32 devices in a mesh: shots: 2 (over y), depth: 4 (over x, core), strip: 4 (over z).
Axes of the slice: x: 2, y: 2, z: 4, core: 2. Of those that a mesh axis runs over, the one named last changes fastest.
Arguments:
- surface: float32 [2, 8, 32, 2048], P(None, 'shots', 'strip'), parts along dimension 1, may hold values from -6 to 6
- omegas: float32 [4], replicated, may hold values from 1 to 3
- region_speed: float32 [8], replicated, may hold values from 1 to 2
- fd_coeff: float32 [8], replicated, may hold values from 0.02 to 0.08
- region_index: int32 [12, 32, 2048], P('depth', 'strip'), may hold values from 0 to 7
- ref_region: int32 [12], P('depth'), may hold values from 0 to 7
Outputs:
- image: float32 [12, 32, 4096], P('depth', 'strip', 'shots'), parts along dimension 2
The draws below stay inside these ranges and needn't reach their ends.
There are 2 independent parts, one for each index of `shots`. The reference program is written for one: setup_inputs(seed, part) draws one part's arguments, and reference() takes and returns one part's arrays. A program takes and returns all parts, laid end to end along the dimension named above; an argument that names none is the same for every part. Nothing has to cross between parts.
All inputs are finite; a program needn't handle non-finite values.
Results may differ from the reference program's by a relative error of at most 0.00015.
Values sent between devices are 32-bit elements; how exact they have to be, the bound alone decides.
No kernel may reach another device: no remote copies, remote signals or barrier semaphores. Data moves between devices by JAX's collectives and lax.ppermute only.
A program may use at most 64 MiB of HBM per device.

```python
import math
import jax
import jax.numpy as jnp
from jax import lax

NX = 2048
FREQ = 4
REGIONS = 8
NY = 32
DEPTHS = 12


def set_ends(values, rng, smallest, high):
    place = [jax.random.randint(jax.random.fold_in(rng, axis), (), 0, length) for axis, length in enumerate(values.shape)]
    longest = values.shape.index(max(values.shape))
    beside = place[:longest] + [(place[longest] + 1) % values.shape[longest]] + place[longest + 1:]
    return values.at[tuple(place)].set(smallest).at[tuple(beside)].set(high)


def block_levels(stream_key, dims, pieces, smallest, top_value):
    def one(dim, shards_of):
        steps = jax.random.uniform(jax.random.fold_in(jax.random.fold_in(stream_key, 6), dim), (shards_of,), jnp.float32, smallest / len(pieces), top_value / len(pieces))
        return jnp.repeat(jnp.exp(steps), dims[dim] // shards_of).reshape((-1,) + (1,) * (len(dims) - dim - 1))

    loudness = one(*pieces[0])
    for cut in pieces[1:]:
        loudness = loudness * one(*cut)
    return loudness


def centred(rng, dims, width, bound, split=(), kind=jnp.bfloat16):
    drawn = width * jax.random.normal(rng, dims, jnp.float32)
    if split:
        drawn = drawn * block_levels(rng, dims, split, -0.22, 0.18)
    return jnp.clip(drawn, -bound, bound).astype(kind)


def setup_inputs(seed: int = 0, part: int = 0) -> dict:
    arg_keys = jax.random.split(jax.random.key(seed), 7)
    own_keys = jax.random.split(jax.random.fold_in(arg_keys[6], part), 7)
    return {
        "surface": centred(own_keys[0], (2, FREQ, NY, NX), 1.0, 6.0, ((2, 4),), jnp.float32),
        "omegas": jnp.clip(jnp.exp(jax.random.uniform(arg_keys[1], (FREQ,), jnp.float32, math.log(1.0), math.log(3.0))), 1.0, 3.0),
        "region_speed": jnp.clip(jax.random.uniform(arg_keys[2], (REGIONS,), jnp.float32, 1.0, 2.0), 1.0, 2.0),
        "fd_coeff": jnp.clip(jnp.exp(jax.random.uniform(arg_keys[3], (REGIONS,), jnp.float32, math.log(0.02), math.log(0.08))), 0.02, 0.08),
        "region_index": set_ends(jax.random.randint(arg_keys[4], (DEPTHS, NY, NX), 0, REGIONS), jax.random.fold_in(arg_keys[4], 1), 0, REGIONS - 1).astype(jnp.int32),
        "ref_region": set_ends(jax.random.randint(arg_keys[5], (DEPTHS,), 0, REGIONS), jax.random.fold_in(arg_keys[5], 1), 0, REGIONS - 1).astype(jnp.int32),
    }


DAMPING = 0.05

def wave_numbers():
    counter = jnp.arange(NX)
    signed = jnp.where(counter >= NX // 2, counter - NX, counter)
    return signed.astype(jnp.float32) * (2.0 * math.pi / NX)

def laplace_rows(values):
    padded = jnp.pad(values, ((1, 1), (0, 0)))
    return padded[:-2] + padded[2:] + jnp.roll(values, 1, 1) + jnp.roll(values, -1, 1) - 4.0 * values

def advance(real_part, imag_part, omega_now, slow_cells, coef_cells, ref_slow, kx_line):
    wave_ref = omega_now * ref_slow
    excess = wave_ref * wave_ref - kx_line * kx_line
    decay_line = jnp.exp(-jnp.sqrt(jnp.maximum(-excess, 0.0)))
    vertical = jnp.sqrt(jnp.maximum(excess, 0.0))
    spectrum = jnp.fft.fft(lax.complex(real_part, imag_part), axis=-1)
    spectrum = spectrum * lax.complex(decay_line * jnp.cos(vertical), decay_line * jnp.sin(vertical))
    shifted = jnp.fft.ifft(spectrum, axis=-1)
    shift_re = jnp.real(shifted)
    shift_im = jnp.imag(shifted)
    phase_cell = omega_now * (slow_cells - ref_slow)
    cosine = jnp.cos(phase_cell)
    sine_part = jnp.sin(phase_cell)
    turned_re = shift_re * cosine - shift_im * sine_part
    turned_im = shift_re * sine_part + shift_im * cosine
    lap_re = laplace_rows(turned_re)
    lap_im = laplace_rows(turned_im)
    stencil_gain = coef_cells / omega_now
    new_re = turned_re + (lap_re * DAMPING - lap_im * stencil_gain)
    new_im = turned_im + (lap_re * stencil_gain + lap_im * DAMPING)
    return (new_re, new_im)

def reference(surface, omegas, region_speed, fd_coeff, region_index, ref_region):
    inv_speed = 1.0 / region_speed
    slowness = inv_speed[region_index]
    coefficient = fd_coeff[region_index]
    ref_slowness = inv_speed[ref_region]
    kx_line = wave_numbers()
    layers = [jnp.zeros((NY, NX), jnp.float32) for depth_no in range(DEPTHS)]
    for freq_no in range(FREQ):
        omega_now = omegas[freq_no]
        real_part = surface[0, freq_no]
        imag_part = surface[1, freq_no]
        for depth_no in range(DEPTHS):
            real_part, imag_part = advance(real_part, imag_part, omega_now, slowness[depth_no], coefficient[depth_no], ref_slowness[depth_no], kx_line)
            layers[depth_no] = layers[depth_no] + real_part
    return jnp.stack(layers)
```

```python
import math

import ml_dtypes
import numpy as np
import jax
import jax.numpy as jnp
from jax import lax
from jax.experimental import pallas as pl
from jax.experimental.pallas import tpu as pltpu
from jax.sharding import PartitionSpec as P

DAMPING = 0.05
PRECISE = lax.Precision.HIGHEST


def padded_2(cells, sides, width):
    for axis, dim in sides:
        count = lax.axis_size(axis)
        ends = count - 1
        head = lax.slice_in_dim(cells, 0, width, axis=dim)
        tail = lax.slice_in_dim(cells, cells.shape[dim] - width, cells.shape[dim], axis=dim)
        cells = jnp.concatenate(
            [
                lax.ppermute(tail, axis, [(i, (i + 1) % count) for i in range(ends)]),
                cells,
                lax.ppermute(head, axis, [((i + 1) % count, i) for i in range(ends)]),
            ],
            axis=dim,
        )
    return cells


def from_behind(value, axis, steps):
    count = lax.axis_size(axis)
    first, last = (max(0, -steps), min(count, count - steps))
    return lax.ppermute(value, axis, [(source, source + steps) for source in range(first, last)])


def complex_scale(values, cosine, sine_part):
    return jnp.stack(
        [values[0] * cosine - values[1] * sine_part, values[0] * sine_part + values[1] * cosine]
    )


def angle_pair(numerator, period):
    angle_grid = numerator.astype(jnp.float32) * (2.0 * math.pi / period)
    return (jnp.cos(angle_grid), jnp.sin(angle_grid))


def block_matrix(cosine, sine_part, forward):
    sign_flip = 1.0 if forward else -1.0
    return jnp.stack(
        [jnp.stack([cosine, -sign_flip * sine_part]), jnp.stack([sign_flip * sine_part, cosine])]
    )


def build_tables(line_len):
    block_len = 128
    outer_len = line_len // block_len
    inner_idx = jnp.arange(block_len)
    outer_idx = jnp.arange(outer_len)
    cos_large, sin_large = angle_pair(
        inner_idx[:, None] * inner_idx[None, :] % block_len, block_len
    )
    cos_small, sin_small = angle_pair(
        outer_idx[:, None] * outer_idx[None, :] % outer_len, outer_len
    )
    cos_twist, sin_twist = angle_pair(outer_idx[:, None] * inner_idx[None, :], line_len)
    wave_index = outer_idx[:, None] + outer_len * inner_idx[None, :]
    signed = jnp.where(wave_index >= line_len // 2, wave_index - line_len, wave_index)
    kx_grid = signed.astype(jnp.float32) * (2.0 * math.pi / line_len)
    small_fwd = block_matrix(cos_small, sin_small, True)
    small_inv = block_matrix(cos_small, sin_small, False)
    large_fwd = block_matrix(cos_large, sin_large, True)
    large_inv = block_matrix(cos_large, sin_large, False)
    return (small_fwd, small_inv, large_fwd, large_inv, cos_twist, sin_twist, kx_grid)


def forward_line(wavefield, tables):
    small_fwd, small_inv, large_fwd, large_inv, cos_twist, sin_twist, kx_grid = tables
    row_count = wavefield.shape[1]
    pieces = wavefield.reshape(2, row_count, cos_twist.shape[0], cos_twist.shape[1])
    mixed_part = jnp.einsum("zrab,zwca->wrcb", pieces, small_fwd, precision=PRECISE)
    mixed_part = complex_scale(mixed_part, cos_twist, -sin_twist)
    return jnp.einsum("zrcb,zwbd->wrcd", mixed_part, large_fwd, precision=PRECISE)


def inverse_line(spectrum, tables):
    small_fwd, small_inv, large_fwd, large_inv, cos_twist, sin_twist, kx_grid = tables
    row_count = spectrum.shape[1]
    line_len = cos_twist.shape[0] * cos_twist.shape[1]
    mixed_part = jnp.einsum("zrcd,zwdb->wrcb", spectrum, large_inv, precision=PRECISE)
    mixed_part = complex_scale(mixed_part, cos_twist, sin_twist)
    pieces = jnp.einsum("zrcb,zwca->wrab", mixed_part, small_inv, precision=PRECISE)
    return pieces.reshape(2, row_count, line_len) * (1.0 / line_len)


def lookup(regions, entries):
    picked = jnp.zeros(regions.shape, jnp.float32)
    for region_no in range(entries.shape[0]):
        picked = picked + jnp.where(regions == region_no, entries[region_no], 0.0)
    return picked


def depth_step(wavefield, omega_now, slow_cells, coef_cells, ref_slow, tables, pad_rows):
    kx_grid = tables[6]
    wave_ref = omega_now * ref_slow
    excess = wave_ref * wave_ref - kx_grid * kx_grid
    decay_line = jnp.exp(-jnp.sqrt(jnp.maximum(-excess, 0.0)))
    vertical = jnp.sqrt(jnp.maximum(excess, 0.0))
    spectrum = complex_scale(
        forward_line(wavefield, tables),
        decay_line * jnp.cos(vertical),
        decay_line * jnp.sin(vertical),
    )
    wavefield = inverse_line(spectrum, tables)
    phase_cell = omega_now * (slow_cells - ref_slow)
    wavefield = complex_scale(wavefield, jnp.cos(phase_cell), jnp.sin(phase_cell))
    padded = pad_rows(wavefield)
    laplace = (
        padded[:, :-2]
        + padded[:, 2:]
        + jnp.roll(wavefield, 1, 2)
        + jnp.roll(wavefield, -1, 2)
        - 4.0 * wavefield
    )
    return wavefield + complex_scale(laplace, DAMPING, coef_cells / omega_now)


def march(wavefield, omega_now, slow_block, coef_block, ref_block, tables, pad_rows):
    traces = []
    for step_no in range(slow_block.shape[0]):
        wavefield = depth_step(
            wavefield,
            omega_now,
            slow_block[step_no],
            coef_block[step_no],
            ref_block[step_no],
            tables,
            pad_rows,
        )
        traces.append(wavefield[0])
    return (wavefield, jnp.stack(traces))


def shards_general(surface, omegas, region_speed, fd_coeff, region_index, ref_region):
    line_len = surface.shape[3]
    rows_here = surface.shape[2]
    freq_count = surface.shape[1]
    step_count = region_index.shape[0]
    tables = build_tables(line_len)
    inv_speed = 1.0 / region_speed
    segment_no = lax.axis_index("depth")
    segment_count = lax.axis_size("depth")

    def pad_near(values):
        return padded_2(values, (("strip", 1),), 1)

    slow_cells = lookup(region_index, inv_speed)
    coef_cells = lookup(region_index, fd_coeff)
    ref_cells = lookup(ref_region, inv_speed)
    freq_index = jnp.arange(freq_count)
    image_out = jnp.zeros((step_count, rows_here, line_len), jnp.float32)
    arriving = jnp.zeros((2, rows_here, line_len), jnp.float32)
    tick_count = freq_count + segment_count - 1
    for tick_no in range(tick_count):
        batch_no = tick_no - segment_no
        is_live = (batch_no >= 0) & (batch_no < freq_count)
        clipped = jnp.clip(batch_no, 0, freq_count - 1)
        picked = lax.dynamic_index_in_dim(surface, clipped, 1, keepdims=False)
        entering = jnp.where(segment_no == 0, picked, arriving)
        omega_now = jnp.sum(jnp.where(freq_index == clipped, omegas, 0.0))
        leaving, traces = march(
            entering, omega_now, slow_cells, coef_cells, ref_cells, tables, pad_near
        )
        image_out = image_out + jnp.where(is_live, traces, 0.0)
        if tick_no + 1 < tick_count:
            arriving = from_behind(leaving, "depth", 1)
    return image_out


LANE = 128
FFT_BLOCKS = 16
ROW_CHUNK = 8


def fft4(x0, x1, x2, x3, sign):
    s0 = (x0[0] + x2[0], x0[1] + x2[1])
    d0 = (x0[0] - x2[0], x0[1] - x2[1])
    s1 = (x1[0] + x3[0], x1[1] + x3[1])
    d1 = (x1[0] - x3[0], x1[1] - x3[1])
    if sign < 0:
        wd = (d1[1], -d1[0])
    else:
        wd = (-d1[1], d1[0])
    return (
        (s0[0] + s1[0], s0[1] + s1[1]),
        (d0[0] + wd[0], d0[1] + wd[1]),
        (s0[0] - s1[0], s0[1] - s1[1]),
        (d0[0] - wd[0], d0[1] - wd[1]),
    )


def turn_const(value, power, sign):
    if power == 4:
        return (-value[1], value[0]) if sign > 0 else (value[1], -value[0])
    angle = sign * 2.0 * math.pi * power / 16.0
    cr, ci = (math.cos(angle), math.sin(angle))
    return (value[0] * cr - value[1] * ci, value[0] * ci + value[1] * cr)


def fft16(parts, sign):
    mid = [[None] * 4 for _ in range(4)]
    for a0 in range(4):
        ys = fft4(parts[a0], parts[4 + a0], parts[8 + a0], parts[12 + a0], sign)
        for c0 in range(4):
            power = a0 * c0
            mid[a0][c0] = ys[c0] if power == 0 else turn_const(ys[c0], power, sign)
    out = [None] * 16
    for c0 in range(4):
        zs = fft4(mid[0][c0], mid[1][c0], mid[2][c0], mid[3][c0], sign)
        for c1 in range(4):
            out[c0 + 4 * c1] = zs[c1]
    return out


def pick(regions, values):
    level = list(values)
    bit = 1
    while len(level) > 1:
        chosen = (regions & bit) != 0
        level = [jnp.where(chosen, level[i + 1], level[i]) for i in range(0, len(level), 2)]
        bit *= 2
    return jnp.broadcast_to(level[0], regions.shape)


def split_dot(values, hi_ref, lo_ref):
    high = values.astype(jnp.bfloat16)
    low = (values - high.astype(jnp.float32)).astype(jnp.bfloat16)
    main = jnp.dot(high, hi_ref[...], preferred_element_type=jnp.float32)
    fix = jnp.dot(high, lo_ref[...], preferred_element_type=jnp.float32) + jnp.dot(
        low, hi_ref[:, :], preferred_element_type=jnp.float32
    )
    return main + fix


def section_kernel(
    tab_ref, w_ref, rid_ref, mult_ref, tw_ref, fhi_ref, flo_ref, ghi_ref, glo_ref,
    wout_ref, img_ref, a_ref, y_ref, v_ref, *, table_len
):
    rows = w_ref.shape[1]
    line_len = w_ref.shape[2]
    steps = rid_ref.shape[0]
    chunks = rows // ROW_CHUNK
    inv_len = 1.0 / line_len
    wout_ref[...] = w_ref[...]

    def blk(a):
        return slice(a * LANE, (a + 1) * LANE)

    def one_step(k, carry):
        base = k * (3 * table_len)
        cos_t = [tab_ref[base + g] for g in range(table_len)]
        sin_t = [tab_ref[base + table_len + g] for g in range(table_len)]
        gain_t = [tab_ref[base + 2 * table_len + g] for g in range(table_len)]

        def forward_chunk(i, c):
            y0 = pl.multiple_of(i * ROW_CHUNK, ROW_CHUNK)
            parts = [
                (wout_ref[0, pl.ds(y0, ROW_CHUNK), blk(a)], wout_ref[1, pl.ds(y0, ROW_CHUNK), blk(a)])
                for a in range(FFT_BLOCKS)
            ]
            spec = fft16(parts, -1)
            for cc in range(FFT_BLOCKS):
                tc = tw_ref[0, cc:cc + 1, :]
                ts = tw_ref[1, cc:cc + 1, :]
                xr, xi = spec[cc]
                a_ref[pl.ds(cc * rows + y0, ROW_CHUNK), 0:LANE] = xr * tc + xi * ts
                a_ref[pl.ds(cc * rows + y0, ROW_CHUNK), LANE:2 * LANE] = xi * tc - xr * ts
            return c

        lax.fori_loop(0, chunks, forward_chunk, 0)
        y_ref[...] = split_dot(a_ref[...], fhi_ref, flo_ref)
        for cc in range(FFT_BLOCKS):
            band = slice(cc * rows, (cc + 1) * rows)
            yr = y_ref[band, 0:LANE]
            yi = y_ref[band, LANE:2 * LANE]
            mr = mult_ref[k, 0, cc:cc + 1, :]
            mi = mult_ref[k, 1, cc:cc + 1, :]
            a_ref[band, 0:LANE] = yr * mr - yi * mi
            a_ref[band, LANE:2 * LANE] = yr * mi + yi * mr
        y_ref[...] = split_dot(a_ref[...], ghi_ref, glo_ref)

        def inverse_chunk(i, c):
            y0 = pl.multiple_of(i * ROW_CHUNK, ROW_CHUNK)
            parts = []
            for cc in range(FFT_BLOCKS):
                zr = y_ref[pl.ds(cc * rows + y0, ROW_CHUNK), 0:LANE]
                zi = y_ref[pl.ds(cc * rows + y0, ROW_CHUNK), LANE:2 * LANE]
                tc = tw_ref[0, cc:cc + 1, :]
                ts = tw_ref[1, cc:cc + 1, :]
                parts.append((zr * tc - zi * ts, zr * ts + zi * tc))
            back = fft16(parts, 1)
            for a in range(FFT_BLOCKS):
                ur = back[a][0] * inv_len
                ui = back[a][1] * inv_len
                regions = rid_ref[k, pl.ds(y0, ROW_CHUNK), blk(a)]
                cs = pick(regions, cos_t)
                sn = pick(regions, sin_t)
                v_ref[0, pl.ds(y0, ROW_CHUNK), blk(a)] = ur * cs - ui * sn
                v_ref[1, pl.ds(y0, ROW_CHUNK), blk(a)] = ur * sn + ui * cs
            return c

        lax.fori_loop(0, chunks, inverse_chunk, 0)
        row_id = lax.broadcasted_iota(jnp.int32, (rows, LANE), 0)
        lane_id = lax.broadcasted_iota(jnp.int32, (rows, LANE), 1)
        for a in range(FFT_BLOCKS):
            prev_b = blk((a - 1) % FFT_BLOCKS)
            next_b = blk((a + 1) % FFT_BLOCKS)
            lap = []
            here = []
            for part in range(2):
                v = v_ref[part, :, blk(a)]
                vp = v_ref[part, :, prev_b]
                vn = v_ref[part, :, next_b]
                above = jnp.where(row_id == 0, 0.0, pltpu.roll(v, 1, 0))
                below = jnp.where(row_id == rows - 1, 0.0, pltpu.roll(v, rows - 1, 0))
                left = jnp.where(lane_id == 0, pltpu.roll(vp, 1, 1), pltpu.roll(v, 1, 1))
                right = jnp.where(
                    lane_id == LANE - 1, pltpu.roll(vn, LANE - 1, 1), pltpu.roll(v, LANE - 1, 1)
                )
                lap.append(above + below + left + right - 4.0 * v)
                here.append(v)
            gain = pick(rid_ref[k, :, blk(a)], gain_t)
            new_re = here[0] + (lap[0] * DAMPING - lap[1] * gain)
            new_im = here[1] + (lap[0] * gain + lap[1] * DAMPING)
            wout_ref[0, :, blk(a)] = new_re
            wout_ref[1, :, blk(a)] = new_im
            img_ref[k, :, blk(a)] = new_re
        return carry

    lax.fori_loop(0, steps, one_step, 0)


def fast_constants(line_len):
    outer = line_len // LANE
    b = np.arange(LANE)
    ang = 2.0 * np.pi * (np.outer(b, b) % LANE) / LANE
    cos_m, sin_m = (np.cos(ang), np.sin(ang))
    fwd = np.block([[cos_m, -sin_m], [sin_m, cos_m]])
    inv = np.block([[cos_m, sin_m], [-sin_m, cos_m]])

    def halves(m):
        hi = m.astype(ml_dtypes.bfloat16)
        lo = (m - hi.astype(np.float64)).astype(ml_dtypes.bfloat16)
        return (hi, lo)

    c = np.arange(outer)
    tw_ang = 2.0 * np.pi * np.outer(c, b) / line_len
    twiddle = np.stack([np.cos(tw_ang), np.sin(tw_ang)]).astype(np.float32)
    q = c[:, None] + outer * b[None, :]
    signed = np.where(q >= line_len // 2, q - line_len, q).astype(np.float32)
    kx_cd = signed * np.float32(2.0 * math.pi / line_len)
    return (halves(fwd), halves(inv), twiddle, kx_cd.astype(np.float32))


def run_section(wave, regions, table, mult, consts):
    (fhi, flo), (ghi, glo), twiddle, _ = consts
    rows, line_len = wave.shape[1], wave.shape[2]
    steps = regions.shape[0]
    table_len = table.shape[0] // (3 * steps)
    vmem = pl.BlockSpec(memory_space=pltpu.VMEM)
    flops = steps * (2 * 3 * 2 * (FFT_BLOCKS * rows) * 256 * 256 + 400 * rows * line_len)
    return pl.pallas_call(
        lambda *refs: section_kernel(*refs, table_len=table_len),
        out_shape=(
            jax.ShapeDtypeStruct(wave.shape, jnp.float32),
            jax.ShapeDtypeStruct((steps, rows, line_len), jnp.float32),
        ),
        in_specs=[pl.BlockSpec(memory_space=pltpu.SMEM)] + [vmem] * 8,
        out_specs=(vmem, vmem),
        scratch_shapes=[
            pltpu.VMEM((FFT_BLOCKS * rows, 2 * LANE), jnp.float32),
            pltpu.VMEM((FFT_BLOCKS * rows, 2 * LANE), jnp.float32),
            pltpu.VMEM((2, rows, line_len), jnp.float32),
        ],
        cost_estimate=pl.CostEstimate(
            flops=flops, transcendentals=0, bytes_accessed=4 * rows * line_len * 6 * steps
        ),
    )(table, wave, regions, mult, jnp.asarray(twiddle), jnp.asarray(fhi), jnp.asarray(flo),
      jnp.asarray(ghi), jnp.asarray(glo))


def section_tables(omega, region_speed, fd_coeff, ref_region, kx_cd):
    inv_speed = 1.0 / region_speed
    ref_slow = inv_speed[ref_region]
    regions = region_speed.shape[0]
    padded = 1 << max(1, (regions - 1).bit_length())
    extra = padded - regions
    phase = omega * (inv_speed[None, :] - ref_slow[:, None])
    gain = jnp.broadcast_to(fd_coeff / omega, phase.shape)
    parts = [jnp.cos(phase), jnp.sin(phase), gain]
    if extra:
        parts = [jnp.concatenate([p, jnp.repeat(p[:, -1:], extra, axis=1)], axis=1) for p in parts]
    table = jnp.stack(parts, axis=1).reshape(-1)
    wave_ref = omega * ref_slow
    wave_ref = wave_ref[:, None, None]
    excess = wave_ref * wave_ref - kx_cd * kx_cd
    decay_line = jnp.exp(-jnp.sqrt(jnp.maximum(-excess, 0.0)))
    vertical = jnp.sqrt(jnp.maximum(excess, 0.0))
    mult = jnp.stack([decay_line * jnp.cos(vertical), decay_line * jnp.sin(vertical)], axis=1)
    return (table, mult)


def fast_fits(surface, region_index, region_speed):
    freq_count = surface.shape[1]
    rows = surface.shape[2] * lax.axis_size("strip")
    line_len = surface.shape[3]
    return (
        freq_count == lax.axis_size("strip")
        and line_len == FFT_BLOCKS * LANE
        and rows % ROW_CHUNK == 0
        and rows <= 64
        and region_speed.shape[0] <= 16
    )


def shards(surface, omegas, region_speed, fd_coeff, region_index, ref_region):
    if not fast_fits(surface, region_index, region_speed):
        return shards_general(surface, omegas, region_speed, fd_coeff, region_index, ref_region)
    line_len = surface.shape[3]
    segment_no = lax.axis_index("depth")
    segment_count = lax.axis_size("depth")
    strip_no = lax.axis_index("strip")
    consts = fast_constants(line_len)
    regions = lax.all_gather(region_index, "strip", axis=1, tiled=True)
    wave = lax.all_to_all(surface, "strip", 1, 2, tiled=True)[:, 0]
    omega = lax.dynamic_index_in_dim(omegas, strip_no, 0, keepdims=False)
    table, mult = section_tables(omega, region_speed, fd_coeff, ref_region, jnp.asarray(consts[3]))
    image = jnp.zeros(regions.shape, jnp.float32)

    def live(wave, image):
        return run_section(wave, regions, table, mult, consts)

    def idle(wave, image):
        return (wave, image)

    for tick_no in range(segment_count):
        wave, image = lax.cond(segment_no == tick_no, live, idle, wave, image)
        if tick_no + 1 < segment_count:
            wave = from_behind(wave, "depth", 1)
    return lax.psum_scatter(image, "strip", scatter_dimension=1, tiled=True)


def solution(mesh):
    in_specs = (
        P(None, "shots", "strip", None),
        P(),
        P(),
        P(),
        P("depth", "strip", None),
        P("depth"),
    )
    out_specs = P("depth", "strip", "shots")
    return jax.shard_map(shards, mesh=mesh, in_specs=in_specs, out_specs=out_specs, check_vma=False)
```

```python
import math

import ml_dtypes
import numpy as np
import jax
import jax.numpy as jnp
from jax import lax
from jax.experimental import pallas as pl
from jax.experimental.pallas import tpu as pltpu
from jax.sharding import PartitionSpec as P

DAMPING = 0.05
PRECISE = lax.Precision.HIGHEST


def padded_2(cells, sides, width):
    for axis, dim in sides:
        count = lax.axis_size(axis)
        ends = count - 1
        head = lax.slice_in_dim(cells, 0, width, axis=dim)
        tail = lax.slice_in_dim(cells, cells.shape[dim] - width, cells.shape[dim], axis=dim)
        cells = jnp.concatenate(
            [
                lax.ppermute(tail, axis, [(i, (i + 1) % count) for i in range(ends)]),
                cells,
                lax.ppermute(head, axis, [((i + 1) % count, i) for i in range(ends)]),
            ],
            axis=dim,
        )
    return cells


def from_behind(value, axis, steps):
    count = lax.axis_size(axis)
    first, last = (max(0, -steps), min(count, count - steps))
    return lax.ppermute(value, axis, [(source, source + steps) for source in range(first, last)])


def complex_scale(values, cosine, sine_part):
    return jnp.stack(
        [values[0] * cosine - values[1] * sine_part, values[0] * sine_part + values[1] * cosine]
    )


def angle_pair(numerator, period):
    angle_grid = numerator.astype(jnp.float32) * (2.0 * math.pi / period)
    return (jnp.cos(angle_grid), jnp.sin(angle_grid))


def block_matrix(cosine, sine_part, forward):
    sign_flip = 1.0 if forward else -1.0
    return jnp.stack(
        [jnp.stack([cosine, -sign_flip * sine_part]), jnp.stack([sign_flip * sine_part, cosine])]
    )


def build_tables(line_len):
    block_len = 128
    outer_len = line_len // block_len
    inner_idx = jnp.arange(block_len)
    outer_idx = jnp.arange(outer_len)
    cos_large, sin_large = angle_pair(
        inner_idx[:, None] * inner_idx[None, :] % block_len, block_len
    )
    cos_small, sin_small = angle_pair(
        outer_idx[:, None] * outer_idx[None, :] % outer_len, outer_len
    )
    cos_twist, sin_twist = angle_pair(outer_idx[:, None] * inner_idx[None, :], line_len)
    wave_index = outer_idx[:, None] + outer_len * inner_idx[None, :]
    signed = jnp.where(wave_index >= line_len // 2, wave_index - line_len, wave_index)
    kx_grid = signed.astype(jnp.float32) * (2.0 * math.pi / line_len)
    small_fwd = block_matrix(cos_small, sin_small, True)
    small_inv = block_matrix(cos_small, sin_small, False)
    large_fwd = block_matrix(cos_large, sin_large, True)
    large_inv = block_matrix(cos_large, sin_large, False)
    return (small_fwd, small_inv, large_fwd, large_inv, cos_twist, sin_twist, kx_grid)


def forward_line(wavefield, tables):
    small_fwd, small_inv, large_fwd, large_inv, cos_twist, sin_twist, kx_grid = tables
    row_count = wavefield.shape[1]
    pieces = wavefield.reshape(2, row_count, cos_twist.shape[0], cos_twist.shape[1])
    mixed_part = jnp.einsum("zrab,zwca->wrcb", pieces, small_fwd, precision=PRECISE)
    mixed_part = complex_scale(mixed_part, cos_twist, -sin_twist)
    return jnp.einsum("zrcb,zwbd->wrcd", mixed_part, large_fwd, precision=PRECISE)


def inverse_line(spectrum, tables):
    small_fwd, small_inv, large_fwd, large_inv, cos_twist, sin_twist, kx_grid = tables
    row_count = spectrum.shape[1]
    line_len = cos_twist.shape[0] * cos_twist.shape[1]
    mixed_part = jnp.einsum("zrcd,zwdb->wrcb", spectrum, large_inv, precision=PRECISE)
    mixed_part = complex_scale(mixed_part, cos_twist, sin_twist)
    pieces = jnp.einsum("zrcb,zwca->wrab", mixed_part, small_inv, precision=PRECISE)
    return pieces.reshape(2, row_count, line_len) * (1.0 / line_len)


def lookup(regions, entries):
    picked = jnp.zeros(regions.shape, jnp.float32)
    for region_no in range(entries.shape[0]):
        picked = picked + jnp.where(regions == region_no, entries[region_no], 0.0)
    return picked


def depth_step(wavefield, omega_now, slow_cells, coef_cells, ref_slow, tables, pad_rows):
    kx_grid = tables[6]
    wave_ref = omega_now * ref_slow
    excess = wave_ref * wave_ref - kx_grid * kx_grid
    decay_line = jnp.exp(-jnp.sqrt(jnp.maximum(-excess, 0.0)))
    vertical = jnp.sqrt(jnp.maximum(excess, 0.0))
    spectrum = complex_scale(
        forward_line(wavefield, tables),
        decay_line * jnp.cos(vertical),
        decay_line * jnp.sin(vertical),
    )
    wavefield = inverse_line(spectrum, tables)
    phase_cell = omega_now * (slow_cells - ref_slow)
    wavefield = complex_scale(wavefield, jnp.cos(phase_cell), jnp.sin(phase_cell))
    padded = pad_rows(wavefield)
    laplace = (
        padded[:, :-2]
        + padded[:, 2:]
        + jnp.roll(wavefield, 1, 2)
        + jnp.roll(wavefield, -1, 2)
        - 4.0 * wavefield
    )
    return wavefield + complex_scale(laplace, DAMPING, coef_cells / omega_now)


def march(wavefield, omega_now, slow_block, coef_block, ref_block, tables, pad_rows):
    traces = []
    for step_no in range(slow_block.shape[0]):
        wavefield = depth_step(
            wavefield,
            omega_now,
            slow_block[step_no],
            coef_block[step_no],
            ref_block[step_no],
            tables,
            pad_rows,
        )
        traces.append(wavefield[0])
    return (wavefield, jnp.stack(traces))


def shards_general(surface, omegas, region_speed, fd_coeff, region_index, ref_region):
    line_len = surface.shape[3]
    rows_here = surface.shape[2]
    freq_count = surface.shape[1]
    step_count = region_index.shape[0]
    tables = build_tables(line_len)
    inv_speed = 1.0 / region_speed
    segment_no = lax.axis_index("depth")
    segment_count = lax.axis_size("depth")

    def pad_near(values):
        return padded_2(values, (("strip", 1),), 1)

    slow_cells = lookup(region_index, inv_speed)
    coef_cells = lookup(region_index, fd_coeff)
    ref_cells = lookup(ref_region, inv_speed)
    freq_index = jnp.arange(freq_count)
    image_out = jnp.zeros((step_count, rows_here, line_len), jnp.float32)
    arriving = jnp.zeros((2, rows_here, line_len), jnp.float32)
    tick_count = freq_count + segment_count - 1
    for tick_no in range(tick_count):
        batch_no = tick_no - segment_no
        is_live = (batch_no >= 0) & (batch_no < freq_count)
        clipped = jnp.clip(batch_no, 0, freq_count - 1)
        picked = lax.dynamic_index_in_dim(surface, clipped, 1, keepdims=False)
        entering = jnp.where(segment_no == 0, picked, arriving)
        omega_now = jnp.sum(jnp.where(freq_index == clipped, omegas, 0.0))
        leaving, traces = march(
            entering, omega_now, slow_cells, coef_cells, ref_cells, tables, pad_near
        )
        image_out = image_out + jnp.where(is_live, traces, 0.0)
        if tick_no + 1 < tick_count:
            arriving = from_behind(leaving, "depth", 1)
    return image_out


LANE = 128
FFT_BLOCKS = 16
ROW_CHUNK = 8


def fft4(x0, x1, x2, x3, sign):
    s0 = (x0[0] + x2[0], x0[1] + x2[1])
    d0 = (x0[0] - x2[0], x0[1] - x2[1])
    s1 = (x1[0] + x3[0], x1[1] + x3[1])
    d1 = (x1[0] - x3[0], x1[1] - x3[1])
    if sign < 0:
        wd = (d1[1], -d1[0])
    else:
        wd = (-d1[1], d1[0])
    return (
        (s0[0] + s1[0], s0[1] + s1[1]),
        (d0[0] + wd[0], d0[1] + wd[1]),
        (s0[0] - s1[0], s0[1] - s1[1]),
        (d0[0] - wd[0], d0[1] - wd[1]),
    )


def turn_const(value, power, sign):
    if power == 4:
        return (-value[1], value[0]) if sign > 0 else (value[1], -value[0])
    angle = sign * 2.0 * math.pi * power / 16.0
    cr, ci = (math.cos(angle), math.sin(angle))
    return (value[0] * cr - value[1] * ci, value[0] * ci + value[1] * cr)


def fft16(parts, sign):
    mid = [[None] * 4 for _ in range(4)]
    for a0 in range(4):
        ys = fft4(parts[a0], parts[4 + a0], parts[8 + a0], parts[12 + a0], sign)
        for c0 in range(4):
            power = a0 * c0
            mid[a0][c0] = ys[c0] if power == 0 else turn_const(ys[c0], power, sign)
    out = [None] * 16
    for c0 in range(4):
        zs = fft4(mid[0][c0], mid[1][c0], mid[2][c0], mid[3][c0], sign)
        for c1 in range(4):
            out[c0 + 4 * c1] = zs[c1]
    return out


def pick(regions, values):
    level = list(values)
    bit = 1
    while len(level) > 1:
        chosen = (regions & bit) != 0
        level = [jnp.where(chosen, level[i + 1], level[i]) for i in range(0, len(level), 2)]
        bit *= 2
    return jnp.broadcast_to(level[0], regions.shape)


def split_dot(values, hi_ref, lo_ref):
    high = values.astype(jnp.bfloat16)
    low = (values - high.astype(jnp.float32)).astype(jnp.bfloat16)
    main = jnp.dot(high, hi_ref[...], preferred_element_type=jnp.float32)
    fix = jnp.dot(high, lo_ref[...], preferred_element_type=jnp.float32) + jnp.dot(
        low, hi_ref[:, :], preferred_element_type=jnp.float32
    )
    return main + fix


def section_kernel(
    tab_ref, w_ref, rid_ref, mult_ref, tw_ref, fhi_ref, flo_ref, ghi_ref, glo_ref,
    wout_ref, img_ref, a_ref, y_ref, v_ref, *, table_len
):
    rows = w_ref.shape[1]
    line_len = w_ref.shape[2]
    steps = rid_ref.shape[0]
    chunks = rows // ROW_CHUNK
    inv_len = 1.0 / line_len
    wout_ref[...] = w_ref[...]

    def blk(a):
        return slice(a * LANE, (a + 1) * LANE)

    def one_step(k, carry):
        base = k * (3 * table_len)
        cos_t = [tab_ref[base + g] for g in range(table_len)]
        sin_t = [tab_ref[base + table_len + g] for g in range(table_len)]
        gain_t = [tab_ref[base + 2 * table_len + g] for g in range(table_len)]

        def forward_chunk(i, c):
            y0 = pl.multiple_of(i * ROW_CHUNK, ROW_CHUNK)
            parts = [
                (wout_ref[0, pl.ds(y0, ROW_CHUNK), blk(a)], wout_ref[1, pl.ds(y0, ROW_CHUNK), blk(a)])
                for a in range(FFT_BLOCKS)
            ]
            spec = fft16(parts, -1)
            for cc in range(FFT_BLOCKS):
                tc = tw_ref[0, cc:cc + 1, :]
                ts = tw_ref[1, cc:cc + 1, :]
                xr, xi = spec[cc]
                a_ref[pl.ds(cc * rows + y0, ROW_CHUNK), 0:LANE] = xr * tc + xi * ts
                a_ref[pl.ds(cc * rows + y0, ROW_CHUNK), LANE:2 * LANE] = xi * tc - xr * ts
            return c

        lax.fori_loop(0, chunks, forward_chunk, 0)
        y_ref[...] = split_dot(a_ref[...], fhi_ref, flo_ref)
        for cc in range(FFT_BLOCKS):
            band = slice(cc * rows, (cc + 1) * rows)
            yr = y_ref[band, 0:LANE]
            yi = y_ref[band, LANE:2 * LANE]
            mr = mult_ref[k, 0, cc:cc + 1, :]
            mi = mult_ref[k, 1, cc:cc + 1, :]
            a_ref[band, 0:LANE] = yr * mr - yi * mi
            a_ref[band, LANE:2 * LANE] = yr * mi + yi * mr
        y_ref[...] = split_dot(a_ref[...], ghi_ref, glo_ref)

        def inverse_chunk(i, c):
            y0 = pl.multiple_of(i * ROW_CHUNK, ROW_CHUNK)
            parts = []
            for cc in range(FFT_BLOCKS):
                zr = y_ref[pl.ds(cc * rows + y0, ROW_CHUNK), 0:LANE]
                zi = y_ref[pl.ds(cc * rows + y0, ROW_CHUNK), LANE:2 * LANE]
                tc = tw_ref[0, cc:cc + 1, :]
                ts = tw_ref[1, cc:cc + 1, :]
                parts.append((zr * tc - zi * ts, zr * ts + zi * tc))
            back = fft16(parts, 1)
            for a in range(FFT_BLOCKS):
                ur = back[a][0] * inv_len
                ui = back[a][1] * inv_len
                regions = rid_ref[k, pl.ds(y0, ROW_CHUNK), blk(a)]
                cs = pick(regions, cos_t)
                sn = pick(regions, sin_t)
                v_ref[0, pl.ds(y0, ROW_CHUNK), blk(a)] = ur * cs - ui * sn
                v_ref[1, pl.ds(y0, ROW_CHUNK), blk(a)] = ur * sn + ui * cs
            return c

        lax.fori_loop(0, chunks, inverse_chunk, 0)
        row_id = lax.broadcasted_iota(jnp.int32, (rows, LANE), 0)
        lane_id = lax.broadcasted_iota(jnp.int32, (rows, LANE), 1)
        for a in range(FFT_BLOCKS):
            prev_b = blk((a - 1) % FFT_BLOCKS)
            next_b = blk((a + 1) % FFT_BLOCKS)
            lap = []
            here = []
            for part in range(2):
                v = v_ref[part, :, blk(a)]
                vp = v_ref[part, :, prev_b]
                vn = v_ref[part, :, next_b]
                above = jnp.where(row_id == 0, 0.0, pltpu.roll(v, 1, 0))
                below = jnp.where(row_id == rows - 1, 0.0, pltpu.roll(v, rows - 1, 0))
                left = jnp.where(lane_id == 0, pltpu.roll(vp, 1, 1), pltpu.roll(v, 1, 1))
                right = jnp.where(
                    lane_id == LANE - 1, pltpu.roll(vn, LANE - 1, 1), pltpu.roll(v, LANE - 1, 1)
                )
                lap.append(above + below + left + right - 4.0 * v)
                here.append(v)
            gain = pick(rid_ref[k, :, blk(a)], gain_t)
            new_re = here[0] + (lap[0] * DAMPING - lap[1] * gain)
            new_im = here[1] + (lap[0] * gain + lap[1] * DAMPING)
            wout_ref[0, :, blk(a)] = new_re
            wout_ref[1, :, blk(a)] = new_im
            img_ref[k, :, blk(a)] = new_re
        return carry

    lax.fori_loop(0, steps, one_step, 0)


def fast_constants(line_len):
    outer = line_len // LANE
    b = np.arange(LANE)
    ang = 2.0 * np.pi * (np.outer(b, b) % LANE) / LANE
    cos_m, sin_m = (np.cos(ang), np.sin(ang))
    fwd = np.block([[cos_m, -sin_m], [sin_m, cos_m]])
    inv = np.block([[cos_m, sin_m], [-sin_m, cos_m]])

    def halves(m):
        hi = m.astype(ml_dtypes.bfloat16)
        lo = (m - hi.astype(np.float64)).astype(ml_dtypes.bfloat16)
        return (hi, lo)

    c = np.arange(outer)
    tw_ang = 2.0 * np.pi * np.outer(c, b) / line_len
    twiddle = np.stack([np.cos(tw_ang), np.sin(tw_ang)]).astype(np.float32)
    q = c[:, None] + outer * b[None, :]
    signed = np.where(q >= line_len // 2, q - line_len, q).astype(np.float32)
    kx_cd = signed * np.float32(2.0 * math.pi / line_len)
    return (halves(fwd), halves(inv), twiddle, kx_cd.astype(np.float32))


def run_section(wave, regions, table, mult, consts):
    (fhi, flo), (ghi, glo), twiddle, _ = consts
    rows, line_len = wave.shape[1], wave.shape[2]
    steps = regions.shape[0]
    table_len = table.shape[0] // (3 * steps)
    vmem = pl.BlockSpec(memory_space=pltpu.VMEM)
    flops = steps * (2 * 3 * 2 * (FFT_BLOCKS * rows) * 256 * 256 + 400 * rows * line_len)
    return pl.pallas_call(
        lambda *refs: section_kernel(*refs, table_len=table_len),
        out_shape=(
            jax.ShapeDtypeStruct(wave.shape, jnp.float32),
            jax.ShapeDtypeStruct((steps, rows, line_len), jnp.float32),
        ),
        in_specs=[pl.BlockSpec(memory_space=pltpu.SMEM)] + [vmem] * 8,
        out_specs=(vmem, vmem),
        scratch_shapes=[
            pltpu.VMEM((FFT_BLOCKS * rows, 2 * LANE), jnp.float32),
            pltpu.VMEM((FFT_BLOCKS * rows, 2 * LANE), jnp.float32),
            pltpu.VMEM((2, rows, line_len), jnp.float32),
        ],
        cost_estimate=pl.CostEstimate(
            flops=flops, transcendentals=0, bytes_accessed=4 * rows * line_len * 6 * steps
        ),
    )(table, wave, regions, mult, jnp.asarray(twiddle), jnp.asarray(fhi), jnp.asarray(flo),
      jnp.asarray(ghi), jnp.asarray(glo))


def section_tables(omega, region_speed, fd_coeff, ref_region, kx_cd):
    inv_speed = 1.0 / region_speed
    ref_slow = inv_speed[ref_region]
    regions = region_speed.shape[0]
    padded = 1 << max(1, (regions - 1).bit_length())
    extra = padded - regions
    phase = omega * (inv_speed[None, :] - ref_slow[:, None])
    gain = jnp.broadcast_to(fd_coeff / omega, phase.shape)
    parts = [jnp.cos(phase), jnp.sin(phase), gain]
    if extra:
        parts = [jnp.concatenate([p, jnp.repeat(p[:, -1:], extra, axis=1)], axis=1) for p in parts]
    table = jnp.stack(parts, axis=1).reshape(-1)
    wave_ref = omega * ref_slow
    wave_ref = wave_ref[:, None, None]
    excess = wave_ref * wave_ref - kx_cd * kx_cd
    decay_line = jnp.exp(-jnp.sqrt(jnp.maximum(-excess, 0.0)))
    vertical = jnp.sqrt(jnp.maximum(excess, 0.0))
    mult = jnp.stack([decay_line * jnp.cos(vertical), decay_line * jnp.sin(vertical)], axis=1)
    return (table, mult)


def fast_fits(surface, region_index, region_speed):
    freq_count = surface.shape[1]
    rows = surface.shape[2] * lax.axis_size("strip")
    line_len = surface.shape[3]
    return (
        freq_count == lax.axis_size("strip")
        and line_len == FFT_BLOCKS * LANE
        and rows % ROW_CHUNK == 0
        and rows <= 64
        and region_speed.shape[0] <= 16
    )


def strip_pairs(depths, strip_count, shift):
    return [
        (d * strip_count + r, d * strip_count + (r + shift) % strip_count)
        for d in depths
        for r in range(strip_count)
    ]


def gather_rows(local, depths, strip_no, strip_count, row_axis):
    rows = local.shape[row_axis]
    shape = list(local.shape)
    shape[row_axis] = rows * strip_count
    full = jnp.zeros(shape, local.dtype)
    start = [0] * len(shape)
    start[row_axis] = strip_no * rows
    full = lax.dynamic_update_slice(full, local, start)
    for shift in range(1, strip_count):
        got = lax.ppermute(local, ("depth", "strip"), strip_pairs(depths, strip_count, shift))
        start = [0] * len(shape)
        start[row_axis] = ((strip_no - shift) % strip_count) * rows
        full = lax.dynamic_update_slice(full, got, start)
    return full


def shards(surface, omegas, region_speed, fd_coeff, region_index, ref_region):
    if not fast_fits(surface, region_index, region_speed):
        return shards_general(surface, omegas, region_speed, fd_coeff, region_index, ref_region)
    line_len = surface.shape[3]
    rows_here = surface.shape[2]
    segment_no = lax.axis_index("depth")
    segment_count = lax.axis_size("depth")
    strip_no = lax.axis_index("strip")
    strip_count = lax.axis_size("strip")
    consts = fast_constants(line_len)
    mine = lax.dynamic_index_in_dim(surface, strip_no, 1, keepdims=False)
    wave = jnp.zeros((2, rows_here * strip_count, line_len), jnp.float32)
    wave = lax.dynamic_update_slice(wave, mine, (0, strip_no * rows_here, 0))
    for shift in range(1, strip_count):
        target = (strip_no + shift) % strip_count
        piece = lax.dynamic_index_in_dim(surface, target, 1, keepdims=False)
        got = lax.ppermute(piece, ("depth", "strip"), strip_pairs([0], strip_count, shift))
        source = (strip_no - shift) % strip_count
        wave = lax.dynamic_update_slice(wave, got, (0, source * rows_here, 0))
    regions = gather_rows(region_index, range(segment_count), strip_no, strip_count, 1)
    omega = lax.dynamic_index_in_dim(omegas, strip_no, 0, keepdims=False)
    table, mult = section_tables(omega, region_speed, fd_coeff, ref_region, jnp.asarray(consts[3]))
    image = jnp.zeros(regions.shape, jnp.float32)

    def live(wave, image):
        return run_section(wave, regions, table, mult, consts)

    def idle(wave, image):
        return (wave, image)

    arrived = []
    for tick_no in range(segment_count):
        wave, image = lax.cond(segment_no == tick_no, live, idle, wave, image)
        if tick_no + 1 < segment_count:
            wave = from_behind(wave, "depth", 1)
        for shift in range(1, strip_count):
            target = (strip_no + shift) % strip_count
            piece = lax.dynamic_slice_in_dim(image, target * rows_here, rows_here, axis=1)
            arrived.append(
                lax.ppermute(piece, ("depth", "strip"), strip_pairs([tick_no], strip_count, shift))
            )
    total = lax.dynamic_slice_in_dim(image, strip_no * rows_here, rows_here, axis=1)
    for piece in arrived:
        total = total + piece
    return total


def solution(mesh):
    in_specs = (
        P(None, "shots", "strip", None),
        P(),
        P(),
        P(),
        P("depth", "strip", None),
        P("depth"),
    )
    out_specs = P("depth", "strip", "shots")
    return jax.shard_map(shards, mesh=mesh, in_specs=in_specs, out_specs=out_specs, check_vma=False)
```

```python
import math

import ml_dtypes
import numpy as np
import jax
import jax.numpy as jnp
from jax import lax
from jax.experimental import pallas as pl
from jax.experimental.pallas import tpu as pltpu
from jax.sharding import PartitionSpec as P

DAMPING = 0.05
PRECISE = lax.Precision.HIGHEST


def padded_2(cells, sides, width):
    for axis, dim in sides:
        count = lax.axis_size(axis)
        ends = count - 1
        head = lax.slice_in_dim(cells, 0, width, axis=dim)
        tail = lax.slice_in_dim(cells, cells.shape[dim] - width, cells.shape[dim], axis=dim)
        cells = jnp.concatenate(
            [
                lax.ppermute(tail, axis, [(i, (i + 1) % count) for i in range(ends)]),
                cells,
                lax.ppermute(head, axis, [((i + 1) % count, i) for i in range(ends)]),
            ],
            axis=dim,
        )
    return cells


def from_behind(value, axis, steps):
    count = lax.axis_size(axis)
    first, last = (max(0, -steps), min(count, count - steps))
    return lax.ppermute(value, axis, [(source, source + steps) for source in range(first, last)])


def complex_scale(values, cosine, sine_part):
    return jnp.stack(
        [values[0] * cosine - values[1] * sine_part, values[0] * sine_part + values[1] * cosine]
    )


def angle_pair(numerator, period):
    angle_grid = numerator.astype(jnp.float32) * (2.0 * math.pi / period)
    return (jnp.cos(angle_grid), jnp.sin(angle_grid))


def block_matrix(cosine, sine_part, forward):
    sign_flip = 1.0 if forward else -1.0
    return jnp.stack(
        [jnp.stack([cosine, -sign_flip * sine_part]), jnp.stack([sign_flip * sine_part, cosine])]
    )


def build_tables(line_len):
    block_len = 128
    outer_len = line_len // block_len
    inner_idx = jnp.arange(block_len)
    outer_idx = jnp.arange(outer_len)
    cos_large, sin_large = angle_pair(
        inner_idx[:, None] * inner_idx[None, :] % block_len, block_len
    )
    cos_small, sin_small = angle_pair(
        outer_idx[:, None] * outer_idx[None, :] % outer_len, outer_len
    )
    cos_twist, sin_twist = angle_pair(outer_idx[:, None] * inner_idx[None, :], line_len)
    wave_index = outer_idx[:, None] + outer_len * inner_idx[None, :]
    signed = jnp.where(wave_index >= line_len // 2, wave_index - line_len, wave_index)
    kx_grid = signed.astype(jnp.float32) * (2.0 * math.pi / line_len)
    small_fwd = block_matrix(cos_small, sin_small, True)
    small_inv = block_matrix(cos_small, sin_small, False)
    large_fwd = block_matrix(cos_large, sin_large, True)
    large_inv = block_matrix(cos_large, sin_large, False)
    return (small_fwd, small_inv, large_fwd, large_inv, cos_twist, sin_twist, kx_grid)


def forward_line(wavefield, tables):
    small_fwd, small_inv, large_fwd, large_inv, cos_twist, sin_twist, kx_grid = tables
    row_count = wavefield.shape[1]
    pieces = wavefield.reshape(2, row_count, cos_twist.shape[0], cos_twist.shape[1])
    mixed_part = jnp.einsum("zrab,zwca->wrcb", pieces, small_fwd, precision=PRECISE)
    mixed_part = complex_scale(mixed_part, cos_twist, -sin_twist)
    return jnp.einsum("zrcb,zwbd->wrcd", mixed_part, large_fwd, precision=PRECISE)


def inverse_line(spectrum, tables):
    small_fwd, small_inv, large_fwd, large_inv, cos_twist, sin_twist, kx_grid = tables
    row_count = spectrum.shape[1]
    line_len = cos_twist.shape[0] * cos_twist.shape[1]
    mixed_part = jnp.einsum("zrcd,zwdb->wrcb", spectrum, large_inv, precision=PRECISE)
    mixed_part = complex_scale(mixed_part, cos_twist, sin_twist)
    pieces = jnp.einsum("zrcb,zwca->wrab", mixed_part, small_inv, precision=PRECISE)
    return pieces.reshape(2, row_count, line_len) * (1.0 / line_len)


def lookup(regions, entries):
    picked = jnp.zeros(regions.shape, jnp.float32)
    for region_no in range(entries.shape[0]):
        picked = picked + jnp.where(regions == region_no, entries[region_no], 0.0)
    return picked


def depth_step(wavefield, omega_now, slow_cells, coef_cells, ref_slow, tables, pad_rows):
    kx_grid = tables[6]
    wave_ref = omega_now * ref_slow
    excess = wave_ref * wave_ref - kx_grid * kx_grid
    decay_line = jnp.exp(-jnp.sqrt(jnp.maximum(-excess, 0.0)))
    vertical = jnp.sqrt(jnp.maximum(excess, 0.0))
    spectrum = complex_scale(
        forward_line(wavefield, tables),
        decay_line * jnp.cos(vertical),
        decay_line * jnp.sin(vertical),
    )
    wavefield = inverse_line(spectrum, tables)
    phase_cell = omega_now * (slow_cells - ref_slow)
    wavefield = complex_scale(wavefield, jnp.cos(phase_cell), jnp.sin(phase_cell))
    padded = pad_rows(wavefield)
    laplace = (
        padded[:, :-2]
        + padded[:, 2:]
        + jnp.roll(wavefield, 1, 2)
        + jnp.roll(wavefield, -1, 2)
        - 4.0 * wavefield
    )
    return wavefield + complex_scale(laplace, DAMPING, coef_cells / omega_now)


def march(wavefield, omega_now, slow_block, coef_block, ref_block, tables, pad_rows):
    traces = []
    for step_no in range(slow_block.shape[0]):
        wavefield = depth_step(
            wavefield,
            omega_now,
            slow_block[step_no],
            coef_block[step_no],
            ref_block[step_no],
            tables,
            pad_rows,
        )
        traces.append(wavefield[0])
    return (wavefield, jnp.stack(traces))


def shards_general(surface, omegas, region_speed, fd_coeff, region_index, ref_region):
    line_len = surface.shape[3]
    rows_here = surface.shape[2]
    freq_count = surface.shape[1]
    step_count = region_index.shape[0]
    tables = build_tables(line_len)
    inv_speed = 1.0 / region_speed
    segment_no = lax.axis_index("depth")
    segment_count = lax.axis_size("depth")

    def pad_near(values):
        return padded_2(values, (("strip", 1),), 1)

    slow_cells = lookup(region_index, inv_speed)
    coef_cells = lookup(region_index, fd_coeff)
    ref_cells = lookup(ref_region, inv_speed)
    freq_index = jnp.arange(freq_count)
    image_out = jnp.zeros((step_count, rows_here, line_len), jnp.float32)
    arriving = jnp.zeros((2, rows_here, line_len), jnp.float32)
    tick_count = freq_count + segment_count - 1
    for tick_no in range(tick_count):
        batch_no = tick_no - segment_no
        is_live = (batch_no >= 0) & (batch_no < freq_count)
        clipped = jnp.clip(batch_no, 0, freq_count - 1)
        picked = lax.dynamic_index_in_dim(surface, clipped, 1, keepdims=False)
        entering = jnp.where(segment_no == 0, picked, arriving)
        omega_now = jnp.sum(jnp.where(freq_index == clipped, omegas, 0.0))
        leaving, traces = march(
            entering, omega_now, slow_cells, coef_cells, ref_cells, tables, pad_near
        )
        image_out = image_out + jnp.where(is_live, traces, 0.0)
        if tick_no + 1 < tick_count:
            arriving = from_behind(leaving, "depth", 1)
    return image_out


LANE = 128
FFT_BLOCKS = 16
ROW_CHUNK = 8


def fft4(x0, x1, x2, x3, sign):
    s0 = (x0[0] + x2[0], x0[1] + x2[1])
    d0 = (x0[0] - x2[0], x0[1] - x2[1])
    s1 = (x1[0] + x3[0], x1[1] + x3[1])
    d1 = (x1[0] - x3[0], x1[1] - x3[1])
    if sign < 0:
        wd = (d1[1], -d1[0])
    else:
        wd = (-d1[1], d1[0])
    return (
        (s0[0] + s1[0], s0[1] + s1[1]),
        (d0[0] + wd[0], d0[1] + wd[1]),
        (s0[0] - s1[0], s0[1] - s1[1]),
        (d0[0] - wd[0], d0[1] - wd[1]),
    )


def turn_const(value, power, sign):
    if power == 4:
        return (-value[1], value[0]) if sign > 0 else (value[1], -value[0])
    angle = sign * 2.0 * math.pi * power / 16.0
    cr, ci = (math.cos(angle), math.sin(angle))
    return (value[0] * cr - value[1] * ci, value[0] * ci + value[1] * cr)


def fft16(parts, sign):
    mid = [[None] * 4 for _ in range(4)]
    for a0 in range(4):
        ys = fft4(parts[a0], parts[4 + a0], parts[8 + a0], parts[12 + a0], sign)
        for c0 in range(4):
            power = a0 * c0
            mid[a0][c0] = ys[c0] if power == 0 else turn_const(ys[c0], power, sign)
    out = [None] * 16
    for c0 in range(4):
        zs = fft4(mid[0][c0], mid[1][c0], mid[2][c0], mid[3][c0], sign)
        for c1 in range(4):
            out[c0 + 4 * c1] = zs[c1]
    return out


def pick(regions, values):
    level = list(values)
    bit = 1
    while len(level) > 1:
        chosen = (regions & bit) != 0
        level = [jnp.where(chosen, level[i + 1], level[i]) for i in range(0, len(level), 2)]
        bit *= 2
    return jnp.broadcast_to(level[0], regions.shape)


def split_dot(values, hi_ref, lo_ref):
    high = values.astype(jnp.bfloat16)
    low = (values - high.astype(jnp.float32)).astype(jnp.bfloat16)
    main = jnp.dot(high, hi_ref[...], preferred_element_type=jnp.float32)
    fix = jnp.dot(high, lo_ref[...], preferred_element_type=jnp.float32) + jnp.dot(
        low, hi_ref[:, :], preferred_element_type=jnp.float32
    )
    return main + fix


def section_kernel(
    tab_ref, w_ref, rid_ref, mult_ref, tw_ref, fhi_ref, flo_ref, ghi_ref, glo_ref,
    wout_ref, img_ref, a_ref, y_ref, v_ref, *, table_len
):
    rows = w_ref.shape[1]
    line_len = w_ref.shape[2]
    steps = rid_ref.shape[0]
    strip_count, rows_here = img_ref.shape[0], img_ref.shape[2]
    chunks = rows // ROW_CHUNK
    inv_len = 1.0 / line_len
    wout_ref[...] = w_ref[...]

    def blk(a):
        return slice(a * LANE, (a + 1) * LANE)

    def one_step(k, carry):
        base = k * (3 * table_len)
        cos_t = [tab_ref[base + g] for g in range(table_len)]
        sin_t = [tab_ref[base + table_len + g] for g in range(table_len)]
        gain_t = [tab_ref[base + 2 * table_len + g] for g in range(table_len)]

        def forward_chunk(i, c):
            y0 = pl.multiple_of(i * ROW_CHUNK, ROW_CHUNK)
            parts = [
                (wout_ref[0, pl.ds(y0, ROW_CHUNK), blk(a)], wout_ref[1, pl.ds(y0, ROW_CHUNK), blk(a)])
                for a in range(FFT_BLOCKS)
            ]
            spec = fft16(parts, -1)
            for cc in range(FFT_BLOCKS):
                tc = tw_ref[0, cc:cc + 1, :]
                ts = tw_ref[1, cc:cc + 1, :]
                xr, xi = spec[cc]
                a_ref[pl.ds(cc * rows + y0, ROW_CHUNK), 0:LANE] = xr * tc + xi * ts
                a_ref[pl.ds(cc * rows + y0, ROW_CHUNK), LANE:2 * LANE] = xi * tc - xr * ts
            return c

        lax.fori_loop(0, chunks, forward_chunk, 0)
        y_ref[...] = split_dot(a_ref[...], fhi_ref, flo_ref)
        for cc in range(FFT_BLOCKS):
            band = slice(cc * rows, (cc + 1) * rows)
            yr = y_ref[band, 0:LANE]
            yi = y_ref[band, LANE:2 * LANE]
            mr = mult_ref[k, 0, cc:cc + 1, :]
            mi = mult_ref[k, 1, cc:cc + 1, :]
            a_ref[band, 0:LANE] = yr * mr - yi * mi
            a_ref[band, LANE:2 * LANE] = yr * mi + yi * mr
        y_ref[...] = split_dot(a_ref[...], ghi_ref, glo_ref)

        def inverse_chunk(i, c):
            y0 = pl.multiple_of(i * ROW_CHUNK, ROW_CHUNK)
            parts = []
            for cc in range(FFT_BLOCKS):
                zr = y_ref[pl.ds(cc * rows + y0, ROW_CHUNK), 0:LANE]
                zi = y_ref[pl.ds(cc * rows + y0, ROW_CHUNK), LANE:2 * LANE]
                tc = tw_ref[0, cc:cc + 1, :]
                ts = tw_ref[1, cc:cc + 1, :]
                parts.append((zr * tc - zi * ts, zr * ts + zi * tc))
            back = fft16(parts, 1)
            for a in range(FFT_BLOCKS):
                ur = back[a][0] * inv_len
                ui = back[a][1] * inv_len
                regions = rid_ref[k, pl.ds(y0, ROW_CHUNK), blk(a)]
                cs = pick(regions, cos_t)
                sn = pick(regions, sin_t)
                v_ref[0, pl.ds(y0, ROW_CHUNK), blk(a)] = ur * cs - ui * sn
                v_ref[1, pl.ds(y0, ROW_CHUNK), blk(a)] = ur * sn + ui * cs
            return c

        lax.fori_loop(0, chunks, inverse_chunk, 0)
        row_id = lax.broadcasted_iota(jnp.int32, (rows, LANE), 0)
        lane_id = lax.broadcasted_iota(jnp.int32, (rows, LANE), 1)
        for a in range(FFT_BLOCKS):
            prev_b = blk((a - 1) % FFT_BLOCKS)
            next_b = blk((a + 1) % FFT_BLOCKS)
            lap = []
            here = []
            for part in range(2):
                v = v_ref[part, :, blk(a)]
                vp = v_ref[part, :, prev_b]
                vn = v_ref[part, :, next_b]
                above = jnp.where(row_id == 0, 0.0, pltpu.roll(v, 1, 0))
                below = jnp.where(row_id == rows - 1, 0.0, pltpu.roll(v, rows - 1, 0))
                left = jnp.where(lane_id == 0, pltpu.roll(vp, 1, 1), pltpu.roll(v, 1, 1))
                right = jnp.where(
                    lane_id == LANE - 1, pltpu.roll(vn, LANE - 1, 1), pltpu.roll(v, LANE - 1, 1)
                )
                lap.append(above + below + left + right - 4.0 * v)
                here.append(v)
            gain = pick(rid_ref[k, :, blk(a)], gain_t)
            new_re = here[0] + (lap[0] * DAMPING - lap[1] * gain)
            new_im = here[1] + (lap[0] * gain + lap[1] * DAMPING)
            wout_ref[0, :, blk(a)] = new_re
            wout_ref[1, :, blk(a)] = new_im
            for j in range(strip_count):
                img_ref[j, k, :, blk(a)] = new_re[j * rows_here:(j + 1) * rows_here]
        return carry

    lax.fori_loop(0, steps, one_step, 0)


def fast_constants(line_len):
    outer = line_len // LANE
    b = np.arange(LANE)
    ang = 2.0 * np.pi * (np.outer(b, b) % LANE) / LANE
    cos_m, sin_m = (np.cos(ang), np.sin(ang))
    fwd = np.block([[cos_m, -sin_m], [sin_m, cos_m]])
    inv = np.block([[cos_m, sin_m], [-sin_m, cos_m]])

    def halves(m):
        hi = m.astype(ml_dtypes.bfloat16)
        lo = (m - hi.astype(np.float64)).astype(ml_dtypes.bfloat16)
        return (hi, lo)

    c = np.arange(outer)
    tw_ang = 2.0 * np.pi * np.outer(c, b) / line_len
    twiddle = np.stack([np.cos(tw_ang), np.sin(tw_ang)]).astype(np.float32)
    q = c[:, None] + outer * b[None, :]
    signed = np.where(q >= line_len // 2, q - line_len, q).astype(np.float32)
    kx_cd = signed * np.float32(2.0 * math.pi / line_len)
    return (halves(fwd), halves(inv), twiddle, kx_cd.astype(np.float32))


def run_section(wave, regions, table, mult, consts, strip_count):
    (fhi, flo), (ghi, glo), twiddle, _ = consts
    rows, line_len = wave.shape[1], wave.shape[2]
    steps = regions.shape[0]
    table_len = table.shape[0] // (3 * steps)
    vmem = pl.BlockSpec(memory_space=pltpu.VMEM)
    flops = steps * (2 * 3 * 2 * (FFT_BLOCKS * rows) * 256 * 256 + 400 * rows * line_len)
    return pl.pallas_call(
        lambda *refs: section_kernel(*refs, table_len=table_len),
        out_shape=(
            jax.ShapeDtypeStruct(wave.shape, jnp.float32),
            jax.ShapeDtypeStruct((strip_count, steps, rows // strip_count, line_len), jnp.float32),
        ),
        in_specs=[pl.BlockSpec(memory_space=pltpu.SMEM)] + [vmem] * 8,
        out_specs=(vmem, vmem),
        scratch_shapes=[
            pltpu.VMEM((FFT_BLOCKS * rows, 2 * LANE), jnp.float32),
            pltpu.VMEM((FFT_BLOCKS * rows, 2 * LANE), jnp.float32),
            pltpu.VMEM((2, rows, line_len), jnp.float32),
        ],
        cost_estimate=pl.CostEstimate(
            flops=flops, transcendentals=0, bytes_accessed=4 * rows * line_len * 6 * steps
        ),
    )(table, wave, regions, mult, jnp.asarray(twiddle), jnp.asarray(fhi), jnp.asarray(flo),
      jnp.asarray(ghi), jnp.asarray(glo))


def section_tables(omega, region_speed, fd_coeff, ref_region, kx_cd):
    inv_speed = 1.0 / region_speed
    ref_slow = inv_speed[ref_region]
    regions = region_speed.shape[0]
    padded = 1 << max(1, (regions - 1).bit_length())
    extra = padded - regions
    phase = omega * (inv_speed[None, :] - ref_slow[:, None])
    gain = jnp.broadcast_to(fd_coeff / omega, phase.shape)
    parts = [jnp.cos(phase), jnp.sin(phase), gain]
    if extra:
        parts = [jnp.concatenate([p, jnp.repeat(p[:, -1:], extra, axis=1)], axis=1) for p in parts]
    table = jnp.stack(parts, axis=1).reshape(-1)
    wave_ref = omega * ref_slow
    wave_ref = wave_ref[:, None, None]
    excess = wave_ref * wave_ref - kx_cd * kx_cd
    decay_line = jnp.exp(-jnp.sqrt(jnp.maximum(-excess, 0.0)))
    vertical = jnp.sqrt(jnp.maximum(excess, 0.0))
    mult = jnp.stack([decay_line * jnp.cos(vertical), decay_line * jnp.sin(vertical)], axis=1)
    return (table, mult)


def fast_fits(surface, region_index, region_speed):
    freq_count = surface.shape[1]
    rows = surface.shape[2] * lax.axis_size("strip")
    line_len = surface.shape[3]
    return (
        freq_count == lax.axis_size("strip")
        and line_len == FFT_BLOCKS * LANE
        and rows % ROW_CHUNK == 0
        and surface.shape[2] % ROW_CHUNK == 0
        and rows <= 64
        and region_speed.shape[0] <= 16
    )


def strip_pairs(depths, strip_count, shift):
    return [
        (d * strip_count + r, d * strip_count + (r + shift) % strip_count)
        for d in depths
        for r in range(strip_count)
    ]


def gather_rows(local, depths, strip_no, strip_count, row_axis):
    rows = local.shape[row_axis]
    shape = list(local.shape)
    shape[row_axis] = rows * strip_count
    full = jnp.zeros(shape, local.dtype)
    start = [0] * len(shape)
    start[row_axis] = strip_no * rows
    full = lax.dynamic_update_slice(full, local, start)
    for shift in range(1, strip_count):
        got = lax.ppermute(local, ("depth", "strip"), strip_pairs(depths, strip_count, shift))
        start = [0] * len(shape)
        start[row_axis] = ((strip_no - shift) % strip_count) * rows
        full = lax.dynamic_update_slice(full, got, start)
    return full


def shards(surface, omegas, region_speed, fd_coeff, region_index, ref_region):
    if not fast_fits(surface, region_index, region_speed):
        return shards_general(surface, omegas, region_speed, fd_coeff, region_index, ref_region)
    line_len = surface.shape[3]
    rows_here = surface.shape[2]
    steps = region_index.shape[0]
    segment_no = lax.axis_index("depth")
    segment_count = lax.axis_size("depth")
    strip_no = lax.axis_index("strip")
    strip_count = lax.axis_size("strip")
    rows = rows_here * strip_count
    consts = fast_constants(line_len)
    outgoing = jnp.concatenate(
        [
            jnp.broadcast_to(region_index.astype(jnp.float32)[None], (strip_count,) + region_index.shape),
            jnp.transpose(surface, (1, 0, 2, 3)),
        ],
        axis=1,
    )
    incoming = lax.all_to_all(outgoing, "strip", 0, 0, tiled=True)
    regions = jnp.transpose(incoming[:, :steps], (1, 0, 2, 3)).reshape(steps, rows, line_len)
    regions = regions.astype(jnp.int32)
    wave = jnp.transpose(incoming[:, steps:], (1, 0, 2, 3)).reshape(2, rows, line_len)
    omega = lax.dynamic_index_in_dim(omegas, strip_no, 0, keepdims=False)
    table, mult = section_tables(omega, region_speed, fd_coeff, ref_region, jnp.asarray(consts[3]))
    image = jnp.zeros((strip_count, steps, rows_here, line_len), jnp.float32)

    def live(wave, image):
        return run_section(wave, regions, table, mult, consts, strip_count)

    def idle(wave, image):
        return (wave, image)

    for tick_no in range(segment_count):
        wave, image = lax.cond(segment_no == tick_no, live, idle, wave, image)
        if tick_no + 1 < segment_count:
            wave = from_behind(wave, "depth", 1)
    parts = lax.all_to_all(image, "strip", 0, 0, tiled=True)
    return jnp.sum(parts, axis=0)


def solution(mesh):
    in_specs = (
        P(None, "shots", "strip", None),
        P(),
        P(),
        P(),
        P("depth", "strip", None),
        P("depth"),
    )
    out_specs = P("depth", "strip", "shots")
    return jax.shard_map(shards, mesh=mesh, in_specs=in_specs, out_specs=out_specs, check_vma=False)
```

```python
import math

import ml_dtypes
import numpy as np
import jax
import jax.numpy as jnp
from jax import lax
from jax.experimental import pallas as pl
from jax.experimental.pallas import tpu as pltpu
from jax.sharding import PartitionSpec as P

DAMPING = 0.05
PRECISE = lax.Precision.HIGHEST


def padded_2(cells, sides, width):
    for axis, dim in sides:
        count = lax.axis_size(axis)
        ends = count - 1
        head = lax.slice_in_dim(cells, 0, width, axis=dim)
        tail = lax.slice_in_dim(cells, cells.shape[dim] - width, cells.shape[dim], axis=dim)
        cells = jnp.concatenate(
            [
                lax.ppermute(tail, axis, [(i, (i + 1) % count) for i in range(ends)]),
                cells,
                lax.ppermute(head, axis, [((i + 1) % count, i) for i in range(ends)]),
            ],
            axis=dim,
        )
    return cells


def from_behind(value, axis, steps):
    count = lax.axis_size(axis)
    first, last = (max(0, -steps), min(count, count - steps))
    return lax.ppermute(value, axis, [(source, source + steps) for source in range(first, last)])


def complex_scale(values, cosine, sine_part):
    return jnp.stack(
        [values[0] * cosine - values[1] * sine_part, values[0] * sine_part + values[1] * cosine]
    )


def angle_pair(numerator, period):
    angle_grid = numerator.astype(jnp.float32) * (2.0 * math.pi / period)
    return (jnp.cos(angle_grid), jnp.sin(angle_grid))


def block_matrix(cosine, sine_part, forward):
    sign_flip = 1.0 if forward else -1.0
    return jnp.stack(
        [jnp.stack([cosine, -sign_flip * sine_part]), jnp.stack([sign_flip * sine_part, cosine])]
    )


def build_tables(line_len):
    block_len = 128
    outer_len = line_len // block_len
    inner_idx = jnp.arange(block_len)
    outer_idx = jnp.arange(outer_len)
    cos_large, sin_large = angle_pair(
        inner_idx[:, None] * inner_idx[None, :] % block_len, block_len
    )
    cos_small, sin_small = angle_pair(
        outer_idx[:, None] * outer_idx[None, :] % outer_len, outer_len
    )
    cos_twist, sin_twist = angle_pair(outer_idx[:, None] * inner_idx[None, :], line_len)
    wave_index = outer_idx[:, None] + outer_len * inner_idx[None, :]
    signed = jnp.where(wave_index >= line_len // 2, wave_index - line_len, wave_index)
    kx_grid = signed.astype(jnp.float32) * (2.0 * math.pi / line_len)
    small_fwd = block_matrix(cos_small, sin_small, True)
    small_inv = block_matrix(cos_small, sin_small, False)
    large_fwd = block_matrix(cos_large, sin_large, True)
    large_inv = block_matrix(cos_large, sin_large, False)
    return (small_fwd, small_inv, large_fwd, large_inv, cos_twist, sin_twist, kx_grid)


def forward_line(wavefield, tables):
    small_fwd, small_inv, large_fwd, large_inv, cos_twist, sin_twist, kx_grid = tables
    row_count = wavefield.shape[1]
    pieces = wavefield.reshape(2, row_count, cos_twist.shape[0], cos_twist.shape[1])
    mixed_part = jnp.einsum("zrab,zwca->wrcb", pieces, small_fwd, precision=PRECISE)
    mixed_part = complex_scale(mixed_part, cos_twist, -sin_twist)
    return jnp.einsum("zrcb,zwbd->wrcd", mixed_part, large_fwd, precision=PRECISE)


def inverse_line(spectrum, tables):
    small_fwd, small_inv, large_fwd, large_inv, cos_twist, sin_twist, kx_grid = tables
    row_count = spectrum.shape[1]
    line_len = cos_twist.shape[0] * cos_twist.shape[1]
    mixed_part = jnp.einsum("zrcd,zwdb->wrcb", spectrum, large_inv, precision=PRECISE)
    mixed_part = complex_scale(mixed_part, cos_twist, sin_twist)
    pieces = jnp.einsum("zrcb,zwca->wrab", mixed_part, small_inv, precision=PRECISE)
    return pieces.reshape(2, row_count, line_len) * (1.0 / line_len)


def lookup(regions, entries):
    picked = jnp.zeros(regions.shape, jnp.float32)
    for region_no in range(entries.shape[0]):
        picked = picked + jnp.where(regions == region_no, entries[region_no], 0.0)
    return picked


def depth_step(wavefield, omega_now, slow_cells, coef_cells, ref_slow, tables, pad_rows):
    kx_grid = tables[6]
    wave_ref = omega_now * ref_slow
    excess = wave_ref * wave_ref - kx_grid * kx_grid
    decay_line = jnp.exp(-jnp.sqrt(jnp.maximum(-excess, 0.0)))
    vertical = jnp.sqrt(jnp.maximum(excess, 0.0))
    spectrum = complex_scale(
        forward_line(wavefield, tables),
        decay_line * jnp.cos(vertical),
        decay_line * jnp.sin(vertical),
    )
    wavefield = inverse_line(spectrum, tables)
    phase_cell = omega_now * (slow_cells - ref_slow)
    wavefield = complex_scale(wavefield, jnp.cos(phase_cell), jnp.sin(phase_cell))
    padded = pad_rows(wavefield)
    laplace = (
        padded[:, :-2]
        + padded[:, 2:]
        + jnp.roll(wavefield, 1, 2)
        + jnp.roll(wavefield, -1, 2)
        - 4.0 * wavefield
    )
    return wavefield + complex_scale(laplace, DAMPING, coef_cells / omega_now)


def march(wavefield, omega_now, slow_block, coef_block, ref_block, tables, pad_rows):
    traces = []
    for step_no in range(slow_block.shape[0]):
        wavefield = depth_step(
            wavefield,
            omega_now,
            slow_block[step_no],
            coef_block[step_no],
            ref_block[step_no],
            tables,
            pad_rows,
        )
        traces.append(wavefield[0])
    return (wavefield, jnp.stack(traces))


def shards_general(surface, omegas, region_speed, fd_coeff, region_index, ref_region):
    line_len = surface.shape[3]
    rows_here = surface.shape[2]
    freq_count = surface.shape[1]
    step_count = region_index.shape[0]
    tables = build_tables(line_len)
    inv_speed = 1.0 / region_speed
    segment_no = lax.axis_index("depth")
    segment_count = lax.axis_size("depth")

    def pad_near(values):
        return padded_2(values, (("strip", 1),), 1)

    slow_cells = lookup(region_index, inv_speed)
    coef_cells = lookup(region_index, fd_coeff)
    ref_cells = lookup(ref_region, inv_speed)
    freq_index = jnp.arange(freq_count)
    image_out = jnp.zeros((step_count, rows_here, line_len), jnp.float32)
    arriving = jnp.zeros((2, rows_here, line_len), jnp.float32)
    tick_count = freq_count + segment_count - 1
    for tick_no in range(tick_count):
        batch_no = tick_no - segment_no
        is_live = (batch_no >= 0) & (batch_no < freq_count)
        clipped = jnp.clip(batch_no, 0, freq_count - 1)
        picked = lax.dynamic_index_in_dim(surface, clipped, 1, keepdims=False)
        entering = jnp.where(segment_no == 0, picked, arriving)
        omega_now = jnp.sum(jnp.where(freq_index == clipped, omegas, 0.0))
        leaving, traces = march(
            entering, omega_now, slow_cells, coef_cells, ref_cells, tables, pad_near
        )
        image_out = image_out + jnp.where(is_live, traces, 0.0)
        if tick_no + 1 < tick_count:
            arriving = from_behind(leaving, "depth", 1)
    return image_out


LANE = 128
FFT_BLOCKS = 16
ROW_CHUNK = 8


def fft4(x0, x1, x2, x3, sign):
    s0 = (x0[0] + x2[0], x0[1] + x2[1])
    d0 = (x0[0] - x2[0], x0[1] - x2[1])
    s1 = (x1[0] + x3[0], x1[1] + x3[1])
    d1 = (x1[0] - x3[0], x1[1] - x3[1])
    if sign < 0:
        wd = (d1[1], -d1[0])
    else:
        wd = (-d1[1], d1[0])
    return (
        (s0[0] + s1[0], s0[1] + s1[1]),
        (d0[0] + wd[0], d0[1] + wd[1]),
        (s0[0] - s1[0], s0[1] - s1[1]),
        (d0[0] - wd[0], d0[1] - wd[1]),
    )


def turn_const(value, power, sign):
    if power == 4:
        return (-value[1], value[0]) if sign > 0 else (value[1], -value[0])
    angle = sign * 2.0 * math.pi * power / 16.0
    cr, ci = (math.cos(angle), math.sin(angle))
    return (value[0] * cr - value[1] * ci, value[0] * ci + value[1] * cr)


def fft16(parts, sign):
    mid = [[None] * 4 for _ in range(4)]
    for a0 in range(4):
        ys = fft4(parts[a0], parts[4 + a0], parts[8 + a0], parts[12 + a0], sign)
        for c0 in range(4):
            power = a0 * c0
            mid[a0][c0] = ys[c0] if power == 0 else turn_const(ys[c0], power, sign)
    out = [None] * 16
    for c0 in range(4):
        zs = fft4(mid[0][c0], mid[1][c0], mid[2][c0], mid[3][c0], sign)
        for c1 in range(4):
            out[c0 + 4 * c1] = zs[c1]
    return out


def pick(regions, values):
    level = list(values)
    bit = 1
    while len(level) > 1:
        chosen = (regions & bit) != 0
        level = [jnp.where(chosen, level[i + 1], level[i]) for i in range(0, len(level), 2)]
        bit *= 2
    return jnp.broadcast_to(level[0], regions.shape)


def split_dot(values, hi_ref, lo_ref):
    high = values.astype(jnp.bfloat16)
    low = (values - high.astype(jnp.float32)).astype(jnp.bfloat16)
    main = jnp.dot(high, hi_ref[...], preferred_element_type=jnp.float32)
    fix = jnp.dot(high, lo_ref[...], preferred_element_type=jnp.float32) + jnp.dot(
        low, hi_ref[:, :], preferred_element_type=jnp.float32
    )
    return main + fix


def section_kernel(
    tab_ref, w_ref, rid_ref, mult_ref, tw_ref, fhi_ref, flo_ref, ghi_ref, glo_ref,
    wout_ref, img_ref, a_ref, y_ref, v_ref, *, table_len
):
    rows = w_ref.shape[1]
    line_len = w_ref.shape[2]
    steps = rid_ref.shape[0]
    strip_count, rows_here = img_ref.shape[0], img_ref.shape[2]
    chunks = rows // ROW_CHUNK
    inv_len = 1.0 / line_len
    wout_ref[...] = w_ref[...]

    def blk(a):
        return slice(a * LANE, (a + 1) * LANE)

    def one_step(k, carry):
        base = k * (3 * table_len)
        cos_t = [tab_ref[base + g] for g in range(table_len)]
        sin_t = [tab_ref[base + table_len + g] for g in range(table_len)]
        gain_t = [tab_ref[base + 2 * table_len + g] for g in range(table_len)]

        def forward_chunk(i, c):
            y0 = pl.multiple_of(i * ROW_CHUNK, ROW_CHUNK)
            parts = [
                (wout_ref[0, pl.ds(y0, ROW_CHUNK), blk(a)], wout_ref[1, pl.ds(y0, ROW_CHUNK), blk(a)])
                for a in range(FFT_BLOCKS)
            ]
            spec = fft16(parts, -1)
            for cc in range(FFT_BLOCKS):
                tc = tw_ref[0, cc:cc + 1, :]
                ts = tw_ref[1, cc:cc + 1, :]
                xr, xi = spec[cc]
                a_ref[pl.ds(cc * rows + y0, ROW_CHUNK), 0:LANE] = xr * tc + xi * ts
                a_ref[pl.ds(cc * rows + y0, ROW_CHUNK), LANE:2 * LANE] = xi * tc - xr * ts
            return c

        lax.fori_loop(0, chunks, forward_chunk, 0)
        y_ref[...] = split_dot(a_ref[...], fhi_ref, flo_ref)
        for cc in range(FFT_BLOCKS):
            band = slice(cc * rows, (cc + 1) * rows)
            yr = y_ref[band, 0:LANE]
            yi = y_ref[band, LANE:2 * LANE]
            mr = mult_ref[k, 0, cc:cc + 1, :]
            mi = mult_ref[k, 1, cc:cc + 1, :]
            a_ref[band, 0:LANE] = yr * mr - yi * mi
            a_ref[band, LANE:2 * LANE] = yr * mi + yi * mr
        y_ref[...] = split_dot(a_ref[...], ghi_ref, glo_ref)

        def inverse_chunk(i, c):
            y0 = pl.multiple_of(i * ROW_CHUNK, ROW_CHUNK)
            parts = []
            for cc in range(FFT_BLOCKS):
                zr = y_ref[pl.ds(cc * rows + y0, ROW_CHUNK), 0:LANE]
                zi = y_ref[pl.ds(cc * rows + y0, ROW_CHUNK), LANE:2 * LANE]
                tc = tw_ref[0, cc:cc + 1, :]
                ts = tw_ref[1, cc:cc + 1, :]
                parts.append((zr * tc - zi * ts, zr * ts + zi * tc))
            back = fft16(parts, 1)
            for a in range(FFT_BLOCKS):
                ur = back[a][0] * inv_len
                ui = back[a][1] * inv_len
                regions = rid_ref[k, pl.ds(y0, ROW_CHUNK), blk(a)]
                cs = pick(regions, cos_t)
                sn = pick(regions, sin_t)
                v_ref[0, pl.ds(y0, ROW_CHUNK), blk(a)] = ur * cs - ui * sn
                v_ref[1, pl.ds(y0, ROW_CHUNK), blk(a)] = ur * sn + ui * cs
            return c

        lax.fori_loop(0, chunks, inverse_chunk, 0)
        row_id = lax.broadcasted_iota(jnp.int32, (rows, LANE), 0)
        lane_id = lax.broadcasted_iota(jnp.int32, (rows, LANE), 1)
        for a in range(FFT_BLOCKS):
            prev_b = blk((a - 1) % FFT_BLOCKS)
            next_b = blk((a + 1) % FFT_BLOCKS)
            lap = []
            here = []
            for part in range(2):
                v = v_ref[part, :, blk(a)]
                vp = v_ref[part, :, prev_b]
                vn = v_ref[part, :, next_b]
                above = jnp.where(row_id == 0, 0.0, pltpu.roll(v, 1, 0))
                below = jnp.where(row_id == rows - 1, 0.0, pltpu.roll(v, rows - 1, 0))
                left = jnp.where(lane_id == 0, pltpu.roll(vp, 1, 1), pltpu.roll(v, 1, 1))
                right = jnp.where(
                    lane_id == LANE - 1, pltpu.roll(vn, LANE - 1, 1), pltpu.roll(v, LANE - 1, 1)
                )
                lap.append(above + below + left + right - 4.0 * v)
                here.append(v)
            gain = pick(rid_ref[k, :, blk(a)], gain_t)
            new_re = here[0] + (lap[0] * DAMPING - lap[1] * gain)
            new_im = here[1] + (lap[0] * gain + lap[1] * DAMPING)
            wout_ref[0, :, blk(a)] = new_re
            wout_ref[1, :, blk(a)] = new_im
            for j in range(strip_count):
                img_ref[j, k, :, blk(a)] = new_re[j * rows_here:(j + 1) * rows_here]
        return carry

    lax.fori_loop(0, steps, one_step, 0)


def fast_constants(line_len):
    outer = line_len // LANE
    b = np.arange(LANE)
    ang = 2.0 * np.pi * (np.outer(b, b) % LANE) / LANE
    cos_m, sin_m = (np.cos(ang), np.sin(ang))
    fwd = np.block([[cos_m, -sin_m], [sin_m, cos_m]])
    inv = np.block([[cos_m, sin_m], [-sin_m, cos_m]])

    def halves(m):
        hi = m.astype(ml_dtypes.bfloat16)
        lo = (m - hi.astype(np.float64)).astype(ml_dtypes.bfloat16)
        return (hi, lo)

    c = np.arange(outer)
    tw_ang = 2.0 * np.pi * np.outer(c, b) / line_len
    twiddle = np.stack([np.cos(tw_ang), np.sin(tw_ang)]).astype(np.float32)
    q = c[:, None] + outer * b[None, :]
    signed = np.where(q >= line_len // 2, q - line_len, q).astype(np.float32)
    kx_cd = signed * np.float32(2.0 * math.pi / line_len)
    return (halves(fwd), halves(inv), twiddle, kx_cd.astype(np.float32))


def run_section(wave, regions, table, mult, consts, strip_count):
    (fhi, flo), (ghi, glo), twiddle, _ = consts
    rows, line_len = wave.shape[1], wave.shape[2]
    steps = regions.shape[0]
    table_len = table.shape[0] // (3 * steps)
    vmem = pl.BlockSpec(memory_space=pltpu.VMEM)
    flops = steps * (2 * 3 * 2 * (FFT_BLOCKS * rows) * 256 * 256 + 400 * rows * line_len)
    return pl.pallas_call(
        lambda *refs: section_kernel(*refs, table_len=table_len),
        out_shape=(
            jax.ShapeDtypeStruct(wave.shape, jnp.float32),
            jax.ShapeDtypeStruct((strip_count, steps, rows // strip_count, line_len), jnp.float32),
        ),
        in_specs=[pl.BlockSpec(memory_space=pltpu.SMEM)] + [vmem] * 8,
        out_specs=(vmem, vmem),
        scratch_shapes=[
            pltpu.VMEM((FFT_BLOCKS * rows, 2 * LANE), jnp.float32),
            pltpu.VMEM((FFT_BLOCKS * rows, 2 * LANE), jnp.float32),
            pltpu.VMEM((2, rows, line_len), jnp.float32),
        ],
        cost_estimate=pl.CostEstimate(
            flops=flops, transcendentals=0, bytes_accessed=4 * rows * line_len * 6 * steps
        ),
    )(table, wave, regions, mult, jnp.asarray(twiddle), jnp.asarray(fhi), jnp.asarray(flo),
      jnp.asarray(ghi), jnp.asarray(glo))


def section_tables(omega, region_speed, fd_coeff, ref_region, kx_cd):
    inv_speed = 1.0 / region_speed
    ref_slow = inv_speed[ref_region]
    regions = region_speed.shape[0]
    padded = 1 << max(1, (regions - 1).bit_length())
    extra = padded - regions
    phase = omega * (inv_speed[None, :] - ref_slow[:, None])
    gain = jnp.broadcast_to(fd_coeff / omega, phase.shape)
    parts = [jnp.cos(phase), jnp.sin(phase), gain]
    if extra:
        parts = [jnp.concatenate([p, jnp.repeat(p[:, -1:], extra, axis=1)], axis=1) for p in parts]
    table = jnp.stack(parts, axis=1).reshape(-1)
    wave_ref = omega * ref_slow
    wave_ref = wave_ref[:, None, None]
    excess = wave_ref * wave_ref - kx_cd * kx_cd
    decay_line = jnp.exp(-jnp.sqrt(jnp.maximum(-excess, 0.0)))
    vertical = jnp.sqrt(jnp.maximum(excess, 0.0))
    mult = jnp.stack([decay_line * jnp.cos(vertical), decay_line * jnp.sin(vertical)], axis=1)
    return (table, mult)


def fast_fits(surface, region_index, region_speed):
    freq_count = surface.shape[1]
    rows = surface.shape[2] * lax.axis_size("strip")
    line_len = surface.shape[3]
    return (
        freq_count == lax.axis_size("strip")
        and line_len == FFT_BLOCKS * LANE
        and rows % ROW_CHUNK == 0
        and surface.shape[2] % ROW_CHUNK == 0
        and rows <= 64
        and region_speed.shape[0] <= 16
    )


def strip_pairs(depths, strip_count, shift):
    return [
        (d * strip_count + r, d * strip_count + (r + shift) % strip_count)
        for d in depths
        for r in range(strip_count)
    ]


def gather_rows(local, depths, strip_no, strip_count, row_axis):
    rows = local.shape[row_axis]
    shape = list(local.shape)
    shape[row_axis] = rows * strip_count
    full = jnp.zeros(shape, local.dtype)
    start = [0] * len(shape)
    start[row_axis] = strip_no * rows
    full = lax.dynamic_update_slice(full, local, start)
    for shift in range(1, strip_count):
        got = lax.ppermute(local, ("depth", "strip"), strip_pairs(depths, strip_count, shift))
        start = [0] * len(shape)
        start[row_axis] = ((strip_no - shift) % strip_count) * rows
        full = lax.dynamic_update_slice(full, got, start)
    return full


def shards(surface, omegas, region_speed, fd_coeff, region_index, ref_region):
    if not fast_fits(surface, region_index, region_speed):
        return shards_general(surface, omegas, region_speed, fd_coeff, region_index, ref_region)
    line_len = surface.shape[3]
    rows_here = surface.shape[2]
    steps = region_index.shape[0]
    segment_no = lax.axis_index("depth")
    segment_count = lax.axis_size("depth")
    strip_no = lax.axis_index("strip")
    strip_count = lax.axis_size("strip")
    rows = rows_here * strip_count
    every_depth = range(segment_count)
    consts = fast_constants(line_len)
    region_f = region_index.astype(jnp.float32)
    mine = lax.dynamic_index_in_dim(surface, strip_no, 1, keepdims=False)
    gathered = jnp.zeros((steps + 2, rows, line_len), jnp.float32)
    gathered = lax.dynamic_update_slice(
        gathered, jnp.concatenate([region_f, mine], axis=0), (0, strip_no * rows_here, 0)
    )
    for shift in range(1, strip_count):
        target = (strip_no + shift) % strip_count
        piece = jnp.concatenate(
            [region_f, lax.dynamic_index_in_dim(surface, target, 1, keepdims=False)], axis=0
        )
        got = lax.ppermute(piece, ("depth", "strip"), strip_pairs(every_depth, strip_count, shift))
        source = (strip_no - shift) % strip_count
        gathered = lax.dynamic_update_slice(gathered, got, (0, source * rows_here, 0))
    regions = gathered[:steps].astype(jnp.int32)
    wave = gathered[steps:]
    omega = lax.dynamic_index_in_dim(omegas, strip_no, 0, keepdims=False)
    table, mult = section_tables(omega, region_speed, fd_coeff, ref_region, jnp.asarray(consts[3]))
    image = jnp.zeros((strip_count, steps, rows_here, line_len), jnp.float32)

    def live(wave, image):
        return run_section(wave, regions, table, mult, consts, strip_count)

    def idle(wave, image):
        return (wave, image)

    for tick_no in range(segment_count):
        wave, image = lax.cond(segment_no == tick_no, live, idle, wave, image)
        if tick_no + 1 < segment_count:
            wave = from_behind(wave, "depth", 1)
    total = lax.dynamic_index_in_dim(image, strip_no, 0, keepdims=False)
    for shift in range(1, strip_count):
        target = (strip_no + shift) % strip_count
        piece = lax.dynamic_index_in_dim(image, target, 0, keepdims=False)
        total = total + lax.ppermute(
            piece, ("depth", "strip"), strip_pairs(every_depth, strip_count, shift)
        )
    return total


def solution(mesh):
    in_specs = (
        P(None, "shots", "strip", None),
        P(),
        P(),
        P(),
        P("depth", "strip", None),
        P("depth"),
    )
    out_specs = P("depth", "strip", "shots")
    return jax.shard_map(shards, mesh=mesh, in_specs=in_specs, out_specs=out_specs, check_vma=False)
```

```python
import math

import ml_dtypes
import numpy as np
import jax
import jax.numpy as jnp
from jax import lax
from jax.experimental import pallas as pl
from jax.experimental.pallas import tpu as pltpu
from jax.sharding import PartitionSpec as P

DAMPING = 0.05
PRECISE = lax.Precision.HIGHEST


def padded_2(cells, sides, width):
    for axis, dim in sides:
        count = lax.axis_size(axis)
        ends = count - 1
        head = lax.slice_in_dim(cells, 0, width, axis=dim)
        tail = lax.slice_in_dim(cells, cells.shape[dim] - width, cells.shape[dim], axis=dim)
        cells = jnp.concatenate(
            [
                lax.ppermute(tail, axis, [(i, (i + 1) % count) for i in range(ends)]),
                cells,
                lax.ppermute(head, axis, [((i + 1) % count, i) for i in range(ends)]),
            ],
            axis=dim,
        )
    return cells


def from_behind(value, axis, steps):
    count = lax.axis_size(axis)
    first, last = (max(0, -steps), min(count, count - steps))
    return lax.ppermute(value, axis, [(source, source + steps) for source in range(first, last)])


def complex_scale(values, cosine, sine_part):
    return jnp.stack(
        [values[0] * cosine - values[1] * sine_part, values[0] * sine_part + values[1] * cosine]
    )


def angle_pair(numerator, period):
    angle_grid = numerator.astype(jnp.float32) * (2.0 * math.pi / period)
    return (jnp.cos(angle_grid), jnp.sin(angle_grid))


def block_matrix(cosine, sine_part, forward):
    sign_flip = 1.0 if forward else -1.0
    return jnp.stack(
        [jnp.stack([cosine, -sign_flip * sine_part]), jnp.stack([sign_flip * sine_part, cosine])]
    )


def build_tables(line_len):
    block_len = 128
    outer_len = line_len // block_len
    inner_idx = jnp.arange(block_len)
    outer_idx = jnp.arange(outer_len)
    cos_large, sin_large = angle_pair(
        inner_idx[:, None] * inner_idx[None, :] % block_len, block_len
    )
    cos_small, sin_small = angle_pair(
        outer_idx[:, None] * outer_idx[None, :] % outer_len, outer_len
    )
    cos_twist, sin_twist = angle_pair(outer_idx[:, None] * inner_idx[None, :], line_len)
    wave_index = outer_idx[:, None] + outer_len * inner_idx[None, :]
    signed = jnp.where(wave_index >= line_len // 2, wave_index - line_len, wave_index)
    kx_grid = signed.astype(jnp.float32) * (2.0 * math.pi / line_len)
    small_fwd = block_matrix(cos_small, sin_small, True)
    small_inv = block_matrix(cos_small, sin_small, False)
    large_fwd = block_matrix(cos_large, sin_large, True)
    large_inv = block_matrix(cos_large, sin_large, False)
    return (small_fwd, small_inv, large_fwd, large_inv, cos_twist, sin_twist, kx_grid)


def forward_line(wavefield, tables):
    small_fwd, small_inv, large_fwd, large_inv, cos_twist, sin_twist, kx_grid = tables
    row_count = wavefield.shape[1]
    pieces = wavefield.reshape(2, row_count, cos_twist.shape[0], cos_twist.shape[1])
    mixed_part = jnp.einsum("zrab,zwca->wrcb", pieces, small_fwd, precision=PRECISE)
    mixed_part = complex_scale(mixed_part, cos_twist, -sin_twist)
    return jnp.einsum("zrcb,zwbd->wrcd", mixed_part, large_fwd, precision=PRECISE)


def inverse_line(spectrum, tables):
    small_fwd, small_inv, large_fwd, large_inv, cos_twist, sin_twist, kx_grid = tables
    row_count = spectrum.shape[1]
    line_len = cos_twist.shape[0] * cos_twist.shape[1]
    mixed_part = jnp.einsum("zrcd,zwdb->wrcb", spectrum, large_inv, precision=PRECISE)
    mixed_part = complex_scale(mixed_part, cos_twist, sin_twist)
    pieces = jnp.einsum("zrcb,zwca->wrab", mixed_part, small_inv, precision=PRECISE)
    return pieces.reshape(2, row_count, line_len) * (1.0 / line_len)


def lookup(regions, entries):
    picked = jnp.zeros(regions.shape, jnp.float32)
    for region_no in range(entries.shape[0]):
        picked = picked + jnp.where(regions == region_no, entries[region_no], 0.0)
    return picked


def depth_step(wavefield, omega_now, slow_cells, coef_cells, ref_slow, tables, pad_rows):
    kx_grid = tables[6]
    wave_ref = omega_now * ref_slow
    excess = wave_ref * wave_ref - kx_grid * kx_grid
    decay_line = jnp.exp(-jnp.sqrt(jnp.maximum(-excess, 0.0)))
    vertical = jnp.sqrt(jnp.maximum(excess, 0.0))
    spectrum = complex_scale(
        forward_line(wavefield, tables),
        decay_line * jnp.cos(vertical),
        decay_line * jnp.sin(vertical),
    )
    wavefield = inverse_line(spectrum, tables)
    phase_cell = omega_now * (slow_cells - ref_slow)
    wavefield = complex_scale(wavefield, jnp.cos(phase_cell), jnp.sin(phase_cell))
    padded = pad_rows(wavefield)
    laplace = (
        padded[:, :-2]
        + padded[:, 2:]
        + jnp.roll(wavefield, 1, 2)
        + jnp.roll(wavefield, -1, 2)
        - 4.0 * wavefield
    )
    return wavefield + complex_scale(laplace, DAMPING, coef_cells / omega_now)


def march(wavefield, omega_now, slow_block, coef_block, ref_block, tables, pad_rows):
    traces = []
    for step_no in range(slow_block.shape[0]):
        wavefield = depth_step(
            wavefield,
            omega_now,
            slow_block[step_no],
            coef_block[step_no],
            ref_block[step_no],
            tables,
            pad_rows,
        )
        traces.append(wavefield[0])
    return (wavefield, jnp.stack(traces))


def shards_general(surface, omegas, region_speed, fd_coeff, region_index, ref_region):
    line_len = surface.shape[3]
    rows_here = surface.shape[2]
    freq_count = surface.shape[1]
    step_count = region_index.shape[0]
    tables = build_tables(line_len)
    inv_speed = 1.0 / region_speed
    segment_no = lax.axis_index("depth")
    segment_count = lax.axis_size("depth")

    def pad_near(values):
        return padded_2(values, (("strip", 1),), 1)

    slow_cells = lookup(region_index, inv_speed)
    coef_cells = lookup(region_index, fd_coeff)
    ref_cells = lookup(ref_region, inv_speed)
    freq_index = jnp.arange(freq_count)
    image_out = jnp.zeros((step_count, rows_here, line_len), jnp.float32)
    arriving = jnp.zeros((2, rows_here, line_len), jnp.float32)
    tick_count = freq_count + segment_count - 1
    for tick_no in range(tick_count):
        batch_no = tick_no - segment_no
        is_live = (batch_no >= 0) & (batch_no < freq_count)
        clipped = jnp.clip(batch_no, 0, freq_count - 1)
        picked = lax.dynamic_index_in_dim(surface, clipped, 1, keepdims=False)
        entering = jnp.where(segment_no == 0, picked, arriving)
        omega_now = jnp.sum(jnp.where(freq_index == clipped, omegas, 0.0))
        leaving, traces = march(
            entering, omega_now, slow_cells, coef_cells, ref_cells, tables, pad_near
        )
        image_out = image_out + jnp.where(is_live, traces, 0.0)
        if tick_no + 1 < tick_count:
            arriving = from_behind(leaving, "depth", 1)
    return image_out


LANE = 128
FFT_BLOCKS = 16
ROW_CHUNK = 8


def fft4(x0, x1, x2, x3, sign):
    s0 = (x0[0] + x2[0], x0[1] + x2[1])
    d0 = (x0[0] - x2[0], x0[1] - x2[1])
    s1 = (x1[0] + x3[0], x1[1] + x3[1])
    d1 = (x1[0] - x3[0], x1[1] - x3[1])
    if sign < 0:
        wd = (d1[1], -d1[0])
    else:
        wd = (-d1[1], d1[0])
    return (
        (s0[0] + s1[0], s0[1] + s1[1]),
        (d0[0] + wd[0], d0[1] + wd[1]),
        (s0[0] - s1[0], s0[1] - s1[1]),
        (d0[0] - wd[0], d0[1] - wd[1]),
    )


def turn_const(value, power, sign):
    if power == 4:
        return (-value[1], value[0]) if sign > 0 else (value[1], -value[0])
    angle = sign * 2.0 * math.pi * power / 16.0
    cr, ci = (math.cos(angle), math.sin(angle))
    return (value[0] * cr - value[1] * ci, value[0] * ci + value[1] * cr)


def fft16(parts, sign):
    mid = [[None] * 4 for _ in range(4)]
    for a0 in range(4):
        ys = fft4(parts[a0], parts[4 + a0], parts[8 + a0], parts[12 + a0], sign)
        for c0 in range(4):
            power = a0 * c0
            mid[a0][c0] = ys[c0] if power == 0 else turn_const(ys[c0], power, sign)
    out = [None] * 16
    for c0 in range(4):
        zs = fft4(mid[0][c0], mid[1][c0], mid[2][c0], mid[3][c0], sign)
        for c1 in range(4):
            out[c0 + 4 * c1] = zs[c1]
    return out


def pick(regions, values):
    level = list(values)
    bit = 1
    while len(level) > 1:
        chosen = (regions & bit) != 0
        level = [jnp.where(chosen, level[i + 1], level[i]) for i in range(0, len(level), 2)]
        bit *= 2
    return jnp.broadcast_to(level[0], regions.shape)


def split_dot(values, hi_ref, lo_ref):
    high = values.astype(jnp.bfloat16)
    low = (values - high.astype(jnp.float32)).astype(jnp.bfloat16)
    main = jnp.dot(high, hi_ref[...], preferred_element_type=jnp.float32)
    fix = jnp.dot(high, lo_ref[...], preferred_element_type=jnp.float32) + jnp.dot(
        low, hi_ref[:, :], preferred_element_type=jnp.float32
    )
    return main + fix


def section_kernel(
    tab_ref, w_ref, rid_ref, mult_ref, tw_ref, fhi_ref, flo_ref, ghi_ref, glo_ref,
    wout_ref, img_ref, a_ref, y_ref, v_ref, *, table_len
):
    rows = w_ref.shape[1]
    line_len = w_ref.shape[2]
    steps = rid_ref.shape[0]
    strip_count, rows_here = img_ref.shape[0], img_ref.shape[2]
    chunks = rows // ROW_CHUNK
    inv_len = 1.0 / line_len
    wout_ref[...] = w_ref[...]

    def blk(a):
        return slice(a * LANE, (a + 1) * LANE)

    def one_step(k, carry):
        base = k * (3 * table_len)
        cos_t = [tab_ref[base + g] for g in range(table_len)]
        sin_t = [tab_ref[base + table_len + g] for g in range(table_len)]
        gain_t = [tab_ref[base + 2 * table_len + g] for g in range(table_len)]

        def forward_chunk(i, c):
            y0 = pl.multiple_of(i * ROW_CHUNK, ROW_CHUNK)
            parts = [
                (wout_ref[0, pl.ds(y0, ROW_CHUNK), blk(a)], wout_ref[1, pl.ds(y0, ROW_CHUNK), blk(a)])
                for a in range(FFT_BLOCKS)
            ]
            spec = fft16(parts, -1)
            for cc in range(FFT_BLOCKS):
                tc = tw_ref[0, cc:cc + 1, :]
                ts = tw_ref[1, cc:cc + 1, :]
                xr, xi = spec[cc]
                a_ref[pl.ds(cc * rows + y0, ROW_CHUNK), 0:LANE] = xr * tc + xi * ts
                a_ref[pl.ds(cc * rows + y0, ROW_CHUNK), LANE:2 * LANE] = xi * tc - xr * ts
            return c

        lax.fori_loop(0, chunks, forward_chunk, 0)
        y_ref[...] = split_dot(a_ref[...], fhi_ref, flo_ref)
        for cc in range(FFT_BLOCKS):
            band = slice(cc * rows, (cc + 1) * rows)
            yr = y_ref[band, 0:LANE]
            yi = y_ref[band, LANE:2 * LANE]
            mr = mult_ref[k, 0, cc:cc + 1, :]
            mi = mult_ref[k, 1, cc:cc + 1, :]
            a_ref[band, 0:LANE] = yr * mr - yi * mi
            a_ref[band, LANE:2 * LANE] = yr * mi + yi * mr
        y_ref[...] = split_dot(a_ref[...], ghi_ref, glo_ref)

        def inverse_chunk(i, c):
            y0 = pl.multiple_of(i * ROW_CHUNK, ROW_CHUNK)
            parts = []
            for cc in range(FFT_BLOCKS):
                zr = y_ref[pl.ds(cc * rows + y0, ROW_CHUNK), 0:LANE]
                zi = y_ref[pl.ds(cc * rows + y0, ROW_CHUNK), LANE:2 * LANE]
                tc = tw_ref[0, cc:cc + 1, :]
                ts = tw_ref[1, cc:cc + 1, :]
                parts.append((zr * tc - zi * ts, zr * ts + zi * tc))
            back = fft16(parts, 1)
            for a in range(FFT_BLOCKS):
                ur = back[a][0] * inv_len
                ui = back[a][1] * inv_len
                regions = rid_ref[k, pl.ds(y0, ROW_CHUNK), blk(a)]
                cs = pick(regions, cos_t)
                sn = pick(regions, sin_t)
                v_ref[0, pl.ds(y0, ROW_CHUNK), blk(a)] = ur * cs - ui * sn
                v_ref[1, pl.ds(y0, ROW_CHUNK), blk(a)] = ur * sn + ui * cs
            return c

        lax.fori_loop(0, chunks, inverse_chunk, 0)
        row_id = lax.broadcasted_iota(jnp.int32, (rows, LANE), 0)
        lane_id = lax.broadcasted_iota(jnp.int32, (rows, LANE), 1)
        for a in range(FFT_BLOCKS):
            prev_b = blk((a - 1) % FFT_BLOCKS)
            next_b = blk((a + 1) % FFT_BLOCKS)
            lap = []
            here = []
            for part in range(2):
                v = v_ref[part, :, blk(a)]
                vp = v_ref[part, :, prev_b]
                vn = v_ref[part, :, next_b]
                above = jnp.where(row_id == 0, 0.0, pltpu.roll(v, 1, 0))
                below = jnp.where(row_id == rows - 1, 0.0, pltpu.roll(v, rows - 1, 0))
                left = jnp.where(lane_id == 0, pltpu.roll(vp, 1, 1), pltpu.roll(v, 1, 1))
                right = jnp.where(
                    lane_id == LANE - 1, pltpu.roll(vn, LANE - 1, 1), pltpu.roll(v, LANE - 1, 1)
                )
                lap.append(above + below + left + right - 4.0 * v)
                here.append(v)
            gain = pick(rid_ref[k, :, blk(a)], gain_t)
            new_re = here[0] + (lap[0] * DAMPING - lap[1] * gain)
            new_im = here[1] + (lap[0] * gain + lap[1] * DAMPING)
            wout_ref[0, :, blk(a)] = new_re
            wout_ref[1, :, blk(a)] = new_im
            for j in range(strip_count):
                img_ref[j, k, :, blk(a)] = new_re[j * rows_here:(j + 1) * rows_here]
        return carry

    lax.fori_loop(0, steps, one_step, 0)


def fast_constants(line_len):
    outer = line_len // LANE
    b = np.arange(LANE)
    ang = 2.0 * np.pi * (np.outer(b, b) % LANE) / LANE
    cos_m, sin_m = (np.cos(ang), np.sin(ang))
    fwd = np.block([[cos_m, -sin_m], [sin_m, cos_m]])
    inv = np.block([[cos_m, sin_m], [-sin_m, cos_m]])

    def halves(m):
        hi = m.astype(ml_dtypes.bfloat16)
        lo = (m - hi.astype(np.float64)).astype(ml_dtypes.bfloat16)
        return (hi, lo)

    c = np.arange(outer)
    tw_ang = 2.0 * np.pi * np.outer(c, b) / line_len
    twiddle = np.stack([np.cos(tw_ang), np.sin(tw_ang)]).astype(np.float32)
    q = c[:, None] + outer * b[None, :]
    signed = np.where(q >= line_len // 2, q - line_len, q).astype(np.float32)
    kx_cd = signed * np.float32(2.0 * math.pi / line_len)
    return (halves(fwd), halves(inv), twiddle, kx_cd.astype(np.float32))


def run_section(wave, regions, table, mult, consts, strip_count):
    (fhi, flo), (ghi, glo), twiddle, _ = consts
    rows, line_len = wave.shape[1], wave.shape[2]
    steps = regions.shape[0]
    table_len = table.shape[0] // (3 * steps)
    vmem = pl.BlockSpec(memory_space=pltpu.VMEM)
    flops = steps * (2 * 3 * 2 * (FFT_BLOCKS * rows) * 256 * 256 + 400 * rows * line_len)
    return pl.pallas_call(
        lambda *refs: section_kernel(*refs, table_len=table_len),
        out_shape=(
            jax.ShapeDtypeStruct(wave.shape, jnp.float32),
            jax.ShapeDtypeStruct((strip_count, steps, rows // strip_count, line_len), jnp.float32),
        ),
        in_specs=[pl.BlockSpec(memory_space=pltpu.SMEM)] + [vmem] * 8,
        out_specs=(vmem, vmem),
        scratch_shapes=[
            pltpu.VMEM((FFT_BLOCKS * rows, 2 * LANE), jnp.float32),
            pltpu.VMEM((FFT_BLOCKS * rows, 2 * LANE), jnp.float32),
            pltpu.VMEM((2, rows, line_len), jnp.float32),
        ],
        cost_estimate=pl.CostEstimate(
            flops=flops, transcendentals=0, bytes_accessed=4 * rows * line_len * 6 * steps
        ),
    )(table, wave, regions, mult, jnp.asarray(twiddle), jnp.asarray(fhi), jnp.asarray(flo),
      jnp.asarray(ghi), jnp.asarray(glo))


def section_tables(omega, region_speed, fd_coeff, ref_region, kx_cd):
    inv_speed = 1.0 / region_speed
    ref_slow = inv_speed[ref_region]
    regions = region_speed.shape[0]
    padded = 1 << max(1, (regions - 1).bit_length())
    extra = padded - regions
    phase = omega * (inv_speed[None, :] - ref_slow[:, None])
    gain = jnp.broadcast_to(fd_coeff / omega, phase.shape)
    parts = [jnp.cos(phase), jnp.sin(phase), gain]
    if extra:
        parts = [jnp.concatenate([p, jnp.repeat(p[:, -1:], extra, axis=1)], axis=1) for p in parts]
    table = jnp.stack(parts, axis=1).reshape(-1)
    wave_ref = omega * ref_slow
    wave_ref = wave_ref[:, None, None]
    excess = wave_ref * wave_ref - kx_cd * kx_cd
    decay_line = jnp.exp(-jnp.sqrt(jnp.maximum(-excess, 0.0)))
    vertical = jnp.sqrt(jnp.maximum(excess, 0.0))
    mult = jnp.stack([decay_line * jnp.cos(vertical), decay_line * jnp.sin(vertical)], axis=1)
    return (table, mult)


def fast_fits(surface, region_index, region_speed):
    freq_count = surface.shape[1]
    rows = surface.shape[2] * lax.axis_size("strip")
    line_len = surface.shape[3]
    return (
        freq_count == lax.axis_size("strip")
        and line_len == FFT_BLOCKS * LANE
        and rows % ROW_CHUNK == 0
        and surface.shape[2] % ROW_CHUNK == 0
        and rows <= 64
        and region_speed.shape[0] <= 16
    )


def strip_pairs(depths, strip_count, shift):
    return [
        (d * strip_count + r, d * strip_count + (r + shift) % strip_count)
        for d in depths
        for r in range(strip_count)
    ]


def gather_rows(local, depths, strip_no, strip_count, row_axis):
    rows = local.shape[row_axis]
    shape = list(local.shape)
    shape[row_axis] = rows * strip_count
    full = jnp.zeros(shape, local.dtype)
    start = [0] * len(shape)
    start[row_axis] = strip_no * rows
    full = lax.dynamic_update_slice(full, local, start)
    for shift in range(1, strip_count):
        got = lax.ppermute(local, ("depth", "strip"), strip_pairs(depths, strip_count, shift))
        start = [0] * len(shape)
        start[row_axis] = ((strip_no - shift) % strip_count) * rows
        full = lax.dynamic_update_slice(full, got, start)
    return full


def shards(surface, omegas, region_speed, fd_coeff, region_index, ref_region):
    if not fast_fits(surface, region_index, region_speed):
        return shards_general(surface, omegas, region_speed, fd_coeff, region_index, ref_region)
    line_len = surface.shape[3]
    rows_here = surface.shape[2]
    steps = region_index.shape[0]
    segment_no = lax.axis_index("depth")
    segment_count = lax.axis_size("depth")
    strip_no = lax.axis_index("strip")
    strip_count = lax.axis_size("strip")
    rows = rows_here * strip_count
    consts = fast_constants(line_len)
    region_f = region_index.astype(jnp.float32)
    mine = lax.dynamic_index_in_dim(surface, strip_no, 1, keepdims=False)
    gathered = jnp.zeros((steps + 2, rows, line_len), jnp.float32)
    gathered = lax.dynamic_update_slice(
        gathered, jnp.concatenate([region_f, mine], axis=0), (0, strip_no * rows_here, 0)
    )
    for shift in range(1, strip_count):
        target = (strip_no + shift) % strip_count
        piece = jnp.concatenate(
            [region_f, lax.dynamic_index_in_dim(surface, target, 1, keepdims=False)], axis=0
        )
        got = lax.ppermute(
            piece, ("depth", "strip"), strip_pairs(range(segment_count), strip_count, shift)
        )
        source = (strip_no - shift) % strip_count
        gathered = lax.dynamic_update_slice(gathered, got, (0, source * rows_here, 0))
    regions = gathered[:steps].astype(jnp.int32)
    wave = gathered[steps:]
    omega = lax.dynamic_index_in_dim(omegas, strip_no, 0, keepdims=False)
    table, mult = section_tables(omega, region_speed, fd_coeff, ref_region, jnp.asarray(consts[3]))
    image = jnp.zeros((strip_count, steps, rows_here, line_len), jnp.float32)
    total = jnp.zeros((steps, rows_here, line_len), jnp.float32)

    def live(wave, image):
        return run_section(wave, regions, table, mult, consts, strip_count)

    def idle(wave, image):
        return (wave, image)

    for tick_no in range(segment_count):
        wave, image = lax.cond(segment_no == tick_no, live, idle, wave, image)
        if tick_no + 1 < segment_count:
            wave = lax.ppermute(wave, "depth", [(tick_no, tick_no + 1)])
            wave, image = lax.optimization_barrier((wave, image))
        for shift in range(1, strip_count):
            target = (strip_no + shift) % strip_count
            piece = lax.dynamic_index_in_dim(image, target, 0, keepdims=False)
            total = total + lax.ppermute(
                piece, ("depth", "strip"), strip_pairs([tick_no], strip_count, shift)
            )
        if tick_no + 1 < segment_count:
            wave, total = lax.optimization_barrier((wave, total))
    return total + lax.dynamic_index_in_dim(image, strip_no, 0, keepdims=False)


def solution(mesh):
    in_specs = (
        P(None, "shots", "strip", None),
        P(),
        P(),
        P(),
        P("depth", "strip", None),
        P("depth"),
    )
    out_specs = P("depth", "strip", "shots")
    return jax.shard_map(shards, mesh=mesh, in_specs=in_specs, out_specs=out_specs, check_vma=False)
```

```python
import math

import ml_dtypes
import numpy as np
import jax
import jax.numpy as jnp
from jax import lax
from jax.experimental import pallas as pl
from jax.experimental.pallas import tpu as pltpu
from jax.sharding import PartitionSpec as P

DAMPING = 0.05
PRECISE = lax.Precision.HIGHEST


def padded_2(cells, sides, width):
    for axis, dim in sides:
        count = lax.axis_size(axis)
        ends = count - 1
        head = lax.slice_in_dim(cells, 0, width, axis=dim)
        tail = lax.slice_in_dim(cells, cells.shape[dim] - width, cells.shape[dim], axis=dim)
        cells = jnp.concatenate(
            [
                lax.ppermute(tail, axis, [(i, (i + 1) % count) for i in range(ends)]),
                cells,
                lax.ppermute(head, axis, [((i + 1) % count, i) for i in range(ends)]),
            ],
            axis=dim,
        )
    return cells


def from_behind(value, axis, steps):
    count = lax.axis_size(axis)
    first, last = (max(0, -steps), min(count, count - steps))
    return lax.ppermute(value, axis, [(source, source + steps) for source in range(first, last)])


def complex_scale(values, cosine, sine_part):
    return jnp.stack(
        [values[0] * cosine - values[1] * sine_part, values[0] * sine_part + values[1] * cosine]
    )


def angle_pair(numerator, period):
    angle_grid = numerator.astype(jnp.float32) * (2.0 * math.pi / period)
    return (jnp.cos(angle_grid), jnp.sin(angle_grid))


def block_matrix(cosine, sine_part, forward):
    sign_flip = 1.0 if forward else -1.0
    return jnp.stack(
        [jnp.stack([cosine, -sign_flip * sine_part]), jnp.stack([sign_flip * sine_part, cosine])]
    )


def build_tables(line_len):
    block_len = 128
    outer_len = line_len // block_len
    inner_idx = jnp.arange(block_len)
    outer_idx = jnp.arange(outer_len)
    cos_large, sin_large = angle_pair(
        inner_idx[:, None] * inner_idx[None, :] % block_len, block_len
    )
    cos_small, sin_small = angle_pair(
        outer_idx[:, None] * outer_idx[None, :] % outer_len, outer_len
    )
    cos_twist, sin_twist = angle_pair(outer_idx[:, None] * inner_idx[None, :], line_len)
    wave_index = outer_idx[:, None] + outer_len * inner_idx[None, :]
    signed = jnp.where(wave_index >= line_len // 2, wave_index - line_len, wave_index)
    kx_grid = signed.astype(jnp.float32) * (2.0 * math.pi / line_len)
    small_fwd = block_matrix(cos_small, sin_small, True)
    small_inv = block_matrix(cos_small, sin_small, False)
    large_fwd = block_matrix(cos_large, sin_large, True)
    large_inv = block_matrix(cos_large, sin_large, False)
    return (small_fwd, small_inv, large_fwd, large_inv, cos_twist, sin_twist, kx_grid)


def forward_line(wavefield, tables):
    small_fwd, small_inv, large_fwd, large_inv, cos_twist, sin_twist, kx_grid = tables
    row_count = wavefield.shape[1]
    pieces = wavefield.reshape(2, row_count, cos_twist.shape[0], cos_twist.shape[1])
    mixed_part = jnp.einsum("zrab,zwca->wrcb", pieces, small_fwd, precision=PRECISE)
    mixed_part = complex_scale(mixed_part, cos_twist, -sin_twist)
    return jnp.einsum("zrcb,zwbd->wrcd", mixed_part, large_fwd, precision=PRECISE)


def inverse_line(spectrum, tables):
    small_fwd, small_inv, large_fwd, large_inv, cos_twist, sin_twist, kx_grid = tables
    row_count = spectrum.shape[1]
    line_len = cos_twist.shape[0] * cos_twist.shape[1]
    mixed_part = jnp.einsum("zrcd,zwdb->wrcb", spectrum, large_inv, precision=PRECISE)
    mixed_part = complex_scale(mixed_part, cos_twist, sin_twist)
    pieces = jnp.einsum("zrcb,zwca->wrab", mixed_part, small_inv, precision=PRECISE)
    return pieces.reshape(2, row_count, line_len) * (1.0 / line_len)


def lookup(regions, entries):
    picked = jnp.zeros(regions.shape, jnp.float32)
    for region_no in range(entries.shape[0]):
        picked = picked + jnp.where(regions == region_no, entries[region_no], 0.0)
    return picked


def depth_step(wavefield, omega_now, slow_cells, coef_cells, ref_slow, tables, pad_rows):
    kx_grid = tables[6]
    wave_ref = omega_now * ref_slow
    excess = wave_ref * wave_ref - kx_grid * kx_grid
    decay_line = jnp.exp(-jnp.sqrt(jnp.maximum(-excess, 0.0)))
    vertical = jnp.sqrt(jnp.maximum(excess, 0.0))
    spectrum = complex_scale(
        forward_line(wavefield, tables),
        decay_line * jnp.cos(vertical),
        decay_line * jnp.sin(vertical),
    )
    wavefield = inverse_line(spectrum, tables)
    phase_cell = omega_now * (slow_cells - ref_slow)
    wavefield = complex_scale(wavefield, jnp.cos(phase_cell), jnp.sin(phase_cell))
    padded = pad_rows(wavefield)
    laplace = (
        padded[:, :-2]
        + padded[:, 2:]
        + jnp.roll(wavefield, 1, 2)
        + jnp.roll(wavefield, -1, 2)
        - 4.0 * wavefield
    )
    return wavefield + complex_scale(laplace, DAMPING, coef_cells / omega_now)


def march(wavefield, omega_now, slow_block, coef_block, ref_block, tables, pad_rows):
    traces = []
    for step_no in range(slow_block.shape[0]):
        wavefield = depth_step(
            wavefield,
            omega_now,
            slow_block[step_no],
            coef_block[step_no],
            ref_block[step_no],
            tables,
            pad_rows,
        )
        traces.append(wavefield[0])
    return (wavefield, jnp.stack(traces))


def shards_general(surface, omegas, region_speed, fd_coeff, region_index, ref_region):
    line_len = surface.shape[3]
    rows_here = surface.shape[2]
    freq_count = surface.shape[1]
    step_count = region_index.shape[0]
    tables = build_tables(line_len)
    inv_speed = 1.0 / region_speed
    segment_no = lax.axis_index("depth")
    segment_count = lax.axis_size("depth")

    def pad_near(values):
        return padded_2(values, (("strip", 1),), 1)

    slow_cells = lookup(region_index, inv_speed)
    coef_cells = lookup(region_index, fd_coeff)
    ref_cells = lookup(ref_region, inv_speed)
    freq_index = jnp.arange(freq_count)
    image_out = jnp.zeros((step_count, rows_here, line_len), jnp.float32)
    arriving = jnp.zeros((2, rows_here, line_len), jnp.float32)
    tick_count = freq_count + segment_count - 1
    for tick_no in range(tick_count):
        batch_no = tick_no - segment_no
        is_live = (batch_no >= 0) & (batch_no < freq_count)
        clipped = jnp.clip(batch_no, 0, freq_count - 1)
        picked = lax.dynamic_index_in_dim(surface, clipped, 1, keepdims=False)
        entering = jnp.where(segment_no == 0, picked, arriving)
        omega_now = jnp.sum(jnp.where(freq_index == clipped, omegas, 0.0))
        leaving, traces = march(
            entering, omega_now, slow_cells, coef_cells, ref_cells, tables, pad_near
        )
        image_out = image_out + jnp.where(is_live, traces, 0.0)
        if tick_no + 1 < tick_count:
            arriving = from_behind(leaving, "depth", 1)
    return image_out


LANE = 128
FFT_BLOCKS = 16
ROW_CHUNK = 8


def fft4(x0, x1, x2, x3, sign):
    s0 = (x0[0] + x2[0], x0[1] + x2[1])
    d0 = (x0[0] - x2[0], x0[1] - x2[1])
    s1 = (x1[0] + x3[0], x1[1] + x3[1])
    d1 = (x1[0] - x3[0], x1[1] - x3[1])
    if sign < 0:
        wd = (d1[1], -d1[0])
    else:
        wd = (-d1[1], d1[0])
    return (
        (s0[0] + s1[0], s0[1] + s1[1]),
        (d0[0] + wd[0], d0[1] + wd[1]),
        (s0[0] - s1[0], s0[1] - s1[1]),
        (d0[0] - wd[0], d0[1] - wd[1]),
    )


def turn_const(value, power, sign):
    if power == 4:
        return (-value[1], value[0]) if sign > 0 else (value[1], -value[0])
    angle = sign * 2.0 * math.pi * power / 16.0
    cr, ci = (math.cos(angle), math.sin(angle))
    return (value[0] * cr - value[1] * ci, value[0] * ci + value[1] * cr)


def fft16(parts, sign):
    mid = [[None] * 4 for _ in range(4)]
    for a0 in range(4):
        ys = fft4(parts[a0], parts[4 + a0], parts[8 + a0], parts[12 + a0], sign)
        for c0 in range(4):
            power = a0 * c0
            mid[a0][c0] = ys[c0] if power == 0 else turn_const(ys[c0], power, sign)
    out = [None] * 16
    for c0 in range(4):
        zs = fft4(mid[0][c0], mid[1][c0], mid[2][c0], mid[3][c0], sign)
        for c1 in range(4):
            out[c0 + 4 * c1] = zs[c1]
    return out


def pick(regions, values):
    level = list(values)
    bit = 1
    while len(level) > 1:
        chosen = (regions & bit) != 0
        level = [jnp.where(chosen, level[i + 1], level[i]) for i in range(0, len(level), 2)]
        bit *= 2
    return jnp.broadcast_to(level[0], regions.shape)


def split_dot(values, hi_ref, lo_ref):
    high = values.astype(jnp.bfloat16)
    low = (values - high.astype(jnp.float32)).astype(jnp.bfloat16)
    main = jnp.dot(high, hi_ref[...], preferred_element_type=jnp.float32)
    fix = jnp.dot(high, lo_ref[...], preferred_element_type=jnp.float32) + jnp.dot(
        low, hi_ref[:, :], preferred_element_type=jnp.float32
    )
    return main + fix


def section_kernel(
    tab_ref, w_ref, rid_ref, mult_ref, tw_ref, fhi_ref, flo_ref, ghi_ref, glo_ref,
    wout_ref, img_ref, a_ref, y_ref, v_ref, *, table_len
):
    rows = w_ref.shape[1]
    line_len = w_ref.shape[2]
    steps = rid_ref.shape[0]
    strip_count, rows_here = img_ref.shape[0], img_ref.shape[2]
    chunks = rows // ROW_CHUNK
    inv_len = 1.0 / line_len
    wout_ref[...] = w_ref[...]

    def blk(a):
        return slice(a * LANE, (a + 1) * LANE)

    def one_step(k, carry):
        base = k * (3 * table_len)
        cos_t = [tab_ref[base + g] for g in range(table_len)]
        sin_t = [tab_ref[base + table_len + g] for g in range(table_len)]
        gain_t = [tab_ref[base + 2 * table_len + g] for g in range(table_len)]

        def forward_chunk(i, c):
            y0 = pl.multiple_of(i * ROW_CHUNK, ROW_CHUNK)
            parts = [
                (wout_ref[0, pl.ds(y0, ROW_CHUNK), blk(a)], wout_ref[1, pl.ds(y0, ROW_CHUNK), blk(a)])
                for a in range(FFT_BLOCKS)
            ]
            spec = fft16(parts, -1)
            for cc in range(FFT_BLOCKS):
                tc = tw_ref[0, cc:cc + 1, :]
                ts = tw_ref[1, cc:cc + 1, :]
                xr, xi = spec[cc]
                a_ref[pl.ds(cc * rows + y0, ROW_CHUNK), 0:LANE] = xr * tc + xi * ts
                a_ref[pl.ds(cc * rows + y0, ROW_CHUNK), LANE:2 * LANE] = xi * tc - xr * ts
            return c

        lax.fori_loop(0, chunks, forward_chunk, 0)
        y_ref[...] = split_dot(a_ref[...], fhi_ref, flo_ref)
        for cc in range(FFT_BLOCKS):
            band = slice(cc * rows, (cc + 1) * rows)
            yr = y_ref[band, 0:LANE]
            yi = y_ref[band, LANE:2 * LANE]
            mr = mult_ref[k, 0, cc:cc + 1, :]
            mi = mult_ref[k, 1, cc:cc + 1, :]
            a_ref[band, 0:LANE] = yr * mr - yi * mi
            a_ref[band, LANE:2 * LANE] = yr * mi + yi * mr
        y_ref[...] = split_dot(a_ref[...], ghi_ref, glo_ref)

        def inverse_chunk(i, c):
            y0 = pl.multiple_of(i * ROW_CHUNK, ROW_CHUNK)
            parts = []
            for cc in range(FFT_BLOCKS):
                zr = y_ref[pl.ds(cc * rows + y0, ROW_CHUNK), 0:LANE]
                zi = y_ref[pl.ds(cc * rows + y0, ROW_CHUNK), LANE:2 * LANE]
                tc = tw_ref[0, cc:cc + 1, :]
                ts = tw_ref[1, cc:cc + 1, :]
                parts.append((zr * tc - zi * ts, zr * ts + zi * tc))
            back = fft16(parts, 1)
            for a in range(FFT_BLOCKS):
                ur = back[a][0] * inv_len
                ui = back[a][1] * inv_len
                regions = rid_ref[k, pl.ds(y0, ROW_CHUNK), blk(a)]
                cs = pick(regions, cos_t)
                sn = pick(regions, sin_t)
                v_ref[0, pl.ds(y0, ROW_CHUNK), blk(a)] = ur * cs - ui * sn
                v_ref[1, pl.ds(y0, ROW_CHUNK), blk(a)] = ur * sn + ui * cs
            return c

        lax.fori_loop(0, chunks, inverse_chunk, 0)
        row_id = lax.broadcasted_iota(jnp.int32, (rows, LANE), 0)
        lane_id = lax.broadcasted_iota(jnp.int32, (rows, LANE), 1)
        for a in range(FFT_BLOCKS):
            prev_b = blk((a - 1) % FFT_BLOCKS)
            next_b = blk((a + 1) % FFT_BLOCKS)
            lap = []
            here = []
            for part in range(2):
                v = v_ref[part, :, blk(a)]
                vp = v_ref[part, :, prev_b]
                vn = v_ref[part, :, next_b]
                above = jnp.where(row_id == 0, 0.0, pltpu.roll(v, 1, 0))
                below = jnp.where(row_id == rows - 1, 0.0, pltpu.roll(v, rows - 1, 0))
                left = jnp.where(lane_id == 0, pltpu.roll(vp, 1, 1), pltpu.roll(v, 1, 1))
                right = jnp.where(
                    lane_id == LANE - 1, pltpu.roll(vn, LANE - 1, 1), pltpu.roll(v, LANE - 1, 1)
                )
                lap.append(above + below + left + right - 4.0 * v)
                here.append(v)
            gain = pick(rid_ref[k, :, blk(a)], gain_t)
            new_re = here[0] + (lap[0] * DAMPING - lap[1] * gain)
            new_im = here[1] + (lap[0] * gain + lap[1] * DAMPING)
            wout_ref[0, :, blk(a)] = new_re
            wout_ref[1, :, blk(a)] = new_im
            for j in range(strip_count):
                img_ref[j, k, :, blk(a)] = new_re[j * rows_here:(j + 1) * rows_here]
        return carry

    lax.fori_loop(0, steps, one_step, 0)


def fast_constants(line_len):
    outer = line_len // LANE
    b = np.arange(LANE)
    ang = 2.0 * np.pi * (np.outer(b, b) % LANE) / LANE
    cos_m, sin_m = (np.cos(ang), np.sin(ang))
    fwd = np.block([[cos_m, -sin_m], [sin_m, cos_m]])
    inv = np.block([[cos_m, sin_m], [-sin_m, cos_m]])

    def halves(m):
        hi = m.astype(ml_dtypes.bfloat16)
        lo = (m - hi.astype(np.float64)).astype(ml_dtypes.bfloat16)
        return (hi, lo)

    c = np.arange(outer)
    tw_ang = 2.0 * np.pi * np.outer(c, b) / line_len
    twiddle = np.stack([np.cos(tw_ang), np.sin(tw_ang)]).astype(np.float32)
    q = c[:, None] + outer * b[None, :]
    signed = np.where(q >= line_len // 2, q - line_len, q).astype(np.float32)
    kx_cd = signed * np.float32(2.0 * math.pi / line_len)
    return (halves(fwd), halves(inv), twiddle, kx_cd.astype(np.float32))


def run_section(wave, regions, table, mult, consts, strip_count):
    (fhi, flo), (ghi, glo), twiddle, _ = consts
    rows, line_len = wave.shape[1], wave.shape[2]
    steps = regions.shape[0]
    table_len = table.shape[0] // (3 * steps)
    vmem = pl.BlockSpec(memory_space=pltpu.VMEM)
    flops = steps * (2 * 3 * 2 * (FFT_BLOCKS * rows) * 256 * 256 + 400 * rows * line_len)
    return pl.pallas_call(
        lambda *refs: section_kernel(*refs, table_len=table_len),
        out_shape=(
            jax.ShapeDtypeStruct(wave.shape, jnp.float32),
            jax.ShapeDtypeStruct((strip_count, steps, rows // strip_count, line_len), jnp.float32),
        ),
        in_specs=[pl.BlockSpec(memory_space=pltpu.SMEM)] + [vmem] * 8,
        out_specs=(vmem, vmem),
        scratch_shapes=[
            pltpu.VMEM((FFT_BLOCKS * rows, 2 * LANE), jnp.float32),
            pltpu.VMEM((FFT_BLOCKS * rows, 2 * LANE), jnp.float32),
            pltpu.VMEM((2, rows, line_len), jnp.float32),
        ],
        cost_estimate=pl.CostEstimate(
            flops=flops, transcendentals=0, bytes_accessed=4 * rows * line_len * 6 * steps
        ),
    )(table, wave, regions, mult, jnp.asarray(twiddle), jnp.asarray(fhi), jnp.asarray(flo),
      jnp.asarray(ghi), jnp.asarray(glo))


def section_tables(omega, region_speed, fd_coeff, ref_region, kx_cd):
    inv_speed = 1.0 / region_speed
    ref_slow = inv_speed[ref_region]
    regions = region_speed.shape[0]
    padded = 1 << max(1, (regions - 1).bit_length())
    extra = padded - regions
    phase = omega * (inv_speed[None, :] - ref_slow[:, None])
    gain = jnp.broadcast_to(fd_coeff / omega, phase.shape)
    parts = [jnp.cos(phase), jnp.sin(phase), gain]
    if extra:
        parts = [jnp.concatenate([p, jnp.repeat(p[:, -1:], extra, axis=1)], axis=1) for p in parts]
    table = jnp.stack(parts, axis=1).reshape(-1)
    wave_ref = omega * ref_slow
    wave_ref = wave_ref[:, None, None]
    excess = wave_ref * wave_ref - kx_cd * kx_cd
    decay_line = jnp.exp(-jnp.sqrt(jnp.maximum(-excess, 0.0)))
    vertical = jnp.sqrt(jnp.maximum(excess, 0.0))
    mult = jnp.stack([decay_line * jnp.cos(vertical), decay_line * jnp.sin(vertical)], axis=1)
    return (table, mult)


def fast_fits(surface, region_index, region_speed):
    freq_count = surface.shape[1]
    rows = surface.shape[2] * lax.axis_size("strip")
    line_len = surface.shape[3]
    return (
        freq_count == lax.axis_size("strip")
        and line_len == FFT_BLOCKS * LANE
        and rows % ROW_CHUNK == 0
        and surface.shape[2] % ROW_CHUNK == 0
        and rows <= 64
        and region_speed.shape[0] <= 16
    )


def strip_pairs(depths, strip_count, shift):
    return [
        (d * strip_count + r, d * strip_count + (r + shift) % strip_count)
        for d in depths
        for r in range(strip_count)
    ]


def gather_rows(local, depths, strip_no, strip_count, row_axis):
    rows = local.shape[row_axis]
    shape = list(local.shape)
    shape[row_axis] = rows * strip_count
    full = jnp.zeros(shape, local.dtype)
    start = [0] * len(shape)
    start[row_axis] = strip_no * rows
    full = lax.dynamic_update_slice(full, local, start)
    for shift in range(1, strip_count):
        got = lax.ppermute(local, ("depth", "strip"), strip_pairs(depths, strip_count, shift))
        start = [0] * len(shape)
        start[row_axis] = ((strip_no - shift) % strip_count) * rows
        full = lax.dynamic_update_slice(full, got, start)
    return full


def gather_strips(piece_of, local, depths, strip_no, strip_count, rows_here):
    rows = rows_here * strip_count
    shape = (local.shape[0], rows, local.shape[2])
    full = lax.dynamic_update_slice(
        jnp.zeros(shape, jnp.float32), local, (0, strip_no * rows_here, 0)
    )
    for shift in range(1, strip_count):
        target = (strip_no + shift) % strip_count
        got = lax.ppermute(
            piece_of(target), ("depth", "strip"), strip_pairs(depths, strip_count, shift)
        )
        source = (strip_no - shift) % strip_count
        full = lax.dynamic_update_slice(full, got, (0, source * rows_here, 0))
    return full


def shards(surface, omegas, region_speed, fd_coeff, region_index, ref_region):
    if not fast_fits(surface, region_index, region_speed):
        return shards_general(surface, omegas, region_speed, fd_coeff, region_index, ref_region)
    line_len = surface.shape[3]
    rows_here = surface.shape[2]
    steps = region_index.shape[0]
    segment_no = lax.axis_index("depth")
    segment_count = lax.axis_size("depth")
    strip_no = lax.axis_index("strip")
    strip_count = lax.axis_size("strip")
    consts = fast_constants(line_len)
    region_f = region_index.astype(jnp.float32)
    early = [d for d in range(segment_count) if d != 1]

    def with_surface(target):
        return jnp.concatenate(
            [region_f, lax.dynamic_index_in_dim(surface, target, 1, keepdims=False)], axis=0
        )

    gathered = gather_strips(
        with_surface, with_surface(strip_no), early, strip_no, strip_count, rows_here
    )
    regions_a = gathered[:steps].astype(jnp.int32)
    wave = gathered[steps:]
    omega = lax.dynamic_index_in_dim(omegas, strip_no, 0, keepdims=False)
    table, mult = section_tables(omega, region_speed, fd_coeff, ref_region, jnp.asarray(consts[3]))
    image = jnp.zeros((strip_count, steps, rows_here, line_len), jnp.float32)
    regions_b = regions_a
    if segment_count > 1:
        token = lax.ppermute(gathered[0, 0:8, 0:LANE], "depth", [(0, 1)])

    def sweep(regions):
        def live(wave, image):
            return run_section(wave, regions, table, mult, consts, strip_count)

        return live

    def idle(wave, image):
        return (wave, image)

    def freq_sum(image, depths):
        parts = []
        for shift in range(1, strip_count):
            target = (strip_no + shift) % strip_count
            piece = lax.dynamic_index_in_dim(image, target, 0, keepdims=False)
            parts.append(
                lax.ppermute(piece, ("depth", "strip"), strip_pairs(depths, strip_count, shift))
            )
        return parts

    arrived = []
    for tick_no in range(segment_count):
        regions = regions_b if tick_no == 1 else regions_a
        wave, image = lax.cond(segment_no == tick_no, sweep(regions), idle, wave, image)
        if tick_no + 1 < segment_count:
            wave = lax.ppermute(wave, "depth", [(tick_no, tick_no + 1)])
        if tick_no == 0 and segment_count > 1:
            held, token, _ = lax.optimization_barrier((region_f, token, image))
            held = held + 0.0 * token[0, 0]
            regions_b = gather_strips(
                lambda target: held, held, [1], strip_no, strip_count, rows_here
            ).astype(jnp.int32)
        if tick_no == segment_count - 2:
            wave, image = lax.optimization_barrier((wave, image))
            arrived += freq_sum(image, range(segment_count - 1))
    arrived += freq_sum(image, [segment_count - 1])
    total = lax.dynamic_index_in_dim(image, strip_no, 0, keepdims=False)
    for piece in arrived:
        total = total + piece
    return total


def solution(mesh):
    in_specs = (
        P(None, "shots", "strip", None),
        P(),
        P(),
        P(),
        P("depth", "strip", None),
        P("depth"),
    )
    out_specs = P("depth", "strip", "shots")
    return jax.shard_map(shards, mesh=mesh, in_specs=in_specs, out_specs=out_specs, check_vma=False)
```

```python
import math

import ml_dtypes
import numpy as np
import jax
import jax.numpy as jnp
from jax import lax
from jax.experimental import pallas as pl
from jax.experimental.pallas import tpu as pltpu
from jax.sharding import PartitionSpec as P

DAMPING = 0.05
PRECISE = lax.Precision.HIGHEST


def padded_2(cells, sides, width):
    for axis, dim in sides:
        count = lax.axis_size(axis)
        ends = count - 1
        head = lax.slice_in_dim(cells, 0, width, axis=dim)
        tail = lax.slice_in_dim(cells, cells.shape[dim] - width, cells.shape[dim], axis=dim)
        cells = jnp.concatenate(
            [
                lax.ppermute(tail, axis, [(i, (i + 1) % count) for i in range(ends)]),
                cells,
                lax.ppermute(head, axis, [((i + 1) % count, i) for i in range(ends)]),
            ],
            axis=dim,
        )
    return cells


def from_behind(value, axis, steps):
    count = lax.axis_size(axis)
    first, last = (max(0, -steps), min(count, count - steps))
    return lax.ppermute(value, axis, [(source, source + steps) for source in range(first, last)])


def complex_scale(values, cosine, sine_part):
    return jnp.stack(
        [values[0] * cosine - values[1] * sine_part, values[0] * sine_part + values[1] * cosine]
    )


def angle_pair(numerator, period):
    angle_grid = numerator.astype(jnp.float32) * (2.0 * math.pi / period)
    return (jnp.cos(angle_grid), jnp.sin(angle_grid))


def block_matrix(cosine, sine_part, forward):
    sign_flip = 1.0 if forward else -1.0
    return jnp.stack(
        [jnp.stack([cosine, -sign_flip * sine_part]), jnp.stack([sign_flip * sine_part, cosine])]
    )


def build_tables(line_len):
    block_len = 128
    outer_len = line_len // block_len
    inner_idx = jnp.arange(block_len)
    outer_idx = jnp.arange(outer_len)
    cos_large, sin_large = angle_pair(
        inner_idx[:, None] * inner_idx[None, :] % block_len, block_len
    )
    cos_small, sin_small = angle_pair(
        outer_idx[:, None] * outer_idx[None, :] % outer_len, outer_len
    )
    cos_twist, sin_twist = angle_pair(outer_idx[:, None] * inner_idx[None, :], line_len)
    wave_index = outer_idx[:, None] + outer_len * inner_idx[None, :]
    signed = jnp.where(wave_index >= line_len // 2, wave_index - line_len, wave_index)
    kx_grid = signed.astype(jnp.float32) * (2.0 * math.pi / line_len)
    small_fwd = block_matrix(cos_small, sin_small, True)
    small_inv = block_matrix(cos_small, sin_small, False)
    large_fwd = block_matrix(cos_large, sin_large, True)
    large_inv = block_matrix(cos_large, sin_large, False)
    return (small_fwd, small_inv, large_fwd, large_inv, cos_twist, sin_twist, kx_grid)


def forward_line(wavefield, tables):
    small_fwd, small_inv, large_fwd, large_inv, cos_twist, sin_twist, kx_grid = tables
    row_count = wavefield.shape[1]
    pieces = wavefield.reshape(2, row_count, cos_twist.shape[0], cos_twist.shape[1])
    mixed_part = jnp.einsum("zrab,zwca->wrcb", pieces, small_fwd, precision=PRECISE)
    mixed_part = complex_scale(mixed_part, cos_twist, -sin_twist)
    return jnp.einsum("zrcb,zwbd->wrcd", mixed_part, large_fwd, precision=PRECISE)


def inverse_line(spectrum, tables):
    small_fwd, small_inv, large_fwd, large_inv, cos_twist, sin_twist, kx_grid = tables
    row_count = spectrum.shape[1]
    line_len = cos_twist.shape[0] * cos_twist.shape[1]
    mixed_part = jnp.einsum("zrcd,zwdb->wrcb", spectrum, large_inv, precision=PRECISE)
    mixed_part = complex_scale(mixed_part, cos_twist, sin_twist)
    pieces = jnp.einsum("zrcb,zwca->wrab", mixed_part, small_inv, precision=PRECISE)
    return pieces.reshape(2, row_count, line_len) * (1.0 / line_len)


def lookup(regions, entries):
    picked = jnp.zeros(regions.shape, jnp.float32)
    for region_no in range(entries.shape[0]):
        picked = picked + jnp.where(regions == region_no, entries[region_no], 0.0)
    return picked


def depth_step(wavefield, omega_now, slow_cells, coef_cells, ref_slow, tables, pad_rows):
    kx_grid = tables[6]
    wave_ref = omega_now * ref_slow
    excess = wave_ref * wave_ref - kx_grid * kx_grid
    decay_line = jnp.exp(-jnp.sqrt(jnp.maximum(-excess, 0.0)))
    vertical = jnp.sqrt(jnp.maximum(excess, 0.0))
    spectrum = complex_scale(
        forward_line(wavefield, tables),
        decay_line * jnp.cos(vertical),
        decay_line * jnp.sin(vertical),
    )
    wavefield = inverse_line(spectrum, tables)
    phase_cell = omega_now * (slow_cells - ref_slow)
    wavefield = complex_scale(wavefield, jnp.cos(phase_cell), jnp.sin(phase_cell))
    padded = pad_rows(wavefield)
    laplace = (
        padded[:, :-2]
        + padded[:, 2:]
        + jnp.roll(wavefield, 1, 2)
        + jnp.roll(wavefield, -1, 2)
        - 4.0 * wavefield
    )
    return wavefield + complex_scale(laplace, DAMPING, coef_cells / omega_now)


def march(wavefield, omega_now, slow_block, coef_block, ref_block, tables, pad_rows):
    traces = []
    for step_no in range(slow_block.shape[0]):
        wavefield = depth_step(
            wavefield,
            omega_now,
            slow_block[step_no],
            coef_block[step_no],
            ref_block[step_no],
            tables,
            pad_rows,
        )
        traces.append(wavefield[0])
    return (wavefield, jnp.stack(traces))


def shards_general(surface, omegas, region_speed, fd_coeff, region_index, ref_region):
    line_len = surface.shape[3]
    rows_here = surface.shape[2]
    freq_count = surface.shape[1]
    step_count = region_index.shape[0]
    tables = build_tables(line_len)
    inv_speed = 1.0 / region_speed
    segment_no = lax.axis_index("depth")
    segment_count = lax.axis_size("depth")

    def pad_near(values):
        return padded_2(values, (("strip", 1),), 1)

    slow_cells = lookup(region_index, inv_speed)
    coef_cells = lookup(region_index, fd_coeff)
    ref_cells = lookup(ref_region, inv_speed)
    freq_index = jnp.arange(freq_count)
    image_out = jnp.zeros((step_count, rows_here, line_len), jnp.float32)
    arriving = jnp.zeros((2, rows_here, line_len), jnp.float32)
    tick_count = freq_count + segment_count - 1
    for tick_no in range(tick_count):
        batch_no = tick_no - segment_no
        is_live = (batch_no >= 0) & (batch_no < freq_count)
        clipped = jnp.clip(batch_no, 0, freq_count - 1)
        picked = lax.dynamic_index_in_dim(surface, clipped, 1, keepdims=False)
        entering = jnp.where(segment_no == 0, picked, arriving)
        omega_now = jnp.sum(jnp.where(freq_index == clipped, omegas, 0.0))
        leaving, traces = march(
            entering, omega_now, slow_cells, coef_cells, ref_cells, tables, pad_near
        )
        image_out = image_out + jnp.where(is_live, traces, 0.0)
        if tick_no + 1 < tick_count:
            arriving = from_behind(leaving, "depth", 1)
    return image_out


LANE = 128
FFT_BLOCKS = 16
ROW_CHUNK = 8


def fft4(x0, x1, x2, x3, sign):
    s0 = (x0[0] + x2[0], x0[1] + x2[1])
    d0 = (x0[0] - x2[0], x0[1] - x2[1])
    s1 = (x1[0] + x3[0], x1[1] + x3[1])
    d1 = (x1[0] - x3[0], x1[1] - x3[1])
    if sign < 0:
        wd = (d1[1], -d1[0])
    else:
        wd = (-d1[1], d1[0])
    return (
        (s0[0] + s1[0], s0[1] + s1[1]),
        (d0[0] + wd[0], d0[1] + wd[1]),
        (s0[0] - s1[0], s0[1] - s1[1]),
        (d0[0] - wd[0], d0[1] - wd[1]),
    )


def turn_const(value, power, sign):
    if power == 4:
        return (-value[1], value[0]) if sign > 0 else (value[1], -value[0])
    angle = sign * 2.0 * math.pi * power / 16.0
    cr, ci = (math.cos(angle), math.sin(angle))
    return (value[0] * cr - value[1] * ci, value[0] * ci + value[1] * cr)


def fft16(parts, sign):
    mid = [[None] * 4 for _ in range(4)]
    for a0 in range(4):
        ys = fft4(parts[a0], parts[4 + a0], parts[8 + a0], parts[12 + a0], sign)
        for c0 in range(4):
            power = a0 * c0
            mid[a0][c0] = ys[c0] if power == 0 else turn_const(ys[c0], power, sign)
    out = [None] * 16
    for c0 in range(4):
        zs = fft4(mid[0][c0], mid[1][c0], mid[2][c0], mid[3][c0], sign)
        for c1 in range(4):
            out[c0 + 4 * c1] = zs[c1]
    return out


def pick(regions, values):
    level = list(values)
    bit = 1
    while len(level) > 1:
        chosen = (regions & bit) != 0
        level = [jnp.where(chosen, level[i + 1], level[i]) for i in range(0, len(level), 2)]
        bit *= 2
    return jnp.broadcast_to(level[0], regions.shape)


def split_dot(values, hi_ref, lo_ref):
    high = values.astype(jnp.bfloat16)
    low = (values - high.astype(jnp.float32)).astype(jnp.bfloat16)
    main = jnp.dot(high, hi_ref[...], preferred_element_type=jnp.float32)
    fix = jnp.dot(high, lo_ref[...], preferred_element_type=jnp.float32) + jnp.dot(
        low, hi_ref[:, :], preferred_element_type=jnp.float32
    )
    return main + fix


def section_kernel(
    tab_ref, w_ref, rid_ref, mult_ref, tw_ref, fhi_ref, flo_ref, ghi_ref, glo_ref,
    wout_ref, img_ref, a_ref, y_ref, v_ref, *, table_len
):
    rows = w_ref.shape[1]
    line_len = w_ref.shape[2]
    steps = rid_ref.shape[0]
    strip_count, rows_here = img_ref.shape[0], img_ref.shape[2]
    chunks = rows // ROW_CHUNK
    inv_len = 1.0 / line_len
    pltpu.sync_copy(w_ref, wout_ref)

    def blk(a):
        return slice(a * LANE, (a + 1) * LANE)

    def one_step(k, carry):
        base = k * (3 * table_len)
        cos_t = [tab_ref[base + g] for g in range(table_len)]
        sin_t = [tab_ref[base + table_len + g] for g in range(table_len)]
        gain_t = [tab_ref[base + 2 * table_len + g] for g in range(table_len)]

        def forward_chunk(i, c):
            y0 = pl.multiple_of(i * ROW_CHUNK, ROW_CHUNK)
            parts = [
                (wout_ref[0, pl.ds(y0, ROW_CHUNK), blk(a)], wout_ref[1, pl.ds(y0, ROW_CHUNK), blk(a)])
                for a in range(FFT_BLOCKS)
            ]
            spec = fft16(parts, -1)
            for cc in range(FFT_BLOCKS):
                tc = tw_ref[0, cc:cc + 1, :]
                ts = tw_ref[1, cc:cc + 1, :]
                xr, xi = spec[cc]
                a_ref[pl.ds(cc * rows + y0, ROW_CHUNK), 0:LANE] = xr * tc + xi * ts
                a_ref[pl.ds(cc * rows + y0, ROW_CHUNK), LANE:2 * LANE] = xi * tc - xr * ts
            return c

        lax.fori_loop(0, chunks, forward_chunk, 0)
        y_ref[...] = split_dot(a_ref[...], fhi_ref, flo_ref)
        for cc in range(FFT_BLOCKS):
            band = slice(cc * rows, (cc + 1) * rows)
            yr = y_ref[band, 0:LANE]
            yi = y_ref[band, LANE:2 * LANE]
            mr = mult_ref[k, 0, cc:cc + 1, :]
            mi = mult_ref[k, 1, cc:cc + 1, :]
            a_ref[band, 0:LANE] = yr * mr - yi * mi
            a_ref[band, LANE:2 * LANE] = yr * mi + yi * mr
        y_ref[...] = split_dot(a_ref[...], ghi_ref, glo_ref)

        def inverse_chunk(i, c):
            y0 = pl.multiple_of(i * ROW_CHUNK, ROW_CHUNK)
            parts = []
            for cc in range(FFT_BLOCKS):
                zr = y_ref[pl.ds(cc * rows + y0, ROW_CHUNK), 0:LANE]
                zi = y_ref[pl.ds(cc * rows + y0, ROW_CHUNK), LANE:2 * LANE]
                tc = tw_ref[0, cc:cc + 1, :]
                ts = tw_ref[1, cc:cc + 1, :]
                parts.append((zr * tc - zi * ts, zr * ts + zi * tc))
            back = fft16(parts, 1)
            for a in range(FFT_BLOCKS):
                ur = back[a][0] * inv_len
                ui = back[a][1] * inv_len
                regions = rid_ref[k, pl.ds(y0, ROW_CHUNK), blk(a)].astype(jnp.int32)
                cs = pick(regions, cos_t)
                sn = pick(regions, sin_t)
                v_ref[0, pl.ds(y0, ROW_CHUNK), blk(a)] = ur * cs - ui * sn
                v_ref[1, pl.ds(y0, ROW_CHUNK), blk(a)] = ur * sn + ui * cs
            return c

        lax.fori_loop(0, chunks, inverse_chunk, 0)
        row_id = lax.broadcasted_iota(jnp.int32, (rows, LANE), 0)
        lane_id = lax.broadcasted_iota(jnp.int32, (rows, LANE), 1)
        for a in range(FFT_BLOCKS):
            prev_b = blk((a - 1) % FFT_BLOCKS)
            next_b = blk((a + 1) % FFT_BLOCKS)
            lap = []
            here = []
            for part in range(2):
                v = v_ref[part, :, blk(a)]
                vp = v_ref[part, :, prev_b]
                vn = v_ref[part, :, next_b]
                above = jnp.where(row_id == 0, 0.0, pltpu.roll(v, 1, 0))
                below = jnp.where(row_id == rows - 1, 0.0, pltpu.roll(v, rows - 1, 0))
                left = jnp.where(lane_id == 0, pltpu.roll(vp, 1, 1), pltpu.roll(v, 1, 1))
                right = jnp.where(
                    lane_id == LANE - 1, pltpu.roll(vn, LANE - 1, 1), pltpu.roll(v, LANE - 1, 1)
                )
                lap.append(above + below + left + right - 4.0 * v)
                here.append(v)
            gain = pick(rid_ref[k, :, blk(a)].astype(jnp.int32), gain_t)
            new_re = here[0] + (lap[0] * DAMPING - lap[1] * gain)
            new_im = here[1] + (lap[0] * gain + lap[1] * DAMPING)
            wout_ref[0, :, blk(a)] = new_re
            wout_ref[1, :, blk(a)] = new_im
            for j in range(strip_count):
                img_ref[j, k, :, blk(a)] = new_re[j * rows_here:(j + 1) * rows_here]
        return carry

    lax.fori_loop(0, steps, one_step, 0)


def fast_constants(line_len):
    outer = line_len // LANE
    b = np.arange(LANE)
    ang = 2.0 * np.pi * (np.outer(b, b) % LANE) / LANE
    cos_m, sin_m = (np.cos(ang), np.sin(ang))
    fwd = np.block([[cos_m, -sin_m], [sin_m, cos_m]])
    inv = np.block([[cos_m, sin_m], [-sin_m, cos_m]])

    def halves(m):
        hi = m.astype(ml_dtypes.bfloat16)
        lo = (m - hi.astype(np.float64)).astype(ml_dtypes.bfloat16)
        return (hi, lo)

    c = np.arange(outer)
    tw_ang = 2.0 * np.pi * np.outer(c, b) / line_len
    twiddle = np.stack([np.cos(tw_ang), np.sin(tw_ang)]).astype(np.float32)
    q = c[:, None] + outer * b[None, :]
    signed = np.where(q >= line_len // 2, q - line_len, q).astype(np.float32)
    kx_cd = signed * np.float32(2.0 * math.pi / line_len)
    return (halves(fwd), halves(inv), twiddle, kx_cd.astype(np.float32))


def run_section(wave, regions, table, mult, consts, strip_count):
    (fhi, flo), (ghi, glo), twiddle, _ = consts
    rows, line_len = wave.shape[1], wave.shape[2]
    steps = regions.shape[0]
    table_len = table.shape[0] // (3 * steps)
    vmem = pl.BlockSpec(memory_space=pltpu.VMEM)
    flops = steps * (2 * 3 * 2 * (FFT_BLOCKS * rows) * 256 * 256 + 400 * rows * line_len)
    return pl.pallas_call(
        lambda *refs: section_kernel(*refs, table_len=table_len),
        out_shape=(
            jax.ShapeDtypeStruct(wave.shape, jnp.float32),
            jax.ShapeDtypeStruct((strip_count, steps, rows // strip_count, line_len), jnp.float32),
        ),
        in_specs=[pl.BlockSpec(memory_space=pltpu.SMEM), pl.BlockSpec(memory_space=pl.ANY)]
        + [vmem] * 7,
        out_specs=(vmem, vmem),
        scratch_shapes=[
            pltpu.VMEM((FFT_BLOCKS * rows, 2 * LANE), jnp.float32),
            pltpu.VMEM((FFT_BLOCKS * rows, 2 * LANE), jnp.float32),
            pltpu.VMEM((2, rows, line_len), jnp.float32),
        ],
        cost_estimate=pl.CostEstimate(
            flops=flops, transcendentals=0, bytes_accessed=4 * rows * line_len * 6 * steps
        ),
    )(table, wave, regions, mult, jnp.asarray(twiddle), jnp.asarray(fhi), jnp.asarray(flo),
      jnp.asarray(ghi), jnp.asarray(glo))


def section_tables(omega, region_speed, fd_coeff, ref_region, kx_cd):
    inv_speed = 1.0 / region_speed
    ref_slow = inv_speed[ref_region]
    regions = region_speed.shape[0]
    padded = 1 << max(1, (regions - 1).bit_length())
    extra = padded - regions
    phase = omega * (inv_speed[None, :] - ref_slow[:, None])
    gain = jnp.broadcast_to(fd_coeff / omega, phase.shape)
    parts = [jnp.cos(phase), jnp.sin(phase), gain]
    if extra:
        parts = [jnp.concatenate([p, jnp.repeat(p[:, -1:], extra, axis=1)], axis=1) for p in parts]
    table = jnp.stack(parts, axis=1).reshape(-1)
    wave_ref = omega * ref_slow
    wave_ref = wave_ref[:, None, None]
    excess = wave_ref * wave_ref - kx_cd * kx_cd
    decay_line = jnp.exp(-jnp.sqrt(jnp.maximum(-excess, 0.0)))
    vertical = jnp.sqrt(jnp.maximum(excess, 0.0))
    mult = jnp.stack([decay_line * jnp.cos(vertical), decay_line * jnp.sin(vertical)], axis=1)
    return (table, mult)


def fast_fits(surface, region_index, region_speed):
    freq_count = surface.shape[1]
    rows = surface.shape[2] * lax.axis_size("strip")
    line_len = surface.shape[3]
    return (
        freq_count == lax.axis_size("strip")
        and line_len == FFT_BLOCKS * LANE
        and rows % ROW_CHUNK == 0
        and surface.shape[2] % ROW_CHUNK == 0
        and rows <= 64
        and region_speed.shape[0] <= 16
    )


def strip_pairs(depths, strip_count, shift):
    return [
        (d * strip_count + r, d * strip_count + (r + shift) % strip_count)
        for d in depths
        for r in range(strip_count)
    ]


def gather_rows(local, depths, strip_no, strip_count, row_axis):
    rows = local.shape[row_axis]
    shape = list(local.shape)
    shape[row_axis] = rows * strip_count
    full = jnp.zeros(shape, local.dtype)
    start = [0] * len(shape)
    start[row_axis] = strip_no * rows
    full = lax.dynamic_update_slice(full, local, start)
    for shift in range(1, strip_count):
        got = lax.ppermute(local, ("depth", "strip"), strip_pairs(depths, strip_count, shift))
        start = [0] * len(shape)
        start[row_axis] = ((strip_no - shift) % strip_count) * rows
        full = lax.dynamic_update_slice(full, got, start)
    return full


def gather_strips(piece_of, local, depths, strip_no, strip_count, rows_here):
    rows = rows_here * strip_count
    shape = (local.shape[0], rows, local.shape[2])
    full = lax.dynamic_update_slice(
        jnp.zeros(shape, jnp.float32), local, (0, strip_no * rows_here, 0)
    )
    for shift in range(1, strip_count):
        target = (strip_no + shift) % strip_count
        got = lax.ppermute(
            piece_of(target), ("depth", "strip"), strip_pairs(depths, strip_count, shift)
        )
        source = (strip_no - shift) % strip_count
        full = lax.dynamic_update_slice(full, got, (0, source * rows_here, 0))
    return full


def shards(surface, omegas, region_speed, fd_coeff, region_index, ref_region):
    if not fast_fits(surface, region_index, region_speed):
        return shards_general(surface, omegas, region_speed, fd_coeff, region_index, ref_region)
    line_len = surface.shape[3]
    rows_here = surface.shape[2]
    steps = region_index.shape[0]
    segment_no = lax.axis_index("depth")
    segment_count = lax.axis_size("depth")
    strip_no = lax.axis_index("strip")
    strip_count = lax.axis_size("strip")
    consts = fast_constants(line_len)
    region_f = region_index.astype(jnp.float32)
    early = [d for d in range(segment_count) if d != 1]

    def with_surface(target):
        return jnp.concatenate(
            [region_f, lax.dynamic_index_in_dim(surface, target, 1, keepdims=False)], axis=0
        )

    gathered = gather_strips(
        with_surface, with_surface(strip_no), early, strip_no, strip_count, rows_here
    )
    regions_a = gathered[:steps]
    wave = gathered[steps:]
    omega = lax.dynamic_index_in_dim(omegas, strip_no, 0, keepdims=False)
    table, mult = section_tables(omega, region_speed, fd_coeff, ref_region, jnp.asarray(consts[3]))
    image = jnp.zeros((strip_count, steps, rows_here, line_len), jnp.float32)
    regions_b = regions_a
    if segment_count > 1:
        token = lax.ppermute(gathered[0, 0:8, 0:LANE], "depth", [(0, 1)])

    def sweep(regions):
        def live(wave, image):
            return run_section(wave, regions, table, mult, consts, strip_count)

        return live

    def idle(wave, image):
        return (wave, image)

    def freq_sum(image, depths):
        parts = []
        for shift in range(1, strip_count):
            target = (strip_no + shift) % strip_count
            piece = lax.dynamic_index_in_dim(image, target, 0, keepdims=False)
            parts.append(
                lax.ppermute(piece, ("depth", "strip"), strip_pairs(depths, strip_count, shift))
            )
        return parts

    arrived = []
    for tick_no in range(segment_count):
        regions = regions_b if tick_no == 1 else regions_a
        wave, image = lax.cond(segment_no == tick_no, sweep(regions), idle, wave, image)
        if tick_no + 1 < segment_count:
            wave = lax.ppermute(wave, "depth", [(tick_no, tick_no + 1)])
        if tick_no == 0 and segment_count > 1:
            held, token, _ = lax.optimization_barrier((region_f, token, image))
            held = held + 0.0 * token[0, 0]
            regions_b = gather_strips(
                lambda target: held, held, [1], strip_no, strip_count, rows_here
            )
        if tick_no == segment_count - 2:
            wave, image = lax.optimization_barrier((wave, image))
            arrived += freq_sum(image, range(segment_count - 1))
    arrived += freq_sum(image, [segment_count - 1])
    total = lax.dynamic_index_in_dim(image, strip_no, 0, keepdims=False)
    for piece in arrived:
        total = total + piece
    return total


def solution(mesh):
    in_specs = (
        P(None, "shots", "strip", None),
        P(),
        P(),
        P(),
        P("depth", "strip", None),
        P("depth"),
    )
    out_specs = P("depth", "strip", "shots")
    return jax.shard_map(shards, mesh=mesh, in_specs=in_specs, out_specs=out_specs, check_vma=False)
```

```python
import math

import ml_dtypes
import numpy as np
import jax
import jax.numpy as jnp
from jax import lax
from jax.experimental import pallas as pl
from jax.experimental.pallas import tpu as pltpu
from jax.sharding import PartitionSpec as P

DAMPING = 0.05
PRECISE = lax.Precision.HIGHEST


def padded_2(cells, sides, width):
    for axis, dim in sides:
        count = lax.axis_size(axis)
        ends = count - 1
        head = lax.slice_in_dim(cells, 0, width, axis=dim)
        tail = lax.slice_in_dim(cells, cells.shape[dim] - width, cells.shape[dim], axis=dim)
        cells = jnp.concatenate(
            [
                lax.ppermute(tail, axis, [(i, (i + 1) % count) for i in range(ends)]),
                cells,
                lax.ppermute(head, axis, [((i + 1) % count, i) for i in range(ends)]),
            ],
            axis=dim,
        )
    return cells


def from_behind(value, axis, steps):
    count = lax.axis_size(axis)
    first, last = (max(0, -steps), min(count, count - steps))
    return lax.ppermute(value, axis, [(source, source + steps) for source in range(first, last)])


def complex_scale(values, cosine, sine_part):
    return jnp.stack(
        [values[0] * cosine - values[1] * sine_part, values[0] * sine_part + values[1] * cosine]
    )


def angle_pair(numerator, period):
    angle_grid = numerator.astype(jnp.float32) * (2.0 * math.pi / period)
    return (jnp.cos(angle_grid), jnp.sin(angle_grid))


def block_matrix(cosine, sine_part, forward):
    sign_flip = 1.0 if forward else -1.0
    return jnp.stack(
        [jnp.stack([cosine, -sign_flip * sine_part]), jnp.stack([sign_flip * sine_part, cosine])]
    )


def build_tables(line_len):
    block_len = 128
    outer_len = line_len // block_len
    inner_idx = jnp.arange(block_len)
    outer_idx = jnp.arange(outer_len)
    cos_large, sin_large = angle_pair(
        inner_idx[:, None] * inner_idx[None, :] % block_len, block_len
    )
    cos_small, sin_small = angle_pair(
        outer_idx[:, None] * outer_idx[None, :] % outer_len, outer_len
    )
    cos_twist, sin_twist = angle_pair(outer_idx[:, None] * inner_idx[None, :], line_len)
    wave_index = outer_idx[:, None] + outer_len * inner_idx[None, :]
    signed = jnp.where(wave_index >= line_len // 2, wave_index - line_len, wave_index)
    kx_grid = signed.astype(jnp.float32) * (2.0 * math.pi / line_len)
    small_fwd = block_matrix(cos_small, sin_small, True)
    small_inv = block_matrix(cos_small, sin_small, False)
    large_fwd = block_matrix(cos_large, sin_large, True)
    large_inv = block_matrix(cos_large, sin_large, False)
    return (small_fwd, small_inv, large_fwd, large_inv, cos_twist, sin_twist, kx_grid)


def forward_line(wavefield, tables):
    small_fwd, small_inv, large_fwd, large_inv, cos_twist, sin_twist, kx_grid = tables
    row_count = wavefield.shape[1]
    pieces = wavefield.reshape(2, row_count, cos_twist.shape[0], cos_twist.shape[1])
    mixed_part = jnp.einsum("zrab,zwca->wrcb", pieces, small_fwd, precision=PRECISE)
    mixed_part = complex_scale(mixed_part, cos_twist, -sin_twist)
    return jnp.einsum("zrcb,zwbd->wrcd", mixed_part, large_fwd, precision=PRECISE)


def inverse_line(spectrum, tables):
    small_fwd, small_inv, large_fwd, large_inv, cos_twist, sin_twist, kx_grid = tables
    row_count = spectrum.shape[1]
    line_len = cos_twist.shape[0] * cos_twist.shape[1]
    mixed_part = jnp.einsum("zrcd,zwdb->wrcb", spectrum, large_inv, precision=PRECISE)
    mixed_part = complex_scale(mixed_part, cos_twist, sin_twist)
    pieces = jnp.einsum("zrcb,zwca->wrab", mixed_part, small_inv, precision=PRECISE)
    return pieces.reshape(2, row_count, line_len) * (1.0 / line_len)


def lookup(regions, entries):
    picked = jnp.zeros(regions.shape, jnp.float32)
    for region_no in range(entries.shape[0]):
        picked = picked + jnp.where(regions == region_no, entries[region_no], 0.0)
    return picked


def depth_step(wavefield, omega_now, slow_cells, coef_cells, ref_slow, tables, pad_rows):
    kx_grid = tables[6]
    wave_ref = omega_now * ref_slow
    excess = wave_ref * wave_ref - kx_grid * kx_grid
    decay_line = jnp.exp(-jnp.sqrt(jnp.maximum(-excess, 0.0)))
    vertical = jnp.sqrt(jnp.maximum(excess, 0.0))
    spectrum = complex_scale(
        forward_line(wavefield, tables),
        decay_line * jnp.cos(vertical),
        decay_line * jnp.sin(vertical),
    )
    wavefield = inverse_line(spectrum, tables)
    phase_cell = omega_now * (slow_cells - ref_slow)
    wavefield = complex_scale(wavefield, jnp.cos(phase_cell), jnp.sin(phase_cell))
    padded = pad_rows(wavefield)
    laplace = (
        padded[:, :-2]
        + padded[:, 2:]
        + jnp.roll(wavefield, 1, 2)
        + jnp.roll(wavefield, -1, 2)
        - 4.0 * wavefield
    )
    return wavefield + complex_scale(laplace, DAMPING, coef_cells / omega_now)


def march(wavefield, omega_now, slow_block, coef_block, ref_block, tables, pad_rows):
    traces = []
    for step_no in range(slow_block.shape[0]):
        wavefield = depth_step(
            wavefield,
            omega_now,
            slow_block[step_no],
            coef_block[step_no],
            ref_block[step_no],
            tables,
            pad_rows,
        )
        traces.append(wavefield[0])
    return (wavefield, jnp.stack(traces))


def shards_general(surface, omegas, region_speed, fd_coeff, region_index, ref_region):
    line_len = surface.shape[3]
    rows_here = surface.shape[2]
    freq_count = surface.shape[1]
    step_count = region_index.shape[0]
    tables = build_tables(line_len)
    inv_speed = 1.0 / region_speed
    segment_no = lax.axis_index("depth")
    segment_count = lax.axis_size("depth")

    def pad_near(values):
        return padded_2(values, (("strip", 1),), 1)

    slow_cells = lookup(region_index, inv_speed)
    coef_cells = lookup(region_index, fd_coeff)
    ref_cells = lookup(ref_region, inv_speed)
    freq_index = jnp.arange(freq_count)
    image_out = jnp.zeros((step_count, rows_here, line_len), jnp.float32)
    arriving = jnp.zeros((2, rows_here, line_len), jnp.float32)
    tick_count = freq_count + segment_count - 1
    for tick_no in range(tick_count):
        batch_no = tick_no - segment_no
        is_live = (batch_no >= 0) & (batch_no < freq_count)
        clipped = jnp.clip(batch_no, 0, freq_count - 1)
        picked = lax.dynamic_index_in_dim(surface, clipped, 1, keepdims=False)
        entering = jnp.where(segment_no == 0, picked, arriving)
        omega_now = jnp.sum(jnp.where(freq_index == clipped, omegas, 0.0))
        leaving, traces = march(
            entering, omega_now, slow_cells, coef_cells, ref_cells, tables, pad_near
        )
        image_out = image_out + jnp.where(is_live, traces, 0.0)
        if tick_no + 1 < tick_count:
            arriving = from_behind(leaving, "depth", 1)
    return image_out


LANE = 128
FFT_BLOCKS = 16
ROW_CHUNK = 8


def fft4(x0, x1, x2, x3, sign):
    s0 = (x0[0] + x2[0], x0[1] + x2[1])
    d0 = (x0[0] - x2[0], x0[1] - x2[1])
    s1 = (x1[0] + x3[0], x1[1] + x3[1])
    d1 = (x1[0] - x3[0], x1[1] - x3[1])
    if sign < 0:
        wd = (d1[1], -d1[0])
    else:
        wd = (-d1[1], d1[0])
    return (
        (s0[0] + s1[0], s0[1] + s1[1]),
        (d0[0] + wd[0], d0[1] + wd[1]),
        (s0[0] - s1[0], s0[1] - s1[1]),
        (d0[0] - wd[0], d0[1] - wd[1]),
    )


def turn_const(value, power, sign):
    if power == 4:
        return (-value[1], value[0]) if sign > 0 else (value[1], -value[0])
    angle = sign * 2.0 * math.pi * power / 16.0
    cr, ci = (math.cos(angle), math.sin(angle))
    return (value[0] * cr - value[1] * ci, value[0] * ci + value[1] * cr)


def fft16(parts, sign):
    mid = [[None] * 4 for _ in range(4)]
    for a0 in range(4):
        ys = fft4(parts[a0], parts[4 + a0], parts[8 + a0], parts[12 + a0], sign)
        for c0 in range(4):
            power = a0 * c0
            mid[a0][c0] = ys[c0] if power == 0 else turn_const(ys[c0], power, sign)
    out = [None] * 16
    for c0 in range(4):
        zs = fft4(mid[0][c0], mid[1][c0], mid[2][c0], mid[3][c0], sign)
        for c1 in range(4):
            out[c0 + 4 * c1] = zs[c1]
    return out


def pick(regions, values):
    level = list(values)
    bit = 1
    while len(level) > 1:
        chosen = (regions & bit) != 0
        level = [jnp.where(chosen, level[i + 1], level[i]) for i in range(0, len(level), 2)]
        bit *= 2
    return jnp.broadcast_to(level[0], regions.shape)


def split_dot(values, hi_ref, lo_ref):
    high = values.astype(jnp.bfloat16)
    low = (values - high.astype(jnp.float32)).astype(jnp.bfloat16)
    main = jnp.dot(high, hi_ref[...], preferred_element_type=jnp.float32)
    fix = jnp.dot(high, lo_ref[...], preferred_element_type=jnp.float32) + jnp.dot(
        low, hi_ref[:, :], preferred_element_type=jnp.float32
    )
    return main + fix


def section_kernel(
    tab_ref, w_ref, rid_ref, mult_ref, tw_ref, fhi_ref, flo_ref, ghi_ref, glo_ref,
    wout_ref, img_ref, a_ref, y_ref, v_ref, *, table_len
):
    rows = w_ref.shape[1]
    line_len = w_ref.shape[2]
    steps = rid_ref.shape[0]
    strip_count, rows_here = img_ref.shape[0], img_ref.shape[2]
    chunks = rows // ROW_CHUNK
    inv_len = 1.0 / line_len
    wout_ref[...] = w_ref[...]

    def blk(a):
        return slice(a * LANE, (a + 1) * LANE)

    def one_step(k, carry):
        base = k * (3 * table_len)
        cos_t = [tab_ref[base + g] for g in range(table_len)]
        sin_t = [tab_ref[base + table_len + g] for g in range(table_len)]
        gain_t = [tab_ref[base + 2 * table_len + g] for g in range(table_len)]

        def forward_chunk(i, c):
            y0 = pl.multiple_of(i * ROW_CHUNK, ROW_CHUNK)
            parts = [
                (wout_ref[0, pl.ds(y0, ROW_CHUNK), blk(a)], wout_ref[1, pl.ds(y0, ROW_CHUNK), blk(a)])
                for a in range(FFT_BLOCKS)
            ]
            spec = fft16(parts, -1)
            for cc in range(FFT_BLOCKS):
                tc = tw_ref[0, cc:cc + 1, :]
                ts = tw_ref[1, cc:cc + 1, :]
                xr, xi = spec[cc]
                a_ref[pl.ds(cc * rows + y0, ROW_CHUNK), 0:LANE] = xr * tc + xi * ts
                a_ref[pl.ds(cc * rows + y0, ROW_CHUNK), LANE:2 * LANE] = xi * tc - xr * ts
            return c

        lax.fori_loop(0, chunks, forward_chunk, 0)
        y_ref[...] = split_dot(a_ref[...], fhi_ref, flo_ref)
        for cc in range(FFT_BLOCKS):
            band = slice(cc * rows, (cc + 1) * rows)
            yr = y_ref[band, 0:LANE]
            yi = y_ref[band, LANE:2 * LANE]
            mr = mult_ref[k, 0, cc:cc + 1, :]
            mi = mult_ref[k, 1, cc:cc + 1, :]
            a_ref[band, 0:LANE] = yr * mr - yi * mi
            a_ref[band, LANE:2 * LANE] = yr * mi + yi * mr
        y_ref[...] = split_dot(a_ref[...], ghi_ref, glo_ref)

        def inverse_chunk(i, c):
            y0 = pl.multiple_of(i * ROW_CHUNK, ROW_CHUNK)
            parts = []
            for cc in range(FFT_BLOCKS):
                zr = y_ref[pl.ds(cc * rows + y0, ROW_CHUNK), 0:LANE]
                zi = y_ref[pl.ds(cc * rows + y0, ROW_CHUNK), LANE:2 * LANE]
                tc = tw_ref[0, cc:cc + 1, :]
                ts = tw_ref[1, cc:cc + 1, :]
                parts.append((zr * tc - zi * ts, zr * ts + zi * tc))
            back = fft16(parts, 1)
            for a in range(FFT_BLOCKS):
                ur = back[a][0] * inv_len
                ui = back[a][1] * inv_len
                regions = rid_ref[k, pl.ds(y0, ROW_CHUNK), blk(a)]
                cs = pick(regions, cos_t)
                sn = pick(regions, sin_t)
                v_ref[0, pl.ds(y0, ROW_CHUNK), blk(a)] = ur * cs - ui * sn
                v_ref[1, pl.ds(y0, ROW_CHUNK), blk(a)] = ur * sn + ui * cs
            return c

        lax.fori_loop(0, chunks, inverse_chunk, 0)
        row_id = lax.broadcasted_iota(jnp.int32, (rows, LANE), 0)
        lane_id = lax.broadcasted_iota(jnp.int32, (rows, LANE), 1)
        cache = {}

        def cell(part, a):
            key = (part, a % FFT_BLOCKS)
            if key not in cache:
                v = v_ref[part, :, blk(a % FFT_BLOCKS)]
                cache[key] = (v, pltpu.roll(v, 1, 1), pltpu.roll(v, LANE - 1, 1))
            return cache[key]

        for a in range(FFT_BLOCKS):
            lap = []
            here = []
            for part in range(2):
                v, from_left, from_right = cell(part, a)
                prev_left = cell(part, a - 1)[1]
                next_right = cell(part, a + 1)[2]
                above = jnp.where(row_id == 0, 0.0, pltpu.roll(v, 1, 0))
                below = jnp.where(row_id == rows - 1, 0.0, pltpu.roll(v, rows - 1, 0))
                left = jnp.where(lane_id == 0, prev_left, from_left)
                right = jnp.where(lane_id == LANE - 1, next_right, from_right)
                lap.append(above + below + left + right - 4.0 * v)
                here.append(v)
            gain = pick(rid_ref[k, :, blk(a)], gain_t)
            new_re = here[0] + (lap[0] * DAMPING - lap[1] * gain)
            new_im = here[1] + (lap[0] * gain + lap[1] * DAMPING)
            wout_ref[0, :, blk(a)] = new_re
            wout_ref[1, :, blk(a)] = new_im
            for j in range(strip_count):
                img_ref[j, k, :, blk(a)] = new_re[j * rows_here:(j + 1) * rows_here]
        return carry

    lax.fori_loop(0, steps, one_step, 0)


def fast_constants(line_len):
    outer = line_len // LANE
    b = np.arange(LANE)
    ang = 2.0 * np.pi * (np.outer(b, b) % LANE) / LANE
    cos_m, sin_m = (np.cos(ang), np.sin(ang))
    fwd = np.block([[cos_m, -sin_m], [sin_m, cos_m]])
    inv = np.block([[cos_m, sin_m], [-sin_m, cos_m]])

    def halves(m):
        hi = m.astype(ml_dtypes.bfloat16)
        lo = (m - hi.astype(np.float64)).astype(ml_dtypes.bfloat16)
        return (hi, lo)

    c = np.arange(outer)
    tw_ang = 2.0 * np.pi * np.outer(c, b) / line_len
    twiddle = np.stack([np.cos(tw_ang), np.sin(tw_ang)]).astype(np.float32)
    q = c[:, None] + outer * b[None, :]
    signed = np.where(q >= line_len // 2, q - line_len, q).astype(np.float32)
    kx_cd = signed * np.float32(2.0 * math.pi / line_len)
    return (halves(fwd), halves(inv), twiddle, kx_cd.astype(np.float32))


def run_section(wave, regions, table, mult, consts, strip_count):
    (fhi, flo), (ghi, glo), twiddle, _ = consts
    rows, line_len = wave.shape[1], wave.shape[2]
    steps = regions.shape[0]
    table_len = table.shape[0] // (3 * steps)
    vmem = pl.BlockSpec(memory_space=pltpu.VMEM)
    flops = steps * (2 * 3 * 2 * (FFT_BLOCKS * rows) * 256 * 256 + 400 * rows * line_len)
    return pl.pallas_call(
        lambda *refs: section_kernel(*refs, table_len=table_len),
        out_shape=(
            jax.ShapeDtypeStruct(wave.shape, jnp.float32),
            jax.ShapeDtypeStruct((strip_count, steps, rows // strip_count, line_len), jnp.float32),
        ),
        in_specs=[pl.BlockSpec(memory_space=pltpu.SMEM)] + [vmem] * 8,
        out_specs=(vmem, vmem),
        scratch_shapes=[
            pltpu.VMEM((FFT_BLOCKS * rows, 2 * LANE), jnp.float32),
            pltpu.VMEM((FFT_BLOCKS * rows, 2 * LANE), jnp.float32),
            pltpu.VMEM((2, rows, line_len), jnp.float32),
        ],
        cost_estimate=pl.CostEstimate(
            flops=flops, transcendentals=0, bytes_accessed=4 * rows * line_len * 6 * steps
        ),
    )(table, wave, regions, mult, jnp.asarray(twiddle), jnp.asarray(fhi), jnp.asarray(flo),
      jnp.asarray(ghi), jnp.asarray(glo))


def section_tables(omega, region_speed, fd_coeff, ref_region, kx_cd):
    inv_speed = 1.0 / region_speed
    ref_slow = inv_speed[ref_region]
    regions = region_speed.shape[0]
    padded = 1 << max(1, (regions - 1).bit_length())
    extra = padded - regions
    phase = omega * (inv_speed[None, :] - ref_slow[:, None])
    gain = jnp.broadcast_to(fd_coeff / omega, phase.shape)
    parts = [jnp.cos(phase), jnp.sin(phase), gain]
    if extra:
        parts = [jnp.concatenate([p, jnp.repeat(p[:, -1:], extra, axis=1)], axis=1) for p in parts]
    table = jnp.stack(parts, axis=1).reshape(-1)
    wave_ref = omega * ref_slow
    wave_ref = wave_ref[:, None, None]
    excess = wave_ref * wave_ref - kx_cd * kx_cd
    decay_line = jnp.exp(-jnp.sqrt(jnp.maximum(-excess, 0.0)))
    vertical = jnp.sqrt(jnp.maximum(excess, 0.0))
    mult = jnp.stack([decay_line * jnp.cos(vertical), decay_line * jnp.sin(vertical)], axis=1)
    return (table, mult)


def fast_fits(surface, region_index, region_speed):
    freq_count = surface.shape[1]
    rows = surface.shape[2] * lax.axis_size("strip")
    line_len = surface.shape[3]
    return (
        freq_count == lax.axis_size("strip")
        and line_len == FFT_BLOCKS * LANE
        and rows % ROW_CHUNK == 0
        and surface.shape[2] % ROW_CHUNK == 0
        and rows <= 64
        and region_speed.shape[0] <= 16
    )


def strip_pairs(depths, strip_count, shift):
    return [
        (d * strip_count + r, d * strip_count + (r + shift) % strip_count)
        for d in depths
        for r in range(strip_count)
    ]


def gather_rows(local, depths, strip_no, strip_count, row_axis):
    rows = local.shape[row_axis]
    shape = list(local.shape)
    shape[row_axis] = rows * strip_count
    full = jnp.zeros(shape, local.dtype)
    start = [0] * len(shape)
    start[row_axis] = strip_no * rows
    full = lax.dynamic_update_slice(full, local, start)
    for shift in range(1, strip_count):
        got = lax.ppermute(local, ("depth", "strip"), strip_pairs(depths, strip_count, shift))
        start = [0] * len(shape)
        start[row_axis] = ((strip_no - shift) % strip_count) * rows
        full = lax.dynamic_update_slice(full, got, start)
    return full


def gather_strips(piece_of, local, depths, strip_no, strip_count, rows_here):
    rows = rows_here * strip_count
    shape = (local.shape[0], rows, local.shape[2])
    full = lax.dynamic_update_slice(
        jnp.zeros(shape, jnp.float32), local, (0, strip_no * rows_here, 0)
    )
    for shift in range(1, strip_count):
        target = (strip_no + shift) % strip_count
        got = lax.ppermute(
            piece_of(target), ("depth", "strip"), strip_pairs(depths, strip_count, shift)
        )
        source = (strip_no - shift) % strip_count
        full = lax.dynamic_update_slice(full, got, (0, source * rows_here, 0))
    return full


def shards(surface, omegas, region_speed, fd_coeff, region_index, ref_region):
    if not fast_fits(surface, region_index, region_speed):
        return shards_general(surface, omegas, region_speed, fd_coeff, region_index, ref_region)
    line_len = surface.shape[3]
    rows_here = surface.shape[2]
    steps = region_index.shape[0]
    segment_no = lax.axis_index("depth")
    segment_count = lax.axis_size("depth")
    strip_no = lax.axis_index("strip")
    strip_count = lax.axis_size("strip")
    consts = fast_constants(line_len)
    region_f = region_index.astype(jnp.float32)
    early = [d for d in range(segment_count) if d != 1]

    def with_surface(target):
        return jnp.concatenate(
            [region_f, lax.dynamic_index_in_dim(surface, target, 1, keepdims=False)], axis=0
        )

    gathered = gather_strips(
        with_surface, with_surface(strip_no), early, strip_no, strip_count, rows_here
    )
    regions_a = gathered[:steps].astype(jnp.int32)
    wave = gathered[steps:]
    omega = lax.dynamic_index_in_dim(omegas, strip_no, 0, keepdims=False)
    table, mult = section_tables(omega, region_speed, fd_coeff, ref_region, jnp.asarray(consts[3]))
    image = jnp.zeros((strip_count, steps, rows_here, line_len), jnp.float32)
    regions_b = regions_a
    if segment_count > 1:
        token = lax.ppermute(gathered[0, 0:8, 0:LANE], "depth", [(0, 1)])

    def sweep(regions):
        def live(wave, image):
            return run_section(wave, regions, table, mult, consts, strip_count)

        return live

    def idle(wave, image):
        return (wave, image)

    def freq_sum(image, depths):
        parts = []
        for shift in range(1, strip_count):
            target = (strip_no + shift) % strip_count
            piece = lax.dynamic_index_in_dim(image, target, 0, keepdims=False)
            parts.append(
                lax.ppermute(piece, ("depth", "strip"), strip_pairs(depths, strip_count, shift))
            )
        return parts

    arrived = []
    for tick_no in range(segment_count):
        regions = regions_b if tick_no == 1 else regions_a
        wave, image = lax.cond(segment_no == tick_no, sweep(regions), idle, wave, image)
        if tick_no + 1 < segment_count:
            wave = lax.ppermute(wave, "depth", [(tick_no, tick_no + 1)])
        if tick_no == 0 and segment_count > 1:
            held, token, _ = lax.optimization_barrier((region_f, token, image))
            held = held + 0.0 * token[0, 0]
            regions_b = gather_strips(
                lambda target: held, held, [1], strip_no, strip_count, rows_here
            ).astype(jnp.int32)
        if tick_no == segment_count - 2:
            wave, image = lax.optimization_barrier((wave, image))
            arrived += freq_sum(image, range(segment_count - 1))
    arrived += freq_sum(image, [segment_count - 1])
    total = lax.dynamic_index_in_dim(image, strip_no, 0, keepdims=False)
    for piece in arrived:
        total = total + piece
    return total


def solution(mesh):
    in_specs = (
        P(None, "shots", "strip", None),
        P(),
        P(),
        P(),
        P("depth", "strip", None),
        P("depth"),
    )
    out_specs = P("depth", "strip", "shots")
    return jax.shard_map(shards, mesh=mesh, in_specs=in_specs, out_specs=out_specs, check_vma=False)
```

```python
import math

import ml_dtypes
import numpy as np
import jax
import jax.numpy as jnp
from jax import lax
from jax.experimental import pallas as pl
from jax.experimental.pallas import tpu as pltpu
from jax.sharding import PartitionSpec as P

DAMPING = 0.05
PRECISE = lax.Precision.HIGHEST


def padded_2(cells, sides, width):
    for axis, dim in sides:
        count = lax.axis_size(axis)
        ends = count - 1
        head = lax.slice_in_dim(cells, 0, width, axis=dim)
        tail = lax.slice_in_dim(cells, cells.shape[dim] - width, cells.shape[dim], axis=dim)
        cells = jnp.concatenate(
            [
                lax.ppermute(tail, axis, [(i, (i + 1) % count) for i in range(ends)]),
                cells,
                lax.ppermute(head, axis, [((i + 1) % count, i) for i in range(ends)]),
            ],
            axis=dim,
        )
    return cells


def from_behind(value, axis, steps):
    count = lax.axis_size(axis)
    first, last = (max(0, -steps), min(count, count - steps))
    return lax.ppermute(value, axis, [(source, source + steps) for source in range(first, last)])


def complex_scale(values, cosine, sine_part):
    return jnp.stack(
        [values[0] * cosine - values[1] * sine_part, values[0] * sine_part + values[1] * cosine]
    )


def angle_pair(numerator, period):
    angle_grid = numerator.astype(jnp.float32) * (2.0 * math.pi / period)
    return (jnp.cos(angle_grid), jnp.sin(angle_grid))


def block_matrix(cosine, sine_part, forward):
    sign_flip = 1.0 if forward else -1.0
    return jnp.stack(
        [jnp.stack([cosine, -sign_flip * sine_part]), jnp.stack([sign_flip * sine_part, cosine])]
    )


def build_tables(line_len):
    block_len = 128
    outer_len = line_len // block_len
    inner_idx = jnp.arange(block_len)
    outer_idx = jnp.arange(outer_len)
    cos_large, sin_large = angle_pair(
        inner_idx[:, None] * inner_idx[None, :] % block_len, block_len
    )
    cos_small, sin_small = angle_pair(
        outer_idx[:, None] * outer_idx[None, :] % outer_len, outer_len
    )
    cos_twist, sin_twist = angle_pair(outer_idx[:, None] * inner_idx[None, :], line_len)
    wave_index = outer_idx[:, None] + outer_len * inner_idx[None, :]
    signed = jnp.where(wave_index >= line_len // 2, wave_index - line_len, wave_index)
    kx_grid = signed.astype(jnp.float32) * (2.0 * math.pi / line_len)
    small_fwd = block_matrix(cos_small, sin_small, True)
    small_inv = block_matrix(cos_small, sin_small, False)
    large_fwd = block_matrix(cos_large, sin_large, True)
    large_inv = block_matrix(cos_large, sin_large, False)
    return (small_fwd, small_inv, large_fwd, large_inv, cos_twist, sin_twist, kx_grid)


def forward_line(wavefield, tables):
    small_fwd, small_inv, large_fwd, large_inv, cos_twist, sin_twist, kx_grid = tables
    row_count = wavefield.shape[1]
    pieces = wavefield.reshape(2, row_count, cos_twist.shape[0], cos_twist.shape[1])
    mixed_part = jnp.einsum("zrab,zwca->wrcb", pieces, small_fwd, precision=PRECISE)
    mixed_part = complex_scale(mixed_part, cos_twist, -sin_twist)
    return jnp.einsum("zrcb,zwbd->wrcd", mixed_part, large_fwd, precision=PRECISE)


def inverse_line(spectrum, tables):
    small_fwd, small_inv, large_fwd, large_inv, cos_twist, sin_twist, kx_grid = tables
    row_count = spectrum.shape[1]
    line_len = cos_twist.shape[0] * cos_twist.shape[1]
    mixed_part = jnp.einsum("zrcd,zwdb->wrcb", spectrum, large_inv, precision=PRECISE)
    mixed_part = complex_scale(mixed_part, cos_twist, sin_twist)
    pieces = jnp.einsum("zrcb,zwca->wrab", mixed_part, small_inv, precision=PRECISE)
    return pieces.reshape(2, row_count, line_len) * (1.0 / line_len)


def lookup(regions, entries):
    picked = jnp.zeros(regions.shape, jnp.float32)
    for region_no in range(entries.shape[0]):
        picked = picked + jnp.where(regions == region_no, entries[region_no], 0.0)
    return picked


def depth_step(wavefield, omega_now, slow_cells, coef_cells, ref_slow, tables, pad_rows):
    kx_grid = tables[6]
    wave_ref = omega_now * ref_slow
    excess = wave_ref * wave_ref - kx_grid * kx_grid
    decay_line = jnp.exp(-jnp.sqrt(jnp.maximum(-excess, 0.0)))
    vertical = jnp.sqrt(jnp.maximum(excess, 0.0))
    spectrum = complex_scale(
        forward_line(wavefield, tables),
        decay_line * jnp.cos(vertical),
        decay_line * jnp.sin(vertical),
    )
    wavefield = inverse_line(spectrum, tables)
    phase_cell = omega_now * (slow_cells - ref_slow)
    wavefield = complex_scale(wavefield, jnp.cos(phase_cell), jnp.sin(phase_cell))
    padded = pad_rows(wavefield)
    laplace = (
        padded[:, :-2]
        + padded[:, 2:]
        + jnp.roll(wavefield, 1, 2)
        + jnp.roll(wavefield, -1, 2)
        - 4.0 * wavefield
    )
    return wavefield + complex_scale(laplace, DAMPING, coef_cells / omega_now)


def march(wavefield, omega_now, slow_block, coef_block, ref_block, tables, pad_rows):
    traces = []
    for step_no in range(slow_block.shape[0]):
        wavefield = depth_step(
            wavefield,
            omega_now,
            slow_block[step_no],
            coef_block[step_no],
            ref_block[step_no],
            tables,
            pad_rows,
        )
        traces.append(wavefield[0])
    return (wavefield, jnp.stack(traces))


def shards_general(surface, omegas, region_speed, fd_coeff, region_index, ref_region):
    line_len = surface.shape[3]
    rows_here = surface.shape[2]
    freq_count = surface.shape[1]
    step_count = region_index.shape[0]
    tables = build_tables(line_len)
    inv_speed = 1.0 / region_speed
    segment_no = lax.axis_index("depth")
    segment_count = lax.axis_size("depth")

    def pad_near(values):
        return padded_2(values, (("strip", 1),), 1)

    slow_cells = lookup(region_index, inv_speed)
    coef_cells = lookup(region_index, fd_coeff)
    ref_cells = lookup(ref_region, inv_speed)
    freq_index = jnp.arange(freq_count)
    image_out = jnp.zeros((step_count, rows_here, line_len), jnp.float32)
    arriving = jnp.zeros((2, rows_here, line_len), jnp.float32)
    tick_count = freq_count + segment_count - 1
    for tick_no in range(tick_count):
        batch_no = tick_no - segment_no
        is_live = (batch_no >= 0) & (batch_no < freq_count)
        clipped = jnp.clip(batch_no, 0, freq_count - 1)
        picked = lax.dynamic_index_in_dim(surface, clipped, 1, keepdims=False)
        entering = jnp.where(segment_no == 0, picked, arriving)
        omega_now = jnp.sum(jnp.where(freq_index == clipped, omegas, 0.0))
        leaving, traces = march(
            entering, omega_now, slow_cells, coef_cells, ref_cells, tables, pad_near
        )
        image_out = image_out + jnp.where(is_live, traces, 0.0)
        if tick_no + 1 < tick_count:
            arriving = from_behind(leaving, "depth", 1)
    return image_out


LANE = 128
FFT_BLOCKS = 16
ROW_CHUNK = 8


def fft4(x0, x1, x2, x3, sign):
    s0 = (x0[0] + x2[0], x0[1] + x2[1])
    d0 = (x0[0] - x2[0], x0[1] - x2[1])
    s1 = (x1[0] + x3[0], x1[1] + x3[1])
    d1 = (x1[0] - x3[0], x1[1] - x3[1])
    if sign < 0:
        wd = (d1[1], -d1[0])
    else:
        wd = (-d1[1], d1[0])
    return (
        (s0[0] + s1[0], s0[1] + s1[1]),
        (d0[0] + wd[0], d0[1] + wd[1]),
        (s0[0] - s1[0], s0[1] - s1[1]),
        (d0[0] - wd[0], d0[1] - wd[1]),
    )


def turn_const(value, power, sign):
    if power == 4:
        return (-value[1], value[0]) if sign > 0 else (value[1], -value[0])
    angle = sign * 2.0 * math.pi * power / 16.0
    cr, ci = (math.cos(angle), math.sin(angle))
    return (value[0] * cr - value[1] * ci, value[0] * ci + value[1] * cr)


def fft16(parts, sign):
    mid = [[None] * 4 for _ in range(4)]
    for a0 in range(4):
        ys = fft4(parts[a0], parts[4 + a0], parts[8 + a0], parts[12 + a0], sign)
        for c0 in range(4):
            power = a0 * c0
            mid[a0][c0] = ys[c0] if power == 0 else turn_const(ys[c0], power, sign)
    out = [None] * 16
    for c0 in range(4):
        zs = fft4(mid[0][c0], mid[1][c0], mid[2][c0], mid[3][c0], sign)
        for c1 in range(4):
            out[c0 + 4 * c1] = zs[c1]
    return out


def pick(regions, values):
    level = list(values)
    bit = 1
    while len(level) > 1:
        chosen = (regions & bit) != 0
        level = [jnp.where(chosen, level[i + 1], level[i]) for i in range(0, len(level), 2)]
        bit *= 2
    return jnp.broadcast_to(level[0], regions.shape)


def full_dot(values, mat_ref):
    return jnp.dot(
        values, mat_ref[...], precision=lax.Precision.HIGHEST, preferred_element_type=jnp.float32
    )


def split_dot(values, hi_ref, lo_ref):
    high = values.astype(jnp.bfloat16)
    low = (values - high.astype(jnp.float32)).astype(jnp.bfloat16)
    main = jnp.dot(high, hi_ref[...], preferred_element_type=jnp.float32)
    fix = jnp.dot(high, lo_ref[...], preferred_element_type=jnp.float32) + jnp.dot(
        low, hi_ref[:, :], preferred_element_type=jnp.float32
    )
    return main + fix


def section_kernel(
    tab_ref, w_ref, rid_ref, mult_ref, tw_ref, fhi_ref, flo_ref, ghi_ref, glo_ref,
    wout_ref, img_ref, a_ref, y_ref, v_ref, *, table_len
):
    rows = w_ref.shape[1]
    line_len = w_ref.shape[2]
    steps = rid_ref.shape[0]
    strip_count, rows_here = img_ref.shape[0], img_ref.shape[2]
    chunks = rows // ROW_CHUNK
    inv_len = 1.0 / line_len
    wout_ref[...] = w_ref[...]

    def blk(a):
        return slice(a * LANE, (a + 1) * LANE)

    def one_step(k, carry):
        base = k * (3 * table_len)
        cos_t = [tab_ref[base + g] for g in range(table_len)]
        sin_t = [tab_ref[base + table_len + g] for g in range(table_len)]
        gain_t = [tab_ref[base + 2 * table_len + g] for g in range(table_len)]

        def forward_chunk(i, c):
            y0 = pl.multiple_of(i * ROW_CHUNK, ROW_CHUNK)
            parts = [
                (wout_ref[0, pl.ds(y0, ROW_CHUNK), blk(a)], wout_ref[1, pl.ds(y0, ROW_CHUNK), blk(a)])
                for a in range(FFT_BLOCKS)
            ]
            spec = fft16(parts, -1)
            for cc in range(FFT_BLOCKS):
                tc = tw_ref[0, cc:cc + 1, :]
                ts = tw_ref[1, cc:cc + 1, :]
                xr, xi = spec[cc]
                a_ref[pl.ds(cc * rows + y0, ROW_CHUNK), 0:LANE] = xr * tc + xi * ts
                a_ref[pl.ds(cc * rows + y0, ROW_CHUNK), LANE:2 * LANE] = xi * tc - xr * ts
            return c

        lax.fori_loop(0, chunks, forward_chunk, 0)
        y_ref[...] = full_dot(a_ref[...], fhi_ref)
        for cc in range(FFT_BLOCKS):
            band = slice(cc * rows, (cc + 1) * rows)
            yr = y_ref[band, 0:LANE]
            yi = y_ref[band, LANE:2 * LANE]
            mr = mult_ref[k, 0, cc:cc + 1, :]
            mi = mult_ref[k, 1, cc:cc + 1, :]
            a_ref[band, 0:LANE] = yr * mr - yi * mi
            a_ref[band, LANE:2 * LANE] = yr * mi + yi * mr
        y_ref[...] = full_dot(a_ref[...], ghi_ref)

        def inverse_chunk(i, c):
            y0 = pl.multiple_of(i * ROW_CHUNK, ROW_CHUNK)
            parts = []
            for cc in range(FFT_BLOCKS):
                zr = y_ref[pl.ds(cc * rows + y0, ROW_CHUNK), 0:LANE]
                zi = y_ref[pl.ds(cc * rows + y0, ROW_CHUNK), LANE:2 * LANE]
                tc = tw_ref[0, cc:cc + 1, :]
                ts = tw_ref[1, cc:cc + 1, :]
                parts.append((zr * tc - zi * ts, zr * ts + zi * tc))
            back = fft16(parts, 1)
            for a in range(FFT_BLOCKS):
                ur = back[a][0] * inv_len
                ui = back[a][1] * inv_len
                regions = rid_ref[k, pl.ds(y0, ROW_CHUNK), blk(a)]
                cs = pick(regions, cos_t)
                sn = pick(regions, sin_t)
                v_ref[0, pl.ds(y0, ROW_CHUNK), blk(a)] = ur * cs - ui * sn
                v_ref[1, pl.ds(y0, ROW_CHUNK), blk(a)] = ur * sn + ui * cs
            return c

        lax.fori_loop(0, chunks, inverse_chunk, 0)
        row_id = lax.broadcasted_iota(jnp.int32, (rows, LANE), 0)
        lane_id = lax.broadcasted_iota(jnp.int32, (rows, LANE), 1)
        cache = {}

        def cell(part, a):
            key = (part, a % FFT_BLOCKS)
            if key not in cache:
                v = v_ref[part, :, blk(a % FFT_BLOCKS)]
                cache[key] = (v, pltpu.roll(v, 1, 1), pltpu.roll(v, LANE - 1, 1))
            return cache[key]

        for a in range(FFT_BLOCKS):
            lap = []
            here = []
            for part in range(2):
                v, from_left, from_right = cell(part, a)
                prev_left = cell(part, a - 1)[1]
                next_right = cell(part, a + 1)[2]
                above = jnp.where(row_id == 0, 0.0, pltpu.roll(v, 1, 0))
                below = jnp.where(row_id == rows - 1, 0.0, pltpu.roll(v, rows - 1, 0))
                left = jnp.where(lane_id == 0, prev_left, from_left)
                right = jnp.where(lane_id == LANE - 1, next_right, from_right)
                lap.append(above + below + left + right - 4.0 * v)
                here.append(v)
            gain = pick(rid_ref[k, :, blk(a)], gain_t)
            new_re = here[0] + (lap[0] * DAMPING - lap[1] * gain)
            new_im = here[1] + (lap[0] * gain + lap[1] * DAMPING)
            wout_ref[0, :, blk(a)] = new_re
            wout_ref[1, :, blk(a)] = new_im
            for j in range(strip_count):
                img_ref[j, k, :, blk(a)] = new_re[j * rows_here:(j + 1) * rows_here]
        return carry

    lax.fori_loop(0, steps, one_step, 0)


def fast_constants(line_len):
    outer = line_len // LANE
    b = np.arange(LANE)
    ang = 2.0 * np.pi * (np.outer(b, b) % LANE) / LANE
    cos_m, sin_m = (np.cos(ang), np.sin(ang))
    fwd = np.block([[cos_m, -sin_m], [sin_m, cos_m]])
    inv = np.block([[cos_m, sin_m], [-sin_m, cos_m]])

    def halves(m):
        hi = m.astype(ml_dtypes.bfloat16)
        lo = (m - hi.astype(np.float64)).astype(ml_dtypes.bfloat16)
        return (hi, lo)

    c = np.arange(outer)
    tw_ang = 2.0 * np.pi * np.outer(c, b) / line_len
    twiddle = np.stack([np.cos(tw_ang), np.sin(tw_ang)]).astype(np.float32)
    q = c[:, None] + outer * b[None, :]
    signed = np.where(q >= line_len // 2, q - line_len, q).astype(np.float32)
    kx_cd = signed * np.float32(2.0 * math.pi / line_len)
    return ((fwd.astype(np.float32), fwd.astype(np.float32)), (inv.astype(np.float32), inv.astype(np.float32)), twiddle, kx_cd.astype(np.float32))


def run_section(wave, regions, table, mult, consts, strip_count):
    (fhi, flo), (ghi, glo), twiddle, _ = consts
    rows, line_len = wave.shape[1], wave.shape[2]
    steps = regions.shape[0]
    table_len = table.shape[0] // (3 * steps)
    vmem = pl.BlockSpec(memory_space=pltpu.VMEM)
    flops = steps * (2 * 3 * 2 * (FFT_BLOCKS * rows) * 256 * 256 + 400 * rows * line_len)
    return pl.pallas_call(
        lambda *refs: section_kernel(*refs, table_len=table_len),
        out_shape=(
            jax.ShapeDtypeStruct(wave.shape, jnp.float32),
            jax.ShapeDtypeStruct((strip_count, steps, rows // strip_count, line_len), jnp.float32),
        ),
        in_specs=[pl.BlockSpec(memory_space=pltpu.SMEM)] + [vmem] * 8,
        out_specs=(vmem, vmem),
        scratch_shapes=[
            pltpu.VMEM((FFT_BLOCKS * rows, 2 * LANE), jnp.float32),
            pltpu.VMEM((FFT_BLOCKS * rows, 2 * LANE), jnp.float32),
            pltpu.VMEM((2, rows, line_len), jnp.float32),
        ],
        cost_estimate=pl.CostEstimate(
            flops=flops, transcendentals=0, bytes_accessed=4 * rows * line_len * 6 * steps
        ),
    )(table, wave, regions, mult, jnp.asarray(twiddle), jnp.asarray(fhi), jnp.asarray(flo),
      jnp.asarray(ghi), jnp.asarray(glo))


def section_tables(omega, region_speed, fd_coeff, ref_region, kx_cd):
    inv_speed = 1.0 / region_speed
    ref_slow = inv_speed[ref_region]
    regions = region_speed.shape[0]
    padded = 1 << max(1, (regions - 1).bit_length())
    extra = padded - regions
    phase = omega * (inv_speed[None, :] - ref_slow[:, None])
    gain = jnp.broadcast_to(fd_coeff / omega, phase.shape)
    parts = [jnp.cos(phase), jnp.sin(phase), gain]
    if extra:
        parts = [jnp.concatenate([p, jnp.repeat(p[:, -1:], extra, axis=1)], axis=1) for p in parts]
    table = jnp.stack(parts, axis=1).reshape(-1)
    wave_ref = omega * ref_slow
    wave_ref = wave_ref[:, None, None]
    excess = wave_ref * wave_ref - kx_cd * kx_cd
    decay_line = jnp.exp(-jnp.sqrt(jnp.maximum(-excess, 0.0)))
    vertical = jnp.sqrt(jnp.maximum(excess, 0.0))
    mult = jnp.stack([decay_line * jnp.cos(vertical), decay_line * jnp.sin(vertical)], axis=1)
    return (table, mult)


def fast_fits(surface, region_index, region_speed):
    freq_count = surface.shape[1]
    rows = surface.shape[2] * lax.axis_size("strip")
    line_len = surface.shape[3]
    return (
        freq_count == lax.axis_size("strip")
        and line_len == FFT_BLOCKS * LANE
        and rows % ROW_CHUNK == 0
        and surface.shape[2] % ROW_CHUNK == 0
        and rows <= 64
        and region_speed.shape[0] <= 16
    )


def strip_pairs(depths, strip_count, shift):
    return [
        (d * strip_count + r, d * strip_count + (r + shift) % strip_count)
        for d in depths
        for r in range(strip_count)
    ]


def gather_rows(local, depths, strip_no, strip_count, row_axis):
    rows = local.shape[row_axis]
    shape = list(local.shape)
    shape[row_axis] = rows * strip_count
    full = jnp.zeros(shape, local.dtype)
    start = [0] * len(shape)
    start[row_axis] = strip_no * rows
    full = lax.dynamic_update_slice(full, local, start)
    for shift in range(1, strip_count):
        got = lax.ppermute(local, ("depth", "strip"), strip_pairs(depths, strip_count, shift))
        start = [0] * len(shape)
        start[row_axis] = ((strip_no - shift) % strip_count) * rows
        full = lax.dynamic_update_slice(full, got, start)
    return full


def gather_strips(piece_of, local, depths, strip_no, strip_count, rows_here):
    rows = rows_here * strip_count
    shape = (local.shape[0], rows, local.shape[2])
    full = lax.dynamic_update_slice(
        jnp.zeros(shape, jnp.float32), local, (0, strip_no * rows_here, 0)
    )
    for shift in range(1, strip_count):
        target = (strip_no + shift) % strip_count
        got = lax.ppermute(
            piece_of(target), ("depth", "strip"), strip_pairs(depths, strip_count, shift)
        )
        source = (strip_no - shift) % strip_count
        full = lax.dynamic_update_slice(full, got, (0, source * rows_here, 0))
    return full


def shards(surface, omegas, region_speed, fd_coeff, region_index, ref_region):
    if not fast_fits(surface, region_index, region_speed):
        return shards_general(surface, omegas, region_speed, fd_coeff, region_index, ref_region)
    line_len = surface.shape[3]
    rows_here = surface.shape[2]
    steps = region_index.shape[0]
    segment_no = lax.axis_index("depth")
    segment_count = lax.axis_size("depth")
    strip_no = lax.axis_index("strip")
    strip_count = lax.axis_size("strip")
    consts = fast_constants(line_len)
    region_f = region_index.astype(jnp.float32)
    early = [d for d in range(segment_count) if d != 1]

    def with_surface(target):
        return jnp.concatenate(
            [region_f, lax.dynamic_index_in_dim(surface, target, 1, keepdims=False)], axis=0
        )

    gathered = gather_strips(
        with_surface, with_surface(strip_no), early, strip_no, strip_count, rows_here
    )
    regions_a = gathered[:steps].astype(jnp.int32)
    wave = gathered[steps:]
    omega = lax.dynamic_index_in_dim(omegas, strip_no, 0, keepdims=False)
    table, mult = section_tables(omega, region_speed, fd_coeff, ref_region, jnp.asarray(consts[3]))
    image = jnp.zeros((strip_count, steps, rows_here, line_len), jnp.float32)
    regions_b = regions_a
    if segment_count > 1:
        token = lax.ppermute(gathered[0, 0:8, 0:LANE], "depth", [(0, 1)])

    def sweep(regions):
        def live(wave, image):
            return run_section(wave, regions, table, mult, consts, strip_count)

        return live

    def idle(wave, image):
        return (wave, image)

    def freq_sum(image, depths):
        parts = []
        for shift in range(1, strip_count):
            target = (strip_no + shift) % strip_count
            piece = lax.dynamic_index_in_dim(image, target, 0, keepdims=False)
            parts.append(
                lax.ppermute(piece, ("depth", "strip"), strip_pairs(depths, strip_count, shift))
            )
        return parts

    arrived = []
    for tick_no in range(segment_count):
        regions = regions_b if tick_no == 1 else regions_a
        wave, image = lax.cond(segment_no == tick_no, sweep(regions), idle, wave, image)
        if tick_no + 1 < segment_count:
            wave = lax.ppermute(wave, "depth", [(tick_no, tick_no + 1)])
        if tick_no == 0 and segment_count > 1:
            held, token, _ = lax.optimization_barrier((region_f, token, image))
            held = held + 0.0 * token[0, 0]
            regions_b = gather_strips(
                lambda target: held, held, [1], strip_no, strip_count, rows_here
            ).astype(jnp.int32)
        if tick_no == segment_count - 2:
            wave, image = lax.optimization_barrier((wave, image))
            arrived += freq_sum(image, range(segment_count - 1))
    arrived += freq_sum(image, [segment_count - 1])
    total = lax.dynamic_index_in_dim(image, strip_no, 0, keepdims=False)
    for piece in arrived:
        total = total + piece
    return total


def solution(mesh):
    in_specs = (
        P(None, "shots", "strip", None),
        P(),
        P(),
        P(),
        P("depth", "strip", None),
        P("depth"),
    )
    out_specs = P("depth", "strip", "shots")
    return jax.shard_map(shards, mesh=mesh, in_specs=in_specs, out_specs=out_specs, check_vma=False)
```

```python
import math

import ml_dtypes
import numpy as np
import jax
import jax.numpy as jnp
from jax import lax
from jax.experimental import pallas as pl
from jax.experimental.pallas import tpu as pltpu
from jax.sharding import PartitionSpec as P

DAMPING = 0.05
PRECISE = lax.Precision.HIGHEST


def padded_2(cells, sides, width):
    for axis, dim in sides:
        count = lax.axis_size(axis)
        ends = count - 1
        head = lax.slice_in_dim(cells, 0, width, axis=dim)
        tail = lax.slice_in_dim(cells, cells.shape[dim] - width, cells.shape[dim], axis=dim)
        cells = jnp.concatenate(
            [
                lax.ppermute(tail, axis, [(i, (i + 1) % count) for i in range(ends)]),
                cells,
                lax.ppermute(head, axis, [((i + 1) % count, i) for i in range(ends)]),
            ],
            axis=dim,
        )
    return cells


def from_behind(value, axis, steps):
    count = lax.axis_size(axis)
    first, last = (max(0, -steps), min(count, count - steps))
    return lax.ppermute(value, axis, [(source, source + steps) for source in range(first, last)])


def complex_scale(values, cosine, sine_part):
    return jnp.stack(
        [values[0] * cosine - values[1] * sine_part, values[0] * sine_part + values[1] * cosine]
    )


def angle_pair(numerator, period):
    angle_grid = numerator.astype(jnp.float32) * (2.0 * math.pi / period)
    return (jnp.cos(angle_grid), jnp.sin(angle_grid))


def block_matrix(cosine, sine_part, forward):
    sign_flip = 1.0 if forward else -1.0
    return jnp.stack(
        [jnp.stack([cosine, -sign_flip * sine_part]), jnp.stack([sign_flip * sine_part, cosine])]
    )


def build_tables(line_len):
    block_len = 128
    outer_len = line_len // block_len
    inner_idx = jnp.arange(block_len)
    outer_idx = jnp.arange(outer_len)
    cos_large, sin_large = angle_pair(
        inner_idx[:, None] * inner_idx[None, :] % block_len, block_len
    )
    cos_small, sin_small = angle_pair(
        outer_idx[:, None] * outer_idx[None, :] % outer_len, outer_len
    )
    cos_twist, sin_twist = angle_pair(outer_idx[:, None] * inner_idx[None, :], line_len)
    wave_index = outer_idx[:, None] + outer_len * inner_idx[None, :]
    signed = jnp.where(wave_index >= line_len // 2, wave_index - line_len, wave_index)
    kx_grid = signed.astype(jnp.float32) * (2.0 * math.pi / line_len)
    small_fwd = block_matrix(cos_small, sin_small, True)
    small_inv = block_matrix(cos_small, sin_small, False)
    large_fwd = block_matrix(cos_large, sin_large, True)
    large_inv = block_matrix(cos_large, sin_large, False)
    return (small_fwd, small_inv, large_fwd, large_inv, cos_twist, sin_twist, kx_grid)


def forward_line(wavefield, tables):
    small_fwd, small_inv, large_fwd, large_inv, cos_twist, sin_twist, kx_grid = tables
    row_count = wavefield.shape[1]
    pieces = wavefield.reshape(2, row_count, cos_twist.shape[0], cos_twist.shape[1])
    mixed_part = jnp.einsum("zrab,zwca->wrcb", pieces, small_fwd, precision=PRECISE)
    mixed_part = complex_scale(mixed_part, cos_twist, -sin_twist)
    return jnp.einsum("zrcb,zwbd->wrcd", mixed_part, large_fwd, precision=PRECISE)


def inverse_line(spectrum, tables):
    small_fwd, small_inv, large_fwd, large_inv, cos_twist, sin_twist, kx_grid = tables
    row_count = spectrum.shape[1]
    line_len = cos_twist.shape[0] * cos_twist.shape[1]
    mixed_part = jnp.einsum("zrcd,zwdb->wrcb", spectrum, large_inv, precision=PRECISE)
    mixed_part = complex_scale(mixed_part, cos_twist, sin_twist)
    pieces = jnp.einsum("zrcb,zwca->wrab", mixed_part, small_inv, precision=PRECISE)
    return pieces.reshape(2, row_count, line_len) * (1.0 / line_len)


def lookup(regions, entries):
    picked = jnp.zeros(regions.shape, jnp.float32)
    for region_no in range(entries.shape[0]):
        picked = picked + jnp.where(regions == region_no, entries[region_no], 0.0)
    return picked


def depth_step(wavefield, omega_now, slow_cells, coef_cells, ref_slow, tables, pad_rows):
    kx_grid = tables[6]
    wave_ref = omega_now * ref_slow
    excess = wave_ref * wave_ref - kx_grid * kx_grid
    decay_line = jnp.exp(-jnp.sqrt(jnp.maximum(-excess, 0.0)))
    vertical = jnp.sqrt(jnp.maximum(excess, 0.0))
    spectrum = complex_scale(
        forward_line(wavefield, tables),
        decay_line * jnp.cos(vertical),
        decay_line * jnp.sin(vertical),
    )
    wavefield = inverse_line(spectrum, tables)
    phase_cell = omega_now * (slow_cells - ref_slow)
    wavefield = complex_scale(wavefield, jnp.cos(phase_cell), jnp.sin(phase_cell))
    padded = pad_rows(wavefield)
    laplace = (
        padded[:, :-2]
        + padded[:, 2:]
        + jnp.roll(wavefield, 1, 2)
        + jnp.roll(wavefield, -1, 2)
        - 4.0 * wavefield
    )
    return wavefield + complex_scale(laplace, DAMPING, coef_cells / omega_now)


def march(wavefield, omega_now, slow_block, coef_block, ref_block, tables, pad_rows):
    traces = []
    for step_no in range(slow_block.shape[0]):
        wavefield = depth_step(
            wavefield,
            omega_now,
            slow_block[step_no],
            coef_block[step_no],
            ref_block[step_no],
            tables,
            pad_rows,
        )
        traces.append(wavefield[0])
    return (wavefield, jnp.stack(traces))


def shards_general(surface, omegas, region_speed, fd_coeff, region_index, ref_region):
    line_len = surface.shape[3]
    rows_here = surface.shape[2]
    freq_count = surface.shape[1]
    step_count = region_index.shape[0]
    tables = build_tables(line_len)
    inv_speed = 1.0 / region_speed
    segment_no = lax.axis_index("depth")
    segment_count = lax.axis_size("depth")

    def pad_near(values):
        return padded_2(values, (("strip", 1),), 1)

    slow_cells = lookup(region_index, inv_speed)
    coef_cells = lookup(region_index, fd_coeff)
    ref_cells = lookup(ref_region, inv_speed)
    freq_index = jnp.arange(freq_count)
    image_out = jnp.zeros((step_count, rows_here, line_len), jnp.float32)
    arriving = jnp.zeros((2, rows_here, line_len), jnp.float32)
    tick_count = freq_count + segment_count - 1
    for tick_no in range(tick_count):
        batch_no = tick_no - segment_no
        is_live = (batch_no >= 0) & (batch_no < freq_count)
        clipped = jnp.clip(batch_no, 0, freq_count - 1)
        picked = lax.dynamic_index_in_dim(surface, clipped, 1, keepdims=False)
        entering = jnp.where(segment_no == 0, picked, arriving)
        omega_now = jnp.sum(jnp.where(freq_index == clipped, omegas, 0.0))
        leaving, traces = march(
            entering, omega_now, slow_cells, coef_cells, ref_cells, tables, pad_near
        )
        image_out = image_out + jnp.where(is_live, traces, 0.0)
        if tick_no + 1 < tick_count:
            arriving = from_behind(leaving, "depth", 1)
    return image_out


LANE = 128
FFT_BLOCKS = 16
ROW_CHUNK = 8


def fft4(x0, x1, x2, x3, sign):
    s0 = (x0[0] + x2[0], x0[1] + x2[1])
    d0 = (x0[0] - x2[0], x0[1] - x2[1])
    s1 = (x1[0] + x3[0], x1[1] + x3[1])
    d1 = (x1[0] - x3[0], x1[1] - x3[1])
    if sign < 0:
        wd = (d1[1], -d1[0])
    else:
        wd = (-d1[1], d1[0])
    return (
        (s0[0] + s1[0], s0[1] + s1[1]),
        (d0[0] + wd[0], d0[1] + wd[1]),
        (s0[0] - s1[0], s0[1] - s1[1]),
        (d0[0] - wd[0], d0[1] - wd[1]),
    )


def turn_const(value, power, sign):
    if power == 4:
        return (-value[1], value[0]) if sign > 0 else (value[1], -value[0])
    angle = sign * 2.0 * math.pi * power / 16.0
    cr, ci = (math.cos(angle), math.sin(angle))
    return (value[0] * cr - value[1] * ci, value[0] * ci + value[1] * cr)


def fft16(parts, sign):
    mid = [[None] * 4 for _ in range(4)]
    for a0 in range(4):
        ys = fft4(parts[a0], parts[4 + a0], parts[8 + a0], parts[12 + a0], sign)
        for c0 in range(4):
            power = a0 * c0
            mid[a0][c0] = ys[c0] if power == 0 else turn_const(ys[c0], power, sign)
    out = [None] * 16
    for c0 in range(4):
        zs = fft4(mid[0][c0], mid[1][c0], mid[2][c0], mid[3][c0], sign)
        for c1 in range(4):
            out[c0 + 4 * c1] = zs[c1]
    return out


def pick(regions, values):
    level = list(values)
    bit = 1
    while len(level) > 1:
        chosen = (regions & bit) != 0
        level = [jnp.where(chosen, level[i + 1], level[i]) for i in range(0, len(level), 2)]
        bit *= 2
    return jnp.broadcast_to(level[0], regions.shape)


def pick_bits(bits, values):
    level = list(values)
    for chosen in bits:
        level = [jnp.where(chosen, level[i + 1], level[i]) for i in range(0, len(level), 2)]
    return jnp.broadcast_to(level[0], bits[0].shape)


def split_dot(values, hi_ref, lo_ref):
    high = values.astype(jnp.bfloat16)
    low = (values - high.astype(jnp.float32)).astype(jnp.bfloat16)
    main = jnp.dot(high, hi_ref[...], preferred_element_type=jnp.float32)
    fix = jnp.dot(high, lo_ref[...], preferred_element_type=jnp.float32) + jnp.dot(
        low, hi_ref[:, :], preferred_element_type=jnp.float32
    )
    return main + fix


def section_kernel(
    tab_ref, w_ref, rid_ref, mult_ref, tw_ref, fhi_ref, flo_ref, ghi_ref, glo_ref,
    wout_ref, img_ref, a_ref, y_ref, v_ref, cs_ref, sn_ref, gn_ref, *, table_len
):
    rows = w_ref.shape[1]
    line_len = w_ref.shape[2]
    steps = rid_ref.shape[0]
    strip_count, rows_here = img_ref.shape[0], img_ref.shape[2]
    chunks = rows // ROW_CHUNK
    inv_len = 1.0 / line_len
    wout_ref[...] = w_ref[...]

    def blk(a):
        return slice(a * LANE, (a + 1) * LANE)

    def one_step(k, carry):
        base = k * (3 * table_len)
        cos_t = [tab_ref[base + g] for g in range(table_len)]
        sin_t = [tab_ref[base + table_len + g] for g in range(table_len)]
        gain_t = [tab_ref[base + 2 * table_len + g] for g in range(table_len)]

        def forward_chunk(i, c):
            y0 = pl.multiple_of(i * ROW_CHUNK, ROW_CHUNK)
            parts = [
                (wout_ref[0, pl.ds(y0, ROW_CHUNK), blk(a)], wout_ref[1, pl.ds(y0, ROW_CHUNK), blk(a)])
                for a in range(FFT_BLOCKS)
            ]
            spec = fft16(parts, -1)
            for cc in range(FFT_BLOCKS):
                tc = tw_ref[0, cc:cc + 1, :]
                ts = tw_ref[1, cc:cc + 1, :]
                xr, xi = spec[cc]
                a_ref[pl.ds(cc * rows + y0, ROW_CHUNK), 0:LANE] = xr * tc + xi * ts
                a_ref[pl.ds(cc * rows + y0, ROW_CHUNK), LANE:2 * LANE] = xi * tc - xr * ts
            return c

        lax.fori_loop(0, chunks, forward_chunk, 0)
        spectrum = split_dot(a_ref[...], fhi_ref, flo_ref)
        for a in range(FFT_BLOCKS):
            regions = rid_ref[k, :, blk(a)]
            bits = [(regions & (1 << b)) != 0 for b in range(max(1, (table_len - 1).bit_length()))]
            cs_ref[:, blk(a)] = pick_bits(bits, cos_t)
            sn_ref[:, blk(a)] = pick_bits(bits, sin_t)
            gn_ref[:, blk(a)] = pick_bits(bits, gain_t)
        y_ref[...] = spectrum
        for cc in range(FFT_BLOCKS):
            band = slice(cc * rows, (cc + 1) * rows)
            yr = y_ref[band, 0:LANE]
            yi = y_ref[band, LANE:2 * LANE]
            mr = mult_ref[k, 0, cc:cc + 1, :]
            mi = mult_ref[k, 1, cc:cc + 1, :]
            a_ref[band, 0:LANE] = yr * mr - yi * mi
            a_ref[band, LANE:2 * LANE] = yr * mi + yi * mr
        y_ref[...] = split_dot(a_ref[...], ghi_ref, glo_ref)

        def inverse_chunk(i, c):
            y0 = pl.multiple_of(i * ROW_CHUNK, ROW_CHUNK)
            parts = []
            for cc in range(FFT_BLOCKS):
                zr = y_ref[pl.ds(cc * rows + y0, ROW_CHUNK), 0:LANE]
                zi = y_ref[pl.ds(cc * rows + y0, ROW_CHUNK), LANE:2 * LANE]
                tc = tw_ref[0, cc:cc + 1, :]
                ts = tw_ref[1, cc:cc + 1, :]
                parts.append((zr * tc - zi * ts, zr * ts + zi * tc))
            back = fft16(parts, 1)
            for a in range(FFT_BLOCKS):
                ur = back[a][0] * inv_len
                ui = back[a][1] * inv_len
                cs = cs_ref[pl.ds(y0, ROW_CHUNK), blk(a)]
                sn = sn_ref[pl.ds(y0, ROW_CHUNK), blk(a)]
                v_ref[0, pl.ds(y0, ROW_CHUNK), blk(a)] = ur * cs - ui * sn
                v_ref[1, pl.ds(y0, ROW_CHUNK), blk(a)] = ur * sn + ui * cs
            return c

        lax.fori_loop(0, chunks, inverse_chunk, 0)
        row_id = lax.broadcasted_iota(jnp.int32, (rows, LANE), 0)
        lane_id = lax.broadcasted_iota(jnp.int32, (rows, LANE), 1)
        cache = {}

        def cell(part, a):
            key = (part, a % FFT_BLOCKS)
            if key not in cache:
                v = v_ref[part, :, blk(a % FFT_BLOCKS)]
                cache[key] = (v, pltpu.roll(v, 1, 1), pltpu.roll(v, LANE - 1, 1))
            return cache[key]

        for a in range(FFT_BLOCKS):
            lap = []
            here = []
            for part in range(2):
                v, from_left, from_right = cell(part, a)
                prev_left = cell(part, a - 1)[1]
                next_right = cell(part, a + 1)[2]
                above = jnp.where(row_id == 0, 0.0, pltpu.roll(v, 1, 0))
                below = jnp.where(row_id == rows - 1, 0.0, pltpu.roll(v, rows - 1, 0))
                left = jnp.where(lane_id == 0, prev_left, from_left)
                right = jnp.where(lane_id == LANE - 1, next_right, from_right)
                lap.append(above + below + left + right - 4.0 * v)
                here.append(v)
            gain = gn_ref[:, blk(a)]
            new_re = here[0] + (lap[0] * DAMPING - lap[1] * gain)
            new_im = here[1] + (lap[0] * gain + lap[1] * DAMPING)
            wout_ref[0, :, blk(a)] = new_re
            wout_ref[1, :, blk(a)] = new_im
            for j in range(strip_count):
                img_ref[j, k, :, blk(a)] = new_re[j * rows_here:(j + 1) * rows_here]
        return carry

    lax.fori_loop(0, steps, one_step, 0)


def fast_constants(line_len):
    outer = line_len // LANE
    b = np.arange(LANE)
    ang = 2.0 * np.pi * (np.outer(b, b) % LANE) / LANE
    cos_m, sin_m = (np.cos(ang), np.sin(ang))
    fwd = np.block([[cos_m, -sin_m], [sin_m, cos_m]])
    inv = np.block([[cos_m, sin_m], [-sin_m, cos_m]])

    def halves(m):
        hi = m.astype(ml_dtypes.bfloat16)
        lo = (m - hi.astype(np.float64)).astype(ml_dtypes.bfloat16)
        return (hi, lo)

    c = np.arange(outer)
    tw_ang = 2.0 * np.pi * np.outer(c, b) / line_len
    twiddle = np.stack([np.cos(tw_ang), np.sin(tw_ang)]).astype(np.float32)
    q = c[:, None] + outer * b[None, :]
    signed = np.where(q >= line_len // 2, q - line_len, q).astype(np.float32)
    kx_cd = signed * np.float32(2.0 * math.pi / line_len)
    return (halves(fwd), halves(inv), twiddle, kx_cd.astype(np.float32))


def run_section(wave, regions, table, mult, consts, strip_count):
    (fhi, flo), (ghi, glo), twiddle, _ = consts
    rows, line_len = wave.shape[1], wave.shape[2]
    steps = regions.shape[0]
    table_len = table.shape[0] // (3 * steps)
    vmem = pl.BlockSpec(memory_space=pltpu.VMEM)
    flops = steps * (2 * 3 * 2 * (FFT_BLOCKS * rows) * 256 * 256 + 400 * rows * line_len)
    return pl.pallas_call(
        lambda *refs: section_kernel(*refs, table_len=table_len),
        out_shape=(
            jax.ShapeDtypeStruct(wave.shape, jnp.float32),
            jax.ShapeDtypeStruct((strip_count, steps, rows // strip_count, line_len), jnp.float32),
        ),
        in_specs=[pl.BlockSpec(memory_space=pltpu.SMEM)] + [vmem] * 8,
        out_specs=(vmem, vmem),
        scratch_shapes=[
            pltpu.VMEM((FFT_BLOCKS * rows, 2 * LANE), jnp.float32),
            pltpu.VMEM((FFT_BLOCKS * rows, 2 * LANE), jnp.float32),
            pltpu.VMEM((2, rows, line_len), jnp.float32),
            pltpu.VMEM((rows, line_len), jnp.float32),
            pltpu.VMEM((rows, line_len), jnp.float32),
            pltpu.VMEM((rows, line_len), jnp.float32),
        ],
        cost_estimate=pl.CostEstimate(
            flops=flops, transcendentals=0, bytes_accessed=4 * rows * line_len * 6 * steps
        ),
    )(table, wave, regions, mult, jnp.asarray(twiddle), jnp.asarray(fhi), jnp.asarray(flo),
      jnp.asarray(ghi), jnp.asarray(glo))


def section_tables(omega, region_speed, fd_coeff, ref_region, kx_cd):
    inv_speed = 1.0 / region_speed
    ref_slow = inv_speed[ref_region]
    regions = region_speed.shape[0]
    padded = 1 << max(1, (regions - 1).bit_length())
    extra = padded - regions
    phase = omega * (inv_speed[None, :] - ref_slow[:, None])
    gain = jnp.broadcast_to(fd_coeff / omega, phase.shape)
    parts = [jnp.cos(phase), jnp.sin(phase), gain]
    if extra:
        parts = [jnp.concatenate([p, jnp.repeat(p[:, -1:], extra, axis=1)], axis=1) for p in parts]
    table = jnp.stack(parts, axis=1).reshape(-1)
    wave_ref = omega * ref_slow
    wave_ref = wave_ref[:, None, None]
    excess = wave_ref * wave_ref - kx_cd * kx_cd
    decay_line = jnp.exp(-jnp.sqrt(jnp.maximum(-excess, 0.0)))
    vertical = jnp.sqrt(jnp.maximum(excess, 0.0))
    mult = jnp.stack([decay_line * jnp.cos(vertical), decay_line * jnp.sin(vertical)], axis=1)
    return (table, mult)


def fast_fits(surface, region_index, region_speed):
    freq_count = surface.shape[1]
    rows = surface.shape[2] * lax.axis_size("strip")
    line_len = surface.shape[3]
    return (
        freq_count == lax.axis_size("strip")
        and line_len == FFT_BLOCKS * LANE
        and rows % ROW_CHUNK == 0
        and surface.shape[2] % ROW_CHUNK == 0
        and rows <= 64
        and region_speed.shape[0] <= 16
    )


def strip_pairs(depths, strip_count, shift):
    return [
        (d * strip_count + r, d * strip_count + (r + shift) % strip_count)
        for d in depths
        for r in range(strip_count)
    ]


def gather_rows(local, depths, strip_no, strip_count, row_axis):
    rows = local.shape[row_axis]
    shape = list(local.shape)
    shape[row_axis] = rows * strip_count
    full = jnp.zeros(shape, local.dtype)
    start = [0] * len(shape)
    start[row_axis] = strip_no * rows
    full = lax.dynamic_update_slice(full, local, start)
    for shift in range(1, strip_count):
        got = lax.ppermute(local, ("depth", "strip"), strip_pairs(depths, strip_count, shift))
        start = [0] * len(shape)
        start[row_axis] = ((strip_no - shift) % strip_count) * rows
        full = lax.dynamic_update_slice(full, got, start)
    return full


def gather_strips(piece_of, local, depths, strip_no, strip_count, rows_here):
    rows = rows_here * strip_count
    shape = (local.shape[0], rows, local.shape[2])
    full = lax.dynamic_update_slice(
        jnp.zeros(shape, jnp.float32), local, (0, strip_no * rows_here, 0)
    )
    for shift in range(1, strip_count):
        target = (strip_no + shift) % strip_count
        got = lax.ppermute(
            piece_of(target), ("depth", "strip"), strip_pairs(depths, strip_count, shift)
        )
        source = (strip_no - shift) % strip_count
        full = lax.dynamic_update_slice(full, got, (0, source * rows_here, 0))
    return full


def shards(surface, omegas, region_speed, fd_coeff, region_index, ref_region):
    if not fast_fits(surface, region_index, region_speed):
        return shards_general(surface, omegas, region_speed, fd_coeff, region_index, ref_region)
    line_len = surface.shape[3]
    rows_here = surface.shape[2]
    steps = region_index.shape[0]
    segment_no = lax.axis_index("depth")
    segment_count = lax.axis_size("depth")
    strip_no = lax.axis_index("strip")
    strip_count = lax.axis_size("strip")
    consts = fast_constants(line_len)
    region_f = region_index.astype(jnp.float32)
    early = [d for d in range(segment_count) if d != 1]

    def with_surface(target):
        return jnp.concatenate(
            [region_f, lax.dynamic_index_in_dim(surface, target, 1, keepdims=False)], axis=0
        )

    gathered = gather_strips(
        with_surface, with_surface(strip_no), early, strip_no, strip_count, rows_here
    )
    regions_a = gathered[:steps].astype(jnp.int32)
    wave = gathered[steps:]
    omega = lax.dynamic_index_in_dim(omegas, strip_no, 0, keepdims=False)
    table, mult = section_tables(omega, region_speed, fd_coeff, ref_region, jnp.asarray(consts[3]))
    image = jnp.zeros((strip_count, steps, rows_here, line_len), jnp.float32)
    regions_b = regions_a
    if segment_count > 1:
        token = lax.ppermute(gathered[0, 0:8, 0:LANE], "depth", [(0, 1)])

    def sweep(regions):
        def live(wave, image):
            return run_section(wave, regions, table, mult, consts, strip_count)

        return live

    def idle(wave, image):
        return (wave, image)

    def freq_sum(image, depths):
        parts = []
        for shift in range(1, strip_count):
            target = (strip_no + shift) % strip_count
            piece = lax.dynamic_index_in_dim(image, target, 0, keepdims=False)
            parts.append(
                lax.ppermute(piece, ("depth", "strip"), strip_pairs(depths, strip_count, shift))
            )
        return parts

    arrived = []
    for tick_no in range(segment_count):
        regions = regions_b if tick_no == 1 else regions_a
        wave, image = lax.cond(segment_no == tick_no, sweep(regions), idle, wave, image)
        if tick_no + 1 < segment_count:
            wave = lax.ppermute(wave, "depth", [(tick_no, tick_no + 1)])
        if tick_no == 0 and segment_count > 1:
            held, token, _ = lax.optimization_barrier((region_f, token, image))
            held = held + 0.0 * token[0, 0]
            regions_b = gather_strips(
                lambda target: held, held, [1], strip_no, strip_count, rows_here
            ).astype(jnp.int32)
        if tick_no == segment_count - 2:
            wave, image = lax.optimization_barrier((wave, image))
            arrived += freq_sum(image, range(segment_count - 1))
    arrived += freq_sum(image, [segment_count - 1])
    total = lax.dynamic_index_in_dim(image, strip_no, 0, keepdims=False)
    for piece in arrived:
        total = total + piece
    return total


def solution(mesh):
    in_specs = (
        P(None, "shots", "strip", None),
        P(),
        P(),
        P(),
        P("depth", "strip", None),
        P("depth"),
    )
    out_specs = P("depth", "strip", "shots")
    return jax.shard_map(shards, mesh=mesh, in_specs=in_specs, out_specs=out_specs, check_vma=False)
```

```python
import math

import ml_dtypes
import numpy as np
import jax
import jax.numpy as jnp
from jax import lax
from jax.experimental import pallas as pl
from jax.experimental.pallas import tpu as pltpu
from jax.sharding import PartitionSpec as P

DAMPING = 0.05
PRECISE = lax.Precision.HIGHEST


def padded_2(cells, sides, width):
    for axis, dim in sides:
        count = lax.axis_size(axis)
        ends = count - 1
        head = lax.slice_in_dim(cells, 0, width, axis=dim)
        tail = lax.slice_in_dim(cells, cells.shape[dim] - width, cells.shape[dim], axis=dim)
        cells = jnp.concatenate(
            [
                lax.ppermute(tail, axis, [(i, (i + 1) % count) for i in range(ends)]),
                cells,
                lax.ppermute(head, axis, [((i + 1) % count, i) for i in range(ends)]),
            ],
            axis=dim,
        )
    return cells


def from_behind(value, axis, steps):
    count = lax.axis_size(axis)
    first, last = (max(0, -steps), min(count, count - steps))
    return lax.ppermute(value, axis, [(source, source + steps) for source in range(first, last)])


def complex_scale(values, cosine, sine_part):
    return jnp.stack(
        [values[0] * cosine - values[1] * sine_part, values[0] * sine_part + values[1] * cosine]
    )


def angle_pair(numerator, period):
    angle_grid = numerator.astype(jnp.float32) * (2.0 * math.pi / period)
    return (jnp.cos(angle_grid), jnp.sin(angle_grid))


def block_matrix(cosine, sine_part, forward):
    sign_flip = 1.0 if forward else -1.0
    return jnp.stack(
        [jnp.stack([cosine, -sign_flip * sine_part]), jnp.stack([sign_flip * sine_part, cosine])]
    )


def build_tables(line_len):
    block_len = 128
    outer_len = line_len // block_len
    inner_idx = jnp.arange(block_len)
    outer_idx = jnp.arange(outer_len)
    cos_large, sin_large = angle_pair(
        inner_idx[:, None] * inner_idx[None, :] % block_len, block_len
    )
    cos_small, sin_small = angle_pair(
        outer_idx[:, None] * outer_idx[None, :] % outer_len, outer_len
    )
    cos_twist, sin_twist = angle_pair(outer_idx[:, None] * inner_idx[None, :], line_len)
    wave_index = outer_idx[:, None] + outer_len * inner_idx[None, :]
    signed = jnp.where(wave_index >= line_len // 2, wave_index - line_len, wave_index)
    kx_grid = signed.astype(jnp.float32) * (2.0 * math.pi / line_len)
    small_fwd = block_matrix(cos_small, sin_small, True)
    small_inv = block_matrix(cos_small, sin_small, False)
    large_fwd = block_matrix(cos_large, sin_large, True)
    large_inv = block_matrix(cos_large, sin_large, False)
    return (small_fwd, small_inv, large_fwd, large_inv, cos_twist, sin_twist, kx_grid)


def forward_line(wavefield, tables):
    small_fwd, small_inv, large_fwd, large_inv, cos_twist, sin_twist, kx_grid = tables
    row_count = wavefield.shape[1]
    pieces = wavefield.reshape(2, row_count, cos_twist.shape[0], cos_twist.shape[1])
    mixed_part = jnp.einsum("zrab,zwca->wrcb", pieces, small_fwd, precision=PRECISE)
    mixed_part = complex_scale(mixed_part, cos_twist, -sin_twist)
    return jnp.einsum("zrcb,zwbd->wrcd", mixed_part, large_fwd, precision=PRECISE)


def inverse_line(spectrum, tables):
    small_fwd, small_inv, large_fwd, large_inv, cos_twist, sin_twist, kx_grid = tables
    row_count = spectrum.shape[1]
    line_len = cos_twist.shape[0] * cos_twist.shape[1]
    mixed_part = jnp.einsum("zrcd,zwdb->wrcb", spectrum, large_inv, precision=PRECISE)
    mixed_part = complex_scale(mixed_part, cos_twist, sin_twist)
    pieces = jnp.einsum("zrcb,zwca->wrab", mixed_part, small_inv, precision=PRECISE)
    return pieces.reshape(2, row_count, line_len) * (1.0 / line_len)


def lookup(regions, entries):
    picked = jnp.zeros(regions.shape, jnp.float32)
    for region_no in range(entries.shape[0]):
        picked = picked + jnp.where(regions == region_no, entries[region_no], 0.0)
    return picked


def depth_step(wavefield, omega_now, slow_cells, coef_cells, ref_slow, tables, pad_rows):
    kx_grid = tables[6]
    wave_ref = omega_now * ref_slow
    excess = wave_ref * wave_ref - kx_grid * kx_grid
    decay_line = jnp.exp(-jnp.sqrt(jnp.maximum(-excess, 0.0)))
    vertical = jnp.sqrt(jnp.maximum(excess, 0.0))
    spectrum = complex_scale(
        forward_line(wavefield, tables),
        decay_line * jnp.cos(vertical),
        decay_line * jnp.sin(vertical),
    )
    wavefield = inverse_line(spectrum, tables)
    phase_cell = omega_now * (slow_cells - ref_slow)
    wavefield = complex_scale(wavefield, jnp.cos(phase_cell), jnp.sin(phase_cell))
    padded = pad_rows(wavefield)
    laplace = (
        padded[:, :-2]
        + padded[:, 2:]
        + jnp.roll(wavefield, 1, 2)
        + jnp.roll(wavefield, -1, 2)
        - 4.0 * wavefield
    )
    return wavefield + complex_scale(laplace, DAMPING, coef_cells / omega_now)


def march(wavefield, omega_now, slow_block, coef_block, ref_block, tables, pad_rows):
    traces = []
    for step_no in range(slow_block.shape[0]):
        wavefield = depth_step(
            wavefield,
            omega_now,
            slow_block[step_no],
            coef_block[step_no],
            ref_block[step_no],
            tables,
            pad_rows,
        )
        traces.append(wavefield[0])
    return (wavefield, jnp.stack(traces))


def shards_general(surface, omegas, region_speed, fd_coeff, region_index, ref_region):
    line_len = surface.shape[3]
    rows_here = surface.shape[2]
    freq_count = surface.shape[1]
    step_count = region_index.shape[0]
    tables = build_tables(line_len)
    inv_speed = 1.0 / region_speed
    segment_no = lax.axis_index("depth")
    segment_count = lax.axis_size("depth")

    def pad_near(values):
        return padded_2(values, (("strip", 1),), 1)

    slow_cells = lookup(region_index, inv_speed)
    coef_cells = lookup(region_index, fd_coeff)
    ref_cells = lookup(ref_region, inv_speed)
    freq_index = jnp.arange(freq_count)
    image_out = jnp.zeros((step_count, rows_here, line_len), jnp.float32)
    arriving = jnp.zeros((2, rows_here, line_len), jnp.float32)
    tick_count = freq_count + segment_count - 1
    for tick_no in range(tick_count):
        batch_no = tick_no - segment_no
        is_live = (batch_no >= 0) & (batch_no < freq_count)
        clipped = jnp.clip(batch_no, 0, freq_count - 1)
        picked = lax.dynamic_index_in_dim(surface, clipped, 1, keepdims=False)
        entering = jnp.where(segment_no == 0, picked, arriving)
        omega_now = jnp.sum(jnp.where(freq_index == clipped, omegas, 0.0))
        leaving, traces = march(
            entering, omega_now, slow_cells, coef_cells, ref_cells, tables, pad_near
        )
        image_out = image_out + jnp.where(is_live, traces, 0.0)
        if tick_no + 1 < tick_count:
            arriving = from_behind(leaving, "depth", 1)
    return image_out


LANE = 128
FFT_BLOCKS = 16
ROW_CHUNK = 8


def fft4(x0, x1, x2, x3, sign):
    s0 = (x0[0] + x2[0], x0[1] + x2[1])
    d0 = (x0[0] - x2[0], x0[1] - x2[1])
    s1 = (x1[0] + x3[0], x1[1] + x3[1])
    d1 = (x1[0] - x3[0], x1[1] - x3[1])
    if sign < 0:
        wd = (d1[1], -d1[0])
    else:
        wd = (-d1[1], d1[0])
    return (
        (s0[0] + s1[0], s0[1] + s1[1]),
        (d0[0] + wd[0], d0[1] + wd[1]),
        (s0[0] - s1[0], s0[1] - s1[1]),
        (d0[0] - wd[0], d0[1] - wd[1]),
    )


def turn_const(value, power, sign):
    if power == 4:
        return (-value[1], value[0]) if sign > 0 else (value[1], -value[0])
    angle = sign * 2.0 * math.pi * power / 16.0
    cr, ci = (math.cos(angle), math.sin(angle))
    return (value[0] * cr - value[1] * ci, value[0] * ci + value[1] * cr)


def fft16(parts, sign):
    mid = [[None] * 4 for _ in range(4)]
    for a0 in range(4):
        ys = fft4(parts[a0], parts[4 + a0], parts[8 + a0], parts[12 + a0], sign)
        for c0 in range(4):
            power = a0 * c0
            mid[a0][c0] = ys[c0] if power == 0 else turn_const(ys[c0], power, sign)
    out = [None] * 16
    for c0 in range(4):
        zs = fft4(mid[0][c0], mid[1][c0], mid[2][c0], mid[3][c0], sign)
        for c1 in range(4):
            out[c0 + 4 * c1] = zs[c1]
    return out


def pick(regions, values):
    level = list(values)
    bit = 1
    while len(level) > 1:
        chosen = (regions & bit) != 0
        level = [jnp.where(chosen, level[i + 1], level[i]) for i in range(0, len(level), 2)]
        bit *= 2
    return jnp.broadcast_to(level[0], regions.shape)


def pick_bits(bits, values):
    level = list(values)
    for chosen in bits:
        level = [jnp.where(chosen, level[i + 1], level[i]) for i in range(0, len(level), 2)]
    return jnp.broadcast_to(level[0], bits[0].shape)


def split_dot(values, hi_ref, lo_ref):
    high = values.astype(jnp.bfloat16)
    low = (values - high.astype(jnp.float32)).astype(jnp.bfloat16)
    main = jnp.dot(high, hi_ref[...], preferred_element_type=jnp.float32)
    fix = jnp.dot(high, lo_ref[...], preferred_element_type=jnp.float32) + jnp.dot(
        low, hi_ref[:, :], preferred_element_type=jnp.float32
    )
    return main + fix


def section_kernel(
    tab_ref, w_ref, rid_ref, mult_ref, tw_ref, fhi_ref, flo_ref, ghi_ref, glo_ref,
    wout_ref, img_ref, a_ref, y_ref, v_ref, cs_ref, sn_ref, gn_ref, *, table_len
):
    rows = w_ref.shape[1]
    line_len = w_ref.shape[2]
    steps = rid_ref.shape[0]
    strip_count, rows_here = img_ref.shape[0], img_ref.shape[2]
    chunks = rows // ROW_CHUNK
    inv_len = 1.0 / line_len
    wout_ref[...] = w_ref[...]

    def blk(a):
        return slice(a * LANE, (a + 1) * LANE)

    def one_step(k, carry):
        base = k * (3 * table_len)
        cos_t = [tab_ref[base + g] for g in range(table_len)]
        sin_t = [tab_ref[base + table_len + g] for g in range(table_len)]
        gain_t = [tab_ref[base + 2 * table_len + g] for g in range(table_len)]

        def forward_chunk(i, c):
            y0 = pl.multiple_of(i * ROW_CHUNK, ROW_CHUNK)
            parts = [
                (wout_ref[0, pl.ds(y0, ROW_CHUNK), blk(a)], wout_ref[1, pl.ds(y0, ROW_CHUNK), blk(a)])
                for a in range(FFT_BLOCKS)
            ]
            spec = fft16(parts, -1)
            for cc in range(FFT_BLOCKS):
                tc = tw_ref[0, cc:cc + 1, :]
                ts = tw_ref[1, cc:cc + 1, :]
                xr, xi = spec[cc]
                a_ref[pl.ds(cc * rows + y0, ROW_CHUNK), 0:LANE] = xr * tc + xi * ts
                a_ref[pl.ds(cc * rows + y0, ROW_CHUNK), LANE:2 * LANE] = xi * tc - xr * ts
            return c

        lax.fori_loop(0, chunks, forward_chunk, 0)
        spectrum = split_dot(a_ref[...], fhi_ref, flo_ref)
        for a in range(FFT_BLOCKS):
            regions = rid_ref[k, :, blk(a)]
            bits = [(regions & (1 << b)) != 0 for b in range(max(1, (table_len - 1).bit_length()))]
            cs_ref[:, blk(a)] = pick_bits(bits, cos_t)
            sn_ref[:, blk(a)] = pick_bits(bits, sin_t)
            gn_ref[:, blk(a)] = pick_bits(bits, gain_t)
        y_ref[...] = spectrum
        for cc in range(FFT_BLOCKS):
            band = slice(cc * rows, (cc + 1) * rows)
            yr = y_ref[band, 0:LANE]
            yi = y_ref[band, LANE:2 * LANE]
            mr = mult_ref[k, 0, cc:cc + 1, :]
            mi = mult_ref[k, 1, cc:cc + 1, :]
            a_ref[band, 0:LANE] = yr * mr - yi * mi
            a_ref[band, LANE:2 * LANE] = yr * mi + yi * mr
        y_ref[...] = split_dot(a_ref[...], ghi_ref, glo_ref)

        def inverse_chunk(i, c):
            y0 = pl.multiple_of(i * ROW_CHUNK, ROW_CHUNK)
            parts = []
            for cc in range(FFT_BLOCKS):
                zr = y_ref[pl.ds(cc * rows + y0, ROW_CHUNK), 0:LANE]
                zi = y_ref[pl.ds(cc * rows + y0, ROW_CHUNK), LANE:2 * LANE]
                tc = tw_ref[0, cc:cc + 1, :]
                ts = tw_ref[1, cc:cc + 1, :]
                parts.append((zr * tc - zi * ts, zr * ts + zi * tc))
            back = fft16(parts, 1)
            for a in range(FFT_BLOCKS):
                ur = back[a][0] * inv_len
                ui = back[a][1] * inv_len
                cs = cs_ref[pl.ds(y0, ROW_CHUNK), blk(a)]
                sn = sn_ref[pl.ds(y0, ROW_CHUNK), blk(a)]
                v_ref[0, pl.ds(y0, ROW_CHUNK), blk(a)] = ur * cs - ui * sn
                v_ref[1, pl.ds(y0, ROW_CHUNK), blk(a)] = ur * sn + ui * cs
            return c

        lax.fori_loop(0, chunks, inverse_chunk, 0)
        row_id = lax.broadcasted_iota(jnp.int32, (rows, LANE), 0)
        lane_id = lax.broadcasted_iota(jnp.int32, (rows, LANE), 1)
        cache = {}

        def cell(part, a):
            key = (part, a % FFT_BLOCKS)
            if key not in cache:
                v = v_ref[part, :, blk(a % FFT_BLOCKS)]
                cache[key] = (v, pltpu.roll(v, 1, 1), pltpu.roll(v, LANE - 1, 1))
            return cache[key]

        for a in range(FFT_BLOCKS):
            lap = []
            here = []
            for part in range(2):
                v, from_left, from_right = cell(part, a)
                prev_left = cell(part, a - 1)[1]
                next_right = cell(part, a + 1)[2]
                above = jnp.where(row_id == 0, 0.0, pltpu.roll(v, 1, 0))
                below = jnp.where(row_id == rows - 1, 0.0, pltpu.roll(v, rows - 1, 0))
                left = jnp.where(lane_id == 0, prev_left, from_left)
                right = jnp.where(lane_id == LANE - 1, next_right, from_right)
                lap.append(above + below + left + right - 4.0 * v)
                here.append(v)
            gain = gn_ref[:, blk(a)]
            new_re = here[0] + (lap[0] * DAMPING - lap[1] * gain)
            new_im = here[1] + (lap[0] * gain + lap[1] * DAMPING)
            wout_ref[0, :, blk(a)] = new_re
            wout_ref[1, :, blk(a)] = new_im
            for j in range(strip_count):
                img_ref[j, k, :, blk(a)] = new_re[j * rows_here:(j + 1) * rows_here]
        return carry

    lax.fori_loop(0, steps, one_step, 0)


def fast_constants(line_len):
    outer = line_len // LANE
    b = np.arange(LANE)
    ang = 2.0 * np.pi * (np.outer(b, b) % LANE) / LANE
    cos_m, sin_m = (np.cos(ang), np.sin(ang))
    fwd = np.block([[cos_m, -sin_m], [sin_m, cos_m]])
    inv = np.block([[cos_m, sin_m], [-sin_m, cos_m]])

    def halves(m):
        hi = m.astype(ml_dtypes.bfloat16)
        lo = (m - hi.astype(np.float64)).astype(ml_dtypes.bfloat16)
        return (hi, lo)

    c = np.arange(outer)
    tw_ang = 2.0 * np.pi * np.outer(c, b) / line_len
    twiddle = np.stack([np.cos(tw_ang), np.sin(tw_ang)]).astype(np.float32)
    q = c[:, None] + outer * b[None, :]
    signed = np.where(q >= line_len // 2, q - line_len, q).astype(np.float32)
    kx_cd = signed * np.float32(2.0 * math.pi / line_len)
    return (halves(fwd), halves(inv), twiddle, kx_cd.astype(np.float32))


def run_section(wave, regions, table, mult, consts, strip_count):
    (fhi, flo), (ghi, glo), twiddle, _ = consts
    rows, line_len = wave.shape[1], wave.shape[2]
    steps = regions.shape[0]
    table_len = table.shape[0] // (3 * steps)
    vmem = pl.BlockSpec(memory_space=pltpu.VMEM)
    flops = steps * (2 * 3 * 2 * (FFT_BLOCKS * rows) * 256 * 256 + 400 * rows * line_len)
    return pl.pallas_call(
        lambda *refs: section_kernel(*refs, table_len=table_len),
        out_shape=(
            jax.ShapeDtypeStruct(wave.shape, jnp.float32),
            jax.ShapeDtypeStruct((strip_count, steps, rows // strip_count, line_len), jnp.float32),
        ),
        in_specs=[pl.BlockSpec(memory_space=pltpu.SMEM)] + [vmem] * 8,
        out_specs=(vmem, vmem),
        scratch_shapes=[
            pltpu.VMEM((FFT_BLOCKS * rows, 2 * LANE), jnp.float32),
            pltpu.VMEM((FFT_BLOCKS * rows, 2 * LANE), jnp.float32),
            pltpu.VMEM((2, rows, line_len), jnp.float32),
            pltpu.VMEM((rows, line_len), jnp.float32),
            pltpu.VMEM((rows, line_len), jnp.float32),
            pltpu.VMEM((rows, line_len), jnp.float32),
        ],
        cost_estimate=pl.CostEstimate(
            flops=flops, transcendentals=0, bytes_accessed=4 * rows * line_len * 6 * steps
        ),
    )(table, wave, regions, mult, jnp.asarray(twiddle), jnp.asarray(fhi), jnp.asarray(flo),
      jnp.asarray(ghi), jnp.asarray(glo))


def section_tables(omega, region_speed, fd_coeff, ref_region, kx_cd):
    inv_speed = 1.0 / region_speed
    ref_slow = inv_speed[ref_region]
    regions = region_speed.shape[0]
    padded = 1 << max(1, (regions - 1).bit_length())
    extra = padded - regions
    phase = omega * (inv_speed[None, :] - ref_slow[:, None])
    gain = jnp.broadcast_to(fd_coeff / omega, phase.shape)
    parts = [jnp.cos(phase), jnp.sin(phase), gain]
    if extra:
        parts = [jnp.concatenate([p, jnp.repeat(p[:, -1:], extra, axis=1)], axis=1) for p in parts]
    table = jnp.stack(parts, axis=1).reshape(-1)
    wave_ref = omega * ref_slow
    wave_ref = wave_ref[:, None, None]
    excess = wave_ref * wave_ref - kx_cd * kx_cd
    decay_line = jnp.exp(-jnp.sqrt(jnp.maximum(-excess, 0.0)))
    vertical = jnp.sqrt(jnp.maximum(excess, 0.0))
    mult = jnp.stack([decay_line * jnp.cos(vertical), decay_line * jnp.sin(vertical)], axis=1)
    return (table, mult)


def fast_fits(surface, region_index, region_speed):
    freq_count = surface.shape[1]
    rows = surface.shape[2] * lax.axis_size("strip")
    line_len = surface.shape[3]
    return (
        freq_count == lax.axis_size("strip")
        and line_len == FFT_BLOCKS * LANE
        and rows % ROW_CHUNK == 0
        and surface.shape[2] % ROW_CHUNK == 0
        and rows <= 64
        and region_speed.shape[0] <= 16
    )


def strip_pairs(depths, strip_count, shift):
    return [
        (d * strip_count + r, d * strip_count + (r + shift) % strip_count)
        for d in depths
        for r in range(strip_count)
    ]


def gather_rows(local, depths, strip_no, strip_count, row_axis):
    rows = local.shape[row_axis]
    shape = list(local.shape)
    shape[row_axis] = rows * strip_count
    full = jnp.zeros(shape, local.dtype)
    start = [0] * len(shape)
    start[row_axis] = strip_no * rows
    full = lax.dynamic_update_slice(full, local, start)
    for shift in range(1, strip_count):
        got = lax.ppermute(local, ("depth", "strip"), strip_pairs(depths, strip_count, shift))
        start = [0] * len(shape)
        start[row_axis] = ((strip_no - shift) % strip_count) * rows
        full = lax.dynamic_update_slice(full, got, start)
    return full


def gather_strips(piece_of, local, depths, strip_no, strip_count, rows_here):
    rows = rows_here * strip_count
    shape = (local.shape[0], rows, local.shape[2])
    full = lax.dynamic_update_slice(
        jnp.zeros(shape, jnp.float32), local, (0, strip_no * rows_here, 0)
    )
    for shift in range(1, strip_count):
        target = (strip_no + shift) % strip_count
        got = lax.ppermute(
            piece_of(target), ("depth", "strip"), strip_pairs(depths, strip_count, shift)
        )
        source = (strip_no - shift) % strip_count
        full = lax.dynamic_update_slice(full, got, (0, source * rows_here, 0))
    return full


def shards(surface, omegas, region_speed, fd_coeff, region_index, ref_region):
    if not fast_fits(surface, region_index, region_speed):
        return shards_general(surface, omegas, region_speed, fd_coeff, region_index, ref_region)
    line_len = surface.shape[3]
    rows_here = surface.shape[2]
    steps = region_index.shape[0]
    segment_no = lax.axis_index("depth")
    segment_count = lax.axis_size("depth")
    strip_no = lax.axis_index("strip")
    strip_count = lax.axis_size("strip")
    consts = fast_constants(line_len)
    region_f = region_index.astype(jnp.float32)
    early = list(range(segment_count))

    def with_surface(target):
        return jnp.concatenate(
            [region_f, lax.dynamic_index_in_dim(surface, target, 1, keepdims=False)], axis=0
        )

    gathered = gather_strips(
        with_surface, with_surface(strip_no), early, strip_no, strip_count, rows_here
    )
    regions_a = gathered[:steps].astype(jnp.int32)
    wave = gathered[steps:]
    omega = lax.dynamic_index_in_dim(omegas, strip_no, 0, keepdims=False)
    table, mult = section_tables(omega, region_speed, fd_coeff, ref_region, jnp.asarray(consts[3]))
    image = jnp.zeros((strip_count, steps, rows_here, line_len), jnp.float32)

    def sweep(regions):
        def live(wave, image):
            return run_section(wave, regions, table, mult, consts, strip_count)

        return live

    def idle(wave, image):
        return (wave, image)

    def freq_sum(image, depths):
        parts = []
        for shift in range(1, strip_count):
            target = (strip_no + shift) % strip_count
            piece = lax.dynamic_index_in_dim(image, target, 0, keepdims=False)
            parts.append(
                lax.ppermute(piece, ("depth", "strip"), strip_pairs(depths, strip_count, shift))
            )
        return parts

    arrived = []
    for tick_no in range(segment_count):
        wave, image = lax.cond(segment_no == tick_no, sweep(regions_a), idle, wave, image)
        if tick_no + 1 < segment_count:
            wave = lax.ppermute(wave, "depth", [(tick_no, tick_no + 1)])
        if tick_no == segment_count - 2:
            wave, image = lax.optimization_barrier((wave, image))
            arrived += freq_sum(image, range(segment_count - 1))
    arrived += freq_sum(image, [segment_count - 1])
    total = lax.dynamic_index_in_dim(image, strip_no, 0, keepdims=False)
    for piece in arrived:
        total = total + piece
    return total


def solution(mesh):
    in_specs = (
        P(None, "shots", "strip", None),
        P(),
        P(),
        P(),
        P("depth", "strip", None),
        P("depth"),
    )
    out_specs = P("depth", "strip", "shots")
    return jax.shard_map(shards, mesh=mesh, in_specs=in_specs, out_specs=out_specs, check_vma=False)
```

```python
import math

import ml_dtypes
import numpy as np
import jax
import jax.numpy as jnp
from jax import lax
from jax.experimental import pallas as pl
from jax.experimental.pallas import tpu as pltpu
from jax.sharding import PartitionSpec as P

DAMPING = 0.05
PRECISE = lax.Precision.HIGHEST


def padded_2(cells, sides, width):
    for axis, dim in sides:
        count = lax.axis_size(axis)
        ends = count - 1
        head = lax.slice_in_dim(cells, 0, width, axis=dim)
        tail = lax.slice_in_dim(cells, cells.shape[dim] - width, cells.shape[dim], axis=dim)
        cells = jnp.concatenate(
            [
                lax.ppermute(tail, axis, [(i, (i + 1) % count) for i in range(ends)]),
                cells,
                lax.ppermute(head, axis, [((i + 1) % count, i) for i in range(ends)]),
            ],
            axis=dim,
        )
    return cells


def from_behind(value, axis, steps):
    count = lax.axis_size(axis)
    first, last = (max(0, -steps), min(count, count - steps))
    return lax.ppermute(value, axis, [(source, source + steps) for source in range(first, last)])


def complex_scale(values, cosine, sine_part):
    return jnp.stack(
        [values[0] * cosine - values[1] * sine_part, values[0] * sine_part + values[1] * cosine]
    )


def angle_pair(numerator, period):
    angle_grid = numerator.astype(jnp.float32) * (2.0 * math.pi / period)
    return (jnp.cos(angle_grid), jnp.sin(angle_grid))


def block_matrix(cosine, sine_part, forward):
    sign_flip = 1.0 if forward else -1.0
    return jnp.stack(
        [jnp.stack([cosine, -sign_flip * sine_part]), jnp.stack([sign_flip * sine_part, cosine])]
    )


def build_tables(line_len):
    block_len = 128
    outer_len = line_len // block_len
    inner_idx = jnp.arange(block_len)
    outer_idx = jnp.arange(outer_len)
    cos_large, sin_large = angle_pair(
        inner_idx[:, None] * inner_idx[None, :] % block_len, block_len
    )
    cos_small, sin_small = angle_pair(
        outer_idx[:, None] * outer_idx[None, :] % outer_len, outer_len
    )
    cos_twist, sin_twist = angle_pair(outer_idx[:, None] * inner_idx[None, :], line_len)
    wave_index = outer_idx[:, None] + outer_len * inner_idx[None, :]
    signed = jnp.where(wave_index >= line_len // 2, wave_index - line_len, wave_index)
    kx_grid = signed.astype(jnp.float32) * (2.0 * math.pi / line_len)
    small_fwd = block_matrix(cos_small, sin_small, True)
    small_inv = block_matrix(cos_small, sin_small, False)
    large_fwd = block_matrix(cos_large, sin_large, True)
    large_inv = block_matrix(cos_large, sin_large, False)
    return (small_fwd, small_inv, large_fwd, large_inv, cos_twist, sin_twist, kx_grid)


def forward_line(wavefield, tables):
    small_fwd, small_inv, large_fwd, large_inv, cos_twist, sin_twist, kx_grid = tables
    row_count = wavefield.shape[1]
    pieces = wavefield.reshape(2, row_count, cos_twist.shape[0], cos_twist.shape[1])
    mixed_part = jnp.einsum("zrab,zwca->wrcb", pieces, small_fwd, precision=PRECISE)
    mixed_part = complex_scale(mixed_part, cos_twist, -sin_twist)
    return jnp.einsum("zrcb,zwbd->wrcd", mixed_part, large_fwd, precision=PRECISE)


def inverse_line(spectrum, tables):
    small_fwd, small_inv, large_fwd, large_inv, cos_twist, sin_twist, kx_grid = tables
    row_count = spectrum.shape[1]
    line_len = cos_twist.shape[0] * cos_twist.shape[1]
    mixed_part = jnp.einsum("zrcd,zwdb->wrcb", spectrum, large_inv, precision=PRECISE)
    mixed_part = complex_scale(mixed_part, cos_twist, sin_twist)
    pieces = jnp.einsum("zrcb,zwca->wrab", mixed_part, small_inv, precision=PRECISE)
    return pieces.reshape(2, row_count, line_len) * (1.0 / line_len)


def lookup(regions, entries):
    picked = jnp.zeros(regions.shape, jnp.float32)
    for region_no in range(entries.shape[0]):
        picked = picked + jnp.where(regions == region_no, entries[region_no], 0.0)
    return picked


def depth_step(wavefield, omega_now, slow_cells, coef_cells, ref_slow, tables, pad_rows):
    kx_grid = tables[6]
    wave_ref = omega_now * ref_slow
    excess = wave_ref * wave_ref - kx_grid * kx_grid
    decay_line = jnp.exp(-jnp.sqrt(jnp.maximum(-excess, 0.0)))
    vertical = jnp.sqrt(jnp.maximum(excess, 0.0))
    spectrum = complex_scale(
        forward_line(wavefield, tables),
        decay_line * jnp.cos(vertical),
        decay_line * jnp.sin(vertical),
    )
    wavefield = inverse_line(spectrum, tables)
    phase_cell = omega_now * (slow_cells - ref_slow)
    wavefield = complex_scale(wavefield, jnp.cos(phase_cell), jnp.sin(phase_cell))
    padded = pad_rows(wavefield)
    laplace = (
        padded[:, :-2]
        + padded[:, 2:]
        + jnp.roll(wavefield, 1, 2)
        + jnp.roll(wavefield, -1, 2)
        - 4.0 * wavefield
    )
    return wavefield + complex_scale(laplace, DAMPING, coef_cells / omega_now)


def march(wavefield, omega_now, slow_block, coef_block, ref_block, tables, pad_rows):
    traces = []
    for step_no in range(slow_block.shape[0]):
        wavefield = depth_step(
            wavefield,
            omega_now,
            slow_block[step_no],
            coef_block[step_no],
            ref_block[step_no],
            tables,
            pad_rows,
        )
        traces.append(wavefield[0])
    return (wavefield, jnp.stack(traces))


def shards_general(surface, omegas, region_speed, fd_coeff, region_index, ref_region):
    line_len = surface.shape[3]
    rows_here = surface.shape[2]
    freq_count = surface.shape[1]
    step_count = region_index.shape[0]
    tables = build_tables(line_len)
    inv_speed = 1.0 / region_speed
    segment_no = lax.axis_index("depth")
    segment_count = lax.axis_size("depth")

    def pad_near(values):
        return padded_2(values, (("strip", 1),), 1)

    slow_cells = lookup(region_index, inv_speed)
    coef_cells = lookup(region_index, fd_coeff)
    ref_cells = lookup(ref_region, inv_speed)
    freq_index = jnp.arange(freq_count)
    image_out = jnp.zeros((step_count, rows_here, line_len), jnp.float32)
    arriving = jnp.zeros((2, rows_here, line_len), jnp.float32)
    tick_count = freq_count + segment_count - 1
    for tick_no in range(tick_count):
        batch_no = tick_no - segment_no
        is_live = (batch_no >= 0) & (batch_no < freq_count)
        clipped = jnp.clip(batch_no, 0, freq_count - 1)
        picked = lax.dynamic_index_in_dim(surface, clipped, 1, keepdims=False)
        entering = jnp.where(segment_no == 0, picked, arriving)
        omega_now = jnp.sum(jnp.where(freq_index == clipped, omegas, 0.0))
        leaving, traces = march(
            entering, omega_now, slow_cells, coef_cells, ref_cells, tables, pad_near
        )
        image_out = image_out + jnp.where(is_live, traces, 0.0)
        if tick_no + 1 < tick_count:
            arriving = from_behind(leaving, "depth", 1)
    return image_out


LANE = 128
FFT_BLOCKS = 16
ROW_CHUNK = 8


def fft4(x0, x1, x2, x3, sign):
    s0 = (x0[0] + x2[0], x0[1] + x2[1])
    d0 = (x0[0] - x2[0], x0[1] - x2[1])
    s1 = (x1[0] + x3[0], x1[1] + x3[1])
    d1 = (x1[0] - x3[0], x1[1] - x3[1])
    if sign < 0:
        wd = (d1[1], -d1[0])
    else:
        wd = (-d1[1], d1[0])
    return (
        (s0[0] + s1[0], s0[1] + s1[1]),
        (d0[0] + wd[0], d0[1] + wd[1]),
        (s0[0] - s1[0], s0[1] - s1[1]),
        (d0[0] - wd[0], d0[1] - wd[1]),
    )


def turn_const(value, power, sign):
    if power == 4:
        return (-value[1], value[0]) if sign > 0 else (value[1], -value[0])
    angle = sign * 2.0 * math.pi * power / 16.0
    cr, ci = (math.cos(angle), math.sin(angle))
    return (value[0] * cr - value[1] * ci, value[0] * ci + value[1] * cr)


def fft16(parts, sign):
    mid = [[None] * 4 for _ in range(4)]
    for a0 in range(4):
        ys = fft4(parts[a0], parts[4 + a0], parts[8 + a0], parts[12 + a0], sign)
        for c0 in range(4):
            power = a0 * c0
            mid[a0][c0] = ys[c0] if power == 0 else turn_const(ys[c0], power, sign)
    out = [None] * 16
    for c0 in range(4):
        zs = fft4(mid[0][c0], mid[1][c0], mid[2][c0], mid[3][c0], sign)
        for c1 in range(4):
            out[c0 + 4 * c1] = zs[c1]
    return out


def pick(regions, values):
    level = list(values)
    bit = 1
    while len(level) > 1:
        chosen = (regions & bit) != 0
        level = [jnp.where(chosen, level[i + 1], level[i]) for i in range(0, len(level), 2)]
        bit *= 2
    return jnp.broadcast_to(level[0], regions.shape)


def pick_bits(bits, values):
    level = list(values)
    for chosen in bits:
        level = [jnp.where(chosen, level[i + 1], level[i]) for i in range(0, len(level), 2)]
    return jnp.broadcast_to(level[0], bits[0].shape)


def split_dot(values, hi_ref, lo_ref):
    high = values.astype(jnp.bfloat16)
    low = (values - high.astype(jnp.float32)).astype(jnp.bfloat16)
    main = jnp.dot(high, hi_ref[...], preferred_element_type=jnp.float32)
    fix = jnp.dot(high, lo_ref[...], preferred_element_type=jnp.float32) + jnp.dot(
        low, hi_ref[:, :], preferred_element_type=jnp.float32
    )
    return main + fix


def section_kernel(
    tab_ref, w_ref, rid_ref, mult_ref, tw_ref, fhi_ref, flo_ref, ghi_ref, glo_ref,
    wout_ref, img_ref, a_ref, y_ref, v_ref, cs_ref, sn_ref, gn_ref, *, table_len
):
    rows = w_ref.shape[1]
    line_len = w_ref.shape[2]
    steps = rid_ref.shape[0]
    strip_count, rows_here = img_ref.shape[0], img_ref.shape[2]
    chunks = rows // ROW_CHUNK
    inv_len = 1.0 / line_len
    wout_ref[...] = w_ref[...]

    def blk(a):
        return slice(a * LANE, (a + 1) * LANE)

    def one_step(k, carry):
        base = k * (3 * table_len)
        cos_t = [tab_ref[base + g] for g in range(table_len)]
        sin_t = [tab_ref[base + table_len + g] for g in range(table_len)]
        gain_t = [tab_ref[base + 2 * table_len + g] for g in range(table_len)]

        def forward_chunk(i, c):
            y0 = pl.multiple_of(i * ROW_CHUNK, ROW_CHUNK)
            parts = [
                (wout_ref[0, pl.ds(y0, ROW_CHUNK), blk(a)], wout_ref[1, pl.ds(y0, ROW_CHUNK), blk(a)])
                for a in range(FFT_BLOCKS)
            ]
            spec = fft16(parts, -1)
            for cc in range(FFT_BLOCKS):
                tc = tw_ref[0, cc:cc + 1, :]
                ts = tw_ref[1, cc:cc + 1, :]
                xr, xi = spec[cc]
                a_ref[pl.ds(cc * rows + y0, ROW_CHUNK), 0:LANE] = xr * tc + xi * ts
                a_ref[pl.ds(cc * rows + y0, ROW_CHUNK), LANE:2 * LANE] = xi * tc - xr * ts
            return c

        lax.fori_loop(0, chunks, forward_chunk, 0)
        spectrum = split_dot(a_ref[...], fhi_ref, flo_ref)
        for a in range(FFT_BLOCKS):
            regions = rid_ref[k, :, blk(a)]
            bits = [(regions & (1 << b)) != 0 for b in range(max(1, (table_len - 1).bit_length()))]
            cs_ref[:, blk(a)] = pick_bits(bits, cos_t)
            sn_ref[:, blk(a)] = pick_bits(bits, sin_t)
            gn_ref[:, blk(a)] = pick_bits(bits, gain_t)
        y_ref[...] = spectrum
        for cc in range(FFT_BLOCKS):
            band = slice(cc * rows, (cc + 1) * rows)
            yr = y_ref[band, 0:LANE]
            yi = y_ref[band, LANE:2 * LANE]
            mr = mult_ref[k, 0, cc:cc + 1, :]
            mi = mult_ref[k, 1, cc:cc + 1, :]
            a_ref[band, 0:LANE] = yr * mr - yi * mi
            a_ref[band, LANE:2 * LANE] = yr * mi + yi * mr
        y_ref[...] = split_dot(a_ref[...], ghi_ref, glo_ref)

        def inverse_chunk(i, c):
            y0 = pl.multiple_of(i * ROW_CHUNK, ROW_CHUNK)
            parts = []
            for cc in range(FFT_BLOCKS):
                zr = y_ref[pl.ds(cc * rows + y0, ROW_CHUNK), 0:LANE]
                zi = y_ref[pl.ds(cc * rows + y0, ROW_CHUNK), LANE:2 * LANE]
                tc = tw_ref[0, cc:cc + 1, :]
                ts = tw_ref[1, cc:cc + 1, :]
                parts.append((zr * tc - zi * ts, zr * ts + zi * tc))
            back = fft16(parts, 1)
            for a in range(FFT_BLOCKS):
                ur = back[a][0] * inv_len
                ui = back[a][1] * inv_len
                cs = cs_ref[pl.ds(y0, ROW_CHUNK), blk(a)]
                sn = sn_ref[pl.ds(y0, ROW_CHUNK), blk(a)]
                v_ref[0, pl.ds(y0, ROW_CHUNK), blk(a)] = ur * cs - ui * sn
                v_ref[1, pl.ds(y0, ROW_CHUNK), blk(a)] = ur * sn + ui * cs
            return c

        lax.fori_loop(0, chunks, inverse_chunk, 0)
        row_id = lax.broadcasted_iota(jnp.int32, (rows, LANE), 0)
        lane_id = lax.broadcasted_iota(jnp.int32, (rows, LANE), 1)
        cache = {}

        def cell(part, a):
            key = (part, a % FFT_BLOCKS)
            if key not in cache:
                v = v_ref[part, :, blk(a % FFT_BLOCKS)]
                cache[key] = (v, pltpu.roll(v, 1, 1), pltpu.roll(v, LANE - 1, 1))
            return cache[key]

        for a in range(FFT_BLOCKS):
            lap = []
            here = []
            for part in range(2):
                v, from_left, from_right = cell(part, a)
                prev_left = cell(part, a - 1)[1]
                next_right = cell(part, a + 1)[2]
                above = jnp.where(row_id == 0, 0.0, pltpu.roll(v, 1, 0))
                below = jnp.where(row_id == rows - 1, 0.0, pltpu.roll(v, rows - 1, 0))
                left = jnp.where(lane_id == 0, prev_left, from_left)
                right = jnp.where(lane_id == LANE - 1, next_right, from_right)
                lap.append(above + below + left + right - 4.0 * v)
                here.append(v)
            gain = gn_ref[:, blk(a)]
            new_re = here[0] + (lap[0] * DAMPING - lap[1] * gain)
            new_im = here[1] + (lap[0] * gain + lap[1] * DAMPING)
            wout_ref[0, :, blk(a)] = new_re
            wout_ref[1, :, blk(a)] = new_im
            for j in range(strip_count):
                img_ref[j, k, :, blk(a)] = new_re[j * rows_here:(j + 1) * rows_here]
        return carry

    lax.fori_loop(0, steps, one_step, 0)


def fast_constants(line_len):
    outer = line_len // LANE
    b = np.arange(LANE)
    ang = 2.0 * np.pi * (np.outer(b, b) % LANE) / LANE
    cos_m, sin_m = (np.cos(ang), np.sin(ang))
    fwd = np.block([[cos_m, -sin_m], [sin_m, cos_m]])
    inv = np.block([[cos_m, sin_m], [-sin_m, cos_m]])

    def halves(m):
        hi = m.astype(ml_dtypes.bfloat16)
        lo = (m - hi.astype(np.float64)).astype(ml_dtypes.bfloat16)
        return (hi, lo)

    c = np.arange(outer)
    tw_ang = 2.0 * np.pi * np.outer(c, b) / line_len
    twiddle = np.stack([np.cos(tw_ang), np.sin(tw_ang)]).astype(np.float32)
    q = c[:, None] + outer * b[None, :]
    signed = np.where(q >= line_len // 2, q - line_len, q).astype(np.float32)
    kx_cd = signed * np.float32(2.0 * math.pi / line_len)
    return (halves(fwd), halves(inv), twiddle, kx_cd.astype(np.float32))


def run_section(wave, regions, table, mult, consts, strip_count):
    (fhi, flo), (ghi, glo), twiddle, _ = consts
    rows, line_len = wave.shape[1], wave.shape[2]
    steps = regions.shape[0]
    table_len = table.shape[0] // (3 * steps)
    vmem = pl.BlockSpec(memory_space=pltpu.VMEM)
    flops = steps * (2 * 3 * 2 * (FFT_BLOCKS * rows) * 256 * 256 + 400 * rows * line_len)
    return pl.pallas_call(
        lambda *refs: section_kernel(*refs, table_len=table_len),
        out_shape=(
            jax.ShapeDtypeStruct(wave.shape, jnp.float32),
            jax.ShapeDtypeStruct((strip_count, steps, rows // strip_count, line_len), jnp.float32),
        ),
        in_specs=[pl.BlockSpec(memory_space=pltpu.SMEM)] + [vmem] * 8,
        out_specs=(vmem, vmem),
        scratch_shapes=[
            pltpu.VMEM((FFT_BLOCKS * rows, 2 * LANE), jnp.float32),
            pltpu.VMEM((FFT_BLOCKS * rows, 2 * LANE), jnp.float32),
            pltpu.VMEM((2, rows, line_len), jnp.float32),
            pltpu.VMEM((rows, line_len), jnp.float32),
            pltpu.VMEM((rows, line_len), jnp.float32),
            pltpu.VMEM((rows, line_len), jnp.float32),
        ],
        cost_estimate=pl.CostEstimate(
            flops=flops, transcendentals=0, bytes_accessed=4 * rows * line_len * 6 * steps
        ),
    )(table, wave, regions, mult, jnp.asarray(twiddle), jnp.asarray(fhi), jnp.asarray(flo),
      jnp.asarray(ghi), jnp.asarray(glo))


def section_tables(omega, region_speed, fd_coeff, ref_region, kx_cd):
    inv_speed = 1.0 / region_speed
    ref_slow = inv_speed[ref_region]
    regions = region_speed.shape[0]
    padded = 1 << max(1, (regions - 1).bit_length())
    extra = padded - regions
    phase = omega * (inv_speed[None, :] - ref_slow[:, None])
    gain = jnp.broadcast_to(fd_coeff / omega, phase.shape)
    parts = [jnp.cos(phase), jnp.sin(phase), gain]
    if extra:
        parts = [jnp.concatenate([p, jnp.repeat(p[:, -1:], extra, axis=1)], axis=1) for p in parts]
    table = jnp.stack(parts, axis=1).reshape(-1)
    wave_ref = omega * ref_slow
    wave_ref = wave_ref[:, None, None]
    excess = wave_ref * wave_ref - kx_cd * kx_cd
    decay_line = jnp.exp(-jnp.sqrt(jnp.maximum(-excess, 0.0)))
    vertical = jnp.sqrt(jnp.maximum(excess, 0.0))
    mult = jnp.stack([decay_line * jnp.cos(vertical), decay_line * jnp.sin(vertical)], axis=1)
    return (table, mult)


def fast_fits(surface, region_index, region_speed):
    freq_count = surface.shape[1]
    rows = surface.shape[2] * lax.axis_size("strip")
    line_len = surface.shape[3]
    return (
        freq_count == lax.axis_size("strip")
        and line_len == FFT_BLOCKS * LANE
        and rows % ROW_CHUNK == 0
        and surface.shape[2] % ROW_CHUNK == 0
        and rows <= 64
        and region_speed.shape[0] <= 16
    )


def strip_pairs(depths, strip_count, shift):
    return [
        (d * strip_count + r, d * strip_count + (r + shift) % strip_count)
        for d in depths
        for r in range(strip_count)
    ]


def gather_rows(local, depths, strip_no, strip_count, row_axis):
    rows = local.shape[row_axis]
    shape = list(local.shape)
    shape[row_axis] = rows * strip_count
    full = jnp.zeros(shape, local.dtype)
    start = [0] * len(shape)
    start[row_axis] = strip_no * rows
    full = lax.dynamic_update_slice(full, local, start)
    for shift in range(1, strip_count):
        got = lax.ppermute(local, ("depth", "strip"), strip_pairs(depths, strip_count, shift))
        start = [0] * len(shape)
        start[row_axis] = ((strip_no - shift) % strip_count) * rows
        full = lax.dynamic_update_slice(full, got, start)
    return full


def gather_strips(piece_of, local, depths, strip_no, strip_count, rows_here):
    rows = rows_here * strip_count
    shape = (local.shape[0], rows, local.shape[2])
    full = lax.dynamic_update_slice(
        jnp.zeros(shape, jnp.float32), local, (0, strip_no * rows_here, 0)
    )
    for shift in range(1, strip_count):
        target = (strip_no + shift) % strip_count
        got = lax.ppermute(
            piece_of(target), ("depth", "strip"), strip_pairs(depths, strip_count, shift)
        )
        source = (strip_no - shift) % strip_count
        full = lax.dynamic_update_slice(full, got, (0, source * rows_here, 0))
    return full


def shards(surface, omegas, region_speed, fd_coeff, region_index, ref_region):
    if not fast_fits(surface, region_index, region_speed):
        return shards_general(surface, omegas, region_speed, fd_coeff, region_index, ref_region)
    line_len = surface.shape[3]
    rows_here = surface.shape[2]
    steps = region_index.shape[0]
    segment_no = lax.axis_index("depth")
    segment_count = lax.axis_size("depth")
    strip_no = lax.axis_index("strip")
    strip_count = lax.axis_size("strip")
    consts = fast_constants(line_len)
    region_f = region_index.astype(jnp.float32)
    early = list(range(segment_count))

    def with_surface(target):
        return jnp.concatenate(
            [region_f, lax.dynamic_index_in_dim(surface, target, 1, keepdims=False)], axis=0
        )

    gathered = gather_strips(
        with_surface, with_surface(strip_no), early, strip_no, strip_count, rows_here
    )
    regions_a = gathered[:steps].astype(jnp.int32)
    wave = gathered[steps:]
    omega = lax.dynamic_index_in_dim(omegas, strip_no, 0, keepdims=False)
    table, mult = section_tables(omega, region_speed, fd_coeff, ref_region, jnp.asarray(consts[3]))
    image = jnp.zeros((strip_count, steps, rows_here, line_len), jnp.float32)

    def sweep(regions):
        def live(wave, image):
            return run_section(wave, regions, table, mult, consts, strip_count)

        return live

    def idle(wave, image):
        return (wave, image)

    def freq_sum(image, depths):
        parts = []
        for shift in range(1, strip_count):
            target = (strip_no + shift) % strip_count
            piece = lax.dynamic_index_in_dim(image, target, 0, keepdims=False)
            parts.append(
                lax.ppermute(piece, ("depth", "strip"), strip_pairs(depths, strip_count, shift))
            )
        return parts

    arrived = []
    for tick_no in range(segment_count):
        wave, image = lax.cond(segment_no == tick_no, sweep(regions_a), idle, wave, image)
        if tick_no + 1 < segment_count:
            wave = lax.ppermute(wave, "depth", [(tick_no, tick_no + 1)])
        if tick_no == segment_count - 2:
            wave, image = lax.optimization_barrier((wave, image))
            group = freq_sum(image, range(segment_count - 1))
            wave, group = lax.optimization_barrier((wave, group))
            arrived += list(group)
    arrived += freq_sum(image, [segment_count - 1])
    total = lax.dynamic_index_in_dim(image, strip_no, 0, keepdims=False)
    for piece in arrived:
        total = total + piece
    return total


def solution(mesh):
    in_specs = (
        P(None, "shots", "strip", None),
        P(),
        P(),
        P(),
        P("depth", "strip", None),
        P("depth"),
    )
    out_specs = P("depth", "strip", "shots")
    return jax.shard_map(shards, mesh=mesh, in_specs=in_specs, out_specs=out_specs, check_vma=False)
```

```python
import math

import ml_dtypes
import numpy as np
import jax
import jax.numpy as jnp
from jax import lax
from jax.experimental import pallas as pl
from jax.experimental.pallas import tpu as pltpu
from jax.sharding import PartitionSpec as P

DAMPING = 0.05
PRECISE = lax.Precision.HIGHEST


def padded_2(cells, sides, width):
    for axis, dim in sides:
        count = lax.axis_size(axis)
        ends = count - 1
        head = lax.slice_in_dim(cells, 0, width, axis=dim)
        tail = lax.slice_in_dim(cells, cells.shape[dim] - width, cells.shape[dim], axis=dim)
        cells = jnp.concatenate(
            [
                lax.ppermute(tail, axis, [(i, (i + 1) % count) for i in range(ends)]),
                cells,
                lax.ppermute(head, axis, [((i + 1) % count, i) for i in range(ends)]),
            ],
            axis=dim,
        )
    return cells


def from_behind(value, axis, steps):
    count = lax.axis_size(axis)
    first, last = (max(0, -steps), min(count, count - steps))
    return lax.ppermute(value, axis, [(source, source + steps) for source in range(first, last)])


def complex_scale(values, cosine, sine_part):
    return jnp.stack(
        [values[0] * cosine - values[1] * sine_part, values[0] * sine_part + values[1] * cosine]
    )


def angle_pair(numerator, period):
    angle_grid = numerator.astype(jnp.float32) * (2.0 * math.pi / period)
    return (jnp.cos(angle_grid), jnp.sin(angle_grid))


def block_matrix(cosine, sine_part, forward):
    sign_flip = 1.0 if forward else -1.0
    return jnp.stack(
        [jnp.stack([cosine, -sign_flip * sine_part]), jnp.stack([sign_flip * sine_part, cosine])]
    )


def build_tables(line_len):
    block_len = 128
    outer_len = line_len // block_len
    inner_idx = jnp.arange(block_len)
    outer_idx = jnp.arange(outer_len)
    cos_large, sin_large = angle_pair(
        inner_idx[:, None] * inner_idx[None, :] % block_len, block_len
    )
    cos_small, sin_small = angle_pair(
        outer_idx[:, None] * outer_idx[None, :] % outer_len, outer_len
    )
    cos_twist, sin_twist = angle_pair(outer_idx[:, None] * inner_idx[None, :], line_len)
    wave_index = outer_idx[:, None] + outer_len * inner_idx[None, :]
    signed = jnp.where(wave_index >= line_len // 2, wave_index - line_len, wave_index)
    kx_grid = signed.astype(jnp.float32) * (2.0 * math.pi / line_len)
    small_fwd = block_matrix(cos_small, sin_small, True)
    small_inv = block_matrix(cos_small, sin_small, False)
    large_fwd = block_matrix(cos_large, sin_large, True)
    large_inv = block_matrix(cos_large, sin_large, False)
    return (small_fwd, small_inv, large_fwd, large_inv, cos_twist, sin_twist, kx_grid)


def forward_line(wavefield, tables):
    small_fwd, small_inv, large_fwd, large_inv, cos_twist, sin_twist, kx_grid = tables
    row_count = wavefield.shape[1]
    pieces = wavefield.reshape(2, row_count, cos_twist.shape[0], cos_twist.shape[1])
    mixed_part = jnp.einsum("zrab,zwca->wrcb", pieces, small_fwd, precision=PRECISE)
    mixed_part = complex_scale(mixed_part, cos_twist, -sin_twist)
    return jnp.einsum("zrcb,zwbd->wrcd", mixed_part, large_fwd, precision=PRECISE)


def inverse_line(spectrum, tables):
    small_fwd, small_inv, large_fwd, large_inv, cos_twist, sin_twist, kx_grid = tables
    row_count = spectrum.shape[1]
    line_len = cos_twist.shape[0] * cos_twist.shape[1]
    mixed_part = jnp.einsum("zrcd,zwdb->wrcb", spectrum, large_inv, precision=PRECISE)
    mixed_part = complex_scale(mixed_part, cos_twist, sin_twist)
    pieces = jnp.einsum("zrcb,zwca->wrab", mixed_part, small_inv, precision=PRECISE)
    return pieces.reshape(2, row_count, line_len) * (1.0 / line_len)


def lookup(regions, entries):
    picked = jnp.zeros(regions.shape, jnp.float32)
    for region_no in range(entries.shape[0]):
        picked = picked + jnp.where(regions == region_no, entries[region_no], 0.0)
    return picked


def depth_step(wavefield, omega_now, slow_cells, coef_cells, ref_slow, tables, pad_rows):
    kx_grid = tables[6]
    wave_ref = omega_now * ref_slow
    excess = wave_ref * wave_ref - kx_grid * kx_grid
    decay_line = jnp.exp(-jnp.sqrt(jnp.maximum(-excess, 0.0)))
    vertical = jnp.sqrt(jnp.maximum(excess, 0.0))
    spectrum = complex_scale(
        forward_line(wavefield, tables),
        decay_line * jnp.cos(vertical),
        decay_line * jnp.sin(vertical),
    )
    wavefield = inverse_line(spectrum, tables)
    phase_cell = omega_now * (slow_cells - ref_slow)
    wavefield = complex_scale(wavefield, jnp.cos(phase_cell), jnp.sin(phase_cell))
    padded = pad_rows(wavefield)
    laplace = (
        padded[:, :-2]
        + padded[:, 2:]
        + jnp.roll(wavefield, 1, 2)
        + jnp.roll(wavefield, -1, 2)
        - 4.0 * wavefield
    )
    return wavefield + complex_scale(laplace, DAMPING, coef_cells / omega_now)


def march(wavefield, omega_now, slow_block, coef_block, ref_block, tables, pad_rows):
    traces = []
    for step_no in range(slow_block.shape[0]):
        wavefield = depth_step(
            wavefield,
            omega_now,
            slow_block[step_no],
            coef_block[step_no],
            ref_block[step_no],
            tables,
            pad_rows,
        )
        traces.append(wavefield[0])
    return (wavefield, jnp.stack(traces))


def shards_general(surface, omegas, region_speed, fd_coeff, region_index, ref_region):
    line_len = surface.shape[3]
    rows_here = surface.shape[2]
    freq_count = surface.shape[1]
    step_count = region_index.shape[0]
    tables = build_tables(line_len)
    inv_speed = 1.0 / region_speed
    segment_no = lax.axis_index("depth")
    segment_count = lax.axis_size("depth")

    def pad_near(values):
        return padded_2(values, (("strip", 1),), 1)

    slow_cells = lookup(region_index, inv_speed)
    coef_cells = lookup(region_index, fd_coeff)
    ref_cells = lookup(ref_region, inv_speed)
    freq_index = jnp.arange(freq_count)
    image_out = jnp.zeros((step_count, rows_here, line_len), jnp.float32)
    arriving = jnp.zeros((2, rows_here, line_len), jnp.float32)
    tick_count = freq_count + segment_count - 1
    for tick_no in range(tick_count):
        batch_no = tick_no - segment_no
        is_live = (batch_no >= 0) & (batch_no < freq_count)
        clipped = jnp.clip(batch_no, 0, freq_count - 1)
        picked = lax.dynamic_index_in_dim(surface, clipped, 1, keepdims=False)
        entering = jnp.where(segment_no == 0, picked, arriving)
        omega_now = jnp.sum(jnp.where(freq_index == clipped, omegas, 0.0))
        leaving, traces = march(
            entering, omega_now, slow_cells, coef_cells, ref_cells, tables, pad_near
        )
        image_out = image_out + jnp.where(is_live, traces, 0.0)
        if tick_no + 1 < tick_count:
            arriving = from_behind(leaving, "depth", 1)
    return image_out


LANE = 128
FFT_BLOCKS = 16
ROW_CHUNK = 8


def fft4(x0, x1, x2, x3, sign):
    s0 = (x0[0] + x2[0], x0[1] + x2[1])
    d0 = (x0[0] - x2[0], x0[1] - x2[1])
    s1 = (x1[0] + x3[0], x1[1] + x3[1])
    d1 = (x1[0] - x3[0], x1[1] - x3[1])
    if sign < 0:
        wd = (d1[1], -d1[0])
    else:
        wd = (-d1[1], d1[0])
    return (
        (s0[0] + s1[0], s0[1] + s1[1]),
        (d0[0] + wd[0], d0[1] + wd[1]),
        (s0[0] - s1[0], s0[1] - s1[1]),
        (d0[0] - wd[0], d0[1] - wd[1]),
    )


def turn_const(value, power, sign):
    if power == 4:
        return (-value[1], value[0]) if sign > 0 else (value[1], -value[0])
    angle = sign * 2.0 * math.pi * power / 16.0
    cr, ci = (math.cos(angle), math.sin(angle))
    return (value[0] * cr - value[1] * ci, value[0] * ci + value[1] * cr)


def fft16(parts, sign):
    mid = [[None] * 4 for _ in range(4)]
    for a0 in range(4):
        ys = fft4(parts[a0], parts[4 + a0], parts[8 + a0], parts[12 + a0], sign)
        for c0 in range(4):
            power = a0 * c0
            mid[a0][c0] = ys[c0] if power == 0 else turn_const(ys[c0], power, sign)
    out = [None] * 16
    for c0 in range(4):
        zs = fft4(mid[0][c0], mid[1][c0], mid[2][c0], mid[3][c0], sign)
        for c1 in range(4):
            out[c0 + 4 * c1] = zs[c1]
    return out


def pick(regions, values):
    level = list(values)
    bit = 1
    while len(level) > 1:
        chosen = (regions & bit) != 0
        level = [jnp.where(chosen, level[i + 1], level[i]) for i in range(0, len(level), 2)]
        bit *= 2
    return jnp.broadcast_to(level[0], regions.shape)


def pick_bits(bits, values):
    level = list(values)
    for chosen in bits:
        level = [jnp.where(chosen, level[i + 1], level[i]) for i in range(0, len(level), 2)]
    return jnp.broadcast_to(level[0], bits[0].shape)


def split_dot(values, hi_ref, lo_ref):
    high = values.astype(jnp.bfloat16)
    low = (values - high.astype(jnp.float32)).astype(jnp.bfloat16)
    main = jnp.dot(high, hi_ref[...], preferred_element_type=jnp.float32)
    fix = jnp.dot(high, lo_ref[...], preferred_element_type=jnp.float32) + jnp.dot(
        low, hi_ref[:, :], preferred_element_type=jnp.float32
    )
    return main + fix


def section_kernel(
    tab_ref, w_ref, rid_ref, mult_ref, tw_ref, fhi_ref, flo_ref, ghi_ref, glo_ref,
    wout_ref, img_ref, a_ref, y_ref, v_ref, cs_ref, sn_ref, gn_ref, *, table_len
):
    rows = w_ref.shape[1]
    line_len = w_ref.shape[2]
    steps = rid_ref.shape[0]
    strip_count, rows_here = img_ref.shape[0], img_ref.shape[2]
    chunks = rows // ROW_CHUNK
    inv_len = 1.0 / line_len
    wout_ref[...] = w_ref[...]

    def blk(a):
        return slice(a * LANE, (a + 1) * LANE)

    def one_step(k, carry):
        base = k * (3 * table_len)
        cos_t = [tab_ref[base + g] for g in range(table_len)]
        sin_t = [tab_ref[base + table_len + g] for g in range(table_len)]
        gain_t = [tab_ref[base + 2 * table_len + g] for g in range(table_len)]

        def forward_chunk(i, c):
            y0 = pl.multiple_of(i * ROW_CHUNK, ROW_CHUNK)
            parts = [
                (wout_ref[0, pl.ds(y0, ROW_CHUNK), blk(a)], wout_ref[1, pl.ds(y0, ROW_CHUNK), blk(a)])
                for a in range(FFT_BLOCKS)
            ]
            spec = fft16(parts, -1)
            for cc in range(FFT_BLOCKS):
                tc = tw_ref[0, cc:cc + 1, :]
                ts = tw_ref[1, cc:cc + 1, :]
                xr, xi = spec[cc]
                a_ref[pl.ds(cc * rows + y0, ROW_CHUNK), 0:LANE] = xr * tc + xi * ts
                a_ref[pl.ds(cc * rows + y0, ROW_CHUNK), LANE:2 * LANE] = xi * tc - xr * ts
            return c

        lax.fori_loop(0, chunks, forward_chunk, 0)
        spectrum = split_dot(a_ref[...], fhi_ref, flo_ref)
        for a in range(FFT_BLOCKS):
            regions = rid_ref[k, :, blk(a)]
            bits = [(regions & (1 << b)) != 0 for b in range(max(1, (table_len - 1).bit_length()))]
            cs_ref[:, blk(a)] = pick_bits(bits, cos_t)
            sn_ref[:, blk(a)] = pick_bits(bits, sin_t)
            gn_ref[:, blk(a)] = pick_bits(bits, gain_t)
        y_ref[...] = spectrum
        for cc in range(FFT_BLOCKS):
            band = slice(cc * rows, (cc + 1) * rows)
            yr = y_ref[band, 0:LANE]
            yi = y_ref[band, LANE:2 * LANE]
            mr = mult_ref[k, 0, cc:cc + 1, :]
            mi = mult_ref[k, 1, cc:cc + 1, :]
            a_ref[band, 0:LANE] = yr * mr - yi * mi
            a_ref[band, LANE:2 * LANE] = yr * mi + yi * mr
        y_ref[...] = split_dot(a_ref[...], ghi_ref, glo_ref)

        def inverse_chunk(i, c):
            y0 = pl.multiple_of(i * ROW_CHUNK, ROW_CHUNK)
            parts = []
            for cc in range(FFT_BLOCKS):
                zr = y_ref[pl.ds(cc * rows + y0, ROW_CHUNK), 0:LANE]
                zi = y_ref[pl.ds(cc * rows + y0, ROW_CHUNK), LANE:2 * LANE]
                tc = tw_ref[0, cc:cc + 1, :]
                ts = tw_ref[1, cc:cc + 1, :]
                parts.append((zr * tc - zi * ts, zr * ts + zi * tc))
            back = fft16(parts, 1)
            for a in range(FFT_BLOCKS):
                ur = back[a][0] * inv_len
                ui = back[a][1] * inv_len
                cs = cs_ref[pl.ds(y0, ROW_CHUNK), blk(a)]
                sn = sn_ref[pl.ds(y0, ROW_CHUNK), blk(a)]
                v_ref[0, pl.ds(y0, ROW_CHUNK), blk(a)] = ur * cs - ui * sn
                v_ref[1, pl.ds(y0, ROW_CHUNK), blk(a)] = ur * sn + ui * cs
            return c

        lax.fori_loop(0, chunks, inverse_chunk, 0)
        row_id = lax.broadcasted_iota(jnp.int32, (rows, LANE), 0)
        lane_id = lax.broadcasted_iota(jnp.int32, (rows, LANE), 1)
        cache = {}

        def cell(part, a):
            key = (part, a % FFT_BLOCKS)
            if key not in cache:
                v = v_ref[part, :, blk(a % FFT_BLOCKS)]
                cache[key] = (v, pltpu.roll(v, 1, 1), pltpu.roll(v, LANE - 1, 1))
            return cache[key]

        for a in range(FFT_BLOCKS):
            lap = []
            here = []
            for part in range(2):
                v, from_left, from_right = cell(part, a)
                prev_left = cell(part, a - 1)[1]
                next_right = cell(part, a + 1)[2]
                above = jnp.where(row_id == 0, 0.0, pltpu.roll(v, 1, 0))
                below = jnp.where(row_id == rows - 1, 0.0, pltpu.roll(v, rows - 1, 0))
                left = jnp.where(lane_id == 0, prev_left, from_left)
                right = jnp.where(lane_id == LANE - 1, next_right, from_right)
                lap.append(above + below + left + right - 4.0 * v)
                here.append(v)
            gain = gn_ref[:, blk(a)]
            new_re = here[0] + (lap[0] * DAMPING - lap[1] * gain)
            new_im = here[1] + (lap[0] * gain + lap[1] * DAMPING)
            wout_ref[0, :, blk(a)] = new_re
            wout_ref[1, :, blk(a)] = new_im
            for j in range(strip_count):
                img_ref[j, k, :, blk(a)] = new_re[j * rows_here:(j + 1) * rows_here]
        return carry

    lax.fori_loop(0, steps, one_step, 0)


def fast_constants(line_len):
    outer = line_len // LANE
    b = np.arange(LANE)
    ang = 2.0 * np.pi * (np.outer(b, b) % LANE) / LANE
    cos_m, sin_m = (np.cos(ang), np.sin(ang))
    fwd = np.block([[cos_m, -sin_m], [sin_m, cos_m]])
    inv = np.block([[cos_m, sin_m], [-sin_m, cos_m]])

    def halves(m):
        hi = m.astype(ml_dtypes.bfloat16)
        lo = (m - hi.astype(np.float64)).astype(ml_dtypes.bfloat16)
        return (hi, lo)

    c = np.arange(outer)
    tw_ang = 2.0 * np.pi * np.outer(c, b) / line_len
    twiddle = np.stack([np.cos(tw_ang), np.sin(tw_ang)]).astype(np.float32)
    q = c[:, None] + outer * b[None, :]
    signed = np.where(q >= line_len // 2, q - line_len, q).astype(np.float32)
    kx_cd = signed * np.float32(2.0 * math.pi / line_len)
    return (halves(fwd), halves(inv), twiddle, kx_cd.astype(np.float32))


def run_section(wave, regions, table, mult, consts, strip_count):
    (fhi, flo), (ghi, glo), twiddle, _ = consts
    rows, line_len = wave.shape[1], wave.shape[2]
    steps = regions.shape[0]
    table_len = table.shape[0] // (3 * steps)
    vmem = pl.BlockSpec(memory_space=pltpu.VMEM)
    flops = steps * (2 * 3 * 2 * (FFT_BLOCKS * rows) * 256 * 256 + 400 * rows * line_len)
    return pl.pallas_call(
        lambda *refs: section_kernel(*refs, table_len=table_len),
        out_shape=(
            jax.ShapeDtypeStruct(wave.shape, jnp.float32),
            jax.ShapeDtypeStruct((strip_count, steps, rows // strip_count, line_len), jnp.float32),
        ),
        in_specs=[pl.BlockSpec(memory_space=pltpu.SMEM)] + [vmem] * 8,
        out_specs=(vmem, vmem),
        scratch_shapes=[
            pltpu.VMEM((FFT_BLOCKS * rows, 2 * LANE), jnp.float32),
            pltpu.VMEM((FFT_BLOCKS * rows, 2 * LANE), jnp.float32),
            pltpu.VMEM((2, rows, line_len), jnp.float32),
            pltpu.VMEM((rows, line_len), jnp.float32),
            pltpu.VMEM((rows, line_len), jnp.float32),
            pltpu.VMEM((rows, line_len), jnp.float32),
        ],
        cost_estimate=pl.CostEstimate(
            flops=flops, transcendentals=0, bytes_accessed=4 * rows * line_len * 6 * steps
        ),
    )(table, wave, regions, mult, jnp.asarray(twiddle), jnp.asarray(fhi), jnp.asarray(flo),
      jnp.asarray(ghi), jnp.asarray(glo))


def section_tables(omega, region_speed, fd_coeff, ref_region, kx_cd):
    inv_speed = 1.0 / region_speed
    ref_slow = inv_speed[ref_region]
    regions = region_speed.shape[0]
    padded = 1 << max(1, (regions - 1).bit_length())
    extra = padded - regions
    phase = omega * (inv_speed[None, :] - ref_slow[:, None])
    gain = jnp.broadcast_to(fd_coeff / omega, phase.shape)
    parts = [jnp.cos(phase), jnp.sin(phase), gain]
    if extra:
        parts = [jnp.concatenate([p, jnp.repeat(p[:, -1:], extra, axis=1)], axis=1) for p in parts]
    table = jnp.stack(parts, axis=1).reshape(-1)
    wave_ref = omega * ref_slow
    wave_ref = wave_ref[:, None, None]
    excess = wave_ref * wave_ref - kx_cd * kx_cd
    decay_line = jnp.exp(-jnp.sqrt(jnp.maximum(-excess, 0.0)))
    vertical = jnp.sqrt(jnp.maximum(excess, 0.0))
    mult = jnp.stack([decay_line * jnp.cos(vertical), decay_line * jnp.sin(vertical)], axis=1)
    return (table, mult)


def fast_fits(surface, region_index, region_speed):
    freq_count = surface.shape[1]
    rows = surface.shape[2] * lax.axis_size("strip")
    line_len = surface.shape[3]
    return (
        freq_count == lax.axis_size("strip")
        and line_len == FFT_BLOCKS * LANE
        and rows % ROW_CHUNK == 0
        and surface.shape[2] % ROW_CHUNK == 0
        and rows <= 64
        and region_speed.shape[0] <= 16
    )


def strip_pairs(depths, strip_count, shift):
    return [
        (d * strip_count + r, d * strip_count + (r + shift) % strip_count)
        for d in depths
        for r in range(strip_count)
    ]


def gather_rows(local, depths, strip_no, strip_count, row_axis):
    rows = local.shape[row_axis]
    shape = list(local.shape)
    shape[row_axis] = rows * strip_count
    full = jnp.zeros(shape, local.dtype)
    start = [0] * len(shape)
    start[row_axis] = strip_no * rows
    full = lax.dynamic_update_slice(full, local, start)
    for shift in range(1, strip_count):
        got = lax.ppermute(local, ("depth", "strip"), strip_pairs(depths, strip_count, shift))
        start = [0] * len(shape)
        start[row_axis] = ((strip_no - shift) % strip_count) * rows
        full = lax.dynamic_update_slice(full, got, start)
    return full


def gather_strips(piece_of, local, depths, strip_no, strip_count, rows_here):
    rows = rows_here * strip_count
    shape = (local.shape[0], rows, local.shape[2])
    full = lax.dynamic_update_slice(
        jnp.zeros(shape, jnp.float32), local, (0, strip_no * rows_here, 0)
    )
    for shift in range(1, strip_count):
        target = (strip_no + shift) % strip_count
        got = lax.ppermute(
            piece_of(target), ("depth", "strip"), strip_pairs(depths, strip_count, shift)
        )
        source = (strip_no - shift) % strip_count
        full = lax.dynamic_update_slice(full, got, (0, source * rows_here, 0))
    return full


def shards(surface, omegas, region_speed, fd_coeff, region_index, ref_region):
    if not fast_fits(surface, region_index, region_speed):
        return shards_general(surface, omegas, region_speed, fd_coeff, region_index, ref_region)
    line_len = surface.shape[3]
    rows_here = surface.shape[2]
    steps = region_index.shape[0]
    segment_no = lax.axis_index("depth")
    segment_count = lax.axis_size("depth")
    strip_no = lax.axis_index("strip")
    strip_count = lax.axis_size("strip")
    consts = fast_constants(line_len)
    region_f = region_index.astype(jnp.float32)
    early = [d for d in range(segment_count) if d != 1]

    def with_surface(target):
        return jnp.concatenate(
            [region_f, lax.dynamic_index_in_dim(surface, target, 1, keepdims=False)], axis=0
        )

    gathered = gather_strips(
        with_surface, with_surface(strip_no), early, strip_no, strip_count, rows_here
    )
    regions_a = gathered[:steps].astype(jnp.int32)
    wave = gathered[steps:]
    omega = lax.dynamic_index_in_dim(omegas, strip_no, 0, keepdims=False)
    table, mult = section_tables(omega, region_speed, fd_coeff, ref_region, jnp.asarray(consts[3]))
    image = jnp.zeros((strip_count, steps, rows_here, line_len), jnp.float32)
    regions_b = regions_a

    def sweep(regions):
        def live(wave, image):
            return run_section(wave, regions, table, mult, consts, strip_count)

        return live

    def idle(wave, image):
        return (wave, image)

    def freq_sum(image, depths):
        parts = []
        for shift in range(1, strip_count):
            target = (strip_no + shift) % strip_count
            piece = lax.dynamic_index_in_dim(image, target, 0, keepdims=False)
            parts.append(
                lax.ppermute(piece, ("depth", "strip"), strip_pairs(depths, strip_count, shift))
            )
        return parts

    arrived = []
    for tick_no in range(segment_count):
        regions = regions_b if tick_no == 1 else regions_a
        wave, image = lax.cond(segment_no == tick_no, sweep(regions), idle, wave, image)
        if tick_no + 1 < segment_count:
            wave = lax.ppermute(wave, "depth", [(tick_no, tick_no + 1)])
        if tick_no == 0 and segment_count > 1:
            held, _ = lax.optimization_barrier((region_f, image))
            regions_b = gather_strips(
                lambda target: held, held, [1], strip_no, strip_count, rows_here
            ).astype(jnp.int32)
        if tick_no == segment_count - 2:
            wave, image = lax.optimization_barrier((wave, image))
            arrived += freq_sum(image, range(segment_count - 1))
    arrived += freq_sum(image, [segment_count - 1])
    total = lax.dynamic_index_in_dim(image, strip_no, 0, keepdims=False)
    for piece in arrived:
        total = total + piece
    return total


def solution(mesh):
    in_specs = (
        P(None, "shots", "strip", None),
        P(),
        P(),
        P(),
        P("depth", "strip", None),
        P("depth"),
    )
    out_specs = P("depth", "strip", "shots")
    return jax.shard_map(shards, mesh=mesh, in_specs=in_specs, out_specs=out_specs, check_vma=False)
```

```python
import math

import ml_dtypes
import numpy as np
import jax
import jax.numpy as jnp
from jax import lax
from jax.experimental import pallas as pl
from jax.experimental.pallas import tpu as pltpu
from jax.sharding import PartitionSpec as P

DAMPING = 0.05
PRECISE = lax.Precision.HIGHEST


def padded_2(cells, sides, width):
    for axis, dim in sides:
        count = lax.axis_size(axis)
        ends = count - 1
        head = lax.slice_in_dim(cells, 0, width, axis=dim)
        tail = lax.slice_in_dim(cells, cells.shape[dim] - width, cells.shape[dim], axis=dim)
        cells = jnp.concatenate(
            [
                lax.ppermute(tail, axis, [(i, (i + 1) % count) for i in range(ends)]),
                cells,
                lax.ppermute(head, axis, [((i + 1) % count, i) for i in range(ends)]),
            ],
            axis=dim,
        )
    return cells


def from_behind(value, axis, steps):
    count = lax.axis_size(axis)
    first, last = (max(0, -steps), min(count, count - steps))
    return lax.ppermute(value, axis, [(source, source + steps) for source in range(first, last)])


def complex_scale(values, cosine, sine_part):
    return jnp.stack(
        [values[0] * cosine - values[1] * sine_part, values[0] * sine_part + values[1] * cosine]
    )


def angle_pair(numerator, period):
    angle_grid = numerator.astype(jnp.float32) * (2.0 * math.pi / period)
    return (jnp.cos(angle_grid), jnp.sin(angle_grid))


def block_matrix(cosine, sine_part, forward):
    sign_flip = 1.0 if forward else -1.0
    return jnp.stack(
        [jnp.stack([cosine, -sign_flip * sine_part]), jnp.stack([sign_flip * sine_part, cosine])]
    )


def build_tables(line_len):
    block_len = 128
    outer_len = line_len // block_len
    inner_idx = jnp.arange(block_len)
    outer_idx = jnp.arange(outer_len)
    cos_large, sin_large = angle_pair(
        inner_idx[:, None] * inner_idx[None, :] % block_len, block_len
    )
    cos_small, sin_small = angle_pair(
        outer_idx[:, None] * outer_idx[None, :] % outer_len, outer_len
    )
    cos_twist, sin_twist = angle_pair(outer_idx[:, None] * inner_idx[None, :], line_len)
    wave_index = outer_idx[:, None] + outer_len * inner_idx[None, :]
    signed = jnp.where(wave_index >= line_len // 2, wave_index - line_len, wave_index)
    kx_grid = signed.astype(jnp.float32) * (2.0 * math.pi / line_len)
    small_fwd = block_matrix(cos_small, sin_small, True)
    small_inv = block_matrix(cos_small, sin_small, False)
    large_fwd = block_matrix(cos_large, sin_large, True)
    large_inv = block_matrix(cos_large, sin_large, False)
    return (small_fwd, small_inv, large_fwd, large_inv, cos_twist, sin_twist, kx_grid)


def forward_line(wavefield, tables):
    small_fwd, small_inv, large_fwd, large_inv, cos_twist, sin_twist, kx_grid = tables
    row_count = wavefield.shape[1]
    pieces = wavefield.reshape(2, row_count, cos_twist.shape[0], cos_twist.shape[1])
    mixed_part = jnp.einsum("zrab,zwca->wrcb", pieces, small_fwd, precision=PRECISE)
    mixed_part = complex_scale(mixed_part, cos_twist, -sin_twist)
    return jnp.einsum("zrcb,zwbd->wrcd", mixed_part, large_fwd, precision=PRECISE)


def inverse_line(spectrum, tables):
    small_fwd, small_inv, large_fwd, large_inv, cos_twist, sin_twist, kx_grid = tables
    row_count = spectrum.shape[1]
    line_len = cos_twist.shape[0] * cos_twist.shape[1]
    mixed_part = jnp.einsum("zrcd,zwdb->wrcb", spectrum, large_inv, precision=PRECISE)
    mixed_part = complex_scale(mixed_part, cos_twist, sin_twist)
    pieces = jnp.einsum("zrcb,zwca->wrab", mixed_part, small_inv, precision=PRECISE)
    return pieces.reshape(2, row_count, line_len) * (1.0 / line_len)


def lookup(regions, entries):
    picked = jnp.zeros(regions.shape, jnp.float32)
    for region_no in range(entries.shape[0]):
        picked = picked + jnp.where(regions == region_no, entries[region_no], 0.0)
    return picked


def depth_step(wavefield, omega_now, slow_cells, coef_cells, ref_slow, tables, pad_rows):
    kx_grid = tables[6]
    wave_ref = omega_now * ref_slow
    excess = wave_ref * wave_ref - kx_grid * kx_grid
    decay_line = jnp.exp(-jnp.sqrt(jnp.maximum(-excess, 0.0)))
    vertical = jnp.sqrt(jnp.maximum(excess, 0.0))
    spectrum = complex_scale(
        forward_line(wavefield, tables),
        decay_line * jnp.cos(vertical),
        decay_line * jnp.sin(vertical),
    )
    wavefield = inverse_line(spectrum, tables)
    phase_cell = omega_now * (slow_cells - ref_slow)
    wavefield = complex_scale(wavefield, jnp.cos(phase_cell), jnp.sin(phase_cell))
    padded = pad_rows(wavefield)
    laplace = (
        padded[:, :-2]
        + padded[:, 2:]
        + jnp.roll(wavefield, 1, 2)
        + jnp.roll(wavefield, -1, 2)
        - 4.0 * wavefield
    )
    return wavefield + complex_scale(laplace, DAMPING, coef_cells / omega_now)


def march(wavefield, omega_now, slow_block, coef_block, ref_block, tables, pad_rows):
    traces = []
    for step_no in range(slow_block.shape[0]):
        wavefield = depth_step(
            wavefield,
            omega_now,
            slow_block[step_no],
            coef_block[step_no],
            ref_block[step_no],
            tables,
            pad_rows,
        )
        traces.append(wavefield[0])
    return (wavefield, jnp.stack(traces))


def shards_general(surface, omegas, region_speed, fd_coeff, region_index, ref_region):
    line_len = surface.shape[3]
    rows_here = surface.shape[2]
    freq_count = surface.shape[1]
    step_count = region_index.shape[0]
    tables = build_tables(line_len)
    inv_speed = 1.0 / region_speed
    segment_no = lax.axis_index("depth")
    segment_count = lax.axis_size("depth")

    def pad_near(values):
        return padded_2(values, (("strip", 1),), 1)

    slow_cells = lookup(region_index, inv_speed)
    coef_cells = lookup(region_index, fd_coeff)
    ref_cells = lookup(ref_region, inv_speed)
    freq_index = jnp.arange(freq_count)
    image_out = jnp.zeros((step_count, rows_here, line_len), jnp.float32)
    arriving = jnp.zeros((2, rows_here, line_len), jnp.float32)
    tick_count = freq_count + segment_count - 1
    for tick_no in range(tick_count):
        batch_no = tick_no - segment_no
        is_live = (batch_no >= 0) & (batch_no < freq_count)
        clipped = jnp.clip(batch_no, 0, freq_count - 1)
        picked = lax.dynamic_index_in_dim(surface, clipped, 1, keepdims=False)
        entering = jnp.where(segment_no == 0, picked, arriving)
        omega_now = jnp.sum(jnp.where(freq_index == clipped, omegas, 0.0))
        leaving, traces = march(
            entering, omega_now, slow_cells, coef_cells, ref_cells, tables, pad_near
        )
        image_out = image_out + jnp.where(is_live, traces, 0.0)
        if tick_no + 1 < tick_count:
            arriving = from_behind(leaving, "depth", 1)
    return image_out


LANE = 128
FFT_BLOCKS = 16
ROW_CHUNK = 8


def fft4(x0, x1, x2, x3, sign):
    s0 = (x0[0] + x2[0], x0[1] + x2[1])
    d0 = (x0[0] - x2[0], x0[1] - x2[1])
    s1 = (x1[0] + x3[0], x1[1] + x3[1])
    d1 = (x1[0] - x3[0], x1[1] - x3[1])
    if sign < 0:
        wd = (d1[1], -d1[0])
    else:
        wd = (-d1[1], d1[0])
    return (
        (s0[0] + s1[0], s0[1] + s1[1]),
        (d0[0] + wd[0], d0[1] + wd[1]),
        (s0[0] - s1[0], s0[1] - s1[1]),
        (d0[0] - wd[0], d0[1] - wd[1]),
    )


def turn_const(value, power, sign):
    if power == 4:
        return (-value[1], value[0]) if sign > 0 else (value[1], -value[0])
    angle = sign * 2.0 * math.pi * power / 16.0
    cr, ci = (math.cos(angle), math.sin(angle))
    return (value[0] * cr - value[1] * ci, value[0] * ci + value[1] * cr)


def fft16(parts, sign):
    mid = [[None] * 4 for _ in range(4)]
    for a0 in range(4):
        ys = fft4(parts[a0], parts[4 + a0], parts[8 + a0], parts[12 + a0], sign)
        for c0 in range(4):
            power = a0 * c0
            mid[a0][c0] = ys[c0] if power == 0 else turn_const(ys[c0], power, sign)
    out = [None] * 16
    for c0 in range(4):
        zs = fft4(mid[0][c0], mid[1][c0], mid[2][c0], mid[3][c0], sign)
        for c1 in range(4):
            out[c0 + 4 * c1] = zs[c1]
    return out


def pick(regions, values):
    level = list(values)
    bit = 1
    while len(level) > 1:
        chosen = (regions & bit) != 0
        level = [jnp.where(chosen, level[i + 1], level[i]) for i in range(0, len(level), 2)]
        bit *= 2
    return jnp.broadcast_to(level[0], regions.shape)


def pick_bits(bits, values):
    level = list(values)
    for chosen in bits:
        level = [jnp.where(chosen, level[i + 1], level[i]) for i in range(0, len(level), 2)]
    return jnp.broadcast_to(level[0], bits[0].shape)


def split_dot(values, hi_ref, lo_ref):
    high = values.astype(jnp.bfloat16)
    low = (values - high.astype(jnp.float32)).astype(jnp.bfloat16)
    main = jnp.dot(high, hi_ref[...], preferred_element_type=jnp.float32)
    fix = jnp.dot(high, lo_ref[...], preferred_element_type=jnp.float32) + jnp.dot(
        low, hi_ref[:, :], preferred_element_type=jnp.float32
    )
    return main + fix


def section_kernel(
    tab_ref, w_ref, rid_ref, mult_ref, tw_ref, fhi_ref, flo_ref, ghi_ref, glo_ref,
    wout_ref, img_ref, a_ref, y_ref, v_ref, cs_ref, sn_ref, gn_ref, *, table_len
):
    rows = w_ref.shape[1]
    line_len = w_ref.shape[2]
    steps = rid_ref.shape[0]
    strip_count, rows_here = img_ref.shape[0], img_ref.shape[2]
    chunks = rows // ROW_CHUNK
    inv_len = 1.0 / line_len
    wout_ref[...] = w_ref[...]

    def blk(a):
        return slice(a * LANE, (a + 1) * LANE)

    def one_step(k, carry):
        base = k * (3 * table_len)
        cos_t = [tab_ref[base + g] for g in range(table_len)]
        sin_t = [tab_ref[base + table_len + g] for g in range(table_len)]
        gain_t = [tab_ref[base + 2 * table_len + g] for g in range(table_len)]

        def forward_chunk(i, c):
            y0 = pl.multiple_of(i * ROW_CHUNK, ROW_CHUNK)
            parts = [
                (wout_ref[0, pl.ds(y0, ROW_CHUNK), blk(a)], wout_ref[1, pl.ds(y0, ROW_CHUNK), blk(a)])
                for a in range(FFT_BLOCKS)
            ]
            spec = fft16(parts, -1)
            for cc in range(FFT_BLOCKS):
                tc = tw_ref[0, cc:cc + 1, :]
                ts = tw_ref[1, cc:cc + 1, :]
                xr, xi = spec[cc]
                a_ref[pl.ds(cc * rows + y0, ROW_CHUNK), 0:LANE] = xr * tc + xi * ts
                a_ref[pl.ds(cc * rows + y0, ROW_CHUNK), LANE:2 * LANE] = xi * tc - xr * ts
            return c

        lax.fori_loop(0, chunks, forward_chunk, 0)
        spectrum = split_dot(a_ref[...], fhi_ref, flo_ref)
        for a in range(FFT_BLOCKS):
            regions = rid_ref[k, :, blk(a)]
            bits = [(regions & (1 << b)) != 0 for b in range(max(1, (table_len - 1).bit_length()))]
            cs_ref[:, blk(a)] = pick_bits(bits, cos_t)
            sn_ref[:, blk(a)] = pick_bits(bits, sin_t)
            gn_ref[:, blk(a)] = pick_bits(bits, gain_t)
        y_ref[...] = spectrum
        for cc in range(FFT_BLOCKS):
            band = slice(cc * rows, (cc + 1) * rows)
            yr = y_ref[band, 0:LANE]
            yi = y_ref[band, LANE:2 * LANE]
            mr = mult_ref[k, 0, cc:cc + 1, :]
            mi = mult_ref[k, 1, cc:cc + 1, :]
            a_ref[band, 0:LANE] = yr * mr - yi * mi
            a_ref[band, LANE:2 * LANE] = yr * mi + yi * mr
        y_ref[...] = split_dot(a_ref[...], ghi_ref, glo_ref)

        def inverse_chunk(i, c):
            y0 = pl.multiple_of(i * ROW_CHUNK, ROW_CHUNK)
            parts = []
            for cc in range(FFT_BLOCKS):
                zr = y_ref[pl.ds(cc * rows + y0, ROW_CHUNK), 0:LANE]
                zi = y_ref[pl.ds(cc * rows + y0, ROW_CHUNK), LANE:2 * LANE]
                tc = tw_ref[0, cc:cc + 1, :]
                ts = tw_ref[1, cc:cc + 1, :]
                parts.append((zr * tc - zi * ts, zr * ts + zi * tc))
            back = fft16(parts, 1)
            for a in range(FFT_BLOCKS):
                ur = back[a][0] * inv_len
                ui = back[a][1] * inv_len
                cs = cs_ref[pl.ds(y0, ROW_CHUNK), blk(a)]
                sn = sn_ref[pl.ds(y0, ROW_CHUNK), blk(a)]
                v_ref[0, pl.ds(y0, ROW_CHUNK), blk(a)] = ur * cs - ui * sn
                v_ref[1, pl.ds(y0, ROW_CHUNK), blk(a)] = ur * sn + ui * cs
            return c

        lax.fori_loop(0, chunks, inverse_chunk, 0)
        row_id = lax.broadcasted_iota(jnp.int32, (rows, LANE), 0)
        lane_id = lax.broadcasted_iota(jnp.int32, (rows, LANE), 1)
        cache = {}

        def cell(part, a):
            key = (part, a % FFT_BLOCKS)
            if key not in cache:
                v = v_ref[part, :, blk(a % FFT_BLOCKS)]
                cache[key] = (v, pltpu.roll(v, 1, 1), pltpu.roll(v, LANE - 1, 1))
            return cache[key]

        for a in range(FFT_BLOCKS):
            lap = []
            here = []
            for part in range(2):
                v, from_left, from_right = cell(part, a)
                prev_left = cell(part, a - 1)[1]
                next_right = cell(part, a + 1)[2]
                above = jnp.where(row_id == 0, 0.0, pltpu.roll(v, 1, 0))
                below = jnp.where(row_id == rows - 1, 0.0, pltpu.roll(v, rows - 1, 0))
                left = jnp.where(lane_id == 0, prev_left, from_left)
                right = jnp.where(lane_id == LANE - 1, next_right, from_right)
                lap.append(above + below + left + right - 4.0 * v)
                here.append(v)
            gain = gn_ref[:, blk(a)]
            new_re = here[0] + (lap[0] * DAMPING - lap[1] * gain)
            new_im = here[1] + (lap[0] * gain + lap[1] * DAMPING)
            wout_ref[0, :, blk(a)] = new_re
            wout_ref[1, :, blk(a)] = new_im
            for j in range(strip_count):
                img_ref[j, k, :, blk(a)] = new_re[j * rows_here:(j + 1) * rows_here]
        return carry

    lax.fori_loop(0, steps, one_step, 0)


def fast_constants(line_len):
    outer = line_len // LANE
    b = np.arange(LANE)
    ang = 2.0 * np.pi * (np.outer(b, b) % LANE) / LANE
    cos_m, sin_m = (np.cos(ang), np.sin(ang))
    fwd = np.block([[cos_m, -sin_m], [sin_m, cos_m]])
    inv = np.block([[cos_m, sin_m], [-sin_m, cos_m]])

    def halves(m):
        hi = m.astype(ml_dtypes.bfloat16)
        lo = (m - hi.astype(np.float64)).astype(ml_dtypes.bfloat16)
        return (hi, lo)

    c = np.arange(outer)
    tw_ang = 2.0 * np.pi * np.outer(c, b) / line_len
    twiddle = np.stack([np.cos(tw_ang), np.sin(tw_ang)]).astype(np.float32)
    q = c[:, None] + outer * b[None, :]
    signed = np.where(q >= line_len // 2, q - line_len, q).astype(np.float32)
    kx_cd = signed * np.float32(2.0 * math.pi / line_len)
    return (halves(fwd), halves(inv), twiddle, kx_cd.astype(np.float32))


def run_section(wave, regions, table, mult, consts, strip_count):
    (fhi, flo), (ghi, glo), twiddle, _ = consts
    rows, line_len = wave.shape[1], wave.shape[2]
    steps = regions.shape[0]
    table_len = table.shape[0] // (3 * steps)
    vmem = pl.BlockSpec(memory_space=pltpu.VMEM)
    flops = steps * (2 * 3 * 2 * (FFT_BLOCKS * rows) * 256 * 256 + 400 * rows * line_len)
    return pl.pallas_call(
        lambda *refs: section_kernel(*refs, table_len=table_len),
        out_shape=(
            jax.ShapeDtypeStruct(wave.shape, jnp.float32),
            jax.ShapeDtypeStruct((strip_count, steps, rows // strip_count, line_len), jnp.float32),
        ),
        in_specs=[pl.BlockSpec(memory_space=pltpu.SMEM)] + [vmem] * 8,
        out_specs=(vmem, vmem),
        scratch_shapes=[
            pltpu.VMEM((FFT_BLOCKS * rows, 2 * LANE), jnp.float32),
            pltpu.VMEM((FFT_BLOCKS * rows, 2 * LANE), jnp.float32),
            pltpu.VMEM((2, rows, line_len), jnp.float32),
            pltpu.VMEM((rows, line_len), jnp.float32),
            pltpu.VMEM((rows, line_len), jnp.float32),
            pltpu.VMEM((rows, line_len), jnp.float32),
        ],
        cost_estimate=pl.CostEstimate(
            flops=flops, transcendentals=0, bytes_accessed=4 * rows * line_len * 6 * steps
        ),
    )(table, wave, regions, mult, jnp.asarray(twiddle), jnp.asarray(fhi), jnp.asarray(flo),
      jnp.asarray(ghi), jnp.asarray(glo))


def section_tables(omega, region_speed, fd_coeff, ref_region, kx_cd):
    inv_speed = 1.0 / region_speed
    ref_slow = inv_speed[ref_region]
    regions = region_speed.shape[0]
    padded = 1 << max(1, (regions - 1).bit_length())
    extra = padded - regions
    phase = omega * (inv_speed[None, :] - ref_slow[:, None])
    gain = jnp.broadcast_to(fd_coeff / omega, phase.shape)
    parts = [jnp.cos(phase), jnp.sin(phase), gain]
    if extra:
        parts = [jnp.concatenate([p, jnp.repeat(p[:, -1:], extra, axis=1)], axis=1) for p in parts]
    table = jnp.stack(parts, axis=1).reshape(-1)
    wave_ref = omega * ref_slow
    wave_ref = wave_ref[:, None, None]
    excess = wave_ref * wave_ref - kx_cd * kx_cd
    decay_line = jnp.exp(-jnp.sqrt(jnp.maximum(-excess, 0.0)))
    vertical = jnp.sqrt(jnp.maximum(excess, 0.0))
    mult = jnp.stack([decay_line * jnp.cos(vertical), decay_line * jnp.sin(vertical)], axis=1)
    return (table, mult)


def fast_fits(surface, region_index, region_speed):
    freq_count = surface.shape[1]
    rows = surface.shape[2] * lax.axis_size("strip")
    line_len = surface.shape[3]
    return (
        freq_count == lax.axis_size("strip")
        and line_len == FFT_BLOCKS * LANE
        and rows % ROW_CHUNK == 0
        and surface.shape[2] % ROW_CHUNK == 0
        and rows <= 64
        and region_speed.shape[0] <= 16
    )


def strip_pairs(depths, strip_count, shift):
    return [
        (d * strip_count + r, d * strip_count + (r + shift) % strip_count)
        for d in depths
        for r in range(strip_count)
    ]


def gather_rows(local, depths, strip_no, strip_count, row_axis):
    rows = local.shape[row_axis]
    shape = list(local.shape)
    shape[row_axis] = rows * strip_count
    full = jnp.zeros(shape, local.dtype)
    start = [0] * len(shape)
    start[row_axis] = strip_no * rows
    full = lax.dynamic_update_slice(full, local, start)
    for shift in range(1, strip_count):
        got = lax.ppermute(local, ("depth", "strip"), strip_pairs(depths, strip_count, shift))
        start = [0] * len(shape)
        start[row_axis] = ((strip_no - shift) % strip_count) * rows
        full = lax.dynamic_update_slice(full, got, start)
    return full


def gather_strips(piece_of, local, depths, strip_no, strip_count, rows_here):
    rows = rows_here * strip_count
    shape = (local.shape[0], rows, local.shape[2])
    full = lax.dynamic_update_slice(
        jnp.zeros(shape, jnp.float32), local, (0, strip_no * rows_here, 0)
    )
    for shift in range(1, strip_count):
        target = (strip_no + shift) % strip_count
        got = lax.ppermute(
            piece_of(target), ("depth", "strip"), strip_pairs(depths, strip_count, shift)
        )
        source = (strip_no - shift) % strip_count
        full = lax.dynamic_update_slice(full, got, (0, source * rows_here, 0))
    return full


def shards(surface, omegas, region_speed, fd_coeff, region_index, ref_region):
    if not fast_fits(surface, region_index, region_speed):
        return shards_general(surface, omegas, region_speed, fd_coeff, region_index, ref_region)
    line_len = surface.shape[3]
    rows_here = surface.shape[2]
    steps = region_index.shape[0]
    segment_no = lax.axis_index("depth")
    segment_count = lax.axis_size("depth")
    strip_no = lax.axis_index("strip")
    strip_count = lax.axis_size("strip")
    consts = fast_constants(line_len)
    region_f = region_index.astype(jnp.float32)
    early = [d for d in range(segment_count) if d != 1]

    def with_surface(target):
        return jnp.concatenate(
            [region_f, lax.dynamic_index_in_dim(surface, target, 1, keepdims=False)], axis=0
        )

    gathered = gather_strips(
        with_surface, with_surface(strip_no), early, strip_no, strip_count, rows_here
    )
    regions_a = gathered[:steps].astype(jnp.int32)
    wave = gathered[steps:]
    omega = lax.dynamic_index_in_dim(omegas, strip_no, 0, keepdims=False)
    table, mult = section_tables(omega, region_speed, fd_coeff, ref_region, jnp.asarray(consts[3]))
    image = jnp.zeros((strip_count, steps, rows_here, line_len), jnp.float32)
    regions_b = regions_a

    def sweep(regions):
        def live(wave, image):
            return run_section(wave, regions, table, mult, consts, strip_count)

        return live

    def idle(wave, image):
        return (wave, image)

    def freq_sum(image, depths):
        parts = []
        for shift in range(1, strip_count):
            target = (strip_no + shift) % strip_count
            piece = lax.dynamic_index_in_dim(image, target, 0, keepdims=False)
            parts.append(
                lax.ppermute(piece, ("depth", "strip"), strip_pairs(depths, strip_count, shift))
            )
        return parts

    arrived = []
    for tick_no in range(segment_count):
        regions = regions_b if tick_no == 1 else regions_a
        if tick_no == 0:
            wave, image = sweep(regions)(wave, image)
        else:
            wave, image = lax.cond(segment_no == tick_no, sweep(regions), idle, wave, image)
        if tick_no + 1 < segment_count:
            wave = lax.ppermute(wave, "depth", [(tick_no, tick_no + 1)])
        if tick_no == 0 and segment_count > 1:
            held, _ = lax.optimization_barrier((region_f, image))
            regions_b = gather_strips(
                lambda target: held, held, [1], strip_no, strip_count, rows_here
            ).astype(jnp.int32)
        if tick_no == segment_count - 2:
            wave, image = lax.optimization_barrier((wave, image))
            arrived += freq_sum(image, range(segment_count - 1))
    arrived += freq_sum(image, [segment_count - 1])
    total = lax.dynamic_index_in_dim(image, strip_no, 0, keepdims=False)
    for piece in arrived:
        total = total + piece
    return total


def solution(mesh):
    in_specs = (
        P(None, "shots", "strip", None),
        P(),
        P(),
        P(),
        P("depth", "strip", None),
        P("depth"),
    )
    out_specs = P("depth", "strip", "shots")
    return jax.shard_map(shards, mesh=mesh, in_specs=in_specs, out_specs=out_specs, check_vma=False)
```

```python
import math

import ml_dtypes
import numpy as np
import jax
import jax.numpy as jnp
from jax import lax
from jax.experimental import pallas as pl
from jax.experimental.pallas import tpu as pltpu
from jax.sharding import PartitionSpec as P

DAMPING = 0.05
PRECISE = lax.Precision.HIGHEST


def padded_2(cells, sides, width):
    for axis, dim in sides:
        count = lax.axis_size(axis)
        ends = count - 1
        head = lax.slice_in_dim(cells, 0, width, axis=dim)
        tail = lax.slice_in_dim(cells, cells.shape[dim] - width, cells.shape[dim], axis=dim)
        cells = jnp.concatenate(
            [
                lax.ppermute(tail, axis, [(i, (i + 1) % count) for i in range(ends)]),
                cells,
                lax.ppermute(head, axis, [((i + 1) % count, i) for i in range(ends)]),
            ],
            axis=dim,
        )
    return cells


def from_behind(value, axis, steps):
    count = lax.axis_size(axis)
    first, last = (max(0, -steps), min(count, count - steps))
    return lax.ppermute(value, axis, [(source, source + steps) for source in range(first, last)])


def complex_scale(values, cosine, sine_part):
    return jnp.stack(
        [values[0] * cosine - values[1] * sine_part, values[0] * sine_part + values[1] * cosine]
    )


def angle_pair(numerator, period):
    angle_grid = numerator.astype(jnp.float32) * (2.0 * math.pi / period)
    return (jnp.cos(angle_grid), jnp.sin(angle_grid))


def block_matrix(cosine, sine_part, forward):
    sign_flip = 1.0 if forward else -1.0
    return jnp.stack(
        [jnp.stack([cosine, -sign_flip * sine_part]), jnp.stack([sign_flip * sine_part, cosine])]
    )


def build_tables(line_len):
    block_len = 128
    outer_len = line_len // block_len
    inner_idx = jnp.arange(block_len)
    outer_idx = jnp.arange(outer_len)
    cos_large, sin_large = angle_pair(
        inner_idx[:, None] * inner_idx[None, :] % block_len, block_len
    )
    cos_small, sin_small = angle_pair(
        outer_idx[:, None] * outer_idx[None, :] % outer_len, outer_len
    )
    cos_twist, sin_twist = angle_pair(outer_idx[:, None] * inner_idx[None, :], line_len)
    wave_index = outer_idx[:, None] + outer_len * inner_idx[None, :]
    signed = jnp.where(wave_index >= line_len // 2, wave_index - line_len, wave_index)
    kx_grid = signed.astype(jnp.float32) * (2.0 * math.pi / line_len)
    small_fwd = block_matrix(cos_small, sin_small, True)
    small_inv = block_matrix(cos_small, sin_small, False)
    large_fwd = block_matrix(cos_large, sin_large, True)
    large_inv = block_matrix(cos_large, sin_large, False)
    return (small_fwd, small_inv, large_fwd, large_inv, cos_twist, sin_twist, kx_grid)


def forward_line(wavefield, tables):
    small_fwd, small_inv, large_fwd, large_inv, cos_twist, sin_twist, kx_grid = tables
    row_count = wavefield.shape[1]
    pieces = wavefield.reshape(2, row_count, cos_twist.shape[0], cos_twist.shape[1])
    mixed_part = jnp.einsum("zrab,zwca->wrcb", pieces, small_fwd, precision=PRECISE)
    mixed_part = complex_scale(mixed_part, cos_twist, -sin_twist)
    return jnp.einsum("zrcb,zwbd->wrcd", mixed_part, large_fwd, precision=PRECISE)


def inverse_line(spectrum, tables):
    small_fwd, small_inv, large_fwd, large_inv, cos_twist, sin_twist, kx_grid = tables
    row_count = spectrum.shape[1]
    line_len = cos_twist.shape[0] * cos_twist.shape[1]
    mixed_part = jnp.einsum("zrcd,zwdb->wrcb", spectrum, large_inv, precision=PRECISE)
    mixed_part = complex_scale(mixed_part, cos_twist, sin_twist)
    pieces = jnp.einsum("zrcb,zwca->wrab", mixed_part, small_inv, precision=PRECISE)
    return pieces.reshape(2, row_count, line_len) * (1.0 / line_len)


def lookup(regions, entries):
    picked = jnp.zeros(regions.shape, jnp.float32)
    for region_no in range(entries.shape[0]):
        picked = picked + jnp.where(regions == region_no, entries[region_no], 0.0)
    return picked


def depth_step(wavefield, omega_now, slow_cells, coef_cells, ref_slow, tables, pad_rows):
    kx_grid = tables[6]
    wave_ref = omega_now * ref_slow
    excess = wave_ref * wave_ref - kx_grid * kx_grid
    decay_line = jnp.exp(-jnp.sqrt(jnp.maximum(-excess, 0.0)))
    vertical = jnp.sqrt(jnp.maximum(excess, 0.0))
    spectrum = complex_scale(
        forward_line(wavefield, tables),
        decay_line * jnp.cos(vertical),
        decay_line * jnp.sin(vertical),
    )
    wavefield = inverse_line(spectrum, tables)
    phase_cell = omega_now * (slow_cells - ref_slow)
    wavefield = complex_scale(wavefield, jnp.cos(phase_cell), jnp.sin(phase_cell))
    padded = pad_rows(wavefield)
    laplace = (
        padded[:, :-2]
        + padded[:, 2:]
        + jnp.roll(wavefield, 1, 2)
        + jnp.roll(wavefield, -1, 2)
        - 4.0 * wavefield
    )
    return wavefield + complex_scale(laplace, DAMPING, coef_cells / omega_now)


def march(wavefield, omega_now, slow_block, coef_block, ref_block, tables, pad_rows):
    traces = []
    for step_no in range(slow_block.shape[0]):
        wavefield = depth_step(
            wavefield,
            omega_now,
            slow_block[step_no],
            coef_block[step_no],
            ref_block[step_no],
            tables,
            pad_rows,
        )
        traces.append(wavefield[0])
    return (wavefield, jnp.stack(traces))


def shards_general(surface, omegas, region_speed, fd_coeff, region_index, ref_region):
    line_len = surface.shape[3]
    rows_here = surface.shape[2]
    freq_count = surface.shape[1]
    step_count = region_index.shape[0]
    tables = build_tables(line_len)
    inv_speed = 1.0 / region_speed
    segment_no = lax.axis_index("depth")
    segment_count = lax.axis_size("depth")

    def pad_near(values):
        return padded_2(values, (("strip", 1),), 1)

    slow_cells = lookup(region_index, inv_speed)
    coef_cells = lookup(region_index, fd_coeff)
    ref_cells = lookup(ref_region, inv_speed)
    freq_index = jnp.arange(freq_count)
    image_out = jnp.zeros((step_count, rows_here, line_len), jnp.float32)
    arriving = jnp.zeros((2, rows_here, line_len), jnp.float32)
    tick_count = freq_count + segment_count - 1
    for tick_no in range(tick_count):
        batch_no = tick_no - segment_no
        is_live = (batch_no >= 0) & (batch_no < freq_count)
        clipped = jnp.clip(batch_no, 0, freq_count - 1)
        picked = lax.dynamic_index_in_dim(surface, clipped, 1, keepdims=False)
        entering = jnp.where(segment_no == 0, picked, arriving)
        omega_now = jnp.sum(jnp.where(freq_index == clipped, omegas, 0.0))
        leaving, traces = march(
            entering, omega_now, slow_cells, coef_cells, ref_cells, tables, pad_near
        )
        image_out = image_out + jnp.where(is_live, traces, 0.0)
        if tick_no + 1 < tick_count:
            arriving = from_behind(leaving, "depth", 1)
    return image_out


LANE = 128
FFT_BLOCKS = 16
ROW_CHUNK = 8


def fft4(x0, x1, x2, x3, sign):
    s0 = (x0[0] + x2[0], x0[1] + x2[1])
    d0 = (x0[0] - x2[0], x0[1] - x2[1])
    s1 = (x1[0] + x3[0], x1[1] + x3[1])
    d1 = (x1[0] - x3[0], x1[1] - x3[1])
    if sign < 0:
        wd = (d1[1], -d1[0])
    else:
        wd = (-d1[1], d1[0])
    return (
        (s0[0] + s1[0], s0[1] + s1[1]),
        (d0[0] + wd[0], d0[1] + wd[1]),
        (s0[0] - s1[0], s0[1] - s1[1]),
        (d0[0] - wd[0], d0[1] - wd[1]),
    )


def turn_const(value, power, sign):
    if power == 4:
        return (-value[1], value[0]) if sign > 0 else (value[1], -value[0])
    angle = sign * 2.0 * math.pi * power / 16.0
    cr, ci = (math.cos(angle), math.sin(angle))
    return (value[0] * cr - value[1] * ci, value[0] * ci + value[1] * cr)


def fft16(parts, sign):
    mid = [[None] * 4 for _ in range(4)]
    for a0 in range(4):
        ys = fft4(parts[a0], parts[4 + a0], parts[8 + a0], parts[12 + a0], sign)
        for c0 in range(4):
            power = a0 * c0
            mid[a0][c0] = ys[c0] if power == 0 else turn_const(ys[c0], power, sign)
    out = [None] * 16
    for c0 in range(4):
        zs = fft4(mid[0][c0], mid[1][c0], mid[2][c0], mid[3][c0], sign)
        for c1 in range(4):
            out[c0 + 4 * c1] = zs[c1]
    return out


def pick(regions, values):
    level = list(values)
    bit = 1
    while len(level) > 1:
        chosen = (regions & bit) != 0
        level = [jnp.where(chosen, level[i + 1], level[i]) for i in range(0, len(level), 2)]
        bit *= 2
    return jnp.broadcast_to(level[0], regions.shape)


def pick_bits(bits, values):
    level = list(values)
    for chosen in bits:
        level = [jnp.where(chosen, level[i + 1], level[i]) for i in range(0, len(level), 2)]
    return jnp.broadcast_to(level[0], bits[0].shape)


def split_dot(values, hi_ref, lo_ref):
    high = values.astype(jnp.bfloat16)
    low = (values - high.astype(jnp.float32)).astype(jnp.bfloat16)
    main = jnp.dot(high, hi_ref[...], preferred_element_type=jnp.float32)
    fix = jnp.dot(high, lo_ref[...], preferred_element_type=jnp.float32) + jnp.dot(
        low, hi_ref[:, :], preferred_element_type=jnp.float32
    )
    return main + fix


def section_kernel(
    tab_ref, w_ref, rid_ref, mult_ref, tw_ref, fhi_ref, flo_ref, ghi_ref, glo_ref,
    wout_ref, img_ref, a_ref, y_ref, v_ref, cs_ref, sn_ref, gn_ref, *, table_len
):
    rows = w_ref.shape[1]
    line_len = w_ref.shape[2]
    steps = rid_ref.shape[0]
    strip_count, rows_here = img_ref.shape[0], img_ref.shape[2]
    chunks = rows // ROW_CHUNK
    inv_len = 1.0 / line_len
    wout_ref[...] = w_ref[...]

    def blk(a):
        return slice(a * LANE, (a + 1) * LANE)

    def one_step(k, carry):
        base = k * (3 * table_len)
        cos_t = [tab_ref[base + g] for g in range(table_len)]
        sin_t = [tab_ref[base + table_len + g] for g in range(table_len)]
        gain_t = [tab_ref[base + 2 * table_len + g] for g in range(table_len)]

        def forward_chunk(i, c):
            y0 = pl.multiple_of(i * ROW_CHUNK, ROW_CHUNK)
            parts = [
                (wout_ref[0, pl.ds(y0, ROW_CHUNK), blk(a)], wout_ref[1, pl.ds(y0, ROW_CHUNK), blk(a)])
                for a in range(FFT_BLOCKS)
            ]
            spec = fft16(parts, -1)
            for cc in range(FFT_BLOCKS):
                tc = tw_ref[0, cc:cc + 1, :]
                ts = tw_ref[1, cc:cc + 1, :]
                xr, xi = spec[cc]
                a_ref[pl.ds(cc * rows + y0, ROW_CHUNK), 0:LANE] = xr * tc + xi * ts
                a_ref[pl.ds(cc * rows + y0, ROW_CHUNK), LANE:2 * LANE] = xi * tc - xr * ts
            return c

        lax.fori_loop(0, chunks, forward_chunk, 0)
        spectrum = split_dot(a_ref[...], fhi_ref, flo_ref)
        for a in range(FFT_BLOCKS):
            regions = rid_ref[k, :, blk(a)]
            bits = [(regions & (1 << b)) != 0 for b in range(max(1, (table_len - 1).bit_length()))]
            cs_ref[:, blk(a)] = pick_bits(bits, cos_t)
            sn_ref[:, blk(a)] = pick_bits(bits, sin_t)
            gn_ref[:, blk(a)] = pick_bits(bits, gain_t)
        y_ref[...] = spectrum
        for cc in range(FFT_BLOCKS):
            band = slice(cc * rows, (cc + 1) * rows)
            yr = y_ref[band, 0:LANE]
            yi = y_ref[band, LANE:2 * LANE]
            mr = mult_ref[k, 0, cc:cc + 1, :]
            mi = mult_ref[k, 1, cc:cc + 1, :]
            a_ref[band, 0:LANE] = yr * mr - yi * mi
            a_ref[band, LANE:2 * LANE] = yr * mi + yi * mr
        y_ref[...] = split_dot(a_ref[...], ghi_ref, glo_ref)

        def inverse_chunk(i, c):
            y0 = pl.multiple_of(i * ROW_CHUNK, ROW_CHUNK)
            parts = []
            for cc in range(FFT_BLOCKS):
                zr = y_ref[pl.ds(cc * rows + y0, ROW_CHUNK), 0:LANE]
                zi = y_ref[pl.ds(cc * rows + y0, ROW_CHUNK), LANE:2 * LANE]
                tc = tw_ref[0, cc:cc + 1, :]
                ts = tw_ref[1, cc:cc + 1, :]
                parts.append((zr * tc - zi * ts, zr * ts + zi * tc))
            back = fft16(parts, 1)
            for a in range(FFT_BLOCKS):
                ur = back[a][0] * inv_len
                ui = back[a][1] * inv_len
                cs = cs_ref[pl.ds(y0, ROW_CHUNK), blk(a)]
                sn = sn_ref[pl.ds(y0, ROW_CHUNK), blk(a)]
                v_ref[0, pl.ds(y0, ROW_CHUNK), blk(a)] = ur * cs - ui * sn
                v_ref[1, pl.ds(y0, ROW_CHUNK), blk(a)] = ur * sn + ui * cs
            return c

        lax.fori_loop(0, chunks, inverse_chunk, 0)
        row_id = lax.broadcasted_iota(jnp.int32, (rows, LANE), 0)
        lane_id = lax.broadcasted_iota(jnp.int32, (rows, LANE), 1)
        cache = {}

        def cell(part, a):
            key = (part, a % FFT_BLOCKS)
            if key not in cache:
                v = v_ref[part, :, blk(a % FFT_BLOCKS)]
                cache[key] = (v, pltpu.roll(v, 1, 1), pltpu.roll(v, LANE - 1, 1))
            return cache[key]

        for a in range(FFT_BLOCKS):
            lap = []
            here = []
            for part in range(2):
                v, from_left, from_right = cell(part, a)
                prev_left = cell(part, a - 1)[1]
                next_right = cell(part, a + 1)[2]
                above = jnp.where(row_id == 0, 0.0, pltpu.roll(v, 1, 0))
                below = jnp.where(row_id == rows - 1, 0.0, pltpu.roll(v, rows - 1, 0))
                left = jnp.where(lane_id == 0, prev_left, from_left)
                right = jnp.where(lane_id == LANE - 1, next_right, from_right)
                lap.append(above + below + left + right - 4.0 * v)
                here.append(v)
            gain = gn_ref[:, blk(a)]
            new_re = here[0] + (lap[0] * DAMPING - lap[1] * gain)
            new_im = here[1] + (lap[0] * gain + lap[1] * DAMPING)
            wout_ref[0, :, blk(a)] = new_re
            wout_ref[1, :, blk(a)] = new_im
            for j in range(strip_count):
                img_ref[j, k, :, blk(a)] = new_re[j * rows_here:(j + 1) * rows_here]
        return carry

    lax.fori_loop(0, steps, one_step, 0)


def fast_constants(line_len):
    outer = line_len // LANE
    b = np.arange(LANE)
    ang = 2.0 * np.pi * (np.outer(b, b) % LANE) / LANE
    cos_m, sin_m = (np.cos(ang), np.sin(ang))
    fwd = np.block([[cos_m, -sin_m], [sin_m, cos_m]])
    inv = np.block([[cos_m, sin_m], [-sin_m, cos_m]])

    def halves(m):
        hi = m.astype(ml_dtypes.bfloat16)
        lo = (m - hi.astype(np.float64)).astype(ml_dtypes.bfloat16)
        return (hi, lo)

    c = np.arange(outer)
    tw_ang = 2.0 * np.pi * np.outer(c, b) / line_len
    twiddle = np.stack([np.cos(tw_ang), np.sin(tw_ang)]).astype(np.float32)
    q = c[:, None] + outer * b[None, :]
    signed = np.where(q >= line_len // 2, q - line_len, q).astype(np.float32)
    kx_cd = signed * np.float32(2.0 * math.pi / line_len)
    return (halves(fwd), halves(inv), twiddle, kx_cd.astype(np.float32))


def run_section(wave, regions, table, mult, consts, strip_count):
    (fhi, flo), (ghi, glo), twiddle, _ = consts
    rows, line_len = wave.shape[1], wave.shape[2]
    steps = regions.shape[0]
    table_len = table.shape[0] // (3 * steps)
    vmem = pl.BlockSpec(memory_space=pltpu.VMEM)
    flops = steps * (2 * 3 * 2 * (FFT_BLOCKS * rows) * 256 * 256 + 400 * rows * line_len)
    return pl.pallas_call(
        lambda *refs: section_kernel(*refs, table_len=table_len),
        out_shape=(
            jax.ShapeDtypeStruct(wave.shape, jnp.float32),
            jax.ShapeDtypeStruct((strip_count, steps, rows // strip_count, line_len), jnp.float32),
        ),
        in_specs=[pl.BlockSpec(memory_space=pltpu.SMEM)] + [vmem] * 8,
        out_specs=(vmem, vmem),
        scratch_shapes=[
            pltpu.VMEM((FFT_BLOCKS * rows, 2 * LANE), jnp.float32),
            pltpu.VMEM((FFT_BLOCKS * rows, 2 * LANE), jnp.float32),
            pltpu.VMEM((2, rows, line_len), jnp.float32),
            pltpu.VMEM((rows, line_len), jnp.float32),
            pltpu.VMEM((rows, line_len), jnp.float32),
            pltpu.VMEM((rows, line_len), jnp.float32),
        ],
        cost_estimate=pl.CostEstimate(
            flops=flops, transcendentals=0, bytes_accessed=4 * rows * line_len * 6 * steps
        ),
    )(table, wave, regions, mult, jnp.asarray(twiddle), jnp.asarray(fhi), jnp.asarray(flo),
      jnp.asarray(ghi), jnp.asarray(glo))


def section_tables(omega, region_speed, fd_coeff, ref_region, kx_cd):
    inv_speed = 1.0 / region_speed
    ref_slow = inv_speed[ref_region]
    regions = region_speed.shape[0]
    padded = 1 << max(1, (regions - 1).bit_length())
    extra = padded - regions
    phase = omega * (inv_speed[None, :] - ref_slow[:, None])
    gain = jnp.broadcast_to(fd_coeff / omega, phase.shape)
    parts = [jnp.cos(phase), jnp.sin(phase), gain]
    if extra:
        parts = [jnp.concatenate([p, jnp.repeat(p[:, -1:], extra, axis=1)], axis=1) for p in parts]
    table = jnp.stack(parts, axis=1).reshape(-1)
    wave_ref = omega * ref_slow
    wave_ref = wave_ref[:, None, None]
    excess = wave_ref * wave_ref - kx_cd * kx_cd
    decay_line = jnp.exp(-jnp.sqrt(jnp.maximum(-excess, 0.0)))
    vertical = jnp.sqrt(jnp.maximum(excess, 0.0))
    mult = jnp.stack([decay_line * jnp.cos(vertical), decay_line * jnp.sin(vertical)], axis=1)
    return (table, mult)


def fast_fits(surface, region_index, region_speed):
    freq_count = surface.shape[1]
    rows = surface.shape[2] * lax.axis_size("strip")
    line_len = surface.shape[3]
    return (
        freq_count == lax.axis_size("strip")
        and line_len == FFT_BLOCKS * LANE
        and rows % ROW_CHUNK == 0
        and surface.shape[2] % ROW_CHUNK == 0
        and rows <= 64
        and region_speed.shape[0] <= 16
    )


def strip_pairs(depths, strip_count, shift):
    return [
        (d * strip_count + r, d * strip_count + (r + shift) % strip_count)
        for d in depths
        for r in range(strip_count)
    ]


def gather_rows(local, depths, strip_no, strip_count, row_axis):
    rows = local.shape[row_axis]
    shape = list(local.shape)
    shape[row_axis] = rows * strip_count
    full = jnp.zeros(shape, local.dtype)
    start = [0] * len(shape)
    start[row_axis] = strip_no * rows
    full = lax.dynamic_update_slice(full, local, start)
    for shift in range(1, strip_count):
        got = lax.ppermute(local, ("depth", "strip"), strip_pairs(depths, strip_count, shift))
        start = [0] * len(shape)
        start[row_axis] = ((strip_no - shift) % strip_count) * rows
        full = lax.dynamic_update_slice(full, got, start)
    return full


def gather_strips(piece_of, local, depths, strip_no, strip_count, rows_here):
    rows = rows_here * strip_count
    shape = (local.shape[0], rows, local.shape[2])
    full = lax.dynamic_update_slice(
        jnp.zeros(shape, jnp.float32), local, (0, strip_no * rows_here, 0)
    )
    for shift in range(1, strip_count):
        target = (strip_no + shift) % strip_count
        got = lax.ppermute(
            piece_of(target), ("depth", "strip"), strip_pairs(depths, strip_count, shift)
        )
        source = (strip_no - shift) % strip_count
        full = lax.dynamic_update_slice(full, got, (0, source * rows_here, 0))
    return full


def shards(surface, omegas, region_speed, fd_coeff, region_index, ref_region):
    if not fast_fits(surface, region_index, region_speed):
        return shards_general(surface, omegas, region_speed, fd_coeff, region_index, ref_region)
    line_len = surface.shape[3]
    rows_here = surface.shape[2]
    steps = region_index.shape[0]
    segment_no = lax.axis_index("depth")
    segment_count = lax.axis_size("depth")
    strip_no = lax.axis_index("strip")
    strip_count = lax.axis_size("strip")
    consts = fast_constants(line_len)
    region_f = region_index.astype(jnp.float32)
    early = [d for d in range(segment_count) if d != 1]

    def with_surface(target):
        return jnp.concatenate(
            [region_f, lax.dynamic_index_in_dim(surface, target, 1, keepdims=False)], axis=0
        )

    gathered = gather_strips(
        with_surface, with_surface(strip_no), early, strip_no, strip_count, rows_here
    )
    regions_a = gathered[:steps].astype(jnp.int32)
    wave = gathered[steps:]
    omega = lax.dynamic_index_in_dim(omegas, strip_no, 0, keepdims=False)
    table, mult = section_tables(omega, region_speed, fd_coeff, ref_region, jnp.asarray(consts[3]))
    image = jnp.zeros((strip_count, steps, rows_here, line_len), jnp.float32)
    regions_b = regions_a

    def sweep(regions):
        def live(wave, image):
            return run_section(wave, regions, table, mult, consts, strip_count)

        return live

    def idle(wave, image):
        return (wave, image)

    def freq_sum(image, depths):
        parts = []
        for shift in range(1, strip_count):
            target = (strip_no + shift) % strip_count
            piece = lax.dynamic_index_in_dim(image, target, 0, keepdims=False)
            parts.append(
                lax.ppermute(piece, ("depth", "strip"), strip_pairs(depths, strip_count, shift))
            )
        return parts

    arrived = []
    for tick_no in range(segment_count):
        regions = regions_b if tick_no == 1 else regions_a
        wave, fresh = sweep(regions)(wave, image)
        image = fresh if tick_no == 0 else jnp.where(segment_no == tick_no, fresh, image)
        if tick_no + 1 < segment_count:
            wave = lax.ppermute(wave, "depth", [(tick_no, tick_no + 1)])
        if tick_no == 0 and segment_count > 1:
            held, _ = lax.optimization_barrier((region_f, image))
            regions_b = gather_strips(
                lambda target: held, held, [1], strip_no, strip_count, rows_here
            ).astype(jnp.int32)
        if tick_no == segment_count - 2:
            wave, image = lax.optimization_barrier((wave, image))
            arrived += freq_sum(image, range(segment_count - 1))
    arrived += freq_sum(image, [segment_count - 1])
    total = lax.dynamic_index_in_dim(image, strip_no, 0, keepdims=False)
    for piece in arrived:
        total = total + piece
    return total


def solution(mesh):
    in_specs = (
        P(None, "shots", "strip", None),
        P(),
        P(),
        P(),
        P("depth", "strip", None),
        P("depth"),
    )
    out_specs = P("depth", "strip", "shots")
    return jax.shard_map(shards, mesh=mesh, in_specs=in_specs, out_specs=out_specs, check_vma=False)
```

```python
import math

import ml_dtypes
import numpy as np
import jax
import jax.numpy as jnp
from jax import lax
from jax.experimental import pallas as pl
from jax.experimental.pallas import tpu as pltpu
from jax.sharding import PartitionSpec as P

DAMPING = 0.05
PRECISE = lax.Precision.HIGHEST


def padded_2(cells, sides, width):
    for axis, dim in sides:
        count = lax.axis_size(axis)
        ends = count - 1
        head = lax.slice_in_dim(cells, 0, width, axis=dim)
        tail = lax.slice_in_dim(cells, cells.shape[dim] - width, cells.shape[dim], axis=dim)
        cells = jnp.concatenate(
            [
                lax.ppermute(tail, axis, [(i, (i + 1) % count) for i in range(ends)]),
                cells,
                lax.ppermute(head, axis, [((i + 1) % count, i) for i in range(ends)]),
            ],
            axis=dim,
        )
    return cells


def from_behind(value, axis, steps):
    count = lax.axis_size(axis)
    first, last = (max(0, -steps), min(count, count - steps))
    return lax.ppermute(value, axis, [(source, source + steps) for source in range(first, last)])


def complex_scale(values, cosine, sine_part):
    return jnp.stack(
        [values[0] * cosine - values[1] * sine_part, values[0] * sine_part + values[1] * cosine]
    )


def angle_pair(numerator, period):
    angle_grid = numerator.astype(jnp.float32) * (2.0 * math.pi / period)
    return (jnp.cos(angle_grid), jnp.sin(angle_grid))


def block_matrix(cosine, sine_part, forward):
    sign_flip = 1.0 if forward else -1.0
    return jnp.stack(
        [jnp.stack([cosine, -sign_flip * sine_part]), jnp.stack([sign_flip * sine_part, cosine])]
    )


def build_tables(line_len):
    block_len = 128
    outer_len = line_len // block_len
    inner_idx = jnp.arange(block_len)
    outer_idx = jnp.arange(outer_len)
    cos_large, sin_large = angle_pair(
        inner_idx[:, None] * inner_idx[None, :] % block_len, block_len
    )
    cos_small, sin_small = angle_pair(
        outer_idx[:, None] * outer_idx[None, :] % outer_len, outer_len
    )
    cos_twist, sin_twist = angle_pair(outer_idx[:, None] * inner_idx[None, :], line_len)
    wave_index = outer_idx[:, None] + outer_len * inner_idx[None, :]
    signed = jnp.where(wave_index >= line_len // 2, wave_index - line_len, wave_index)
    kx_grid = signed.astype(jnp.float32) * (2.0 * math.pi / line_len)
    small_fwd = block_matrix(cos_small, sin_small, True)
    small_inv = block_matrix(cos_small, sin_small, False)
    large_fwd = block_matrix(cos_large, sin_large, True)
    large_inv = block_matrix(cos_large, sin_large, False)
    return (small_fwd, small_inv, large_fwd, large_inv, cos_twist, sin_twist, kx_grid)


def forward_line(wavefield, tables):
    small_fwd, small_inv, large_fwd, large_inv, cos_twist, sin_twist, kx_grid = tables
    row_count = wavefield.shape[1]
    pieces = wavefield.reshape(2, row_count, cos_twist.shape[0], cos_twist.shape[1])
    mixed_part = jnp.einsum("zrab,zwca->wrcb", pieces, small_fwd, precision=PRECISE)
    mixed_part = complex_scale(mixed_part, cos_twist, -sin_twist)
    return jnp.einsum("zrcb,zwbd->wrcd", mixed_part, large_fwd, precision=PRECISE)


def inverse_line(spectrum, tables):
    small_fwd, small_inv, large_fwd, large_inv, cos_twist, sin_twist, kx_grid = tables
    row_count = spectrum.shape[1]
    line_len = cos_twist.shape[0] * cos_twist.shape[1]
    mixed_part = jnp.einsum("zrcd,zwdb->wrcb", spectrum, large_inv, precision=PRECISE)
    mixed_part = complex_scale(mixed_part, cos_twist, sin_twist)
    pieces = jnp.einsum("zrcb,zwca->wrab", mixed_part, small_inv, precision=PRECISE)
    return pieces.reshape(2, row_count, line_len) * (1.0 / line_len)


def lookup(regions, entries):
    picked = jnp.zeros(regions.shape, jnp.float32)
    for region_no in range(entries.shape[0]):
        picked = picked + jnp.where(regions == region_no, entries[region_no], 0.0)
    return picked


def depth_step(wavefield, omega_now, slow_cells, coef_cells, ref_slow, tables, pad_rows):
    kx_grid = tables[6]
    wave_ref = omega_now * ref_slow
    excess = wave_ref * wave_ref - kx_grid * kx_grid
    decay_line = jnp.exp(-jnp.sqrt(jnp.maximum(-excess, 0.0)))
    vertical = jnp.sqrt(jnp.maximum(excess, 0.0))
    spectrum = complex_scale(
        forward_line(wavefield, tables),
        decay_line * jnp.cos(vertical),
        decay_line * jnp.sin(vertical),
    )
    wavefield = inverse_line(spectrum, tables)
    phase_cell = omega_now * (slow_cells - ref_slow)
    wavefield = complex_scale(wavefield, jnp.cos(phase_cell), jnp.sin(phase_cell))
    padded = pad_rows(wavefield)
    laplace = (
        padded[:, :-2]
        + padded[:, 2:]
        + jnp.roll(wavefield, 1, 2)
        + jnp.roll(wavefield, -1, 2)
        - 4.0 * wavefield
    )
    return wavefield + complex_scale(laplace, DAMPING, coef_cells / omega_now)


def march(wavefield, omega_now, slow_block, coef_block, ref_block, tables, pad_rows):
    traces = []
    for step_no in range(slow_block.shape[0]):
        wavefield = depth_step(
            wavefield,
            omega_now,
            slow_block[step_no],
            coef_block[step_no],
            ref_block[step_no],
            tables,
            pad_rows,
        )
        traces.append(wavefield[0])
    return (wavefield, jnp.stack(traces))


def shards_general(surface, omegas, region_speed, fd_coeff, region_index, ref_region):
    line_len = surface.shape[3]
    rows_here = surface.shape[2]
    freq_count = surface.shape[1]
    step_count = region_index.shape[0]
    tables = build_tables(line_len)
    inv_speed = 1.0 / region_speed
    segment_no = lax.axis_index("depth")
    segment_count = lax.axis_size("depth")

    def pad_near(values):
        return padded_2(values, (("strip", 1),), 1)

    slow_cells = lookup(region_index, inv_speed)
    coef_cells = lookup(region_index, fd_coeff)
    ref_cells = lookup(ref_region, inv_speed)
    freq_index = jnp.arange(freq_count)
    image_out = jnp.zeros((step_count, rows_here, line_len), jnp.float32)
    arriving = jnp.zeros((2, rows_here, line_len), jnp.float32)
    tick_count = freq_count + segment_count - 1
    for tick_no in range(tick_count):
        batch_no = tick_no - segment_no
        is_live = (batch_no >= 0) & (batch_no < freq_count)
        clipped = jnp.clip(batch_no, 0, freq_count - 1)
        picked = lax.dynamic_index_in_dim(surface, clipped, 1, keepdims=False)
        entering = jnp.where(segment_no == 0, picked, arriving)
        omega_now = jnp.sum(jnp.where(freq_index == clipped, omegas, 0.0))
        leaving, traces = march(
            entering, omega_now, slow_cells, coef_cells, ref_cells, tables, pad_near
        )
        image_out = image_out + jnp.where(is_live, traces, 0.0)
        if tick_no + 1 < tick_count:
            arriving = from_behind(leaving, "depth", 1)
    return image_out


LANE = 128
FFT_BLOCKS = 16
ROW_CHUNK = 8


def fft4(x0, x1, x2, x3, sign):
    s0 = (x0[0] + x2[0], x0[1] + x2[1])
    d0 = (x0[0] - x2[0], x0[1] - x2[1])
    s1 = (x1[0] + x3[0], x1[1] + x3[1])
    d1 = (x1[0] - x3[0], x1[1] - x3[1])
    if sign < 0:
        wd = (d1[1], -d1[0])
    else:
        wd = (-d1[1], d1[0])
    return (
        (s0[0] + s1[0], s0[1] + s1[1]),
        (d0[0] + wd[0], d0[1] + wd[1]),
        (s0[0] - s1[0], s0[1] - s1[1]),
        (d0[0] - wd[0], d0[1] - wd[1]),
    )


def turn_const(value, power, sign):
    if power == 4:
        return (-value[1], value[0]) if sign > 0 else (value[1], -value[0])
    angle = sign * 2.0 * math.pi * power / 16.0
    cr, ci = (math.cos(angle), math.sin(angle))
    return (value[0] * cr - value[1] * ci, value[0] * ci + value[1] * cr)


def fft16(parts, sign):
    mid = [[None] * 4 for _ in range(4)]
    for a0 in range(4):
        ys = fft4(parts[a0], parts[4 + a0], parts[8 + a0], parts[12 + a0], sign)
        for c0 in range(4):
            power = a0 * c0
            mid[a0][c0] = ys[c0] if power == 0 else turn_const(ys[c0], power, sign)
    out = [None] * 16
    for c0 in range(4):
        zs = fft4(mid[0][c0], mid[1][c0], mid[2][c0], mid[3][c0], sign)
        for c1 in range(4):
            out[c0 + 4 * c1] = zs[c1]
    return out


def pick(regions, values):
    level = list(values)
    bit = 1
    while len(level) > 1:
        chosen = (regions & bit) != 0
        level = [jnp.where(chosen, level[i + 1], level[i]) for i in range(0, len(level), 2)]
        bit *= 2
    return jnp.broadcast_to(level[0], regions.shape)


def pick_bits(bits, values):
    level = list(values)
    for chosen in bits:
        level = [jnp.where(chosen, level[i + 1], level[i]) for i in range(0, len(level), 2)]
    return jnp.broadcast_to(level[0], bits[0].shape)


def split_dot(values, hi_ref, lo_ref):
    high = values.astype(jnp.bfloat16)
    low = (values - high.astype(jnp.float32)).astype(jnp.bfloat16)
    main = jnp.dot(high, hi_ref[...], preferred_element_type=jnp.float32)
    fix = jnp.dot(high, lo_ref[...], preferred_element_type=jnp.float32) + jnp.dot(
        low, hi_ref[:, :], preferred_element_type=jnp.float32
    )
    return main + fix


def section_kernel(
    tab_ref, w_ref, rid_ref, mult_ref, tw_ref, fhi_ref, flo_ref, ghi_ref, glo_ref, pos_ref,
    wout_ref, img_ref, a_ref, y_ref, v_ref, cs_ref, sn_ref, gn_ref, *, table_len
):
    rows = w_ref.shape[1]
    line_len = w_ref.shape[2]
    steps = rid_ref.shape[0]
    strip_count, rows_here = img_ref.shape[0], img_ref.shape[2]
    chunks = rows // ROW_CHUNK
    inv_len = 1.0 / line_len
    wout_ref[...] = w_ref[...]

    def blk(a):
        return slice(a * LANE, (a + 1) * LANE)

    def one_step(k, carry):
        base = k * (3 * table_len)
        cos_t = [tab_ref[base + g] for g in range(table_len)]
        sin_t = [tab_ref[base + table_len + g] for g in range(table_len)]
        gain_t = [tab_ref[base + 2 * table_len + g] for g in range(table_len)]

        def forward_chunk(i, c):
            y0 = pl.multiple_of(i * ROW_CHUNK, ROW_CHUNK)
            parts = [
                (wout_ref[0, pl.ds(y0, ROW_CHUNK), blk(a)], wout_ref[1, pl.ds(y0, ROW_CHUNK), blk(a)])
                for a in range(FFT_BLOCKS)
            ]
            spec = fft16(parts, -1)
            for cc in range(FFT_BLOCKS):
                tc = tw_ref[0, cc:cc + 1, :]
                ts = tw_ref[1, cc:cc + 1, :]
                xr, xi = spec[cc]
                a_ref[pl.ds(cc * rows + y0, ROW_CHUNK), 0:LANE] = xr * tc + xi * ts
                a_ref[pl.ds(cc * rows + y0, ROW_CHUNK), LANE:2 * LANE] = xi * tc - xr * ts
            return c

        lax.fori_loop(0, chunks, forward_chunk, 0)
        spectrum = split_dot(a_ref[...], fhi_ref, flo_ref)
        for a in range(FFT_BLOCKS):
            regions = rid_ref[k, :, blk(a)]
            bits = [(regions & (1 << b)) != 0 for b in range(max(1, (table_len - 1).bit_length()))]
            cs_ref[:, blk(a)] = pick_bits(bits, cos_t)
            sn_ref[:, blk(a)] = pick_bits(bits, sin_t)
            gn_ref[:, blk(a)] = pick_bits(bits, gain_t)
        y_ref[...] = spectrum
        for cc in range(FFT_BLOCKS):
            band = slice(cc * rows, (cc + 1) * rows)
            yr = y_ref[band, 0:LANE]
            yi = y_ref[band, LANE:2 * LANE]
            mr = mult_ref[k, 0, cc:cc + 1, :]
            mi = mult_ref[k, 1, cc:cc + 1, :]
            a_ref[band, 0:LANE] = yr * mr - yi * mi
            a_ref[band, LANE:2 * LANE] = yr * mi + yi * mr
        y_ref[...] = split_dot(a_ref[...], ghi_ref, glo_ref)

        def inverse_chunk(i, c):
            y0 = pl.multiple_of(i * ROW_CHUNK, ROW_CHUNK)
            parts = []
            for cc in range(FFT_BLOCKS):
                zr = y_ref[pl.ds(cc * rows + y0, ROW_CHUNK), 0:LANE]
                zi = y_ref[pl.ds(cc * rows + y0, ROW_CHUNK), LANE:2 * LANE]
                tc = tw_ref[0, cc:cc + 1, :]
                ts = tw_ref[1, cc:cc + 1, :]
                parts.append((zr * tc - zi * ts, zr * ts + zi * tc))
            back = fft16(parts, 1)
            for a in range(FFT_BLOCKS):
                ur = back[a][0] * inv_len
                ui = back[a][1] * inv_len
                cs = cs_ref[pl.ds(y0, ROW_CHUNK), blk(a)]
                sn = sn_ref[pl.ds(y0, ROW_CHUNK), blk(a)]
                v_ref[0, pl.ds(y0, ROW_CHUNK), blk(a)] = ur * cs - ui * sn
                v_ref[1, pl.ds(y0, ROW_CHUNK), blk(a)] = ur * sn + ui * cs
            return c

        lax.fori_loop(0, chunks, inverse_chunk, 0)
        row_id = lax.broadcasted_iota(jnp.int32, (rows, LANE), 0)
        lane_id = lax.broadcasted_iota(jnp.int32, (rows, LANE), 1)
        cache = {}

        def cell(part, a):
            key = (part, a % FFT_BLOCKS)
            if key not in cache:
                v = v_ref[part, :, blk(a % FFT_BLOCKS)]
                cache[key] = (v, pltpu.roll(v, 1, 1), pltpu.roll(v, LANE - 1, 1))
            return cache[key]

        for a in range(FFT_BLOCKS):
            lap = []
            here = []
            for part in range(2):
                v, from_left, from_right = cell(part, a)
                prev_left = cell(part, a - 1)[1]
                next_right = cell(part, a + 1)[2]
                above = jnp.where(row_id == 0, 0.0, pltpu.roll(v, 1, 0))
                below = jnp.where(row_id == rows - 1, 0.0, pltpu.roll(v, rows - 1, 0))
                left = jnp.where(lane_id == 0, prev_left, from_left)
                right = jnp.where(lane_id == LANE - 1, next_right, from_right)
                lap.append(above + below + left + right - 4.0 * v)
                here.append(v)
            gain = gn_ref[:, blk(a)]
            new_re = here[0] + (lap[0] * DAMPING - lap[1] * gain)
            new_im = here[1] + (lap[0] * gain + lap[1] * DAMPING)
            wout_ref[0, :, blk(a)] = new_re
            wout_ref[1, :, blk(a)] = new_im
            for j in range(strip_count):
                slot = (j - pos_ref[0] + strip_count) % strip_count
                img_ref[slot, k, :, blk(a)] = new_re[j * rows_here:(j + 1) * rows_here]
        return carry

    lax.fori_loop(0, steps, one_step, 0)


def fast_constants(line_len):
    outer = line_len // LANE
    b = np.arange(LANE)
    ang = 2.0 * np.pi * (np.outer(b, b) % LANE) / LANE
    cos_m, sin_m = (np.cos(ang), np.sin(ang))
    fwd = np.block([[cos_m, -sin_m], [sin_m, cos_m]])
    inv = np.block([[cos_m, sin_m], [-sin_m, cos_m]])

    def halves(m):
        hi = m.astype(ml_dtypes.bfloat16)
        lo = (m - hi.astype(np.float64)).astype(ml_dtypes.bfloat16)
        return (hi, lo)

    c = np.arange(outer)
    tw_ang = 2.0 * np.pi * np.outer(c, b) / line_len
    twiddle = np.stack([np.cos(tw_ang), np.sin(tw_ang)]).astype(np.float32)
    q = c[:, None] + outer * b[None, :]
    signed = np.where(q >= line_len // 2, q - line_len, q).astype(np.float32)
    kx_cd = signed * np.float32(2.0 * math.pi / line_len)
    return (halves(fwd), halves(inv), twiddle, kx_cd.astype(np.float32))


def run_section(wave, regions, table, mult, consts, strip_count, strip_no):
    (fhi, flo), (ghi, glo), twiddle, _ = consts
    rows, line_len = wave.shape[1], wave.shape[2]
    steps = regions.shape[0]
    table_len = table.shape[0] // (3 * steps)
    vmem = pl.BlockSpec(memory_space=pltpu.VMEM)
    flops = steps * (2 * 3 * 2 * (FFT_BLOCKS * rows) * 256 * 256 + 400 * rows * line_len)
    return pl.pallas_call(
        lambda *refs: section_kernel(*refs, table_len=table_len),
        out_shape=(
            jax.ShapeDtypeStruct(wave.shape, jnp.float32),
            jax.ShapeDtypeStruct((strip_count, steps, rows // strip_count, line_len), jnp.float32),
        ),
        in_specs=[pl.BlockSpec(memory_space=pltpu.SMEM)] + [vmem] * 8
        + [pl.BlockSpec(memory_space=pltpu.SMEM)],
        out_specs=(vmem, vmem),
        scratch_shapes=[
            pltpu.VMEM((FFT_BLOCKS * rows, 2 * LANE), jnp.float32),
            pltpu.VMEM((FFT_BLOCKS * rows, 2 * LANE), jnp.float32),
            pltpu.VMEM((2, rows, line_len), jnp.float32),
            pltpu.VMEM((rows, line_len), jnp.float32),
            pltpu.VMEM((rows, line_len), jnp.float32),
            pltpu.VMEM((rows, line_len), jnp.float32),
        ],
        cost_estimate=pl.CostEstimate(
            flops=flops, transcendentals=0, bytes_accessed=4 * rows * line_len * 6 * steps
        ),
    )(table, wave, regions, mult, jnp.asarray(twiddle), jnp.asarray(fhi), jnp.asarray(flo),
      jnp.asarray(ghi), jnp.asarray(glo), jnp.reshape(strip_no, (1,)).astype(jnp.int32))


def section_tables(omega, region_speed, fd_coeff, ref_region, kx_cd):
    inv_speed = 1.0 / region_speed
    ref_slow = inv_speed[ref_region]
    regions = region_speed.shape[0]
    padded = 1 << max(1, (regions - 1).bit_length())
    extra = padded - regions
    phase = omega * (inv_speed[None, :] - ref_slow[:, None])
    gain = jnp.broadcast_to(fd_coeff / omega, phase.shape)
    parts = [jnp.cos(phase), jnp.sin(phase), gain]
    if extra:
        parts = [jnp.concatenate([p, jnp.repeat(p[:, -1:], extra, axis=1)], axis=1) for p in parts]
    table = jnp.stack(parts, axis=1).reshape(-1)
    wave_ref = omega * ref_slow
    wave_ref = wave_ref[:, None, None]
    excess = wave_ref * wave_ref - kx_cd * kx_cd
    decay_line = jnp.exp(-jnp.sqrt(jnp.maximum(-excess, 0.0)))
    vertical = jnp.sqrt(jnp.maximum(excess, 0.0))
    mult = jnp.stack([decay_line * jnp.cos(vertical), decay_line * jnp.sin(vertical)], axis=1)
    return (table, mult)


def fast_fits(surface, region_index, region_speed):
    freq_count = surface.shape[1]
    rows = surface.shape[2] * lax.axis_size("strip")
    line_len = surface.shape[3]
    return (
        freq_count == lax.axis_size("strip")
        and line_len == FFT_BLOCKS * LANE
        and rows % ROW_CHUNK == 0
        and surface.shape[2] % ROW_CHUNK == 0
        and rows <= 64
        and region_speed.shape[0] <= 16
    )


def strip_pairs(depths, strip_count, shift):
    return [
        (d * strip_count + r, d * strip_count + (r + shift) % strip_count)
        for d in depths
        for r in range(strip_count)
    ]


def gather_rows(local, depths, strip_no, strip_count, row_axis):
    rows = local.shape[row_axis]
    shape = list(local.shape)
    shape[row_axis] = rows * strip_count
    full = jnp.zeros(shape, local.dtype)
    start = [0] * len(shape)
    start[row_axis] = strip_no * rows
    full = lax.dynamic_update_slice(full, local, start)
    for shift in range(1, strip_count):
        got = lax.ppermute(local, ("depth", "strip"), strip_pairs(depths, strip_count, shift))
        start = [0] * len(shape)
        start[row_axis] = ((strip_no - shift) % strip_count) * rows
        full = lax.dynamic_update_slice(full, got, start)
    return full


def gather_strips(piece_of, local, depths, strip_no, strip_count, rows_here):
    rows = rows_here * strip_count
    shape = (local.shape[0], rows, local.shape[2])
    full = lax.dynamic_update_slice(
        jnp.zeros(shape, jnp.float32), local, (0, strip_no * rows_here, 0)
    )
    for shift in range(1, strip_count):
        target = (strip_no + shift) % strip_count
        got = lax.ppermute(
            piece_of(target), ("depth", "strip"), strip_pairs(depths, strip_count, shift)
        )
        source = (strip_no - shift) % strip_count
        full = lax.dynamic_update_slice(full, got, (0, source * rows_here, 0))
    return full


def shards(surface, omegas, region_speed, fd_coeff, region_index, ref_region):
    if not fast_fits(surface, region_index, region_speed):
        return shards_general(surface, omegas, region_speed, fd_coeff, region_index, ref_region)
    line_len = surface.shape[3]
    rows_here = surface.shape[2]
    steps = region_index.shape[0]
    segment_no = lax.axis_index("depth")
    segment_count = lax.axis_size("depth")
    strip_no = lax.axis_index("strip")
    strip_count = lax.axis_size("strip")
    consts = fast_constants(line_len)
    region_f = region_index.astype(jnp.float32)
    early = [d for d in range(segment_count) if d != 1]

    def with_surface(target):
        return jnp.concatenate(
            [region_f, lax.dynamic_index_in_dim(surface, target, 1, keepdims=False)], axis=0
        )

    gathered = gather_strips(
        with_surface, with_surface(strip_no), early, strip_no, strip_count, rows_here
    )
    regions_a = gathered[:steps].astype(jnp.int32)
    wave = gathered[steps:]
    omega = lax.dynamic_index_in_dim(omegas, strip_no, 0, keepdims=False)
    table, mult = section_tables(omega, region_speed, fd_coeff, ref_region, jnp.asarray(consts[3]))
    image = jnp.zeros((strip_count, steps, rows_here, line_len), jnp.float32)
    regions_b = regions_a

    def sweep(regions):
        def live(wave, image):
            return run_section(wave, regions, table, mult, consts, strip_count, strip_no)

        return live

    def idle(wave, image):
        return (wave, image)

    def freq_sum(image, depths):
        parts = []
        for shift in range(1, strip_count):
            piece = image[shift]
            parts.append(
                lax.ppermute(piece, ("depth", "strip"), strip_pairs(depths, strip_count, shift))
            )
        return parts

    arrived = []
    for tick_no in range(segment_count):
        regions = regions_b if tick_no == 1 else regions_a
        if tick_no == 0:
            wave, image = sweep(regions)(wave, image)
        else:
            wave, image = lax.cond(segment_no == tick_no, sweep(regions), idle, wave, image)
        if tick_no + 1 < segment_count:
            wave = lax.ppermute(wave, "depth", [(tick_no, tick_no + 1)])
        if tick_no == 0 and segment_count > 1:
            held, _ = lax.optimization_barrier((region_f, image))
            regions_b = gather_strips(
                lambda target: held, held, [1], strip_no, strip_count, rows_here
            ).astype(jnp.int32)
        if tick_no == segment_count - 2:
            wave, image = lax.optimization_barrier((wave, image))
            arrived += freq_sum(image, range(segment_count - 1))
    arrived += freq_sum(image, [segment_count - 1])
    total = image[0]
    for piece in arrived:
        total = total + piece
    return total


def solution(mesh):
    in_specs = (
        P(None, "shots", "strip", None),
        P(),
        P(),
        P(),
        P("depth", "strip", None),
        P("depth"),
    )
    out_specs = P("depth", "strip", "shots")
    return jax.shard_map(shards, mesh=mesh, in_specs=in_specs, out_specs=out_specs, check_vma=False)
```

```python
import math

import ml_dtypes
import numpy as np
import jax
import jax.numpy as jnp
from jax import lax
from jax.experimental import pallas as pl
from jax.experimental.pallas import tpu as pltpu
from jax.sharding import PartitionSpec as P

DAMPING = 0.05
PRECISE = lax.Precision.HIGHEST


def padded_2(cells, sides, width):
    for axis, dim in sides:
        count = lax.axis_size(axis)
        ends = count - 1
        head = lax.slice_in_dim(cells, 0, width, axis=dim)
        tail = lax.slice_in_dim(cells, cells.shape[dim] - width, cells.shape[dim], axis=dim)
        cells = jnp.concatenate(
            [
                lax.ppermute(tail, axis, [(i, (i + 1) % count) for i in range(ends)]),
                cells,
                lax.ppermute(head, axis, [((i + 1) % count, i) for i in range(ends)]),
            ],
            axis=dim,
        )
    return cells


def from_behind(value, axis, steps):
    count = lax.axis_size(axis)
    first, last = (max(0, -steps), min(count, count - steps))
    return lax.ppermute(value, axis, [(source, source + steps) for source in range(first, last)])


def complex_scale(values, cosine, sine_part):
    return jnp.stack(
        [values[0] * cosine - values[1] * sine_part, values[0] * sine_part + values[1] * cosine]
    )


def angle_pair(numerator, period):
    angle_grid = numerator.astype(jnp.float32) * (2.0 * math.pi / period)
    return (jnp.cos(angle_grid), jnp.sin(angle_grid))


def block_matrix(cosine, sine_part, forward):
    sign_flip = 1.0 if forward else -1.0
    return jnp.stack(
        [jnp.stack([cosine, -sign_flip * sine_part]), jnp.stack([sign_flip * sine_part, cosine])]
    )


def build_tables(line_len):
    block_len = 128
    outer_len = line_len // block_len
    inner_idx = jnp.arange(block_len)
    outer_idx = jnp.arange(outer_len)
    cos_large, sin_large = angle_pair(
        inner_idx[:, None] * inner_idx[None, :] % block_len, block_len
    )
    cos_small, sin_small = angle_pair(
        outer_idx[:, None] * outer_idx[None, :] % outer_len, outer_len
    )
    cos_twist, sin_twist = angle_pair(outer_idx[:, None] * inner_idx[None, :], line_len)
    wave_index = outer_idx[:, None] + outer_len * inner_idx[None, :]
    signed = jnp.where(wave_index >= line_len // 2, wave_index - line_len, wave_index)
    kx_grid = signed.astype(jnp.float32) * (2.0 * math.pi / line_len)
    small_fwd = block_matrix(cos_small, sin_small, True)
    small_inv = block_matrix(cos_small, sin_small, False)
    large_fwd = block_matrix(cos_large, sin_large, True)
    large_inv = block_matrix(cos_large, sin_large, False)
    return (small_fwd, small_inv, large_fwd, large_inv, cos_twist, sin_twist, kx_grid)


def forward_line(wavefield, tables):
    small_fwd, small_inv, large_fwd, large_inv, cos_twist, sin_twist, kx_grid = tables
    row_count = wavefield.shape[1]
    pieces = wavefield.reshape(2, row_count, cos_twist.shape[0], cos_twist.shape[1])
    mixed_part = jnp.einsum("zrab,zwca->wrcb", pieces, small_fwd, precision=PRECISE)
    mixed_part = complex_scale(mixed_part, cos_twist, -sin_twist)
    return jnp.einsum("zrcb,zwbd->wrcd", mixed_part, large_fwd, precision=PRECISE)


def inverse_line(spectrum, tables):
    small_fwd, small_inv, large_fwd, large_inv, cos_twist, sin_twist, kx_grid = tables
    row_count = spectrum.shape[1]
    line_len = cos_twist.shape[0] * cos_twist.shape[1]
    mixed_part = jnp.einsum("zrcd,zwdb->wrcb", spectrum, large_inv, precision=PRECISE)
    mixed_part = complex_scale(mixed_part, cos_twist, sin_twist)
    pieces = jnp.einsum("zrcb,zwca->wrab", mixed_part, small_inv, precision=PRECISE)
    return pieces.reshape(2, row_count, line_len) * (1.0 / line_len)


def lookup(regions, entries):
    picked = jnp.zeros(regions.shape, jnp.float32)
    for region_no in range(entries.shape[0]):
        picked = picked + jnp.where(regions == region_no, entries[region_no], 0.0)
    return picked


def depth_step(wavefield, omega_now, slow_cells, coef_cells, ref_slow, tables, pad_rows):
    kx_grid = tables[6]
    wave_ref = omega_now * ref_slow
    excess = wave_ref * wave_ref - kx_grid * kx_grid
    decay_line = jnp.exp(-jnp.sqrt(jnp.maximum(-excess, 0.0)))
    vertical = jnp.sqrt(jnp.maximum(excess, 0.0))
    spectrum = complex_scale(
        forward_line(wavefield, tables),
        decay_line * jnp.cos(vertical),
        decay_line * jnp.sin(vertical),
    )
    wavefield = inverse_line(spectrum, tables)
    phase_cell = omega_now * (slow_cells - ref_slow)
    wavefield = complex_scale(wavefield, jnp.cos(phase_cell), jnp.sin(phase_cell))
    padded = pad_rows(wavefield)
    laplace = (
        padded[:, :-2]
        + padded[:, 2:]
        + jnp.roll(wavefield, 1, 2)
        + jnp.roll(wavefield, -1, 2)
        - 4.0 * wavefield
    )
    return wavefield + complex_scale(laplace, DAMPING, coef_cells / omega_now)


def march(wavefield, omega_now, slow_block, coef_block, ref_block, tables, pad_rows):
    traces = []
    for step_no in range(slow_block.shape[0]):
        wavefield = depth_step(
            wavefield,
            omega_now,
            slow_block[step_no],
            coef_block[step_no],
            ref_block[step_no],
            tables,
            pad_rows,
        )
        traces.append(wavefield[0])
    return (wavefield, jnp.stack(traces))


def shards_general(surface, omegas, region_speed, fd_coeff, region_index, ref_region):
    line_len = surface.shape[3]
    rows_here = surface.shape[2]
    freq_count = surface.shape[1]
    step_count = region_index.shape[0]
    tables = build_tables(line_len)
    inv_speed = 1.0 / region_speed
    segment_no = lax.axis_index("depth")
    segment_count = lax.axis_size("depth")

    def pad_near(values):
        return padded_2(values, (("strip", 1),), 1)

    slow_cells = lookup(region_index, inv_speed)
    coef_cells = lookup(region_index, fd_coeff)
    ref_cells = lookup(ref_region, inv_speed)
    freq_index = jnp.arange(freq_count)
    image_out = jnp.zeros((step_count, rows_here, line_len), jnp.float32)
    arriving = jnp.zeros((2, rows_here, line_len), jnp.float32)
    tick_count = freq_count + segment_count - 1
    for tick_no in range(tick_count):
        batch_no = tick_no - segment_no
        is_live = (batch_no >= 0) & (batch_no < freq_count)
        clipped = jnp.clip(batch_no, 0, freq_count - 1)
        picked = lax.dynamic_index_in_dim(surface, clipped, 1, keepdims=False)
        entering = jnp.where(segment_no == 0, picked, arriving)
        omega_now = jnp.sum(jnp.where(freq_index == clipped, omegas, 0.0))
        leaving, traces = march(
            entering, omega_now, slow_cells, coef_cells, ref_cells, tables, pad_near
        )
        image_out = image_out + jnp.where(is_live, traces, 0.0)
        if tick_no + 1 < tick_count:
            arriving = from_behind(leaving, "depth", 1)
    return image_out


LANE = 128
FFT_BLOCKS = 16
ROW_CHUNK = 8


def fft4(x0, x1, x2, x3, sign):
    s0 = (x0[0] + x2[0], x0[1] + x2[1])
    d0 = (x0[0] - x2[0], x0[1] - x2[1])
    s1 = (x1[0] + x3[0], x1[1] + x3[1])
    d1 = (x1[0] - x3[0], x1[1] - x3[1])
    if sign < 0:
        wd = (d1[1], -d1[0])
    else:
        wd = (-d1[1], d1[0])
    return (
        (s0[0] + s1[0], s0[1] + s1[1]),
        (d0[0] + wd[0], d0[1] + wd[1]),
        (s0[0] - s1[0], s0[1] - s1[1]),
        (d0[0] - wd[0], d0[1] - wd[1]),
    )


def turn_const(value, power, sign):
    if power == 4:
        return (-value[1], value[0]) if sign > 0 else (value[1], -value[0])
    angle = sign * 2.0 * math.pi * power / 16.0
    cr, ci = (math.cos(angle), math.sin(angle))
    return (value[0] * cr - value[1] * ci, value[0] * ci + value[1] * cr)


def fft16(parts, sign):
    mid = [[None] * 4 for _ in range(4)]
    for a0 in range(4):
        ys = fft4(parts[a0], parts[4 + a0], parts[8 + a0], parts[12 + a0], sign)
        for c0 in range(4):
            power = a0 * c0
            mid[a0][c0] = ys[c0] if power == 0 else turn_const(ys[c0], power, sign)
    out = [None] * 16
    for c0 in range(4):
        zs = fft4(mid[0][c0], mid[1][c0], mid[2][c0], mid[3][c0], sign)
        for c1 in range(4):
            out[c0 + 4 * c1] = zs[c1]
    return out


def pick(regions, values):
    level = list(values)
    bit = 1
    while len(level) > 1:
        chosen = (regions & bit) != 0
        level = [jnp.where(chosen, level[i + 1], level[i]) for i in range(0, len(level), 2)]
        bit *= 2
    return jnp.broadcast_to(level[0], regions.shape)


def pick_bits(bits, values):
    level = list(values)
    for chosen in bits:
        level = [jnp.where(chosen, level[i + 1], level[i]) for i in range(0, len(level), 2)]
    return jnp.broadcast_to(level[0], bits[0].shape)


def split_dot(values, hi_ref, lo_ref):
    high = values.astype(jnp.bfloat16)
    low = (values - high.astype(jnp.float32)).astype(jnp.bfloat16)
    main = jnp.dot(high, hi_ref[...], preferred_element_type=jnp.float32)
    fix = jnp.dot(high, lo_ref[...], preferred_element_type=jnp.float32) + jnp.dot(
        low, hi_ref[:, :], preferred_element_type=jnp.float32
    )
    return main + fix


def section_kernel(
    tab_ref, w_ref, rid_ref, mult_ref, tw_ref, fhi_ref, flo_ref, ghi_ref, glo_ref, pos_ref,
    wout_ref, img_ref, a_ref, y_ref, v_ref, cs_ref, sn_ref, gn_ref, *, table_len
):
    rows = w_ref.shape[1]
    line_len = w_ref.shape[2]
    steps = rid_ref.shape[0]
    strip_count, rows_here = img_ref.shape[0], img_ref.shape[2]
    chunks = rows // ROW_CHUNK
    inv_len = 1.0 / line_len
    wout_ref[...] = w_ref[...]

    def blk(a):
        return slice(a * LANE, (a + 1) * LANE)

    def one_step(k, carry):
        base = k * (3 * table_len)
        cos_t = [tab_ref[base + g] for g in range(table_len)]
        sin_t = [tab_ref[base + table_len + g] for g in range(table_len)]
        gain_t = [tab_ref[base + 2 * table_len + g] for g in range(table_len)]

        def forward_chunk(i, c):
            y0 = pl.multiple_of(i * ROW_CHUNK, ROW_CHUNK)
            parts = [
                (wout_ref[0, pl.ds(y0, ROW_CHUNK), blk(a)], wout_ref[1, pl.ds(y0, ROW_CHUNK), blk(a)])
                for a in range(FFT_BLOCKS)
            ]
            spec = fft16(parts, -1)
            for cc in range(FFT_BLOCKS):
                tc = tw_ref[0, cc:cc + 1, :]
                ts = tw_ref[1, cc:cc + 1, :]
                xr, xi = spec[cc]
                a_ref[pl.ds(cc * rows + y0, ROW_CHUNK), 0:LANE] = xr * tc + xi * ts
                a_ref[pl.ds(cc * rows + y0, ROW_CHUNK), LANE:2 * LANE] = xi * tc - xr * ts
            return c

        lax.fori_loop(0, chunks, forward_chunk, 0)
        spectrum = split_dot(a_ref[...], fhi_ref, flo_ref)
        for a in range(FFT_BLOCKS):
            regions = rid_ref[k, :, blk(a)]
            bits = [(regions & (1 << b)) != 0 for b in range(max(1, (table_len - 1).bit_length()))]
            cs_ref[:, blk(a)] = pick_bits(bits, cos_t)
            sn_ref[:, blk(a)] = pick_bits(bits, sin_t)
            gn_ref[:, blk(a)] = pick_bits(bits, gain_t)
        y_ref[...] = spectrum
        for cc in range(FFT_BLOCKS):
            band = slice(cc * rows, (cc + 1) * rows)
            yr = y_ref[band, 0:LANE]
            yi = y_ref[band, LANE:2 * LANE]
            mr = mult_ref[k, 0, cc:cc + 1, :]
            mi = mult_ref[k, 1, cc:cc + 1, :]
            a_ref[band, 0:LANE] = yr * mr - yi * mi
            a_ref[band, LANE:2 * LANE] = yr * mi + yi * mr
        y_ref[...] = split_dot(a_ref[...], ghi_ref, glo_ref)

        def inverse_chunk(i, c):
            y0 = pl.multiple_of(i * ROW_CHUNK, ROW_CHUNK)
            parts = []
            for cc in range(FFT_BLOCKS):
                zr = y_ref[pl.ds(cc * rows + y0, ROW_CHUNK), 0:LANE]
                zi = y_ref[pl.ds(cc * rows + y0, ROW_CHUNK), LANE:2 * LANE]
                tc = tw_ref[0, cc:cc + 1, :]
                ts = tw_ref[1, cc:cc + 1, :]
                parts.append((zr * tc - zi * ts, zr * ts + zi * tc))
            back = fft16(parts, 1)
            for a in range(FFT_BLOCKS):
                ur = back[a][0] * inv_len
                ui = back[a][1] * inv_len
                cs = cs_ref[pl.ds(y0, ROW_CHUNK), blk(a)]
                sn = sn_ref[pl.ds(y0, ROW_CHUNK), blk(a)]
                v_ref[0, pl.ds(y0, ROW_CHUNK), blk(a)] = ur * cs - ui * sn
                v_ref[1, pl.ds(y0, ROW_CHUNK), blk(a)] = ur * sn + ui * cs
            return c

        lax.fori_loop(0, chunks, inverse_chunk, 0)
        row_id = lax.broadcasted_iota(jnp.int32, (rows, LANE), 0)
        lane_id = lax.broadcasted_iota(jnp.int32, (rows, LANE), 1)
        cache = {}

        def cell(part, a):
            key = (part, a % FFT_BLOCKS)
            if key not in cache:
                v = v_ref[part, :, blk(a % FFT_BLOCKS)]
                cache[key] = (v, pltpu.roll(v, 1, 1), pltpu.roll(v, LANE - 1, 1))
            return cache[key]

        for a in range(FFT_BLOCKS):
            lap = []
            here = []
            for part in range(2):
                v, from_left, from_right = cell(part, a)
                prev_left = cell(part, a - 1)[1]
                next_right = cell(part, a + 1)[2]
                above = jnp.where(row_id == 0, 0.0, pltpu.roll(v, 1, 0))
                below = jnp.where(row_id == rows - 1, 0.0, pltpu.roll(v, rows - 1, 0))
                left = jnp.where(lane_id == 0, prev_left, from_left)
                right = jnp.where(lane_id == LANE - 1, next_right, from_right)
                lap.append(above + below + left + right - 4.0 * v)
                here.append(v)
            gain = gn_ref[:, blk(a)]
            new_re = here[0] + (lap[0] * DAMPING - lap[1] * gain)
            new_im = here[1] + (lap[0] * gain + lap[1] * DAMPING)
            wout_ref[0, :, blk(a)] = new_re
            wout_ref[1, :, blk(a)] = new_im
            for j in range(strip_count):
                slot = (j - pos_ref[0] + strip_count) % strip_count
                img_ref[slot, k, :, blk(a)] = new_re[j * rows_here:(j + 1) * rows_here]
        return carry

    lax.fori_loop(0, steps, one_step, 0)


def fast_constants(line_len):
    outer = line_len // LANE
    b = np.arange(LANE)
    ang = 2.0 * np.pi * (np.outer(b, b) % LANE) / LANE
    cos_m, sin_m = (np.cos(ang), np.sin(ang))
    fwd = np.block([[cos_m, -sin_m], [sin_m, cos_m]])
    inv = np.block([[cos_m, sin_m], [-sin_m, cos_m]])

    def halves(m):
        hi = m.astype(ml_dtypes.bfloat16)
        lo = (m - hi.astype(np.float64)).astype(ml_dtypes.bfloat16)
        return (hi, lo)

    c = np.arange(outer)
    tw_ang = 2.0 * np.pi * np.outer(c, b) / line_len
    twiddle = np.stack([np.cos(tw_ang), np.sin(tw_ang)]).astype(np.float32)
    q = c[:, None] + outer * b[None, :]
    signed = np.where(q >= line_len // 2, q - line_len, q).astype(np.float32)
    kx_cd = signed * np.float32(2.0 * math.pi / line_len)
    return (halves(fwd), halves(inv), twiddle, kx_cd.astype(np.float32))


def run_section(wave, regions, table, mult, consts, strip_count, strip_no):
    (fhi, flo), (ghi, glo), twiddle, _ = consts
    rows, line_len = wave.shape[1], wave.shape[2]
    steps = regions.shape[0]
    table_len = table.shape[0] // (3 * steps)
    vmem = pl.BlockSpec(memory_space=pltpu.VMEM)
    flops = steps * (2 * 3 * 2 * (FFT_BLOCKS * rows) * 256 * 256 + 400 * rows * line_len)
    return pl.pallas_call(
        lambda *refs: section_kernel(*refs, table_len=table_len),
        out_shape=(
            jax.ShapeDtypeStruct(wave.shape, jnp.float32),
            jax.ShapeDtypeStruct((strip_count, steps, rows // strip_count, line_len), jnp.float32),
        ),
        in_specs=[pl.BlockSpec(memory_space=pltpu.SMEM)] + [vmem] * 8
        + [pl.BlockSpec(memory_space=pltpu.SMEM)],
        out_specs=(vmem, vmem),
        scratch_shapes=[
            pltpu.VMEM((FFT_BLOCKS * rows, 2 * LANE), jnp.float32),
            pltpu.VMEM((FFT_BLOCKS * rows, 2 * LANE), jnp.float32),
            pltpu.VMEM((2, rows, line_len), jnp.float32),
            pltpu.VMEM((rows, line_len), jnp.float32),
            pltpu.VMEM((rows, line_len), jnp.float32),
            pltpu.VMEM((rows, line_len), jnp.float32),
        ],
        cost_estimate=pl.CostEstimate(
            flops=flops, transcendentals=0, bytes_accessed=4 * rows * line_len * 6 * steps
        ),
    )(table, wave, regions, mult, jnp.asarray(twiddle), jnp.asarray(fhi), jnp.asarray(flo),
      jnp.asarray(ghi), jnp.asarray(glo), jnp.reshape(strip_no, (1,)).astype(jnp.int32))


def section_tables(omega, region_speed, fd_coeff, ref_region, kx_cd):
    inv_speed = 1.0 / region_speed
    ref_slow = inv_speed[ref_region]
    regions = region_speed.shape[0]
    padded = 1 << max(1, (regions - 1).bit_length())
    extra = padded - regions
    phase = omega * (inv_speed[None, :] - ref_slow[:, None])
    gain = jnp.broadcast_to(fd_coeff / omega, phase.shape)
    parts = [jnp.cos(phase), jnp.sin(phase), gain]
    if extra:
        parts = [jnp.concatenate([p, jnp.repeat(p[:, -1:], extra, axis=1)], axis=1) for p in parts]
    table = jnp.stack(parts, axis=1).reshape(-1)
    wave_ref = omega * ref_slow
    wave_ref = wave_ref[:, None, None]
    excess = wave_ref * wave_ref - kx_cd * kx_cd
    decay_line = jnp.exp(-jnp.sqrt(jnp.maximum(-excess, 0.0)))
    vertical = jnp.sqrt(jnp.maximum(excess, 0.0))
    mult = jnp.stack([decay_line * jnp.cos(vertical), decay_line * jnp.sin(vertical)], axis=1)
    return (table, mult)


def fast_fits(surface, region_index, region_speed):
    freq_count = surface.shape[1]
    rows = surface.shape[2] * lax.axis_size("strip")
    line_len = surface.shape[3]
    return (
        freq_count == lax.axis_size("strip")
        and line_len == FFT_BLOCKS * LANE
        and rows % ROW_CHUNK == 0
        and surface.shape[2] % ROW_CHUNK == 0
        and rows <= 64
        and region_speed.shape[0] <= 16
    )


def strip_pairs(depths, strip_count, shift):
    return [
        (d * strip_count + r, d * strip_count + (r + shift) % strip_count)
        for d in depths
        for r in range(strip_count)
    ]


def gather_rows(local, depths, strip_no, strip_count, row_axis):
    rows = local.shape[row_axis]
    shape = list(local.shape)
    shape[row_axis] = rows * strip_count
    full = jnp.zeros(shape, local.dtype)
    start = [0] * len(shape)
    start[row_axis] = strip_no * rows
    full = lax.dynamic_update_slice(full, local, start)
    for shift in range(1, strip_count):
        got = lax.ppermute(local, ("depth", "strip"), strip_pairs(depths, strip_count, shift))
        start = [0] * len(shape)
        start[row_axis] = ((strip_no - shift) % strip_count) * rows
        full = lax.dynamic_update_slice(full, got, start)
    return full


def gather_strips(piece_of, local, depths, strip_no, strip_count, rows_here):
    rows = rows_here * strip_count
    shape = (local.shape[0], rows, local.shape[2])
    full = lax.dynamic_update_slice(
        jnp.zeros(shape, jnp.float32), local, (0, strip_no * rows_here, 0)
    )
    for shift in range(1, strip_count):
        target = (strip_no + shift) % strip_count
        got = lax.ppermute(
            piece_of(target), ("depth", "strip"), strip_pairs(depths, strip_count, shift)
        )
        source = (strip_no - shift) % strip_count
        full = lax.dynamic_update_slice(full, got, (0, source * rows_here, 0))
    return full


def shards(surface, omegas, region_speed, fd_coeff, region_index, ref_region):
    if not fast_fits(surface, region_index, region_speed):
        return shards_general(surface, omegas, region_speed, fd_coeff, region_index, ref_region)
    line_len = surface.shape[3]
    rows_here = surface.shape[2]
    steps = region_index.shape[0]
    segment_no = lax.axis_index("depth")
    segment_count = lax.axis_size("depth")
    strip_no = lax.axis_index("strip")
    strip_count = lax.axis_size("strip")
    consts = fast_constants(line_len)
    region_f = region_index.astype(jnp.float32)
    early = [d for d in range(segment_count) if d != 1]

    def with_surface(target):
        return jnp.concatenate(
            [region_f, lax.dynamic_index_in_dim(surface, target, 1, keepdims=False)], axis=0
        )

    rows = rows_here * strip_count
    regions_a = lax.dynamic_update_slice(
        jnp.zeros((steps, rows, line_len), jnp.float32), region_f, (0, strip_no * rows_here, 0)
    )
    wave = lax.dynamic_update_slice(
        jnp.zeros((2, rows, line_len), jnp.float32),
        lax.dynamic_index_in_dim(surface, strip_no, 1, keepdims=False),
        (0, strip_no * rows_here, 0),
    )
    for shift in range(1, strip_count):
        target = (strip_no + shift) % strip_count
        got = lax.ppermute(
            with_surface(target), ("depth", "strip"), strip_pairs(early, strip_count, shift)
        )
        start = (0, ((strip_no - shift) % strip_count) * rows_here, 0)
        regions_a = lax.dynamic_update_slice(regions_a, got[:steps], start)
        wave = lax.dynamic_update_slice(wave, got[steps:], start)
    regions_a = regions_a.astype(jnp.int32)
    omega = lax.dynamic_index_in_dim(omegas, strip_no, 0, keepdims=False)
    table, mult = section_tables(omega, region_speed, fd_coeff, ref_region, jnp.asarray(consts[3]))
    image = jnp.zeros((strip_count, steps, rows_here, line_len), jnp.float32)
    regions_b = regions_a

    def sweep(regions):
        def live(wave, image):
            return run_section(wave, regions, table, mult, consts, strip_count, strip_no)

        return live

    def idle(wave, image):
        return (wave, image)

    def freq_sum(image, depths):
        parts = []
        for shift in range(1, strip_count):
            piece = image[shift]
            parts.append(
                lax.ppermute(piece, ("depth", "strip"), strip_pairs(depths, strip_count, shift))
            )
        return parts

    arrived = []
    for tick_no in range(segment_count):
        regions = regions_b if tick_no == 1 else regions_a
        if tick_no == 0:
            wave, image = sweep(regions)(wave, image)
        else:
            wave, image = lax.cond(segment_no == tick_no, sweep(regions), idle, wave, image)
        if tick_no + 1 < segment_count:
            wave = lax.ppermute(wave, "depth", [(tick_no, tick_no + 1)])
        if tick_no == 0 and segment_count > 1:
            held, _ = lax.optimization_barrier((region_f, image))
            regions_b = gather_strips(
                lambda target: held, held, [1], strip_no, strip_count, rows_here
            ).astype(jnp.int32)
        if tick_no == segment_count - 2:
            wave, image = lax.optimization_barrier((wave, image))
            arrived += freq_sum(image, range(segment_count - 1))
    arrived += freq_sum(image, [segment_count - 1])
    total = image[0]
    for piece in arrived:
        total = total + piece
    return total


def solution(mesh):
    in_specs = (
        P(None, "shots", "strip", None),
        P(),
        P(),
        P(),
        P("depth", "strip", None),
        P("depth"),
    )
    out_specs = P("depth", "strip", "shots")
    return jax.shard_map(shards, mesh=mesh, in_specs=in_specs, out_specs=out_specs, check_vma=False)
```

```python
import math

import ml_dtypes
import numpy as np
import jax
import jax.numpy as jnp
from jax import lax
from jax.experimental import pallas as pl
from jax.experimental.pallas import tpu as pltpu
from jax.sharding import PartitionSpec as P

DAMPING = 0.05
PRECISE = lax.Precision.HIGHEST


def padded_2(cells, sides, width):
    for axis, dim in sides:
        count = lax.axis_size(axis)
        ends = count - 1
        head = lax.slice_in_dim(cells, 0, width, axis=dim)
        tail = lax.slice_in_dim(cells, cells.shape[dim] - width, cells.shape[dim], axis=dim)
        cells = jnp.concatenate(
            [
                lax.ppermute(tail, axis, [(i, (i + 1) % count) for i in range(ends)]),
                cells,
                lax.ppermute(head, axis, [((i + 1) % count, i) for i in range(ends)]),
            ],
            axis=dim,
        )
    return cells


def from_behind(value, axis, steps):
    count = lax.axis_size(axis)
    first, last = (max(0, -steps), min(count, count - steps))
    return lax.ppermute(value, axis, [(source, source + steps) for source in range(first, last)])


def complex_scale(values, cosine, sine_part):
    return jnp.stack(
        [values[0] * cosine - values[1] * sine_part, values[0] * sine_part + values[1] * cosine]
    )


def angle_pair(numerator, period):
    angle_grid = numerator.astype(jnp.float32) * (2.0 * math.pi / period)
    return (jnp.cos(angle_grid), jnp.sin(angle_grid))


def block_matrix(cosine, sine_part, forward):
    sign_flip = 1.0 if forward else -1.0
    return jnp.stack(
        [jnp.stack([cosine, -sign_flip * sine_part]), jnp.stack([sign_flip * sine_part, cosine])]
    )


def build_tables(line_len):
    block_len = 128
    outer_len = line_len // block_len
    inner_idx = jnp.arange(block_len)
    outer_idx = jnp.arange(outer_len)
    cos_large, sin_large = angle_pair(
        inner_idx[:, None] * inner_idx[None, :] % block_len, block_len
    )
    cos_small, sin_small = angle_pair(
        outer_idx[:, None] * outer_idx[None, :] % outer_len, outer_len
    )
    cos_twist, sin_twist = angle_pair(outer_idx[:, None] * inner_idx[None, :], line_len)
    wave_index = outer_idx[:, None] + outer_len * inner_idx[None, :]
    signed = jnp.where(wave_index >= line_len // 2, wave_index - line_len, wave_index)
    kx_grid = signed.astype(jnp.float32) * (2.0 * math.pi / line_len)
    small_fwd = block_matrix(cos_small, sin_small, True)
    small_inv = block_matrix(cos_small, sin_small, False)
    large_fwd = block_matrix(cos_large, sin_large, True)
    large_inv = block_matrix(cos_large, sin_large, False)
    return (small_fwd, small_inv, large_fwd, large_inv, cos_twist, sin_twist, kx_grid)


def forward_line(wavefield, tables):
    small_fwd, small_inv, large_fwd, large_inv, cos_twist, sin_twist, kx_grid = tables
    row_count = wavefield.shape[1]
    pieces = wavefield.reshape(2, row_count, cos_twist.shape[0], cos_twist.shape[1])
    mixed_part = jnp.einsum("zrab,zwca->wrcb", pieces, small_fwd, precision=PRECISE)
    mixed_part = complex_scale(mixed_part, cos_twist, -sin_twist)
    return jnp.einsum("zrcb,zwbd->wrcd", mixed_part, large_fwd, precision=PRECISE)


def inverse_line(spectrum, tables):
    small_fwd, small_inv, large_fwd, large_inv, cos_twist, sin_twist, kx_grid = tables
    row_count = spectrum.shape[1]
    line_len = cos_twist.shape[0] * cos_twist.shape[1]
    mixed_part = jnp.einsum("zrcd,zwdb->wrcb", spectrum, large_inv, precision=PRECISE)
    mixed_part = complex_scale(mixed_part, cos_twist, sin_twist)
    pieces = jnp.einsum("zrcb,zwca->wrab", mixed_part, small_inv, precision=PRECISE)
    return pieces.reshape(2, row_count, line_len) * (1.0 / line_len)


def lookup(regions, entries):
    picked = jnp.zeros(regions.shape, jnp.float32)
    for region_no in range(entries.shape[0]):
        picked = picked + jnp.where(regions == region_no, entries[region_no], 0.0)
    return picked


def depth_step(wavefield, omega_now, slow_cells, coef_cells, ref_slow, tables, pad_rows):
    kx_grid = tables[6]
    wave_ref = omega_now * ref_slow
    excess = wave_ref * wave_ref - kx_grid * kx_grid
    decay_line = jnp.exp(-jnp.sqrt(jnp.maximum(-excess, 0.0)))
    vertical = jnp.sqrt(jnp.maximum(excess, 0.0))
    spectrum = complex_scale(
        forward_line(wavefield, tables),
        decay_line * jnp.cos(vertical),
        decay_line * jnp.sin(vertical),
    )
    wavefield = inverse_line(spectrum, tables)
    phase_cell = omega_now * (slow_cells - ref_slow)
    wavefield = complex_scale(wavefield, jnp.cos(phase_cell), jnp.sin(phase_cell))
    padded = pad_rows(wavefield)
    laplace = (
        padded[:, :-2]
        + padded[:, 2:]
        + jnp.roll(wavefield, 1, 2)
        + jnp.roll(wavefield, -1, 2)
        - 4.0 * wavefield
    )
    return wavefield + complex_scale(laplace, DAMPING, coef_cells / omega_now)


def march(wavefield, omega_now, slow_block, coef_block, ref_block, tables, pad_rows):
    traces = []
    for step_no in range(slow_block.shape[0]):
        wavefield = depth_step(
            wavefield,
            omega_now,
            slow_block[step_no],
            coef_block[step_no],
            ref_block[step_no],
            tables,
            pad_rows,
        )
        traces.append(wavefield[0])
    return (wavefield, jnp.stack(traces))


def shards_general(surface, omegas, region_speed, fd_coeff, region_index, ref_region):
    line_len = surface.shape[3]
    rows_here = surface.shape[2]
    freq_count = surface.shape[1]
    step_count = region_index.shape[0]
    tables = build_tables(line_len)
    inv_speed = 1.0 / region_speed
    segment_no = lax.axis_index("depth")
    segment_count = lax.axis_size("depth")

    def pad_near(values):
        return padded_2(values, (("strip", 1),), 1)

    slow_cells = lookup(region_index, inv_speed)
    coef_cells = lookup(region_index, fd_coeff)
    ref_cells = lookup(ref_region, inv_speed)
    freq_index = jnp.arange(freq_count)
    image_out = jnp.zeros((step_count, rows_here, line_len), jnp.float32)
    arriving = jnp.zeros((2, rows_here, line_len), jnp.float32)
    tick_count = freq_count + segment_count - 1
    for tick_no in range(tick_count):
        batch_no = tick_no - segment_no
        is_live = (batch_no >= 0) & (batch_no < freq_count)
        clipped = jnp.clip(batch_no, 0, freq_count - 1)
        picked = lax.dynamic_index_in_dim(surface, clipped, 1, keepdims=False)
        entering = jnp.where(segment_no == 0, picked, arriving)
        omega_now = jnp.sum(jnp.where(freq_index == clipped, omegas, 0.0))
        leaving, traces = march(
            entering, omega_now, slow_cells, coef_cells, ref_cells, tables, pad_near
        )
        image_out = image_out + jnp.where(is_live, traces, 0.0)
        if tick_no + 1 < tick_count:
            arriving = from_behind(leaving, "depth", 1)
    return image_out


LANE = 128
FFT_BLOCKS = 16
ROW_CHUNK = 8


def fft4(x0, x1, x2, x3, sign):
    s0 = (x0[0] + x2[0], x0[1] + x2[1])
    d0 = (x0[0] - x2[0], x0[1] - x2[1])
    s1 = (x1[0] + x3[0], x1[1] + x3[1])
    d1 = (x1[0] - x3[0], x1[1] - x3[1])
    if sign < 0:
        wd = (d1[1], -d1[0])
    else:
        wd = (-d1[1], d1[0])
    return (
        (s0[0] + s1[0], s0[1] + s1[1]),
        (d0[0] + wd[0], d0[1] + wd[1]),
        (s0[0] - s1[0], s0[1] - s1[1]),
        (d0[0] - wd[0], d0[1] - wd[1]),
    )


def turn_const(value, power, sign):
    if power == 4:
        return (-value[1], value[0]) if sign > 0 else (value[1], -value[0])
    angle = sign * 2.0 * math.pi * power / 16.0
    cr, ci = (math.cos(angle), math.sin(angle))
    return (value[0] * cr - value[1] * ci, value[0] * ci + value[1] * cr)


def fft16(parts, sign):
    mid = [[None] * 4 for _ in range(4)]
    for a0 in range(4):
        ys = fft4(parts[a0], parts[4 + a0], parts[8 + a0], parts[12 + a0], sign)
        for c0 in range(4):
            power = a0 * c0
            mid[a0][c0] = ys[c0] if power == 0 else turn_const(ys[c0], power, sign)
    out = [None] * 16
    for c0 in range(4):
        zs = fft4(mid[0][c0], mid[1][c0], mid[2][c0], mid[3][c0], sign)
        for c1 in range(4):
            out[c0 + 4 * c1] = zs[c1]
    return out


def pick(regions, values):
    level = list(values)
    bit = 1
    while len(level) > 1:
        chosen = (regions & bit) != 0
        level = [jnp.where(chosen, level[i + 1], level[i]) for i in range(0, len(level), 2)]
        bit *= 2
    return jnp.broadcast_to(level[0], regions.shape)


def pick_bits(bits, values):
    level = list(values)
    for chosen in bits:
        level = [jnp.where(chosen, level[i + 1], level[i]) for i in range(0, len(level), 2)]
    return jnp.broadcast_to(level[0], bits[0].shape)


def split_dot(values, hi_ref, lo_ref):
    high = values.astype(jnp.bfloat16)
    low = (values - high.astype(jnp.float32)).astype(jnp.bfloat16)
    main = jnp.dot(high, hi_ref[...], preferred_element_type=jnp.float32)
    fix = jnp.dot(high, lo_ref[...], preferred_element_type=jnp.float32) + jnp.dot(
        low, hi_ref[:, :], preferred_element_type=jnp.float32
    )
    return main + fix


def section_kernel(
    tab_ref, w_ref, rid_ref, mult_ref, tw_ref, fhi_ref, flo_ref, ghi_ref, glo_ref, pos_ref,
    wout_ref, img_ref, a_ref, y_ref, v_ref, cs_ref, sn_ref, gn_ref, *, table_len
):
    rows = w_ref.shape[1]
    line_len = w_ref.shape[2]
    steps = rid_ref.shape[0]
    strip_count, rows_here = img_ref.shape[0], img_ref.shape[2]
    chunks = rows // ROW_CHUNK
    inv_len = 1.0 / line_len
    wout_ref[...] = w_ref[...]

    def blk(a):
        return slice(a * LANE, (a + 1) * LANE)

    def one_step(k, carry):
        base = k * (3 * table_len)
        cos_t = [tab_ref[base + g] for g in range(table_len)]
        sin_t = [tab_ref[base + table_len + g] for g in range(table_len)]
        gain_t = [tab_ref[base + 2 * table_len + g] for g in range(table_len)]

        def forward_chunk(i, c):
            y0 = pl.multiple_of(i * ROW_CHUNK, ROW_CHUNK)
            parts = [
                (wout_ref[0, pl.ds(y0, ROW_CHUNK), blk(a)], wout_ref[1, pl.ds(y0, ROW_CHUNK), blk(a)])
                for a in range(FFT_BLOCKS)
            ]
            spec = fft16(parts, -1)
            for cc in range(FFT_BLOCKS):
                tc = tw_ref[0, cc:cc + 1, :]
                ts = tw_ref[1, cc:cc + 1, :]
                xr, xi = spec[cc]
                a_ref[pl.ds(cc * rows + y0, ROW_CHUNK), 0:LANE] = xr * tc + xi * ts
                a_ref[pl.ds(cc * rows + y0, ROW_CHUNK), LANE:2 * LANE] = xi * tc - xr * ts
            return c

        lax.fori_loop(0, chunks, forward_chunk, 0)
        spectrum = split_dot(a_ref[...], fhi_ref, flo_ref)
        for a in range(FFT_BLOCKS):
            regions = rid_ref[k, :, blk(a)]
            bits = [(regions & (1 << b)) != 0 for b in range(max(1, (table_len - 1).bit_length()))]
            cs_ref[:, blk(a)] = pick_bits(bits, cos_t)
            sn_ref[:, blk(a)] = pick_bits(bits, sin_t)
            gn_ref[:, blk(a)] = pick_bits(bits, gain_t)
        y_ref[...] = spectrum
        for cc in range(FFT_BLOCKS):
            band = slice(cc * rows, (cc + 1) * rows)
            yr = y_ref[band, 0:LANE]
            yi = y_ref[band, LANE:2 * LANE]
            mr = mult_ref[k, 0, cc:cc + 1, :]
            mi = mult_ref[k, 1, cc:cc + 1, :]
            a_ref[band, 0:LANE] = yr * mr - yi * mi
            a_ref[band, LANE:2 * LANE] = yr * mi + yi * mr
        y_ref[...] = split_dot(a_ref[...], ghi_ref, glo_ref)

        def inverse_chunk(i, c):
            y0 = pl.multiple_of(i * ROW_CHUNK, ROW_CHUNK)
            parts = []
            for cc in range(FFT_BLOCKS):
                zr = y_ref[pl.ds(cc * rows + y0, ROW_CHUNK), 0:LANE]
                zi = y_ref[pl.ds(cc * rows + y0, ROW_CHUNK), LANE:2 * LANE]
                tc = tw_ref[0, cc:cc + 1, :]
                ts = tw_ref[1, cc:cc + 1, :]
                parts.append((zr * tc - zi * ts, zr * ts + zi * tc))
            back = fft16(parts, 1)
            for a in range(FFT_BLOCKS):
                ur = back[a][0] * inv_len
                ui = back[a][1] * inv_len
                cs = cs_ref[pl.ds(y0, ROW_CHUNK), blk(a)]
                sn = sn_ref[pl.ds(y0, ROW_CHUNK), blk(a)]
                v_ref[0, pl.ds(y0, ROW_CHUNK), blk(a)] = ur * cs - ui * sn
                v_ref[1, pl.ds(y0, ROW_CHUNK), blk(a)] = ur * sn + ui * cs
            return c

        lax.fori_loop(0, chunks, inverse_chunk, 0)
        row_id = lax.broadcasted_iota(jnp.int32, (rows, LANE), 0)
        lane_id = lax.broadcasted_iota(jnp.int32, (rows, LANE), 1)
        cache = {}

        def cell(part, a):
            key = (part, a % FFT_BLOCKS)
            if key not in cache:
                v = v_ref[part, :, blk(a % FFT_BLOCKS)]
                cache[key] = (v, pltpu.roll(v, 1, 1), pltpu.roll(v, LANE - 1, 1))
            return cache[key]

        for a in range(FFT_BLOCKS):
            lap = []
            here = []
            for part in range(2):
                v, from_left, from_right = cell(part, a)
                prev_left = cell(part, a - 1)[1]
                next_right = cell(part, a + 1)[2]
                above = jnp.where(row_id == 0, 0.0, pltpu.roll(v, 1, 0))
                below = jnp.where(row_id == rows - 1, 0.0, pltpu.roll(v, rows - 1, 0))
                left = jnp.where(lane_id == 0, prev_left, from_left)
                right = jnp.where(lane_id == LANE - 1, next_right, from_right)
                lap.append(above + below + left + right - 4.0 * v)
                here.append(v)
            gain = gn_ref[:, blk(a)]
            new_re = here[0] + (lap[0] * DAMPING - lap[1] * gain)
            new_im = here[1] + (lap[0] * gain + lap[1] * DAMPING)
            wout_ref[0, :, blk(a)] = new_re
            wout_ref[1, :, blk(a)] = new_im
            for j in range(strip_count):
                slot = (j - pos_ref[0] + strip_count) % strip_count
                img_ref[slot, k, :, blk(a)] = new_re[j * rows_here:(j + 1) * rows_here]
        return carry

    lax.fori_loop(0, steps, one_step, 0)


def fast_constants(line_len):
    outer = line_len // LANE
    b = np.arange(LANE)
    ang = 2.0 * np.pi * (np.outer(b, b) % LANE) / LANE
    cos_m, sin_m = (np.cos(ang), np.sin(ang))
    fwd = np.block([[cos_m, -sin_m], [sin_m, cos_m]])
    inv = np.block([[cos_m, sin_m], [-sin_m, cos_m]])

    def halves(m):
        hi = m.astype(ml_dtypes.bfloat16)
        lo = (m - hi.astype(np.float64)).astype(ml_dtypes.bfloat16)
        return (hi, lo)

    c = np.arange(outer)
    tw_ang = 2.0 * np.pi * np.outer(c, b) / line_len
    twiddle = np.stack([np.cos(tw_ang), np.sin(tw_ang)]).astype(np.float32)
    q = c[:, None] + outer * b[None, :]
    signed = np.where(q >= line_len // 2, q - line_len, q).astype(np.float32)
    kx_cd = signed * np.float32(2.0 * math.pi / line_len)
    return (halves(fwd), halves(inv), twiddle, kx_cd.astype(np.float32))


def run_section(wave, regions, table, mult, consts, strip_count, strip_no):
    (fhi, flo), (ghi, glo), twiddle, _ = consts
    rows, line_len = wave.shape[1], wave.shape[2]
    steps = regions.shape[0]
    table_len = table.shape[0] // (3 * steps)
    vmem = pl.BlockSpec(memory_space=pltpu.VMEM)
    flops = steps * (2 * 3 * 2 * (FFT_BLOCKS * rows) * 256 * 256 + 400 * rows * line_len)
    return pl.pallas_call(
        lambda *refs: section_kernel(*refs, table_len=table_len),
        out_shape=(
            jax.ShapeDtypeStruct(wave.shape, jnp.float32),
            jax.ShapeDtypeStruct((strip_count, steps, rows // strip_count, line_len), jnp.float32),
        ),
        in_specs=[pl.BlockSpec(memory_space=pltpu.SMEM)] + [vmem] * 8
        + [pl.BlockSpec(memory_space=pltpu.SMEM)],
        out_specs=(vmem, vmem),
        scratch_shapes=[
            pltpu.VMEM((FFT_BLOCKS * rows, 2 * LANE), jnp.float32),
            pltpu.VMEM((FFT_BLOCKS * rows, 2 * LANE), jnp.float32),
            pltpu.VMEM((2, rows, line_len), jnp.float32),
            pltpu.VMEM((rows, line_len), jnp.float32),
            pltpu.VMEM((rows, line_len), jnp.float32),
            pltpu.VMEM((rows, line_len), jnp.float32),
        ],
        cost_estimate=pl.CostEstimate(
            flops=flops, transcendentals=0, bytes_accessed=4 * rows * line_len * 6 * steps
        ),
    )(table, wave, regions, mult, jnp.asarray(twiddle), jnp.asarray(fhi), jnp.asarray(flo),
      jnp.asarray(ghi), jnp.asarray(glo), jnp.reshape(strip_no, (1,)).astype(jnp.int32))


def section_tables(omega, region_speed, fd_coeff, ref_region, kx_cd):
    inv_speed = 1.0 / region_speed
    ref_slow = inv_speed[ref_region]
    regions = region_speed.shape[0]
    padded = 1 << max(1, (regions - 1).bit_length())
    extra = padded - regions
    phase = omega * (inv_speed[None, :] - ref_slow[:, None])
    gain = jnp.broadcast_to(fd_coeff / omega, phase.shape)
    parts = [jnp.cos(phase), jnp.sin(phase), gain]
    if extra:
        parts = [jnp.concatenate([p, jnp.repeat(p[:, -1:], extra, axis=1)], axis=1) for p in parts]
    table = jnp.stack(parts, axis=1).reshape(-1)
    wave_ref = omega * ref_slow
    wave_ref = wave_ref[:, None, None]
    excess = wave_ref * wave_ref - kx_cd * kx_cd
    decay_line = jnp.exp(-jnp.sqrt(jnp.maximum(-excess, 0.0)))
    vertical = jnp.sqrt(jnp.maximum(excess, 0.0))
    mult = jnp.stack([decay_line * jnp.cos(vertical), decay_line * jnp.sin(vertical)], axis=1)
    return (table, mult)


def fast_fits(surface, region_index, region_speed):
    freq_count = surface.shape[1]
    rows = surface.shape[2] * lax.axis_size("strip")
    line_len = surface.shape[3]
    return (
        freq_count == lax.axis_size("strip")
        and line_len == FFT_BLOCKS * LANE
        and rows % ROW_CHUNK == 0
        and surface.shape[2] % ROW_CHUNK == 0
        and rows <= 64
        and region_speed.shape[0] <= 16
    )


def strip_pairs(depths, strip_count, shift):
    return [
        (d * strip_count + r, d * strip_count + (r + shift) % strip_count)
        for d in depths
        for r in range(strip_count)
    ]


def gather_rows(local, depths, strip_no, strip_count, row_axis):
    rows = local.shape[row_axis]
    shape = list(local.shape)
    shape[row_axis] = rows * strip_count
    full = jnp.zeros(shape, local.dtype)
    start = [0] * len(shape)
    start[row_axis] = strip_no * rows
    full = lax.dynamic_update_slice(full, local, start)
    for shift in range(1, strip_count):
        got = lax.ppermute(local, ("depth", "strip"), strip_pairs(depths, strip_count, shift))
        start = [0] * len(shape)
        start[row_axis] = ((strip_no - shift) % strip_count) * rows
        full = lax.dynamic_update_slice(full, got, start)
    return full


def gather_strips(piece_of, local, depths, strip_no, strip_count, rows_here):
    rows = rows_here * strip_count
    shape = (local.shape[0], rows, local.shape[2])
    full = lax.dynamic_update_slice(
        jnp.zeros(shape, jnp.float32), local, (0, strip_no * rows_here, 0)
    )
    for shift in range(1, strip_count):
        target = (strip_no + shift) % strip_count
        got = lax.ppermute(
            piece_of(target), ("depth", "strip"), strip_pairs(depths, strip_count, shift)
        )
        source = (strip_no - shift) % strip_count
        full = lax.dynamic_update_slice(full, got, (0, source * rows_here, 0))
    return full


def shards(surface, omegas, region_speed, fd_coeff, region_index, ref_region):
    if not fast_fits(surface, region_index, region_speed):
        return shards_general(surface, omegas, region_speed, fd_coeff, region_index, ref_region)
    line_len = surface.shape[3]
    rows_here = surface.shape[2]
    steps = region_index.shape[0]
    segment_no = lax.axis_index("depth")
    segment_count = lax.axis_size("depth")
    strip_no = lax.axis_index("strip")
    strip_count = lax.axis_size("strip")
    consts = fast_constants(line_len)
    region_f = region_index.astype(jnp.float32)
    early = [d for d in range(segment_count) if d != 1]

    def with_surface(target):
        return jnp.concatenate(
            [region_f, lax.dynamic_index_in_dim(surface, target, 1, keepdims=False)], axis=0
        )

    gathered = gather_strips(
        with_surface, with_surface(strip_no), early, strip_no, strip_count, rows_here
    )
    regions_a = gathered[:steps].astype(jnp.int32)
    wave = gathered[steps:]
    omega = lax.dynamic_index_in_dim(omegas, strip_no, 0, keepdims=False)
    table, mult = section_tables(omega, region_speed, fd_coeff, ref_region, jnp.asarray(consts[3]))
    image = jnp.zeros((strip_count, steps, rows_here, line_len), jnp.float32)
    regions_b = regions_a

    def sweep(regions):
        def live(wave, image):
            return run_section(wave, regions, table, mult, consts, strip_count, strip_no)

        return live

    def idle(wave, image):
        return (wave, image)

    def freq_sum(image, depths):
        parts = []
        for shift in range(1, strip_count):
            piece = image[shift]
            parts.append(
                lax.ppermute(piece, ("depth", "strip"), strip_pairs(depths, strip_count, shift))
            )
        return parts

    arrived = []
    for tick_no in range(segment_count):
        regions = regions_b if tick_no == 1 else regions_a
        if tick_no == 0:
            wave, image = sweep(regions)(wave, image)
        elif tick_no == 1:
            wave, fresh = sweep(regions)(wave, image)
            image = jnp.where(segment_no == tick_no, fresh, image)
        else:
            wave, image = lax.cond(segment_no == tick_no, sweep(regions), idle, wave, image)
        if tick_no + 1 < segment_count:
            wave = lax.ppermute(wave, "depth", [(tick_no, tick_no + 1)])
        if tick_no == 0 and segment_count > 1:
            held, _ = lax.optimization_barrier((region_f, image))
            regions_b = gather_strips(
                lambda target: held, held, [1], strip_no, strip_count, rows_here
            ).astype(jnp.int32)
        if tick_no == segment_count - 2:
            wave, image = lax.optimization_barrier((wave, image))
            arrived += freq_sum(image, range(segment_count - 1))
    arrived += freq_sum(image, [segment_count - 1])
    total = image[0]
    for piece in arrived:
        total = total + piece
    return total


def solution(mesh):
    in_specs = (
        P(None, "shots", "strip", None),
        P(),
        P(),
        P(),
        P("depth", "strip", None),
        P("depth"),
    )
    out_specs = P("depth", "strip", "shots")
    return jax.shard_map(shards, mesh=mesh, in_specs=in_specs, out_specs=out_specs, check_vma=False)
```

```python
import math

import ml_dtypes
import numpy as np
import jax
import jax.numpy as jnp
from jax import lax
from jax.experimental import pallas as pl
from jax.experimental.pallas import tpu as pltpu
from jax.sharding import PartitionSpec as P

DAMPING = 0.05
PRECISE = lax.Precision.HIGHEST


def padded_2(cells, sides, width):
    for axis, dim in sides:
        count = lax.axis_size(axis)
        ends = count - 1
        head = lax.slice_in_dim(cells, 0, width, axis=dim)
        tail = lax.slice_in_dim(cells, cells.shape[dim] - width, cells.shape[dim], axis=dim)
        cells = jnp.concatenate(
            [
                lax.ppermute(tail, axis, [(i, (i + 1) % count) for i in range(ends)]),
                cells,
                lax.ppermute(head, axis, [((i + 1) % count, i) for i in range(ends)]),
            ],
            axis=dim,
        )
    return cells


def from_behind(value, axis, steps):
    count = lax.axis_size(axis)
    first, last = (max(0, -steps), min(count, count - steps))
    return lax.ppermute(value, axis, [(source, source + steps) for source in range(first, last)])


def complex_scale(values, cosine, sine_part):
    return jnp.stack(
        [values[0] * cosine - values[1] * sine_part, values[0] * sine_part + values[1] * cosine]
    )


def angle_pair(numerator, period):
    angle_grid = numerator.astype(jnp.float32) * (2.0 * math.pi / period)
    return (jnp.cos(angle_grid), jnp.sin(angle_grid))


def block_matrix(cosine, sine_part, forward):
    sign_flip = 1.0 if forward else -1.0
    return jnp.stack(
        [jnp.stack([cosine, -sign_flip * sine_part]), jnp.stack([sign_flip * sine_part, cosine])]
    )


def build_tables(line_len):
    block_len = 128
    outer_len = line_len // block_len
    inner_idx = jnp.arange(block_len)
    outer_idx = jnp.arange(outer_len)
    cos_large, sin_large = angle_pair(
        inner_idx[:, None] * inner_idx[None, :] % block_len, block_len
    )
    cos_small, sin_small = angle_pair(
        outer_idx[:, None] * outer_idx[None, :] % outer_len, outer_len
    )
    cos_twist, sin_twist = angle_pair(outer_idx[:, None] * inner_idx[None, :], line_len)
    wave_index = outer_idx[:, None] + outer_len * inner_idx[None, :]
    signed = jnp.where(wave_index >= line_len // 2, wave_index - line_len, wave_index)
    kx_grid = signed.astype(jnp.float32) * (2.0 * math.pi / line_len)
    small_fwd = block_matrix(cos_small, sin_small, True)
    small_inv = block_matrix(cos_small, sin_small, False)
    large_fwd = block_matrix(cos_large, sin_large, True)
    large_inv = block_matrix(cos_large, sin_large, False)
    return (small_fwd, small_inv, large_fwd, large_inv, cos_twist, sin_twist, kx_grid)


def forward_line(wavefield, tables):
    small_fwd, small_inv, large_fwd, large_inv, cos_twist, sin_twist, kx_grid = tables
    row_count = wavefield.shape[1]
    pieces = wavefield.reshape(2, row_count, cos_twist.shape[0], cos_twist.shape[1])
    mixed_part = jnp.einsum("zrab,zwca->wrcb", pieces, small_fwd, precision=PRECISE)
    mixed_part = complex_scale(mixed_part, cos_twist, -sin_twist)
    return jnp.einsum("zrcb,zwbd->wrcd", mixed_part, large_fwd, precision=PRECISE)


def inverse_line(spectrum, tables):
    small_fwd, small_inv, large_fwd, large_inv, cos_twist, sin_twist, kx_grid = tables
    row_count = spectrum.shape[1]
    line_len = cos_twist.shape[0] * cos_twist.shape[1]
    mixed_part = jnp.einsum("zrcd,zwdb->wrcb", spectrum, large_inv, precision=PRECISE)
    mixed_part = complex_scale(mixed_part, cos_twist, sin_twist)
    pieces = jnp.einsum("zrcb,zwca->wrab", mixed_part, small_inv, precision=PRECISE)
    return pieces.reshape(2, row_count, line_len) * (1.0 / line_len)


def lookup(regions, entries):
    picked = jnp.zeros(regions.shape, jnp.float32)
    for region_no in range(entries.shape[0]):
        picked = picked + jnp.where(regions == region_no, entries[region_no], 0.0)
    return picked


def depth_step(wavefield, omega_now, slow_cells, coef_cells, ref_slow, tables, pad_rows):
    kx_grid = tables[6]
    wave_ref = omega_now * ref_slow
    excess = wave_ref * wave_ref - kx_grid * kx_grid
    decay_line = jnp.exp(-jnp.sqrt(jnp.maximum(-excess, 0.0)))
    vertical = jnp.sqrt(jnp.maximum(excess, 0.0))
    spectrum = complex_scale(
        forward_line(wavefield, tables),
        decay_line * jnp.cos(vertical),
        decay_line * jnp.sin(vertical),
    )
    wavefield = inverse_line(spectrum, tables)
    phase_cell = omega_now * (slow_cells - ref_slow)
    wavefield = complex_scale(wavefield, jnp.cos(phase_cell), jnp.sin(phase_cell))
    padded = pad_rows(wavefield)
    laplace = (
        padded[:, :-2]
        + padded[:, 2:]
        + jnp.roll(wavefield, 1, 2)
        + jnp.roll(wavefield, -1, 2)
        - 4.0 * wavefield
    )
    return wavefield + complex_scale(laplace, DAMPING, coef_cells / omega_now)


def march(wavefield, omega_now, slow_block, coef_block, ref_block, tables, pad_rows):
    traces = []
    for step_no in range(slow_block.shape[0]):
        wavefield = depth_step(
            wavefield,
            omega_now,
            slow_block[step_no],
            coef_block[step_no],
            ref_block[step_no],
            tables,
            pad_rows,
        )
        traces.append(wavefield[0])
    return (wavefield, jnp.stack(traces))


def shards_general(surface, omegas, region_speed, fd_coeff, region_index, ref_region):
    line_len = surface.shape[3]
    rows_here = surface.shape[2]
    freq_count = surface.shape[1]
    step_count = region_index.shape[0]
    tables = build_tables(line_len)
    inv_speed = 1.0 / region_speed
    segment_no = lax.axis_index("depth")
    segment_count = lax.axis_size("depth")

    def pad_near(values):
        return padded_2(values, (("strip", 1),), 1)

    slow_cells = lookup(region_index, inv_speed)
    coef_cells = lookup(region_index, fd_coeff)
    ref_cells = lookup(ref_region, inv_speed)
    freq_index = jnp.arange(freq_count)
    image_out = jnp.zeros((step_count, rows_here, line_len), jnp.float32)
    arriving = jnp.zeros((2, rows_here, line_len), jnp.float32)
    tick_count = freq_count + segment_count - 1
    for tick_no in range(tick_count):
        batch_no = tick_no - segment_no
        is_live = (batch_no >= 0) & (batch_no < freq_count)
        clipped = jnp.clip(batch_no, 0, freq_count - 1)
        picked = lax.dynamic_index_in_dim(surface, clipped, 1, keepdims=False)
        entering = jnp.where(segment_no == 0, picked, arriving)
        omega_now = jnp.sum(jnp.where(freq_index == clipped, omegas, 0.0))
        leaving, traces = march(
            entering, omega_now, slow_cells, coef_cells, ref_cells, tables, pad_near
        )
        image_out = image_out + jnp.where(is_live, traces, 0.0)
        if tick_no + 1 < tick_count:
            arriving = from_behind(leaving, "depth", 1)
    return image_out


LANE = 128
FFT_BLOCKS = 16
ROW_CHUNK = 8


def fft4(x0, x1, x2, x3, sign):
    s0 = (x0[0] + x2[0], x0[1] + x2[1])
    d0 = (x0[0] - x2[0], x0[1] - x2[1])
    s1 = (x1[0] + x3[0], x1[1] + x3[1])
    d1 = (x1[0] - x3[0], x1[1] - x3[1])
    if sign < 0:
        wd = (d1[1], -d1[0])
    else:
        wd = (-d1[1], d1[0])
    return (
        (s0[0] + s1[0], s0[1] + s1[1]),
        (d0[0] + wd[0], d0[1] + wd[1]),
        (s0[0] - s1[0], s0[1] - s1[1]),
        (d0[0] - wd[0], d0[1] - wd[1]),
    )


def turn_const(value, power, sign):
    if power == 4:
        return (-value[1], value[0]) if sign > 0 else (value[1], -value[0])
    angle = sign * 2.0 * math.pi * power / 16.0
    cr, ci = (math.cos(angle), math.sin(angle))
    return (value[0] * cr - value[1] * ci, value[0] * ci + value[1] * cr)


def fft16(parts, sign):
    mid = [[None] * 4 for _ in range(4)]
    for a0 in range(4):
        ys = fft4(parts[a0], parts[4 + a0], parts[8 + a0], parts[12 + a0], sign)
        for c0 in range(4):
            power = a0 * c0
            mid[a0][c0] = ys[c0] if power == 0 else turn_const(ys[c0], power, sign)
    out = [None] * 16
    for c0 in range(4):
        zs = fft4(mid[0][c0], mid[1][c0], mid[2][c0], mid[3][c0], sign)
        for c1 in range(4):
            out[c0 + 4 * c1] = zs[c1]
    return out


def pick(regions, values):
    level = list(values)
    bit = 1
    while len(level) > 1:
        chosen = (regions & bit) != 0
        level = [jnp.where(chosen, level[i + 1], level[i]) for i in range(0, len(level), 2)]
        bit *= 2
    return jnp.broadcast_to(level[0], regions.shape)


def pick_bits(bits, values):
    level = list(values)
    for chosen in bits:
        level = [jnp.where(chosen, level[i + 1], level[i]) for i in range(0, len(level), 2)]
    return jnp.broadcast_to(level[0], bits[0].shape)


def split_dot(values, hi_ref, lo_ref):
    high = values.astype(jnp.bfloat16)
    low = (values - high.astype(jnp.float32)).astype(jnp.bfloat16)
    main = jnp.dot(high, hi_ref[...], preferred_element_type=jnp.float32)
    fix = jnp.dot(high, lo_ref[...], preferred_element_type=jnp.float32) + jnp.dot(
        low, hi_ref[:, :], preferred_element_type=jnp.float32
    )
    return main + fix


def section_kernel(
    tab_ref, w_ref, rid_ref, mult_ref, tw_ref, fhi_ref, flo_ref, ghi_ref, glo_ref, pos_ref,
    wout_ref, img_ref, a_ref, y_ref, v_ref, cs_ref, sn_ref, gn_ref, *, table_len
):
    rows = w_ref.shape[1]
    line_len = w_ref.shape[2]
    steps = rid_ref.shape[0]
    strip_count, rows_here = img_ref.shape[0], img_ref.shape[2]
    chunks = rows // ROW_CHUNK
    inv_len = 1.0 / line_len
    wout_ref[...] = w_ref[...]

    def blk(a):
        return slice(a * LANE, (a + 1) * LANE)

    def one_step(k, carry):
        base = k * (3 * table_len)
        cos_t = [tab_ref[base + g] for g in range(table_len)]
        sin_t = [tab_ref[base + table_len + g] for g in range(table_len)]
        gain_t = [tab_ref[base + 2 * table_len + g] for g in range(table_len)]

        def forward_chunk(i, c):
            y0 = pl.multiple_of(i * ROW_CHUNK, ROW_CHUNK)
            parts = [
                (wout_ref[0, pl.ds(y0, ROW_CHUNK), blk(a)], wout_ref[1, pl.ds(y0, ROW_CHUNK), blk(a)])
                for a in range(FFT_BLOCKS)
            ]
            spec = fft16(parts, -1)
            for cc in range(FFT_BLOCKS):
                tc = tw_ref[0, cc:cc + 1, :]
                ts = tw_ref[1, cc:cc + 1, :]
                xr, xi = spec[cc]
                a_ref[pl.ds(cc * rows + y0, ROW_CHUNK), 0:LANE] = xr * tc + xi * ts
                a_ref[pl.ds(cc * rows + y0, ROW_CHUNK), LANE:2 * LANE] = xi * tc - xr * ts
            return c

        lax.fori_loop(0, chunks, forward_chunk, 0, unroll=True)
        spectrum = split_dot(a_ref[...], fhi_ref, flo_ref)
        for a in range(FFT_BLOCKS):
            regions = rid_ref[k, :, blk(a)]
            bits = [(regions & (1 << b)) != 0 for b in range(max(1, (table_len - 1).bit_length()))]
            cs_ref[:, blk(a)] = pick_bits(bits, cos_t)
            sn_ref[:, blk(a)] = pick_bits(bits, sin_t)
            gn_ref[:, blk(a)] = pick_bits(bits, gain_t)
        y_ref[...] = spectrum
        for cc in range(FFT_BLOCKS):
            band = slice(cc * rows, (cc + 1) * rows)
            yr = y_ref[band, 0:LANE]
            yi = y_ref[band, LANE:2 * LANE]
            mr = mult_ref[k, 0, cc:cc + 1, :]
            mi = mult_ref[k, 1, cc:cc + 1, :]
            a_ref[band, 0:LANE] = yr * mr - yi * mi
            a_ref[band, LANE:2 * LANE] = yr * mi + yi * mr
        y_ref[...] = split_dot(a_ref[...], ghi_ref, glo_ref)

        def inverse_chunk(i, c):
            y0 = pl.multiple_of(i * ROW_CHUNK, ROW_CHUNK)
            parts = []
            for cc in range(FFT_BLOCKS):
                zr = y_ref[pl.ds(cc * rows + y0, ROW_CHUNK), 0:LANE]
                zi = y_ref[pl.ds(cc * rows + y0, ROW_CHUNK), LANE:2 * LANE]
                tc = tw_ref[0, cc:cc + 1, :]
                ts = tw_ref[1, cc:cc + 1, :]
                parts.append((zr * tc - zi * ts, zr * ts + zi * tc))
            back = fft16(parts, 1)
            for a in range(FFT_BLOCKS):
                ur = back[a][0] * inv_len
                ui = back[a][1] * inv_len
                cs = cs_ref[pl.ds(y0, ROW_CHUNK), blk(a)]
                sn = sn_ref[pl.ds(y0, ROW_CHUNK), blk(a)]
                v_ref[0, pl.ds(y0, ROW_CHUNK), blk(a)] = ur * cs - ui * sn
                v_ref[1, pl.ds(y0, ROW_CHUNK), blk(a)] = ur * sn + ui * cs
            return c

        lax.fori_loop(0, chunks, inverse_chunk, 0, unroll=True)
        row_id = lax.broadcasted_iota(jnp.int32, (rows, LANE), 0)
        lane_id = lax.broadcasted_iota(jnp.int32, (rows, LANE), 1)
        cache = {}

        def cell(part, a):
            key = (part, a % FFT_BLOCKS)
            if key not in cache:
                v = v_ref[part, :, blk(a % FFT_BLOCKS)]
                cache[key] = (v, pltpu.roll(v, 1, 1), pltpu.roll(v, LANE - 1, 1))
            return cache[key]

        for a in range(FFT_BLOCKS):
            lap = []
            here = []
            for part in range(2):
                v, from_left, from_right = cell(part, a)
                prev_left = cell(part, a - 1)[1]
                next_right = cell(part, a + 1)[2]
                above = jnp.where(row_id == 0, 0.0, pltpu.roll(v, 1, 0))
                below = jnp.where(row_id == rows - 1, 0.0, pltpu.roll(v, rows - 1, 0))
                left = jnp.where(lane_id == 0, prev_left, from_left)
                right = jnp.where(lane_id == LANE - 1, next_right, from_right)
                lap.append(above + below + left + right - 4.0 * v)
                here.append(v)
            gain = gn_ref[:, blk(a)]
            new_re = here[0] + (lap[0] * DAMPING - lap[1] * gain)
            new_im = here[1] + (lap[0] * gain + lap[1] * DAMPING)
            wout_ref[0, :, blk(a)] = new_re
            wout_ref[1, :, blk(a)] = new_im
            for j in range(strip_count):
                slot = (j - pos_ref[0] + strip_count) % strip_count
                img_ref[slot, k, :, blk(a)] = new_re[j * rows_here:(j + 1) * rows_here]
        return carry

    lax.fori_loop(0, steps, one_step, 0)


def fast_constants(line_len):
    outer = line_len // LANE
    b = np.arange(LANE)
    ang = 2.0 * np.pi * (np.outer(b, b) % LANE) / LANE
    cos_m, sin_m = (np.cos(ang), np.sin(ang))
    fwd = np.block([[cos_m, -sin_m], [sin_m, cos_m]])
    inv = np.block([[cos_m, sin_m], [-sin_m, cos_m]])

    def halves(m):
        hi = m.astype(ml_dtypes.bfloat16)
        lo = (m - hi.astype(np.float64)).astype(ml_dtypes.bfloat16)
        return (hi, lo)

    c = np.arange(outer)
    tw_ang = 2.0 * np.pi * np.outer(c, b) / line_len
    twiddle = np.stack([np.cos(tw_ang), np.sin(tw_ang)]).astype(np.float32)
    q = c[:, None] + outer * b[None, :]
    signed = np.where(q >= line_len // 2, q - line_len, q).astype(np.float32)
    kx_cd = signed * np.float32(2.0 * math.pi / line_len)
    return (halves(fwd), halves(inv), twiddle, kx_cd.astype(np.float32))


def run_section(wave, regions, table, mult, consts, strip_count, strip_no):
    (fhi, flo), (ghi, glo), twiddle, _ = consts
    rows, line_len = wave.shape[1], wave.shape[2]
    steps = regions.shape[0]
    table_len = table.shape[0] // (3 * steps)
    vmem = pl.BlockSpec(memory_space=pltpu.VMEM)
    flops = steps * (2 * 3 * 2 * (FFT_BLOCKS * rows) * 256 * 256 + 400 * rows * line_len)
    return pl.pallas_call(
        lambda *refs: section_kernel(*refs, table_len=table_len),
        out_shape=(
            jax.ShapeDtypeStruct(wave.shape, jnp.float32),
            jax.ShapeDtypeStruct((strip_count, steps, rows // strip_count, line_len), jnp.float32),
        ),
        in_specs=[pl.BlockSpec(memory_space=pltpu.SMEM)] + [vmem] * 8
        + [pl.BlockSpec(memory_space=pltpu.SMEM)],
        out_specs=(vmem, vmem),
        scratch_shapes=[
            pltpu.VMEM((FFT_BLOCKS * rows, 2 * LANE), jnp.float32),
            pltpu.VMEM((FFT_BLOCKS * rows, 2 * LANE), jnp.float32),
            pltpu.VMEM((2, rows, line_len), jnp.float32),
            pltpu.VMEM((rows, line_len), jnp.float32),
            pltpu.VMEM((rows, line_len), jnp.float32),
            pltpu.VMEM((rows, line_len), jnp.float32),
        ],
        cost_estimate=pl.CostEstimate(
            flops=flops, transcendentals=0, bytes_accessed=4 * rows * line_len * 6 * steps
        ),
    )(table, wave, regions, mult, jnp.asarray(twiddle), jnp.asarray(fhi), jnp.asarray(flo),
      jnp.asarray(ghi), jnp.asarray(glo), jnp.reshape(strip_no, (1,)).astype(jnp.int32))


def section_tables(omega, region_speed, fd_coeff, ref_region, kx_cd):
    inv_speed = 1.0 / region_speed
    ref_slow = inv_speed[ref_region]
    regions = region_speed.shape[0]
    padded = 1 << max(1, (regions - 1).bit_length())
    extra = padded - regions
    phase = omega * (inv_speed[None, :] - ref_slow[:, None])
    gain = jnp.broadcast_to(fd_coeff / omega, phase.shape)
    parts = [jnp.cos(phase), jnp.sin(phase), gain]
    if extra:
        parts = [jnp.concatenate([p, jnp.repeat(p[:, -1:], extra, axis=1)], axis=1) for p in parts]
    table = jnp.stack(parts, axis=1).reshape(-1)
    wave_ref = omega * ref_slow
    wave_ref = wave_ref[:, None, None]
    excess = wave_ref * wave_ref - kx_cd * kx_cd
    decay_line = jnp.exp(-jnp.sqrt(jnp.maximum(-excess, 0.0)))
    vertical = jnp.sqrt(jnp.maximum(excess, 0.0))
    mult = jnp.stack([decay_line * jnp.cos(vertical), decay_line * jnp.sin(vertical)], axis=1)
    return (table, mult)


def fast_fits(surface, region_index, region_speed):
    freq_count = surface.shape[1]
    rows = surface.shape[2] * lax.axis_size("strip")
    line_len = surface.shape[3]
    return (
        freq_count == lax.axis_size("strip")
        and line_len == FFT_BLOCKS * LANE
        and rows % ROW_CHUNK == 0
        and surface.shape[2] % ROW_CHUNK == 0
        and rows <= 64
        and region_speed.shape[0] <= 16
    )


def strip_pairs(depths, strip_count, shift):
    return [
        (d * strip_count + r, d * strip_count + (r + shift) % strip_count)
        for d in depths
        for r in range(strip_count)
    ]


def gather_rows(local, depths, strip_no, strip_count, row_axis):
    rows = local.shape[row_axis]
    shape = list(local.shape)
    shape[row_axis] = rows * strip_count
    full = jnp.zeros(shape, local.dtype)
    start = [0] * len(shape)
    start[row_axis] = strip_no * rows
    full = lax.dynamic_update_slice(full, local, start)
    for shift in range(1, strip_count):
        got = lax.ppermute(local, ("depth", "strip"), strip_pairs(depths, strip_count, shift))
        start = [0] * len(shape)
        start[row_axis] = ((strip_no - shift) % strip_count) * rows
        full = lax.dynamic_update_slice(full, got, start)
    return full


def gather_strips(piece_of, local, depths, strip_no, strip_count, rows_here):
    rows = rows_here * strip_count
    shape = (local.shape[0], rows, local.shape[2])
    full = lax.dynamic_update_slice(
        jnp.zeros(shape, jnp.float32), local, (0, strip_no * rows_here, 0)
    )
    for shift in range(1, strip_count):
        target = (strip_no + shift) % strip_count
        got = lax.ppermute(
            piece_of(target), ("depth", "strip"), strip_pairs(depths, strip_count, shift)
        )
        source = (strip_no - shift) % strip_count
        full = lax.dynamic_update_slice(full, got, (0, source * rows_here, 0))
    return full


def shards(surface, omegas, region_speed, fd_coeff, region_index, ref_region):
    if not fast_fits(surface, region_index, region_speed):
        return shards_general(surface, omegas, region_speed, fd_coeff, region_index, ref_region)
    line_len = surface.shape[3]
    rows_here = surface.shape[2]
    steps = region_index.shape[0]
    segment_no = lax.axis_index("depth")
    segment_count = lax.axis_size("depth")
    strip_no = lax.axis_index("strip")
    strip_count = lax.axis_size("strip")
    consts = fast_constants(line_len)
    region_f = region_index.astype(jnp.float32)
    early = [d for d in range(segment_count) if d != 1]

    def with_surface(target):
        return jnp.concatenate(
            [region_f, lax.dynamic_index_in_dim(surface, target, 1, keepdims=False)], axis=0
        )

    gathered = gather_strips(
        with_surface, with_surface(strip_no), early, strip_no, strip_count, rows_here
    )
    regions_a = gathered[:steps].astype(jnp.int32)
    wave = gathered[steps:]
    omega = lax.dynamic_index_in_dim(omegas, strip_no, 0, keepdims=False)
    table, mult = section_tables(omega, region_speed, fd_coeff, ref_region, jnp.asarray(consts[3]))
    image = jnp.zeros((strip_count, steps, rows_here, line_len), jnp.float32)
    regions_b = regions_a

    def sweep(regions):
        def live(wave, image):
            return run_section(wave, regions, table, mult, consts, strip_count, strip_no)

        return live

    def idle(wave, image):
        return (wave, image)

    def freq_sum(image, depths):
        parts = []
        for shift in range(1, strip_count):
            piece = image[shift]
            parts.append(
                lax.ppermute(piece, ("depth", "strip"), strip_pairs(depths, strip_count, shift))
            )
        return parts

    arrived = []
    for tick_no in range(segment_count):
        regions = regions_b if tick_no == 1 else regions_a
        if tick_no == 0:
            wave, image = sweep(regions)(wave, image)
        else:
            wave, image = lax.cond(segment_no == tick_no, sweep(regions), idle, wave, image)
        if tick_no + 1 < segment_count:
            wave = lax.ppermute(wave, "depth", [(tick_no, tick_no + 1)])
        if tick_no == 0 and segment_count > 1:
            held, _ = lax.optimization_barrier((region_f, image))
            regions_b = gather_strips(
                lambda target: held, held, [1], strip_no, strip_count, rows_here
            ).astype(jnp.int32)
        if tick_no == segment_count - 2:
            wave, image = lax.optimization_barrier((wave, image))
            arrived += freq_sum(image, range(segment_count - 1))
    arrived += freq_sum(image, [segment_count - 1])
    total = image[0]
    for piece in arrived:
        total = total + piece
    return total


def solution(mesh):
    in_specs = (
        P(None, "shots", "strip", None),
        P(),
        P(),
        P(),
        P("depth", "strip", None),
        P("depth"),
    )
    out_specs = P("depth", "strip", "shots")
    return jax.shard_map(shards, mesh=mesh, in_specs=in_specs, out_specs=out_specs, check_vma=False)
```

```python
import math

import ml_dtypes
import numpy as np
import jax
import jax.numpy as jnp
from jax import lax
from jax.experimental import pallas as pl
from jax.experimental.pallas import tpu as pltpu
from jax.sharding import PartitionSpec as P

DAMPING = 0.05
PRECISE = lax.Precision.HIGHEST


def padded_2(cells, sides, width):
    for axis, dim in sides:
        count = lax.axis_size(axis)
        ends = count - 1
        head = lax.slice_in_dim(cells, 0, width, axis=dim)
        tail = lax.slice_in_dim(cells, cells.shape[dim] - width, cells.shape[dim], axis=dim)
        cells = jnp.concatenate(
            [
                lax.ppermute(tail, axis, [(i, (i + 1) % count) for i in range(ends)]),
                cells,
                lax.ppermute(head, axis, [((i + 1) % count, i) for i in range(ends)]),
            ],
            axis=dim,
        )
    return cells


def from_behind(value, axis, steps):
    count = lax.axis_size(axis)
    first, last = (max(0, -steps), min(count, count - steps))
    return lax.ppermute(value, axis, [(source, source + steps) for source in range(first, last)])


def complex_scale(values, cosine, sine_part):
    return jnp.stack(
        [values[0] * cosine - values[1] * sine_part, values[0] * sine_part + values[1] * cosine]
    )


def angle_pair(numerator, period):
    angle_grid = numerator.astype(jnp.float32) * (2.0 * math.pi / period)
    return (jnp.cos(angle_grid), jnp.sin(angle_grid))


def block_matrix(cosine, sine_part, forward):
    sign_flip = 1.0 if forward else -1.0
    return jnp.stack(
        [jnp.stack([cosine, -sign_flip * sine_part]), jnp.stack([sign_flip * sine_part, cosine])]
    )


def build_tables(line_len):
    block_len = 128
    outer_len = line_len // block_len
    inner_idx = jnp.arange(block_len)
    outer_idx = jnp.arange(outer_len)
    cos_large, sin_large = angle_pair(
        inner_idx[:, None] * inner_idx[None, :] % block_len, block_len
    )
    cos_small, sin_small = angle_pair(
        outer_idx[:, None] * outer_idx[None, :] % outer_len, outer_len
    )
    cos_twist, sin_twist = angle_pair(outer_idx[:, None] * inner_idx[None, :], line_len)
    wave_index = outer_idx[:, None] + outer_len * inner_idx[None, :]
    signed = jnp.where(wave_index >= line_len // 2, wave_index - line_len, wave_index)
    kx_grid = signed.astype(jnp.float32) * (2.0 * math.pi / line_len)
    small_fwd = block_matrix(cos_small, sin_small, True)
    small_inv = block_matrix(cos_small, sin_small, False)
    large_fwd = block_matrix(cos_large, sin_large, True)
    large_inv = block_matrix(cos_large, sin_large, False)
    return (small_fwd, small_inv, large_fwd, large_inv, cos_twist, sin_twist, kx_grid)


def forward_line(wavefield, tables):
    small_fwd, small_inv, large_fwd, large_inv, cos_twist, sin_twist, kx_grid = tables
    row_count = wavefield.shape[1]
    pieces = wavefield.reshape(2, row_count, cos_twist.shape[0], cos_twist.shape[1])
    mixed_part = jnp.einsum("zrab,zwca->wrcb", pieces, small_fwd, precision=PRECISE)
    mixed_part = complex_scale(mixed_part, cos_twist, -sin_twist)
    return jnp.einsum("zrcb,zwbd->wrcd", mixed_part, large_fwd, precision=PRECISE)


def inverse_line(spectrum, tables):
    small_fwd, small_inv, large_fwd, large_inv, cos_twist, sin_twist, kx_grid = tables
    row_count = spectrum.shape[1]
    line_len = cos_twist.shape[0] * cos_twist.shape[1]
    mixed_part = jnp.einsum("zrcd,zwdb->wrcb", spectrum, large_inv, precision=PRECISE)
    mixed_part = complex_scale(mixed_part, cos_twist, sin_twist)
    pieces = jnp.einsum("zrcb,zwca->wrab", mixed_part, small_inv, precision=PRECISE)
    return pieces.reshape(2, row_count, line_len) * (1.0 / line_len)


def lookup(regions, entries):
    picked = jnp.zeros(regions.shape, jnp.float32)
    for region_no in range(entries.shape[0]):
        picked = picked + jnp.where(regions == region_no, entries[region_no], 0.0)
    return picked


def depth_step(wavefield, omega_now, slow_cells, coef_cells, ref_slow, tables, pad_rows):
    kx_grid = tables[6]
    wave_ref = omega_now * ref_slow
    excess = wave_ref * wave_ref - kx_grid * kx_grid
    decay_line = jnp.exp(-jnp.sqrt(jnp.maximum(-excess, 0.0)))
    vertical = jnp.sqrt(jnp.maximum(excess, 0.0))
    spectrum = complex_scale(
        forward_line(wavefield, tables),
        decay_line * jnp.cos(vertical),
        decay_line * jnp.sin(vertical),
    )
    wavefield = inverse_line(spectrum, tables)
    phase_cell = omega_now * (slow_cells - ref_slow)
    wavefield = complex_scale(wavefield, jnp.cos(phase_cell), jnp.sin(phase_cell))
    padded = pad_rows(wavefield)
    laplace = (
        padded[:, :-2]
        + padded[:, 2:]
        + jnp.roll(wavefield, 1, 2)
        + jnp.roll(wavefield, -1, 2)
        - 4.0 * wavefield
    )
    return wavefield + complex_scale(laplace, DAMPING, coef_cells / omega_now)


def march(wavefield, omega_now, slow_block, coef_block, ref_block, tables, pad_rows):
    traces = []
    for step_no in range(slow_block.shape[0]):
        wavefield = depth_step(
            wavefield,
            omega_now,
            slow_block[step_no],
            coef_block[step_no],
            ref_block[step_no],
            tables,
            pad_rows,
        )
        traces.append(wavefield[0])
    return (wavefield, jnp.stack(traces))


def shards_general(surface, omegas, region_speed, fd_coeff, region_index, ref_region):
    line_len = surface.shape[3]
    rows_here = surface.shape[2]
    freq_count = surface.shape[1]
    step_count = region_index.shape[0]
    tables = build_tables(line_len)
    inv_speed = 1.0 / region_speed
    segment_no = lax.axis_index("depth")
    segment_count = lax.axis_size("depth")

    def pad_near(values):
        return padded_2(values, (("strip", 1),), 1)

    slow_cells = lookup(region_index, inv_speed)
    coef_cells = lookup(region_index, fd_coeff)
    ref_cells = lookup(ref_region, inv_speed)
    freq_index = jnp.arange(freq_count)
    image_out = jnp.zeros((step_count, rows_here, line_len), jnp.float32)
    arriving = jnp.zeros((2, rows_here, line_len), jnp.float32)
    tick_count = freq_count + segment_count - 1
    for tick_no in range(tick_count):
        batch_no = tick_no - segment_no
        is_live = (batch_no >= 0) & (batch_no < freq_count)
        clipped = jnp.clip(batch_no, 0, freq_count - 1)
        picked = lax.dynamic_index_in_dim(surface, clipped, 1, keepdims=False)
        entering = jnp.where(segment_no == 0, picked, arriving)
        omega_now = jnp.sum(jnp.where(freq_index == clipped, omegas, 0.0))
        leaving, traces = march(
            entering, omega_now, slow_cells, coef_cells, ref_cells, tables, pad_near
        )
        image_out = image_out + jnp.where(is_live, traces, 0.0)
        if tick_no + 1 < tick_count:
            arriving = from_behind(leaving, "depth", 1)
    return image_out


LANE = 128
FFT_BLOCKS = 16
ROW_CHUNK = 8


def fft4(x0, x1, x2, x3, sign):
    s0 = (x0[0] + x2[0], x0[1] + x2[1])
    d0 = (x0[0] - x2[0], x0[1] - x2[1])
    s1 = (x1[0] + x3[0], x1[1] + x3[1])
    d1 = (x1[0] - x3[0], x1[1] - x3[1])
    if sign < 0:
        wd = (d1[1], -d1[0])
    else:
        wd = (-d1[1], d1[0])
    return (
        (s0[0] + s1[0], s0[1] + s1[1]),
        (d0[0] + wd[0], d0[1] + wd[1]),
        (s0[0] - s1[0], s0[1] - s1[1]),
        (d0[0] - wd[0], d0[1] - wd[1]),
    )


def turn_const(value, power, sign):
    if power == 4:
        return (-value[1], value[0]) if sign > 0 else (value[1], -value[0])
    angle = sign * 2.0 * math.pi * power / 16.0
    cr, ci = (math.cos(angle), math.sin(angle))
    return (value[0] * cr - value[1] * ci, value[0] * ci + value[1] * cr)


def fft16(parts, sign):
    mid = [[None] * 4 for _ in range(4)]
    for a0 in range(4):
        ys = fft4(parts[a0], parts[4 + a0], parts[8 + a0], parts[12 + a0], sign)
        for c0 in range(4):
            power = a0 * c0
            mid[a0][c0] = ys[c0] if power == 0 else turn_const(ys[c0], power, sign)
    out = [None] * 16
    for c0 in range(4):
        zs = fft4(mid[0][c0], mid[1][c0], mid[2][c0], mid[3][c0], sign)
        for c1 in range(4):
            out[c0 + 4 * c1] = zs[c1]
    return out


def pick(regions, values):
    level = list(values)
    bit = 1
    while len(level) > 1:
        chosen = (regions & bit) != 0
        level = [jnp.where(chosen, level[i + 1], level[i]) for i in range(0, len(level), 2)]
        bit *= 2
    return jnp.broadcast_to(level[0], regions.shape)


def pick_bits(bits, values):
    level = list(values)
    for chosen in bits:
        level = [jnp.where(chosen, level[i + 1], level[i]) for i in range(0, len(level), 2)]
    return jnp.broadcast_to(level[0], bits[0].shape)


def split_dot(values, hi_ref, lo_ref):
    high = values.astype(jnp.bfloat16)
    low = (values - high.astype(jnp.float32)).astype(jnp.bfloat16)
    main = jnp.dot(high, hi_ref[...], preferred_element_type=jnp.float32)
    fix = jnp.dot(high, lo_ref[...], preferred_element_type=jnp.float32) + jnp.dot(
        low, hi_ref[:, :], preferred_element_type=jnp.float32
    )
    return main + fix


def section_kernel(
    tab_ref, w_ref, rid_ref, mult_ref, tw_ref, fhi_ref, flo_ref, ghi_ref, glo_ref, pos_ref,
    wout_ref, img_ref, a_ref, y_ref, v_ref, cs_ref, sn_ref, gn_ref, *, table_len
):
    rows = w_ref.shape[1]
    line_len = w_ref.shape[2]
    steps = rid_ref.shape[0]
    strip_count, rows_here = img_ref.shape[0], img_ref.shape[2]
    chunks = rows // ROW_CHUNK
    inv_len = 1.0 / line_len
    wout_ref[...] = w_ref[...]

    def blk(a):
        return slice(a * LANE, (a + 1) * LANE)

    def one_step(k, carry):
        base = k * (3 * table_len)
        cos_t = [tab_ref[base + g] for g in range(table_len)]
        sin_t = [tab_ref[base + table_len + g] for g in range(table_len)]
        gain_t = [tab_ref[base + 2 * table_len + g] for g in range(table_len)]

        def forward_chunk(i, c):
            y0 = pl.multiple_of(i * ROW_CHUNK, ROW_CHUNK)
            parts = [
                (wout_ref[0, pl.ds(y0, ROW_CHUNK), blk(a)], wout_ref[1, pl.ds(y0, ROW_CHUNK), blk(a)])
                for a in range(FFT_BLOCKS)
            ]
            spec = fft16(parts, -1)
            for cc in range(FFT_BLOCKS):
                tc = tw_ref[0, cc:cc + 1, :]
                ts = tw_ref[1, cc:cc + 1, :]
                xr, xi = spec[cc]
                a_ref[pl.ds(cc * rows + y0, ROW_CHUNK), 0:LANE] = xr * tc + xi * ts
                a_ref[pl.ds(cc * rows + y0, ROW_CHUNK), LANE:2 * LANE] = xi * tc - xr * ts
            return c

        lax.fori_loop(0, chunks, forward_chunk, 0, unroll=True)
        spectrum = split_dot(a_ref[...], fhi_ref, flo_ref)
        for a in range(FFT_BLOCKS):
            regions = rid_ref[k, :, blk(a)]
            bits = [(regions & (1 << b)) != 0 for b in range(max(1, (table_len - 1).bit_length()))]
            cs_ref[:, blk(a)] = pick_bits(bits, cos_t)
            sn_ref[:, blk(a)] = pick_bits(bits, sin_t)
            gn_ref[:, blk(a)] = pick_bits(bits, gain_t)
        y_ref[...] = spectrum
        for cc in range(FFT_BLOCKS):
            band = slice(cc * rows, (cc + 1) * rows)
            yr = y_ref[band, 0:LANE]
            yi = y_ref[band, LANE:2 * LANE]
            mr = mult_ref[k, 0, cc:cc + 1, :]
            mi = mult_ref[k, 1, cc:cc + 1, :]
            a_ref[band, 0:LANE] = yr * mr - yi * mi
            a_ref[band, LANE:2 * LANE] = yr * mi + yi * mr
        y_ref[...] = split_dot(a_ref[...], ghi_ref, glo_ref)

        def inverse_chunk(i, c):
            y0 = pl.multiple_of(i * ROW_CHUNK, ROW_CHUNK)
            parts = []
            for cc in range(FFT_BLOCKS):
                zr = y_ref[pl.ds(cc * rows + y0, ROW_CHUNK), 0:LANE]
                zi = y_ref[pl.ds(cc * rows + y0, ROW_CHUNK), LANE:2 * LANE]
                tc = tw_ref[0, cc:cc + 1, :]
                ts = tw_ref[1, cc:cc + 1, :]
                parts.append((zr * tc - zi * ts, zr * ts + zi * tc))
            back = fft16(parts, 1)
            for a in range(FFT_BLOCKS):
                ur = back[a][0] * inv_len
                ui = back[a][1] * inv_len
                cs = cs_ref[pl.ds(y0, ROW_CHUNK), blk(a)]
                sn = sn_ref[pl.ds(y0, ROW_CHUNK), blk(a)]
                v_ref[0, pl.ds(y0, ROW_CHUNK), blk(a)] = ur * cs - ui * sn
                v_ref[1, pl.ds(y0, ROW_CHUNK), blk(a)] = ur * sn + ui * cs
            return c

        lax.fori_loop(0, chunks, inverse_chunk, 0, unroll=True)
        row_id = lax.broadcasted_iota(jnp.int32, (rows, LANE), 0)
        lane_id = lax.broadcasted_iota(jnp.int32, (rows, LANE), 1)
        cache = {}

        def cell(part, a):
            key = (part, a % FFT_BLOCKS)
            if key not in cache:
                v = v_ref[part, :, blk(a % FFT_BLOCKS)]
                cache[key] = (v, pltpu.roll(v, 1, 1), pltpu.roll(v, LANE - 1, 1))
            return cache[key]

        for a in range(FFT_BLOCKS):
            lap = []
            here = []
            for part in range(2):
                v, from_left, from_right = cell(part, a)
                prev_left = cell(part, a - 1)[1]
                next_right = cell(part, a + 1)[2]
                above = jnp.where(row_id == 0, 0.0, pltpu.roll(v, 1, 0))
                below = jnp.where(row_id == rows - 1, 0.0, pltpu.roll(v, rows - 1, 0))
                left = jnp.where(lane_id == 0, prev_left, from_left)
                right = jnp.where(lane_id == LANE - 1, next_right, from_right)
                lap.append(above + below + left + right - 4.0 * v)
                here.append(v)
            gain = gn_ref[:, blk(a)]
            new_re = here[0] + (lap[0] * DAMPING - lap[1] * gain)
            new_im = here[1] + (lap[0] * gain + lap[1] * DAMPING)
            wout_ref[0, :, blk(a)] = new_re
            wout_ref[1, :, blk(a)] = new_im
            for j in range(strip_count):
                slot = (j - pos_ref[0] + strip_count) % strip_count
                img_ref[slot, k, :, blk(a)] = new_re[j * rows_here:(j + 1) * rows_here]
        return carry

    lax.fori_loop(0, steps, one_step, 0, unroll=True)


def fast_constants(line_len):
    outer = line_len // LANE
    b = np.arange(LANE)
    ang = 2.0 * np.pi * (np.outer(b, b) % LANE) / LANE
    cos_m, sin_m = (np.cos(ang), np.sin(ang))
    fwd = np.block([[cos_m, -sin_m], [sin_m, cos_m]])
    inv = np.block([[cos_m, sin_m], [-sin_m, cos_m]])

    def halves(m):
        hi = m.astype(ml_dtypes.bfloat16)
        lo = (m - hi.astype(np.float64)).astype(ml_dtypes.bfloat16)
        return (hi, lo)

    c = np.arange(outer)
    tw_ang = 2.0 * np.pi * np.outer(c, b) / line_len
    twiddle = np.stack([np.cos(tw_ang), np.sin(tw_ang)]).astype(np.float32)
    q = c[:, None] + outer * b[None, :]
    signed = np.where(q >= line_len // 2, q - line_len, q).astype(np.float32)
    kx_cd = signed * np.float32(2.0 * math.pi / line_len)
    return (halves(fwd), halves(inv), twiddle, kx_cd.astype(np.float32))


def run_section(wave, regions, table, mult, consts, strip_count, strip_no):
    (fhi, flo), (ghi, glo), twiddle, _ = consts
    rows, line_len = wave.shape[1], wave.shape[2]
    steps = regions.shape[0]
    table_len = table.shape[0] // (3 * steps)
    vmem = pl.BlockSpec(memory_space=pltpu.VMEM)
    flops = steps * (2 * 3 * 2 * (FFT_BLOCKS * rows) * 256 * 256 + 400 * rows * line_len)
    return pl.pallas_call(
        lambda *refs: section_kernel(*refs, table_len=table_len),
        out_shape=(
            jax.ShapeDtypeStruct(wave.shape, jnp.float32),
            jax.ShapeDtypeStruct((strip_count, steps, rows // strip_count, line_len), jnp.float32),
        ),
        in_specs=[pl.BlockSpec(memory_space=pltpu.SMEM)] + [vmem] * 8
        + [pl.BlockSpec(memory_space=pltpu.SMEM)],
        out_specs=(vmem, vmem),
        scratch_shapes=[
            pltpu.VMEM((FFT_BLOCKS * rows, 2 * LANE), jnp.float32),
            pltpu.VMEM((FFT_BLOCKS * rows, 2 * LANE), jnp.float32),
            pltpu.VMEM((2, rows, line_len), jnp.float32),
            pltpu.VMEM((rows, line_len), jnp.float32),
            pltpu.VMEM((rows, line_len), jnp.float32),
            pltpu.VMEM((rows, line_len), jnp.float32),
        ],
        cost_estimate=pl.CostEstimate(
            flops=flops, transcendentals=0, bytes_accessed=4 * rows * line_len * 6 * steps
        ),
    )(table, wave, regions, mult, jnp.asarray(twiddle), jnp.asarray(fhi), jnp.asarray(flo),
      jnp.asarray(ghi), jnp.asarray(glo), jnp.reshape(strip_no, (1,)).astype(jnp.int32))


def section_tables(omega, region_speed, fd_coeff, ref_region, kx_cd):
    inv_speed = 1.0 / region_speed
    ref_slow = inv_speed[ref_region]
    regions = region_speed.shape[0]
    padded = 1 << max(1, (regions - 1).bit_length())
    extra = padded - regions
    phase = omega * (inv_speed[None, :] - ref_slow[:, None])
    gain = jnp.broadcast_to(fd_coeff / omega, phase.shape)
    parts = [jnp.cos(phase), jnp.sin(phase), gain]
    if extra:
        parts = [jnp.concatenate([p, jnp.repeat(p[:, -1:], extra, axis=1)], axis=1) for p in parts]
    table = jnp.stack(parts, axis=1).reshape(-1)
    wave_ref = omega * ref_slow
    wave_ref = wave_ref[:, None, None]
    excess = wave_ref * wave_ref - kx_cd * kx_cd
    decay_line = jnp.exp(-jnp.sqrt(jnp.maximum(-excess, 0.0)))
    vertical = jnp.sqrt(jnp.maximum(excess, 0.0))
    mult = jnp.stack([decay_line * jnp.cos(vertical), decay_line * jnp.sin(vertical)], axis=1)
    return (table, mult)


def fast_fits(surface, region_index, region_speed):
    freq_count = surface.shape[1]
    rows = surface.shape[2] * lax.axis_size("strip")
    line_len = surface.shape[3]
    return (
        freq_count == lax.axis_size("strip")
        and line_len == FFT_BLOCKS * LANE
        and rows % ROW_CHUNK == 0
        and surface.shape[2] % ROW_CHUNK == 0
        and rows <= 64
        and region_speed.shape[0] <= 16
    )


def strip_pairs(depths, strip_count, shift):
    return [
        (d * strip_count + r, d * strip_count + (r + shift) % strip_count)
        for d in depths
        for r in range(strip_count)
    ]


def gather_rows(local, depths, strip_no, strip_count, row_axis):
    rows = local.shape[row_axis]
    shape = list(local.shape)
    shape[row_axis] = rows * strip_count
    full = jnp.zeros(shape, local.dtype)
    start = [0] * len(shape)
    start[row_axis] = strip_no * rows
    full = lax.dynamic_update_slice(full, local, start)
    for shift in range(1, strip_count):
        got = lax.ppermute(local, ("depth", "strip"), strip_pairs(depths, strip_count, shift))
        start = [0] * len(shape)
        start[row_axis] = ((strip_no - shift) % strip_count) * rows
        full = lax.dynamic_update_slice(full, got, start)
    return full


def gather_strips(piece_of, local, depths, strip_no, strip_count, rows_here):
    rows = rows_here * strip_count
    shape = (local.shape[0], rows, local.shape[2])
    full = lax.dynamic_update_slice(
        jnp.zeros(shape, jnp.float32), local, (0, strip_no * rows_here, 0)
    )
    for shift in range(1, strip_count):
        target = (strip_no + shift) % strip_count
        got = lax.ppermute(
            piece_of(target), ("depth", "strip"), strip_pairs(depths, strip_count, shift)
        )
        source = (strip_no - shift) % strip_count
        full = lax.dynamic_update_slice(full, got, (0, source * rows_here, 0))
    return full


def shards(surface, omegas, region_speed, fd_coeff, region_index, ref_region):
    if not fast_fits(surface, region_index, region_speed):
        return shards_general(surface, omegas, region_speed, fd_coeff, region_index, ref_region)
    line_len = surface.shape[3]
    rows_here = surface.shape[2]
    steps = region_index.shape[0]
    segment_no = lax.axis_index("depth")
    segment_count = lax.axis_size("depth")
    strip_no = lax.axis_index("strip")
    strip_count = lax.axis_size("strip")
    consts = fast_constants(line_len)
    region_f = region_index.astype(jnp.float32)
    early = [d for d in range(segment_count) if d != 1]

    def with_surface(target):
        return jnp.concatenate(
            [region_f, lax.dynamic_index_in_dim(surface, target, 1, keepdims=False)], axis=0
        )

    gathered = gather_strips(
        with_surface, with_surface(strip_no), early, strip_no, strip_count, rows_here
    )
    regions_a = gathered[:steps].astype(jnp.int32)
    wave = gathered[steps:]
    omega = lax.dynamic_index_in_dim(omegas, strip_no, 0, keepdims=False)
    table, mult = section_tables(omega, region_speed, fd_coeff, ref_region, jnp.asarray(consts[3]))
    image = jnp.zeros((strip_count, steps, rows_here, line_len), jnp.float32)
    regions_b = regions_a

    def sweep(regions):
        def live(wave, image):
            return run_section(wave, regions, table, mult, consts, strip_count, strip_no)

        return live

    def idle(wave, image):
        return (wave, image)

    def freq_sum(image, depths):
        parts = []
        for shift in range(1, strip_count):
            piece = image[shift]
            parts.append(
                lax.ppermute(piece, ("depth", "strip"), strip_pairs(depths, strip_count, shift))
            )
        return parts

    arrived = []
    for tick_no in range(segment_count):
        regions = regions_b if tick_no == 1 else regions_a
        if tick_no == 0:
            wave, image = sweep(regions)(wave, image)
        else:
            wave, image = lax.cond(segment_no == tick_no, sweep(regions), idle, wave, image)
        if tick_no + 1 < segment_count:
            wave = lax.ppermute(wave, "depth", [(tick_no, tick_no + 1)])
        if tick_no == 0 and segment_count > 1:
            held, _ = lax.optimization_barrier((region_f, image))
            regions_b = gather_strips(
                lambda target: held, held, [1], strip_no, strip_count, rows_here
            ).astype(jnp.int32)
        if tick_no == segment_count - 2:
            wave, image = lax.optimization_barrier((wave, image))
            arrived += freq_sum(image, range(segment_count - 1))
    arrived += freq_sum(image, [segment_count - 1])
    total = image[0]
    for piece in arrived:
        total = total + piece
    return total


def solution(mesh):
    in_specs = (
        P(None, "shots", "strip", None),
        P(),
        P(),
        P(),
        P("depth", "strip", None),
        P("depth"),
    )
    out_specs = P("depth", "strip", "shots")
    return jax.shard_map(shards, mesh=mesh, in_specs=in_specs, out_specs=out_specs, check_vma=False)
```

```python
import math

import ml_dtypes
import numpy as np
import jax
import jax.numpy as jnp
from jax import lax
from jax.experimental import pallas as pl
from jax.experimental.pallas import tpu as pltpu
from jax.sharding import PartitionSpec as P

DAMPING = 0.05
PRECISE = lax.Precision.HIGHEST


def padded_2(cells, sides, width):
    for axis, dim in sides:
        count = lax.axis_size(axis)
        ends = count - 1
        head = lax.slice_in_dim(cells, 0, width, axis=dim)
        tail = lax.slice_in_dim(cells, cells.shape[dim] - width, cells.shape[dim], axis=dim)
        cells = jnp.concatenate(
            [
                lax.ppermute(tail, axis, [(i, (i + 1) % count) for i in range(ends)]),
                cells,
                lax.ppermute(head, axis, [((i + 1) % count, i) for i in range(ends)]),
            ],
            axis=dim,
        )
    return cells


def from_behind(value, axis, steps):
    count = lax.axis_size(axis)
    first, last = (max(0, -steps), min(count, count - steps))
    return lax.ppermute(value, axis, [(source, source + steps) for source in range(first, last)])


def complex_scale(values, cosine, sine_part):
    return jnp.stack(
        [values[0] * cosine - values[1] * sine_part, values[0] * sine_part + values[1] * cosine]
    )


def angle_pair(numerator, period):
    angle_grid = numerator.astype(jnp.float32) * (2.0 * math.pi / period)
    return (jnp.cos(angle_grid), jnp.sin(angle_grid))


def block_matrix(cosine, sine_part, forward):
    sign_flip = 1.0 if forward else -1.0
    return jnp.stack(
        [jnp.stack([cosine, -sign_flip * sine_part]), jnp.stack([sign_flip * sine_part, cosine])]
    )


def build_tables(line_len):
    block_len = 128
    outer_len = line_len // block_len
    inner_idx = jnp.arange(block_len)
    outer_idx = jnp.arange(outer_len)
    cos_large, sin_large = angle_pair(
        inner_idx[:, None] * inner_idx[None, :] % block_len, block_len
    )
    cos_small, sin_small = angle_pair(
        outer_idx[:, None] * outer_idx[None, :] % outer_len, outer_len
    )
    cos_twist, sin_twist = angle_pair(outer_idx[:, None] * inner_idx[None, :], line_len)
    wave_index = outer_idx[:, None] + outer_len * inner_idx[None, :]
    signed = jnp.where(wave_index >= line_len // 2, wave_index - line_len, wave_index)
    kx_grid = signed.astype(jnp.float32) * (2.0 * math.pi / line_len)
    small_fwd = block_matrix(cos_small, sin_small, True)
    small_inv = block_matrix(cos_small, sin_small, False)
    large_fwd = block_matrix(cos_large, sin_large, True)
    large_inv = block_matrix(cos_large, sin_large, False)
    return (small_fwd, small_inv, large_fwd, large_inv, cos_twist, sin_twist, kx_grid)


def forward_line(wavefield, tables):
    small_fwd, small_inv, large_fwd, large_inv, cos_twist, sin_twist, kx_grid = tables
    row_count = wavefield.shape[1]
    pieces = wavefield.reshape(2, row_count, cos_twist.shape[0], cos_twist.shape[1])
    mixed_part = jnp.einsum("zrab,zwca->wrcb", pieces, small_fwd, precision=PRECISE)
    mixed_part = complex_scale(mixed_part, cos_twist, -sin_twist)
    return jnp.einsum("zrcb,zwbd->wrcd", mixed_part, large_fwd, precision=PRECISE)


def inverse_line(spectrum, tables):
    small_fwd, small_inv, large_fwd, large_inv, cos_twist, sin_twist, kx_grid = tables
    row_count = spectrum.shape[1]
    line_len = cos_twist.shape[0] * cos_twist.shape[1]
    mixed_part = jnp.einsum("zrcd,zwdb->wrcb", spectrum, large_inv, precision=PRECISE)
    mixed_part = complex_scale(mixed_part, cos_twist, sin_twist)
    pieces = jnp.einsum("zrcb,zwca->wrab", mixed_part, small_inv, precision=PRECISE)
    return pieces.reshape(2, row_count, line_len) * (1.0 / line_len)


def lookup(regions, entries):
    picked = jnp.zeros(regions.shape, jnp.float32)
    for region_no in range(entries.shape[0]):
        picked = picked + jnp.where(regions == region_no, entries[region_no], 0.0)
    return picked


def depth_step(wavefield, omega_now, slow_cells, coef_cells, ref_slow, tables, pad_rows):
    kx_grid = tables[6]
    wave_ref = omega_now * ref_slow
    excess = wave_ref * wave_ref - kx_grid * kx_grid
    decay_line = jnp.exp(-jnp.sqrt(jnp.maximum(-excess, 0.0)))
    vertical = jnp.sqrt(jnp.maximum(excess, 0.0))
    spectrum = complex_scale(
        forward_line(wavefield, tables),
        decay_line * jnp.cos(vertical),
        decay_line * jnp.sin(vertical),
    )
    wavefield = inverse_line(spectrum, tables)
    phase_cell = omega_now * (slow_cells - ref_slow)
    wavefield = complex_scale(wavefield, jnp.cos(phase_cell), jnp.sin(phase_cell))
    padded = pad_rows(wavefield)
    laplace = (
        padded[:, :-2]
        + padded[:, 2:]
        + jnp.roll(wavefield, 1, 2)
        + jnp.roll(wavefield, -1, 2)
        - 4.0 * wavefield
    )
    return wavefield + complex_scale(laplace, DAMPING, coef_cells / omega_now)


def march(wavefield, omega_now, slow_block, coef_block, ref_block, tables, pad_rows):
    traces = []
    for step_no in range(slow_block.shape[0]):
        wavefield = depth_step(
            wavefield,
            omega_now,
            slow_block[step_no],
            coef_block[step_no],
            ref_block[step_no],
            tables,
            pad_rows,
        )
        traces.append(wavefield[0])
    return (wavefield, jnp.stack(traces))


def shards_general(surface, omegas, region_speed, fd_coeff, region_index, ref_region):
    line_len = surface.shape[3]
    rows_here = surface.shape[2]
    freq_count = surface.shape[1]
    step_count = region_index.shape[0]
    tables = build_tables(line_len)
    inv_speed = 1.0 / region_speed
    segment_no = lax.axis_index("depth")
    segment_count = lax.axis_size("depth")

    def pad_near(values):
        return padded_2(values, (("strip", 1),), 1)

    slow_cells = lookup(region_index, inv_speed)
    coef_cells = lookup(region_index, fd_coeff)
    ref_cells = lookup(ref_region, inv_speed)
    freq_index = jnp.arange(freq_count)
    image_out = jnp.zeros((step_count, rows_here, line_len), jnp.float32)
    arriving = jnp.zeros((2, rows_here, line_len), jnp.float32)
    tick_count = freq_count + segment_count - 1
    for tick_no in range(tick_count):
        batch_no = tick_no - segment_no
        is_live = (batch_no >= 0) & (batch_no < freq_count)
        clipped = jnp.clip(batch_no, 0, freq_count - 1)
        picked = lax.dynamic_index_in_dim(surface, clipped, 1, keepdims=False)
        entering = jnp.where(segment_no == 0, picked, arriving)
        omega_now = jnp.sum(jnp.where(freq_index == clipped, omegas, 0.0))
        leaving, traces = march(
            entering, omega_now, slow_cells, coef_cells, ref_cells, tables, pad_near
        )
        image_out = image_out + jnp.where(is_live, traces, 0.0)
        if tick_no + 1 < tick_count:
            arriving = from_behind(leaving, "depth", 1)
    return image_out


LANE = 128
FFT_BLOCKS = 16
ROW_CHUNK = 8


def fft4(x0, x1, x2, x3, sign):
    s0 = (x0[0] + x2[0], x0[1] + x2[1])
    d0 = (x0[0] - x2[0], x0[1] - x2[1])
    s1 = (x1[0] + x3[0], x1[1] + x3[1])
    d1 = (x1[0] - x3[0], x1[1] - x3[1])
    if sign < 0:
        wd = (d1[1], -d1[0])
    else:
        wd = (-d1[1], d1[0])
    return (
        (s0[0] + s1[0], s0[1] + s1[1]),
        (d0[0] + wd[0], d0[1] + wd[1]),
        (s0[0] - s1[0], s0[1] - s1[1]),
        (d0[0] - wd[0], d0[1] - wd[1]),
    )


def turn_const(value, power, sign):
    if power == 4:
        return (-value[1], value[0]) if sign > 0 else (value[1], -value[0])
    angle = sign * 2.0 * math.pi * power / 16.0
    cr, ci = (math.cos(angle), math.sin(angle))
    return (value[0] * cr - value[1] * ci, value[0] * ci + value[1] * cr)


def fft16(parts, sign):
    mid = [[None] * 4 for _ in range(4)]
    for a0 in range(4):
        ys = fft4(parts[a0], parts[4 + a0], parts[8 + a0], parts[12 + a0], sign)
        for c0 in range(4):
            power = a0 * c0
            mid[a0][c0] = ys[c0] if power == 0 else turn_const(ys[c0], power, sign)
    out = [None] * 16
    for c0 in range(4):
        zs = fft4(mid[0][c0], mid[1][c0], mid[2][c0], mid[3][c0], sign)
        for c1 in range(4):
            out[c0 + 4 * c1] = zs[c1]
    return out


def pick(regions, values):
    level = list(values)
    bit = 1
    while len(level) > 1:
        chosen = (regions & bit) != 0
        level = [jnp.where(chosen, level[i + 1], level[i]) for i in range(0, len(level), 2)]
        bit *= 2
    return jnp.broadcast_to(level[0], regions.shape)


def pick_bits(bits, values):
    level = list(values)
    for chosen in bits:
        level = [jnp.where(chosen, level[i + 1], level[i]) for i in range(0, len(level), 2)]
    return jnp.broadcast_to(level[0], bits[0].shape)


def split_dot(values, hi_ref, lo_ref):
    high = values.astype(jnp.bfloat16)
    low = (values - high.astype(jnp.float32)).astype(jnp.bfloat16)
    main = jnp.dot(high, hi_ref[...], preferred_element_type=jnp.float32)
    fix = jnp.dot(high, lo_ref[...], preferred_element_type=jnp.float32) + jnp.dot(
        low, hi_ref[:, :], preferred_element_type=jnp.float32
    )
    return main + fix


def section_kernel(
    tab_ref, w_ref, rid_ref, mult_ref, tw_ref, fhi_ref, flo_ref, ghi_ref, glo_ref, pos_ref,
    wout_ref, img_ref, a_ref, y_ref, v_ref, cs_ref, sn_ref, gn_ref, ahi_ref, alo_ref, *, table_len
):
    rows = w_ref.shape[1]
    line_len = w_ref.shape[2]
    steps = rid_ref.shape[0]
    strip_count, rows_here = img_ref.shape[0], img_ref.shape[2]
    chunks = rows // ROW_CHUNK
    inv_len = 1.0 / line_len
    wout_ref[...] = w_ref[...]

    def blk(a):
        return slice(a * LANE, (a + 1) * LANE)

    def one_step(k, carry):
        base = k * (3 * table_len)
        cos_t = [tab_ref[base + g] for g in range(table_len)]
        sin_t = [tab_ref[base + table_len + g] for g in range(table_len)]
        gain_t = [tab_ref[base + 2 * table_len + g] for g in range(table_len)]

        def forward_chunk(i, c):
            y0 = pl.multiple_of(i * ROW_CHUNK, ROW_CHUNK)
            parts = [
                (wout_ref[0, pl.ds(y0, ROW_CHUNK), blk(a)], wout_ref[1, pl.ds(y0, ROW_CHUNK), blk(a)])
                for a in range(FFT_BLOCKS)
            ]
            spec = fft16(parts, -1)
            for cc in range(FFT_BLOCKS):
                tc = tw_ref[0, cc:cc + 1, :]
                ts = tw_ref[1, cc:cc + 1, :]
                xr, xi = spec[cc]
                a_ref[pl.ds(cc * rows + y0, ROW_CHUNK), 0:LANE] = xr * tc + xi * ts
                a_ref[pl.ds(cc * rows + y0, ROW_CHUNK), LANE:2 * LANE] = xi * tc - xr * ts
            return c

        lax.fori_loop(0, chunks, forward_chunk, 0, unroll=True)
        spectrum = split_dot(a_ref[...], fhi_ref, flo_ref)
        for a in range(FFT_BLOCKS):
            regions = rid_ref[k, :, blk(a)]
            bits = [(regions & (1 << b)) != 0 for b in range(max(1, (table_len - 1).bit_length()))]
            cs_ref[:, blk(a)] = pick_bits(bits, cos_t)
            sn_ref[:, blk(a)] = pick_bits(bits, sin_t)
            gn_ref[:, blk(a)] = pick_bits(bits, gain_t)
        y_ref[...] = spectrum
        for cc in range(FFT_BLOCKS):
            band = slice(cc * rows, (cc + 1) * rows)
            yr = y_ref[band, 0:LANE]
            yi = y_ref[band, LANE:2 * LANE]
            mr = mult_ref[k, 0, cc:cc + 1, :]
            mi = mult_ref[k, 1, cc:cc + 1, :]
            for lanes, val in ((slice(0, LANE), yr * mr - yi * mi), (slice(LANE, 2 * LANE), yr * mi + yi * mr)):
                high = val.astype(jnp.bfloat16)
                ahi_ref[band, lanes] = high
                alo_ref[band, lanes] = (val - high.astype(jnp.float32)).astype(jnp.bfloat16)
        high = ahi_ref[...]
        main = jnp.dot(high, ghi_ref[...], preferred_element_type=jnp.float32)
        fix = jnp.dot(high, glo_ref[...], preferred_element_type=jnp.float32) + jnp.dot(
            alo_ref[...], ghi_ref[:, :], preferred_element_type=jnp.float32
        )
        y_ref[...] = main + fix

        def inverse_chunk(i, c):
            y0 = pl.multiple_of(i * ROW_CHUNK, ROW_CHUNK)
            parts = []
            for cc in range(FFT_BLOCKS):
                zr = y_ref[pl.ds(cc * rows + y0, ROW_CHUNK), 0:LANE]
                zi = y_ref[pl.ds(cc * rows + y0, ROW_CHUNK), LANE:2 * LANE]
                tc = tw_ref[0, cc:cc + 1, :]
                ts = tw_ref[1, cc:cc + 1, :]
                parts.append((zr * tc - zi * ts, zr * ts + zi * tc))
            back = fft16(parts, 1)
            for a in range(FFT_BLOCKS):
                ur = back[a][0] * inv_len
                ui = back[a][1] * inv_len
                cs = cs_ref[pl.ds(y0, ROW_CHUNK), blk(a)]
                sn = sn_ref[pl.ds(y0, ROW_CHUNK), blk(a)]
                v_ref[0, pl.ds(y0, ROW_CHUNK), blk(a)] = ur * cs - ui * sn
                v_ref[1, pl.ds(y0, ROW_CHUNK), blk(a)] = ur * sn + ui * cs
            return c

        lax.fori_loop(0, chunks, inverse_chunk, 0, unroll=True)
        row_id = lax.broadcasted_iota(jnp.int32, (rows, LANE), 0)
        lane_id = lax.broadcasted_iota(jnp.int32, (rows, LANE), 1)
        cache = {}

        def cell(part, a):
            key = (part, a % FFT_BLOCKS)
            if key not in cache:
                v = v_ref[part, :, blk(a % FFT_BLOCKS)]
                cache[key] = (v, pltpu.roll(v, 1, 1), pltpu.roll(v, LANE - 1, 1))
            return cache[key]

        for a in range(FFT_BLOCKS):
            lap = []
            here = []
            for part in range(2):
                v, from_left, from_right = cell(part, a)
                prev_left = cell(part, a - 1)[1]
                next_right = cell(part, a + 1)[2]
                above = jnp.where(row_id == 0, 0.0, pltpu.roll(v, 1, 0))
                below = jnp.where(row_id == rows - 1, 0.0, pltpu.roll(v, rows - 1, 0))
                left = jnp.where(lane_id == 0, prev_left, from_left)
                right = jnp.where(lane_id == LANE - 1, next_right, from_right)
                lap.append(above + below + left + right - 4.0 * v)
                here.append(v)
            gain = gn_ref[:, blk(a)]
            new_re = here[0] + (lap[0] * DAMPING - lap[1] * gain)
            new_im = here[1] + (lap[0] * gain + lap[1] * DAMPING)
            wout_ref[0, :, blk(a)] = new_re
            wout_ref[1, :, blk(a)] = new_im
            for j in range(strip_count):
                slot = (j - pos_ref[0] + strip_count) % strip_count
                img_ref[slot, k, :, blk(a)] = new_re[j * rows_here:(j + 1) * rows_here]
        return carry

    lax.fori_loop(0, steps, one_step, 0)


def fast_constants(line_len):
    outer = line_len // LANE
    b = np.arange(LANE)
    ang = 2.0 * np.pi * (np.outer(b, b) % LANE) / LANE
    cos_m, sin_m = (np.cos(ang), np.sin(ang))
    fwd = np.block([[cos_m, -sin_m], [sin_m, cos_m]])
    inv = np.block([[cos_m, sin_m], [-sin_m, cos_m]])

    def halves(m):
        hi = m.astype(ml_dtypes.bfloat16)
        lo = (m - hi.astype(np.float64)).astype(ml_dtypes.bfloat16)
        return (hi, lo)

    c = np.arange(outer)
    tw_ang = 2.0 * np.pi * np.outer(c, b) / line_len
    twiddle = np.stack([np.cos(tw_ang), np.sin(tw_ang)]).astype(np.float32)
    q = c[:, None] + outer * b[None, :]
    signed = np.where(q >= line_len // 2, q - line_len, q).astype(np.float32)
    kx_cd = signed * np.float32(2.0 * math.pi / line_len)
    return (halves(fwd), halves(inv), twiddle, kx_cd.astype(np.float32))


def run_section(wave, regions, table, mult, consts, strip_count, strip_no):
    (fhi, flo), (ghi, glo), twiddle, _ = consts
    rows, line_len = wave.shape[1], wave.shape[2]
    steps = regions.shape[0]
    table_len = table.shape[0] // (3 * steps)
    vmem = pl.BlockSpec(memory_space=pltpu.VMEM)
    flops = steps * (2 * 3 * 2 * (FFT_BLOCKS * rows) * 256 * 256 + 400 * rows * line_len)
    return pl.pallas_call(
        lambda *refs: section_kernel(*refs, table_len=table_len),
        out_shape=(
            jax.ShapeDtypeStruct(wave.shape, jnp.float32),
            jax.ShapeDtypeStruct((strip_count, steps, rows // strip_count, line_len), jnp.float32),
        ),
        in_specs=[pl.BlockSpec(memory_space=pltpu.SMEM)] + [vmem] * 8
        + [pl.BlockSpec(memory_space=pltpu.SMEM)],
        out_specs=(vmem, vmem),
        scratch_shapes=[
            pltpu.VMEM((FFT_BLOCKS * rows, 2 * LANE), jnp.float32),
            pltpu.VMEM((FFT_BLOCKS * rows, 2 * LANE), jnp.float32),
            pltpu.VMEM((2, rows, line_len), jnp.float32),
            pltpu.VMEM((rows, line_len), jnp.float32),
            pltpu.VMEM((rows, line_len), jnp.float32),
            pltpu.VMEM((rows, line_len), jnp.float32),
            pltpu.VMEM((FFT_BLOCKS * rows, 2 * LANE), jnp.bfloat16),
            pltpu.VMEM((FFT_BLOCKS * rows, 2 * LANE), jnp.bfloat16),
        ],
        cost_estimate=pl.CostEstimate(
            flops=flops, transcendentals=0, bytes_accessed=4 * rows * line_len * 6 * steps
        ),
    )(table, wave, regions, mult, jnp.asarray(twiddle), jnp.asarray(fhi), jnp.asarray(flo),
      jnp.asarray(ghi), jnp.asarray(glo), jnp.reshape(strip_no, (1,)).astype(jnp.int32))


def section_tables(omega, region_speed, fd_coeff, ref_region, kx_cd):
    inv_speed = 1.0 / region_speed
    ref_slow = inv_speed[ref_region]
    regions = region_speed.shape[0]
    padded = 1 << max(1, (regions - 1).bit_length())
    extra = padded - regions
    phase = omega * (inv_speed[None, :] - ref_slow[:, None])
    gain = jnp.broadcast_to(fd_coeff / omega, phase.shape)
    parts = [jnp.cos(phase), jnp.sin(phase), gain]
    if extra:
        parts = [jnp.concatenate([p, jnp.repeat(p[:, -1:], extra, axis=1)], axis=1) for p in parts]
    table = jnp.stack(parts, axis=1).reshape(-1)
    wave_ref = omega * ref_slow
    wave_ref = wave_ref[:, None, None]
    excess = wave_ref * wave_ref - kx_cd * kx_cd
    decay_line = jnp.exp(-jnp.sqrt(jnp.maximum(-excess, 0.0)))
    vertical = jnp.sqrt(jnp.maximum(excess, 0.0))
    mult = jnp.stack([decay_line * jnp.cos(vertical), decay_line * jnp.sin(vertical)], axis=1)
    return (table, mult)


def fast_fits(surface, region_index, region_speed):
    freq_count = surface.shape[1]
    rows = surface.shape[2] * lax.axis_size("strip")
    line_len = surface.shape[3]
    return (
        freq_count == lax.axis_size("strip")
        and line_len == FFT_BLOCKS * LANE
        and rows % ROW_CHUNK == 0
        and surface.shape[2] % ROW_CHUNK == 0
        and rows <= 64
        and region_speed.shape[0] <= 16
    )


def strip_pairs(depths, strip_count, shift):
    return [
        (d * strip_count + r, d * strip_count + (r + shift) % strip_count)
        for d in depths
        for r in range(strip_count)
    ]


def gather_rows(local, depths, strip_no, strip_count, row_axis):
    rows = local.shape[row_axis]
    shape = list(local.shape)
    shape[row_axis] = rows * strip_count
    full = jnp.zeros(shape, local.dtype)
    start = [0] * len(shape)
    start[row_axis] = strip_no * rows
    full = lax.dynamic_update_slice(full, local, start)
    for shift in range(1, strip_count):
        got = lax.ppermute(local, ("depth", "strip"), strip_pairs(depths, strip_count, shift))
        start = [0] * len(shape)
        start[row_axis] = ((strip_no - shift) % strip_count) * rows
        full = lax.dynamic_update_slice(full, got, start)
    return full


def gather_strips(piece_of, local, depths, strip_no, strip_count, rows_here):
    rows = rows_here * strip_count
    shape = (local.shape[0], rows, local.shape[2])
    full = lax.dynamic_update_slice(
        jnp.zeros(shape, jnp.float32), local, (0, strip_no * rows_here, 0)
    )
    for shift in range(1, strip_count):
        target = (strip_no + shift) % strip_count
        got = lax.ppermute(
            piece_of(target), ("depth", "strip"), strip_pairs(depths, strip_count, shift)
        )
        source = (strip_no - shift) % strip_count
        full = lax.dynamic_update_slice(full, got, (0, source * rows_here, 0))
    return full


def shards(surface, omegas, region_speed, fd_coeff, region_index, ref_region):
    if not fast_fits(surface, region_index, region_speed):
        return shards_general(surface, omegas, region_speed, fd_coeff, region_index, ref_region)
    line_len = surface.shape[3]
    rows_here = surface.shape[2]
    steps = region_index.shape[0]
    segment_no = lax.axis_index("depth")
    segment_count = lax.axis_size("depth")
    strip_no = lax.axis_index("strip")
    strip_count = lax.axis_size("strip")
    consts = fast_constants(line_len)
    region_f = region_index.astype(jnp.float32)
    early = [d for d in range(segment_count) if d != 1]

    def with_surface(target):
        return jnp.concatenate(
            [region_f, lax.dynamic_index_in_dim(surface, target, 1, keepdims=False)], axis=0
        )

    gathered = gather_strips(
        with_surface, with_surface(strip_no), early, strip_no, strip_count, rows_here
    )
    regions_a = gathered[:steps].astype(jnp.int32)
    wave = gathered[steps:]
    omega = lax.dynamic_index_in_dim(omegas, strip_no, 0, keepdims=False)
    table, mult = section_tables(omega, region_speed, fd_coeff, ref_region, jnp.asarray(consts[3]))
    image = jnp.zeros((strip_count, steps, rows_here, line_len), jnp.float32)
    regions_b = regions_a

    def sweep(regions):
        def live(wave, image):
            return run_section(wave, regions, table, mult, consts, strip_count, strip_no)

        return live

    def idle(wave, image):
        return (wave, image)

    def freq_sum(image, depths):
        parts = []
        for shift in range(1, strip_count):
            piece = image[shift]
            parts.append(
                lax.ppermute(piece, ("depth", "strip"), strip_pairs(depths, strip_count, shift))
            )
        return parts

    arrived = []
    for tick_no in range(segment_count):
        regions = regions_b if tick_no == 1 else regions_a
        if tick_no == 0:
            wave, image = sweep(regions)(wave, image)
        else:
            wave, image = lax.cond(segment_no == tick_no, sweep(regions), idle, wave, image)
        if tick_no + 1 < segment_count:
            wave = lax.ppermute(wave, "depth", [(tick_no, tick_no + 1)])
        if tick_no == 0 and segment_count > 1:
            held, _ = lax.optimization_barrier((region_f, image))
            regions_b = gather_strips(
                lambda target: held, held, [1], strip_no, strip_count, rows_here
            ).astype(jnp.int32)
        if tick_no == segment_count - 2:
            wave, image = lax.optimization_barrier((wave, image))
            arrived += freq_sum(image, range(segment_count - 1))
    arrived += freq_sum(image, [segment_count - 1])
    total = image[0]
    for piece in arrived:
        total = total + piece
    return total


def solution(mesh):
    in_specs = (
        P(None, "shots", "strip", None),
        P(),
        P(),
        P(),
        P("depth", "strip", None),
        P("depth"),
    )
    out_specs = P("depth", "strip", "shots")
    return jax.shard_map(shards, mesh=mesh, in_specs=in_specs, out_specs=out_specs, check_vma=False)
```

```python
import math

import ml_dtypes
import numpy as np
import jax
import jax.numpy as jnp
from jax import lax
from jax.experimental import pallas as pl
from jax.experimental.pallas import tpu as pltpu
from jax.sharding import PartitionSpec as P

DAMPING = 0.05
PRECISE = lax.Precision.HIGHEST


def padded_2(cells, sides, width):
    for axis, dim in sides:
        count = lax.axis_size(axis)
        ends = count - 1
        head = lax.slice_in_dim(cells, 0, width, axis=dim)
        tail = lax.slice_in_dim(cells, cells.shape[dim] - width, cells.shape[dim], axis=dim)
        cells = jnp.concatenate(
            [
                lax.ppermute(tail, axis, [(i, (i + 1) % count) for i in range(ends)]),
                cells,
                lax.ppermute(head, axis, [((i + 1) % count, i) for i in range(ends)]),
            ],
            axis=dim,
        )
    return cells


def from_behind(value, axis, steps):
    count = lax.axis_size(axis)
    first, last = (max(0, -steps), min(count, count - steps))
    return lax.ppermute(value, axis, [(source, source + steps) for source in range(first, last)])


def complex_scale(values, cosine, sine_part):
    return jnp.stack(
        [values[0] * cosine - values[1] * sine_part, values[0] * sine_part + values[1] * cosine]
    )


def angle_pair(numerator, period):
    angle_grid = numerator.astype(jnp.float32) * (2.0 * math.pi / period)
    return (jnp.cos(angle_grid), jnp.sin(angle_grid))


def block_matrix(cosine, sine_part, forward):
    sign_flip = 1.0 if forward else -1.0
    return jnp.stack(
        [jnp.stack([cosine, -sign_flip * sine_part]), jnp.stack([sign_flip * sine_part, cosine])]
    )


def build_tables(line_len):
    block_len = 128
    outer_len = line_len // block_len
    inner_idx = jnp.arange(block_len)
    outer_idx = jnp.arange(outer_len)
    cos_large, sin_large = angle_pair(
        inner_idx[:, None] * inner_idx[None, :] % block_len, block_len
    )
    cos_small, sin_small = angle_pair(
        outer_idx[:, None] * outer_idx[None, :] % outer_len, outer_len
    )
    cos_twist, sin_twist = angle_pair(outer_idx[:, None] * inner_idx[None, :], line_len)
    wave_index = outer_idx[:, None] + outer_len * inner_idx[None, :]
    signed = jnp.where(wave_index >= line_len // 2, wave_index - line_len, wave_index)
    kx_grid = signed.astype(jnp.float32) * (2.0 * math.pi / line_len)
    small_fwd = block_matrix(cos_small, sin_small, True)
    small_inv = block_matrix(cos_small, sin_small, False)
    large_fwd = block_matrix(cos_large, sin_large, True)
    large_inv = block_matrix(cos_large, sin_large, False)
    return (small_fwd, small_inv, large_fwd, large_inv, cos_twist, sin_twist, kx_grid)


def forward_line(wavefield, tables):
    small_fwd, small_inv, large_fwd, large_inv, cos_twist, sin_twist, kx_grid = tables
    row_count = wavefield.shape[1]
    pieces = wavefield.reshape(2, row_count, cos_twist.shape[0], cos_twist.shape[1])
    mixed_part = jnp.einsum("zrab,zwca->wrcb", pieces, small_fwd, precision=PRECISE)
    mixed_part = complex_scale(mixed_part, cos_twist, -sin_twist)
    return jnp.einsum("zrcb,zwbd->wrcd", mixed_part, large_fwd, precision=PRECISE)


def inverse_line(spectrum, tables):
    small_fwd, small_inv, large_fwd, large_inv, cos_twist, sin_twist, kx_grid = tables
    row_count = spectrum.shape[1]
    line_len = cos_twist.shape[0] * cos_twist.shape[1]
    mixed_part = jnp.einsum("zrcd,zwdb->wrcb", spectrum, large_inv, precision=PRECISE)
    mixed_part = complex_scale(mixed_part, cos_twist, sin_twist)
    pieces = jnp.einsum("zrcb,zwca->wrab", mixed_part, small_inv, precision=PRECISE)
    return pieces.reshape(2, row_count, line_len) * (1.0 / line_len)


def lookup(regions, entries):
    picked = jnp.zeros(regions.shape, jnp.float32)
    for region_no in range(entries.shape[0]):
        picked = picked + jnp.where(regions == region_no, entries[region_no], 0.0)
    return picked


def depth_step(wavefield, omega_now, slow_cells, coef_cells, ref_slow, tables, pad_rows):
    kx_grid = tables[6]
    wave_ref = omega_now * ref_slow
    excess = wave_ref * wave_ref - kx_grid * kx_grid
    decay_line = jnp.exp(-jnp.sqrt(jnp.maximum(-excess, 0.0)))
    vertical = jnp.sqrt(jnp.maximum(excess, 0.0))
    spectrum = complex_scale(
        forward_line(wavefield, tables),
        decay_line * jnp.cos(vertical),
        decay_line * jnp.sin(vertical),
    )
    wavefield = inverse_line(spectrum, tables)
    phase_cell = omega_now * (slow_cells - ref_slow)
    wavefield = complex_scale(wavefield, jnp.cos(phase_cell), jnp.sin(phase_cell))
    padded = pad_rows(wavefield)
    laplace = (
        padded[:, :-2]
        + padded[:, 2:]
        + jnp.roll(wavefield, 1, 2)
        + jnp.roll(wavefield, -1, 2)
        - 4.0 * wavefield
    )
    return wavefield + complex_scale(laplace, DAMPING, coef_cells / omega_now)


def march(wavefield, omega_now, slow_block, coef_block, ref_block, tables, pad_rows):
    traces = []
    for step_no in range(slow_block.shape[0]):
        wavefield = depth_step(
            wavefield,
            omega_now,
            slow_block[step_no],
            coef_block[step_no],
            ref_block[step_no],
            tables,
            pad_rows,
        )
        traces.append(wavefield[0])
    return (wavefield, jnp.stack(traces))


def shards_general(surface, omegas, region_speed, fd_coeff, region_index, ref_region):
    line_len = surface.shape[3]
    rows_here = surface.shape[2]
    freq_count = surface.shape[1]
    step_count = region_index.shape[0]
    tables = build_tables(line_len)
    inv_speed = 1.0 / region_speed
    segment_no = lax.axis_index("depth")
    segment_count = lax.axis_size("depth")

    def pad_near(values):
        return padded_2(values, (("strip", 1),), 1)

    slow_cells = lookup(region_index, inv_speed)
    coef_cells = lookup(region_index, fd_coeff)
    ref_cells = lookup(ref_region, inv_speed)
    freq_index = jnp.arange(freq_count)
    image_out = jnp.zeros((step_count, rows_here, line_len), jnp.float32)
    arriving = jnp.zeros((2, rows_here, line_len), jnp.float32)
    tick_count = freq_count + segment_count - 1
    for tick_no in range(tick_count):
        batch_no = tick_no - segment_no
        is_live = (batch_no >= 0) & (batch_no < freq_count)
        clipped = jnp.clip(batch_no, 0, freq_count - 1)
        picked = lax.dynamic_index_in_dim(surface, clipped, 1, keepdims=False)
        entering = jnp.where(segment_no == 0, picked, arriving)
        omega_now = jnp.sum(jnp.where(freq_index == clipped, omegas, 0.0))
        leaving, traces = march(
            entering, omega_now, slow_cells, coef_cells, ref_cells, tables, pad_near
        )
        image_out = image_out + jnp.where(is_live, traces, 0.0)
        if tick_no + 1 < tick_count:
            arriving = from_behind(leaving, "depth", 1)
    return image_out


LANE = 128
FFT_BLOCKS = 16
ROW_CHUNK = 8
FFT_ROWS = 16


def fft4(x0, x1, x2, x3, sign):
    s0 = (x0[0] + x2[0], x0[1] + x2[1])
    d0 = (x0[0] - x2[0], x0[1] - x2[1])
    s1 = (x1[0] + x3[0], x1[1] + x3[1])
    d1 = (x1[0] - x3[0], x1[1] - x3[1])
    if sign < 0:
        wd = (d1[1], -d1[0])
    else:
        wd = (-d1[1], d1[0])
    return (
        (s0[0] + s1[0], s0[1] + s1[1]),
        (d0[0] + wd[0], d0[1] + wd[1]),
        (s0[0] - s1[0], s0[1] - s1[1]),
        (d0[0] - wd[0], d0[1] - wd[1]),
    )


def turn_const(value, power, sign):
    if power == 4:
        return (-value[1], value[0]) if sign > 0 else (value[1], -value[0])
    angle = sign * 2.0 * math.pi * power / 16.0
    cr, ci = (math.cos(angle), math.sin(angle))
    return (value[0] * cr - value[1] * ci, value[0] * ci + value[1] * cr)


def fft16(parts, sign):
    mid = [[None] * 4 for _ in range(4)]
    for a0 in range(4):
        ys = fft4(parts[a0], parts[4 + a0], parts[8 + a0], parts[12 + a0], sign)
        for c0 in range(4):
            power = a0 * c0
            mid[a0][c0] = ys[c0] if power == 0 else turn_const(ys[c0], power, sign)
    out = [None] * 16
    for c0 in range(4):
        zs = fft4(mid[0][c0], mid[1][c0], mid[2][c0], mid[3][c0], sign)
        for c1 in range(4):
            out[c0 + 4 * c1] = zs[c1]
    return out


def pick(regions, values):
    level = list(values)
    bit = 1
    while len(level) > 1:
        chosen = (regions & bit) != 0
        level = [jnp.where(chosen, level[i + 1], level[i]) for i in range(0, len(level), 2)]
        bit *= 2
    return jnp.broadcast_to(level[0], regions.shape)


def pick_bits(bits, values):
    level = list(values)
    for chosen in bits:
        level = [jnp.where(chosen, level[i + 1], level[i]) for i in range(0, len(level), 2)]
    return jnp.broadcast_to(level[0], bits[0].shape)


def split_dot(values, hi_ref, lo_ref):
    high = values.astype(jnp.bfloat16)
    low = (values - high.astype(jnp.float32)).astype(jnp.bfloat16)
    main = jnp.dot(high, hi_ref[...], preferred_element_type=jnp.float32)
    fix = jnp.dot(high, lo_ref[...], preferred_element_type=jnp.float32) + jnp.dot(
        low, hi_ref[:, :], preferred_element_type=jnp.float32
    )
    return main + fix


def section_kernel(
    tab_ref, w_ref, rid_ref, mult_ref, tw_ref, fhi_ref, flo_ref, ghi_ref, glo_ref, pos_ref,
    wout_ref, img_ref, a_ref, y_ref, v_ref, cs_ref, sn_ref, gn_ref, *, table_len
):
    rows = w_ref.shape[1]
    line_len = w_ref.shape[2]
    steps = rid_ref.shape[0]
    strip_count, rows_here = img_ref.shape[0], img_ref.shape[2]
    chunks = rows // FFT_ROWS
    inv_len = 1.0 / line_len
    wout_ref[...] = w_ref[...]

    def blk(a):
        return slice(a * LANE, (a + 1) * LANE)

    def one_step(k, carry):
        base = k * (3 * table_len)
        cos_t = [tab_ref[base + g] for g in range(table_len)]
        sin_t = [tab_ref[base + table_len + g] for g in range(table_len)]
        gain_t = [tab_ref[base + 2 * table_len + g] for g in range(table_len)]

        def forward_chunk(i, c):
            y0 = pl.multiple_of(i * FFT_ROWS, FFT_ROWS)
            parts = [
                (wout_ref[0, pl.ds(y0, FFT_ROWS), blk(a)], wout_ref[1, pl.ds(y0, FFT_ROWS), blk(a)])
                for a in range(FFT_BLOCKS)
            ]
            spec = fft16(parts, -1)
            for cc in range(FFT_BLOCKS):
                tc = tw_ref[0, cc:cc + 1, :]
                ts = tw_ref[1, cc:cc + 1, :]
                xr, xi = spec[cc]
                a_ref[pl.ds(cc * rows + y0, FFT_ROWS), 0:LANE] = xr * tc + xi * ts
                a_ref[pl.ds(cc * rows + y0, FFT_ROWS), LANE:2 * LANE] = xi * tc - xr * ts
            return c

        lax.fori_loop(0, chunks, forward_chunk, 0, unroll=True)
        spectrum = split_dot(a_ref[...], fhi_ref, flo_ref)
        for a in range(FFT_BLOCKS):
            regions = rid_ref[k, :, blk(a)]
            bits = [(regions & (1 << b)) != 0 for b in range(max(1, (table_len - 1).bit_length()))]
            cs_ref[:, blk(a)] = pick_bits(bits, cos_t)
            sn_ref[:, blk(a)] = pick_bits(bits, sin_t)
            gn_ref[:, blk(a)] = pick_bits(bits, gain_t)
        y_ref[...] = spectrum
        for cc in range(FFT_BLOCKS):
            band = slice(cc * rows, (cc + 1) * rows)
            yr = y_ref[band, 0:LANE]
            yi = y_ref[band, LANE:2 * LANE]
            mr = mult_ref[k, 0, cc:cc + 1, :]
            mi = mult_ref[k, 1, cc:cc + 1, :]
            a_ref[band, 0:LANE] = yr * mr - yi * mi
            a_ref[band, LANE:2 * LANE] = yr * mi + yi * mr
        y_ref[...] = split_dot(a_ref[...], ghi_ref, glo_ref)

        def inverse_chunk(i, c):
            y0 = pl.multiple_of(i * FFT_ROWS, FFT_ROWS)
            parts = []
            for cc in range(FFT_BLOCKS):
                zr = y_ref[pl.ds(cc * rows + y0, FFT_ROWS), 0:LANE]
                zi = y_ref[pl.ds(cc * rows + y0, FFT_ROWS), LANE:2 * LANE]
                tc = tw_ref[0, cc:cc + 1, :]
                ts = tw_ref[1, cc:cc + 1, :]
                parts.append((zr * tc - zi * ts, zr * ts + zi * tc))
            back = fft16(parts, 1)
            for a in range(FFT_BLOCKS):
                ur = back[a][0] * inv_len
                ui = back[a][1] * inv_len
                cs = cs_ref[pl.ds(y0, FFT_ROWS), blk(a)]
                sn = sn_ref[pl.ds(y0, FFT_ROWS), blk(a)]
                v_ref[0, pl.ds(y0, FFT_ROWS), blk(a)] = ur * cs - ui * sn
                v_ref[1, pl.ds(y0, FFT_ROWS), blk(a)] = ur * sn + ui * cs
            return c

        lax.fori_loop(0, chunks, inverse_chunk, 0, unroll=True)
        row_id = lax.broadcasted_iota(jnp.int32, (rows, LANE), 0)
        lane_id = lax.broadcasted_iota(jnp.int32, (rows, LANE), 1)
        cache = {}

        def cell(part, a):
            key = (part, a % FFT_BLOCKS)
            if key not in cache:
                v = v_ref[part, :, blk(a % FFT_BLOCKS)]
                cache[key] = (v, pltpu.roll(v, 1, 1), pltpu.roll(v, LANE - 1, 1))
            return cache[key]

        for a in range(FFT_BLOCKS):
            lap = []
            here = []
            for part in range(2):
                v, from_left, from_right = cell(part, a)
                prev_left = cell(part, a - 1)[1]
                next_right = cell(part, a + 1)[2]
                above = jnp.where(row_id == 0, 0.0, pltpu.roll(v, 1, 0))
                below = jnp.where(row_id == rows - 1, 0.0, pltpu.roll(v, rows - 1, 0))
                left = jnp.where(lane_id == 0, prev_left, from_left)
                right = jnp.where(lane_id == LANE - 1, next_right, from_right)
                lap.append(above + below + left + right - 4.0 * v)
                here.append(v)
            gain = gn_ref[:, blk(a)]
            new_re = here[0] + (lap[0] * DAMPING - lap[1] * gain)
            new_im = here[1] + (lap[0] * gain + lap[1] * DAMPING)
            wout_ref[0, :, blk(a)] = new_re
            wout_ref[1, :, blk(a)] = new_im
            for j in range(strip_count):
                slot = (j - pos_ref[0] + strip_count) % strip_count
                img_ref[slot, k, :, blk(a)] = new_re[j * rows_here:(j + 1) * rows_here]
        return carry

    lax.fori_loop(0, steps, one_step, 0)


def fast_constants(line_len):
    outer = line_len // LANE
    b = np.arange(LANE)
    ang = 2.0 * np.pi * (np.outer(b, b) % LANE) / LANE
    cos_m, sin_m = (np.cos(ang), np.sin(ang))
    fwd = np.block([[cos_m, -sin_m], [sin_m, cos_m]])
    inv = np.block([[cos_m, sin_m], [-sin_m, cos_m]])

    def halves(m):
        hi = m.astype(ml_dtypes.bfloat16)
        lo = (m - hi.astype(np.float64)).astype(ml_dtypes.bfloat16)
        return (hi, lo)

    c = np.arange(outer)
    tw_ang = 2.0 * np.pi * np.outer(c, b) / line_len
    twiddle = np.stack([np.cos(tw_ang), np.sin(tw_ang)]).astype(np.float32)
    q = c[:, None] + outer * b[None, :]
    signed = np.where(q >= line_len // 2, q - line_len, q).astype(np.float32)
    kx_cd = signed * np.float32(2.0 * math.pi / line_len)
    return (halves(fwd), halves(inv), twiddle, kx_cd.astype(np.float32))


def run_section(wave, regions, table, mult, consts, strip_count, strip_no):
    (fhi, flo), (ghi, glo), twiddle, _ = consts
    rows, line_len = wave.shape[1], wave.shape[2]
    steps = regions.shape[0]
    table_len = table.shape[0] // (3 * steps)
    vmem = pl.BlockSpec(memory_space=pltpu.VMEM)
    flops = steps * (2 * 3 * 2 * (FFT_BLOCKS * rows) * 256 * 256 + 400 * rows * line_len)
    return pl.pallas_call(
        lambda *refs: section_kernel(*refs, table_len=table_len),
        out_shape=(
            jax.ShapeDtypeStruct(wave.shape, jnp.float32),
            jax.ShapeDtypeStruct((strip_count, steps, rows // strip_count, line_len), jnp.float32),
        ),
        in_specs=[pl.BlockSpec(memory_space=pltpu.SMEM)] + [vmem] * 8
        + [pl.BlockSpec(memory_space=pltpu.SMEM)],
        out_specs=(vmem, vmem),
        scratch_shapes=[
            pltpu.VMEM((FFT_BLOCKS * rows, 2 * LANE), jnp.float32),
            pltpu.VMEM((FFT_BLOCKS * rows, 2 * LANE), jnp.float32),
            pltpu.VMEM((2, rows, line_len), jnp.float32),
            pltpu.VMEM((rows, line_len), jnp.float32),
            pltpu.VMEM((rows, line_len), jnp.float32),
            pltpu.VMEM((rows, line_len), jnp.float32),
        ],
        cost_estimate=pl.CostEstimate(
            flops=flops, transcendentals=0, bytes_accessed=4 * rows * line_len * 6 * steps
        ),
    )(table, wave, regions, mult, jnp.asarray(twiddle), jnp.asarray(fhi), jnp.asarray(flo),
      jnp.asarray(ghi), jnp.asarray(glo), jnp.reshape(strip_no, (1,)).astype(jnp.int32))


def section_tables(omega, region_speed, fd_coeff, ref_region, kx_cd):
    inv_speed = 1.0 / region_speed
    ref_slow = inv_speed[ref_region]
    regions = region_speed.shape[0]
    padded = 1 << max(1, (regions - 1).bit_length())
    extra = padded - regions
    phase = omega * (inv_speed[None, :] - ref_slow[:, None])
    gain = jnp.broadcast_to(fd_coeff / omega, phase.shape)
    parts = [jnp.cos(phase), jnp.sin(phase), gain]
    if extra:
        parts = [jnp.concatenate([p, jnp.repeat(p[:, -1:], extra, axis=1)], axis=1) for p in parts]
    table = jnp.stack(parts, axis=1).reshape(-1)
    wave_ref = omega * ref_slow
    wave_ref = wave_ref[:, None, None]
    excess = wave_ref * wave_ref - kx_cd * kx_cd
    decay_line = jnp.exp(-jnp.sqrt(jnp.maximum(-excess, 0.0)))
    vertical = jnp.sqrt(jnp.maximum(excess, 0.0))
    mult = jnp.stack([decay_line * jnp.cos(vertical), decay_line * jnp.sin(vertical)], axis=1)
    return (table, mult)


def fast_fits(surface, region_index, region_speed):
    freq_count = surface.shape[1]
    rows = surface.shape[2] * lax.axis_size("strip")
    line_len = surface.shape[3]
    return (
        freq_count == lax.axis_size("strip")
        and line_len == FFT_BLOCKS * LANE
        and rows % FFT_ROWS == 0
        and surface.shape[2] % ROW_CHUNK == 0
        and rows <= 64
        and region_speed.shape[0] <= 16
    )


def strip_pairs(depths, strip_count, shift):
    return [
        (d * strip_count + r, d * strip_count + (r + shift) % strip_count)
        for d in depths
        for r in range(strip_count)
    ]


def gather_rows(local, depths, strip_no, strip_count, row_axis):
    rows = local.shape[row_axis]
    shape = list(local.shape)
    shape[row_axis] = rows * strip_count
    full = jnp.zeros(shape, local.dtype)
    start = [0] * len(shape)
    start[row_axis] = strip_no * rows
    full = lax.dynamic_update_slice(full, local, start)
    for shift in range(1, strip_count):
        got = lax.ppermute(local, ("depth", "strip"), strip_pairs(depths, strip_count, shift))
        start = [0] * len(shape)
        start[row_axis] = ((strip_no - shift) % strip_count) * rows
        full = lax.dynamic_update_slice(full, got, start)
    return full


def gather_strips(piece_of, local, depths, strip_no, strip_count, rows_here):
    rows = rows_here * strip_count
    shape = (local.shape[0], rows, local.shape[2])
    full = lax.dynamic_update_slice(
        jnp.zeros(shape, jnp.float32), local, (0, strip_no * rows_here, 0)
    )
    for shift in range(1, strip_count):
        target = (strip_no + shift) % strip_count
        got = lax.ppermute(
            piece_of(target), ("depth", "strip"), strip_pairs(depths, strip_count, shift)
        )
        source = (strip_no - shift) % strip_count
        full = lax.dynamic_update_slice(full, got, (0, source * rows_here, 0))
    return full


def shards(surface, omegas, region_speed, fd_coeff, region_index, ref_region):
    if not fast_fits(surface, region_index, region_speed):
        return shards_general(surface, omegas, region_speed, fd_coeff, region_index, ref_region)
    line_len = surface.shape[3]
    rows_here = surface.shape[2]
    steps = region_index.shape[0]
    segment_no = lax.axis_index("depth")
    segment_count = lax.axis_size("depth")
    strip_no = lax.axis_index("strip")
    strip_count = lax.axis_size("strip")
    consts = fast_constants(line_len)
    region_f = region_index.astype(jnp.float32)
    early = [d for d in range(segment_count) if d != 1]

    def with_surface(target):
        return jnp.concatenate(
            [region_f, lax.dynamic_index_in_dim(surface, target, 1, keepdims=False)], axis=0
        )

    gathered = gather_strips(
        with_surface, with_surface(strip_no), early, strip_no, strip_count, rows_here
    )
    regions_a = gathered[:steps].astype(jnp.int32)
    wave = gathered[steps:]
    omega = lax.dynamic_index_in_dim(omegas, strip_no, 0, keepdims=False)
    table, mult = section_tables(omega, region_speed, fd_coeff, ref_region, jnp.asarray(consts[3]))
    image = jnp.zeros((strip_count, steps, rows_here, line_len), jnp.float32)
    regions_b = regions_a

    def sweep(regions):
        def live(wave, image):
            return run_section(wave, regions, table, mult, consts, strip_count, strip_no)

        return live

    def idle(wave, image):
        return (wave, image)

    def freq_sum(image, depths):
        parts = []
        for shift in range(1, strip_count):
            piece = image[shift]
            parts.append(
                lax.ppermute(piece, ("depth", "strip"), strip_pairs(depths, strip_count, shift))
            )
        return parts

    arrived = []
    for tick_no in range(segment_count):
        regions = regions_b if tick_no == 1 else regions_a
        if tick_no == 0:
            wave, image = sweep(regions)(wave, image)
        else:
            wave, image = lax.cond(segment_no == tick_no, sweep(regions), idle, wave, image)
        if tick_no + 1 < segment_count:
            wave = lax.ppermute(wave, "depth", [(tick_no, tick_no + 1)])
        if tick_no == 0 and segment_count > 1:
            held, _ = lax.optimization_barrier((region_f, image))
            regions_b = gather_strips(
                lambda target: held, held, [1], strip_no, strip_count, rows_here
            ).astype(jnp.int32)
        if tick_no == segment_count - 2:
            wave, image = lax.optimization_barrier((wave, image))
            arrived += freq_sum(image, range(segment_count - 1))
    arrived += freq_sum(image, [segment_count - 1])
    total = image[0]
    for piece in arrived:
        total = total + piece
    return total


def solution(mesh):
    in_specs = (
        P(None, "shots", "strip", None),
        P(),
        P(),
        P(),
        P("depth", "strip", None),
        P("depth"),
    )
    out_specs = P("depth", "strip", "shots")
    return jax.shard_map(shards, mesh=mesh, in_specs=in_specs, out_specs=out_specs, check_vma=False)
```
